32 devices in a mesh: rep: 2 (over y), fsdp: 16 (over z, x, core).
Axes of the slice: x: 2, y: 2, z: 4, core: 2. Of those that a mesh axis runs over, the one named last changes fastest.
Arguments:
- inputs: bfloat16 [16384, 768], P(('rep', 'fsdp')), may hold values from -6 to 6
- times: float32 [16384], P(('rep', 'fsdp')), may hold values from 0 to 1
- positions: float32 [3, 16384], P(None, ('rep', 'fsdp')), may hold values from -8 to 8
- atom_types: int32 [16384], P(('rep', 'fsdp')), may hold values from 0 to 63
- molecule_ids: int32 [16384], P(('rep', 'fsdp')), may hold values from 0 to 255, never falling along the last dimension, each value on 1 to 128 neighbouring positions
- pad_mask: int32 [16384], P(('rep', 'fsdp')), may hold values 0 or 1
- cotangent: bfloat16 [16384, 768], P(('rep', 'fsdp')), may hold values from -6 to 6
- norm_gains: bfloat16 [2, 768], P(None, 'fsdp'), may hold values from 0.5 to 1.5
- bias_rows: bfloat16 [6, 768], P(None, 'fsdp'), may hold values from -3 to 3
- up_bias: bfloat16 [3072], P('fsdp'), may hold values from -3 to 3
- input_weight: bfloat16 [768, 2304], P(None, 'fsdp'), may hold values from -0.21875 to 0.21875
- output_weight: bfloat16 [768, 768], P(None, 'fsdp'), may hold values from -0.875 to 0.875
- up_weight: bfloat16 [768, 3072], P(None, 'fsdp'), may hold values from -0.21875 to 0.21875
- down_weight: bfloat16 [3072, 768], P(None, 'fsdp'), may hold values from -0.109375 to 0.109375
- kernel_means: bfloat16 [128], P('fsdp'), may hold values from 0 to 6
- kernel_widths: bfloat16 [128], P('fsdp'), may hold values from 0.5 to 3
- pair_scale: bfloat16 [4096], P('fsdp'), may hold values from 0.5 to 1.5
- pair_shift: bfloat16 [4096], P('fsdp'), may hold values from -1 to 1
- kernel_heads: bfloat16 [128, 32], P('fsdp'), may hold values from -3 to 3
Outputs:
- rows: bfloat16 [16384, 768], P(('rep', 'fsdp'))
- inputs_grad: float32 [16384, 768], P(('rep', 'fsdp'))
- norm_gains_grad: float32 [2, 768], P(None, 'fsdp')
- bias_rows_grad: float32 [6, 768], P(None, 'fsdp')
- up_bias_grad: float32 [3072], P('fsdp')
- input_weight_grad: float32 [768, 2304], P(None, 'fsdp')
- output_weight_grad: float32 [768, 768], P(None, 'fsdp')
- up_weight_grad: float32 [768, 3072], P(None, 'fsdp')
- down_weight_grad: float32 [3072, 768], P(None, 'fsdp')
- kernel_means_grad: float32 [128], P('fsdp')
- kernel_widths_grad: float32 [128], P('fsdp')
- pair_scale_grad: float32 [4096], P('fsdp')
- pair_shift_grad: float32 [4096], P('fsdp')
- kernel_heads_grad: float32 [128, 32], P('fsdp')
The draws below stay inside these ranges and needn't reach their ends.
Inputs may be any that keep to these rules, and one draw needn't show every extreme that they name: `molecule_ids`: molecule ids are non-decreasing along the atoms; a molecule holds 1 to 128 atoms and one holds exactly 128.
All inputs are finite; a program needn't handle non-finite values. No bound on the sum of `pad_mask` on one device may be relied on, other than what follows from the above.
Results may differ from the reference program's by a relative error of at most 0.022.
Values may be sent and summed in bfloat16 or wider, within the bound.
No kernel may reach another device: no remote copies, remote signals or barrier semaphores. Data moves between devices by JAX's collectives and lax.ppermute only.
A program may use at most 128 MiB of HBM per device.

```python
import math
import jax
import jax.numpy as jnp
import numpy as np
from jax import lax

D = 768
HEADS = 32
HEAD_SIZE = 24
FF = 3072
KERNELS = 128
ATOM_TYPES = 64
MOL_MOST = 128
BLK = 128
ATOMS = 16384


def with_ends(values, stream_key, low, largest):
    dims = values.shape
    spot = [jax.random.randint(jax.random.fold_in(stream_key, axis), (), 0, dims[axis]) for axis in range(len(dims))]
    values = values.at[tuple(spot)].set(low)
    longest = dims.index(max(dims))
    spot[longest] = (spot[longest] + 1) % dims[longest]
    return values.at[tuple(spot)].set(largest)


def raised(result, stream_key, source, target, parts, factor):
    owner, partner = [(jnp.arange(result.shape[axis_at]) // (result.shape[axis_at] // parts)).reshape([-1 if axis == axis_at else 1 for axis in range(result.ndim)]) for axis_at in (source, target)]
    chosen = jax.random.permutation(stream_key, parts)[partner]
    strong = (owner == chosen) | (owner == (partner + parts // 2) % parts)
    return jnp.where(strong, factor * result, result)


def block_levels(own_key, shape, shards, least, top_value):
    factor_of = 1.0
    for dim, parts in shards:
        heights = jax.random.uniform(jax.random.fold_in(jax.random.fold_in(own_key, 6), dim), (parts,), jnp.float32, least / len(shards), top_value / len(shards))
        factor_of = factor_of * jnp.repeat(jnp.exp(heights), shape[dim] // parts).reshape((-1,) + (1,) * (len(shape) - 1 - dim))
    return factor_of


def length_profile(number_of, total, reach, slope):
    loads = [(1 << 20) // math.isqrt(rank ** slope) + 1 for rank in range(2, number_of + 1)]
    surplus, holding = total - reach - (number_of - 1), [1] * (number_of - 1)
    while surplus > 0:
        candidates = [i for i in range(number_of - 1) if holding[i] < reach]
        whole, remaining = sum([loads[i] for i in candidates]), surplus
        for i in candidates:
            more = min(reach - holding[i], max(1, remaining * loads[i] // whole), surplus)
            holding[i] = holding[i] + more
            surplus = surplus - more
    return np.array([reach] + holding)


def uneven_parts(key, number_of, total, limit, slope):
    if number_of == 2:
        one = jax.random.randint(key, (), max(1, total - limit), min(limit, total - 1) + 1)
        return jnp.stack([one, total - one])
    sizes = jnp.asarray(length_profile(number_of, total, limit, slope), jnp.int32)
    couples = (number_of - 1) // 2
    source_of, taker = sizes[1:1 + 2 * couples:2], sizes[2:2 + 2 * couples:2]
    margin = jnp.minimum(source_of - 1, limit - taker)
    shifted = jax.random.randint(jax.random.fold_in(key, 1), (couples,), 0, 1 << 20) % (margin + 1)
    sizes = sizes.at[1:1 + 2 * couples:2].set(source_of - shifted).at[2:2 + 2 * couples:2].set(taker + shifted)
    return sizes[jax.random.permutation(jax.random.fold_in(key, 2), number_of)]


def bell_draw(key, shape, width, reach, shards=(), held_as=jnp.bfloat16):
    values = jax.random.normal(key, shape, jnp.float32) * width
    if len(shards) > 0:
        values = block_levels(key, shape, shards, -0.22, 0.18) * values
    return jnp.clip(values, min=-reach, max=reach).astype(held_as)


def noise_with(stream_key, shape, scale, most, cuts, heavy, kind=jnp.bfloat16):
    drawn = scale * jax.random.normal(stream_key, shape, jnp.float32)
    if cuts:
        drawn = drawn * block_levels(stream_key, shape, cuts, -0.22, 0.18)
    return jnp.clip(raised(drawn, jax.random.fold_in(stream_key, 3), *heavy), -most, most).astype(kind)


def setup_inputs(seed: int = 0) -> dict:
    key_list = jax.random.split(jax.random.key(seed), 20)
    inputs = bell_draw(key_list[0], (ATOMS, D), 1.0, 6.0, ((0, 32),))
    times = jnp.clip(1.0 * jax.random.uniform(key_list[1], (ATOMS,), jnp.float32) ** block_levels(key_list[1], (ATOMS,), ((0, 32),), -0.2, 0.2), 0.0, 1.0)
    positions = bell_draw(key_list[2], (3, ATOMS), 1.5, 8.0, ((1, 32),), jnp.float32)
    atom_types = with_ends(jax.random.randint(key_list[3], (ATOMS,), 0, ATOM_TYPES), jax.random.fold_in(key_list[3], 1), 0, ATOM_TYPES - 1).astype(jnp.int32)
    molecule_ids = jnp.searchsorted(jnp.cumsum(uneven_parts(key_list[4], ATOMS // 64, ATOMS, MOL_MOST, 1)), jnp.arange(ATOMS), side="right").astype(jnp.int32)
    pad_mask = with_ends((jax.random.randint(key_list[5], (ATOMS,), 0, 8) < 7).astype(jnp.int32), jax.random.fold_in(key_list[5], 1), 0, 1)
    cotangent = noise_with(key_list[6], (ATOMS, D), 1.0, 6.0, ((0, 32),), (0, 1, 32, 2.75))
    norm_gains = jnp.clip(1.0 + 0.1 * jax.random.normal(key_list[7], (2, D), jnp.float32), 0.5, 1.5).astype(jnp.bfloat16)
    bias_rows = bell_draw(key_list[8], (6, D), 0.5, 3.0, ((1, 16),))
    up_bias = bell_draw(key_list[9], (FF,), 0.5, 3.0, ((0, 16),))
    input_weight = bell_draw(key_list[10], (D, 3 * D), D ** -0.5, 0.21875, ((1, 16),))
    output_weight = bell_draw(key_list[11], (D, D), (D // 16) ** -0.5, 0.875, ((1, 16),))
    up_weight = bell_draw(key_list[12], (D, FF), D ** -0.5, 0.21875, ((1, 16),))
    down_weight = bell_draw(key_list[13], (FF, D), FF ** -0.5, 0.109375, ((1, 16),))
    kernel_means = jnp.clip(6.0 * jax.random.uniform(key_list[14], (KERNELS,), jnp.float32) ** block_levels(key_list[14], (KERNELS,), ((0, 16),), -0.2, 0.2), 0.0, 6.0).astype(jnp.bfloat16)
    kernel_widths = jnp.clip(0.5 + 2.5 * jax.random.uniform(key_list[15], (KERNELS,), jnp.float32) ** block_levels(key_list[15], (KERNELS,), ((0, 16),), -0.2, 0.2), 0.5, 3.0).astype(jnp.bfloat16)
    pair_scale = jnp.clip(0.5 + 1.0 * jax.random.uniform(key_list[16], (ATOM_TYPES * ATOM_TYPES,), jnp.float32) ** block_levels(key_list[16], (ATOM_TYPES * ATOM_TYPES,), ((0, 16),), -0.2, 0.2), 0.5, 1.5).astype(jnp.bfloat16)
    pair_shift = jnp.clip(jax.random.uniform(key_list[17], (ATOM_TYPES * ATOM_TYPES,), jnp.float32, -1.0, 1.0) * block_levels(key_list[17], (ATOM_TYPES * ATOM_TYPES,), ((0, 16),), -0.4, 0.0), -1.0, 1.0).astype(jnp.bfloat16)
    kernel_heads = bell_draw(key_list[18], (KERNELS, HEADS), (KERNELS // 32) ** -0.5, 3.0, ((0, 16),))
    return {"inputs": inputs, "times": times, "positions": positions, "atom_types": atom_types, "molecule_ids": molecule_ids, "pad_mask": pad_mask, "cotangent": cotangent, "norm_gains": norm_gains, "bias_rows": bias_rows, "up_bias": up_bias, "input_weight": input_weight, "output_weight": output_weight, "up_weight": up_weight, "down_weight": down_weight, "kernel_means": kernel_means, "kernel_widths": kernel_widths, "pair_scale": pair_scale, "pair_shift": pair_shift, "kernel_heads": kernel_heads}


epsilon = 1e-05
masked_score = -1000000000.0
time_scale = 1000.0
root_two_pi = math.sqrt(2.0 * math.pi)
highest = lax.Precision.HIGHEST

@jax.custom_vjp
def low(v):
    return lax.optimization_barrier(v.astype(jnp.bfloat16)).astype(jnp.float32)

@jax.custom_vjp
def low_back(v):
    return v

def low_keep(v):
    return (low(v), None)

def low_pass(kept, grad):
    return (grad,)

def back_keep(v):
    return (v, None)

def back_low(kept, grad):
    return (low(grad),)
low.defvjp(low_keep, low_pass)
low_back.defvjp(back_keep, back_low)

def time_embedding(times, model_width):
    half_width = model_width // 2
    counter = jnp.arange(half_width, dtype=jnp.float32)
    frequency = jnp.exp(counter * (-math.log(10000.0) / half_width))
    angles = (time_scale * times)[:, None] * frequency[None, :]
    return jnp.concatenate([jnp.sin(angles), jnp.cos(angles)], axis=1)

def layer_norm(values, gain_row, shift_row):
    center = values - lax.optimization_barrier(jnp.mean(values, axis=1, keepdims=True))
    inv_std = lax.rsqrt(lax.optimization_barrier(jnp.mean(center * center, axis=1, keepdims=True)) + epsilon)
    return center * inv_std * gain_row + shift_row

def gelu_value(values):
    return values * (0.5 + 0.5 * lax.erf(values * math.sqrt(0.5)))

def attend_block(pieces, tables):
    queries, key_block, value_block, positions, types, mols, pads = pieces
    kernel_means, kernel_widths, pair_scale, pair_shift, kernel_heads = tables
    offsets = positions[:, :, None] - positions[:, None, :]
    distance = jnp.sqrt(lax.optimization_barrier(jnp.sum(offsets * offsets, axis=0)))
    pair_index = types[:, None] * ATOM_TYPES + types[None, :]
    stretched = jnp.take(pair_scale, pair_index) * distance + jnp.take(pair_shift, pair_index)
    kernel_gap = (stretched[:, :, None] - kernel_means) / kernel_widths
    kernels = low(jnp.exp(-0.5 * kernel_gap * kernel_gap) / (root_two_pi * kernel_widths))
    pair_bias = jnp.einsum('ijk,kh->hij', kernels, kernel_heads, precision=highest)
    raw_scores = jnp.einsum('ihd,jhd->hij', queries, key_block, precision=highest)
    atom_ids = jnp.arange(BLK, dtype=jnp.int32)
    same_mol = mols[:, None] == mols[None, :]
    key_live = (pads[None, :] == 1) | (atom_ids[:, None] == atom_ids[None, :])
    allowed = same_mol & key_live
    scores = low_back(jnp.where(allowed[None], raw_scores * (1.0 / math.sqrt(HEAD_SIZE)) + pair_bias, masked_score))
    row_max = lax.optimization_barrier(jnp.max(scores, axis=2, keepdims=True))
    exponent = jnp.exp(scores - row_max)
    attn_probs = exponent / lax.optimization_barrier(jnp.sum(exponent, axis=2, keepdims=True))
    attended = jnp.einsum('hij,jhd->ihd', low(attn_probs), value_block, precision=highest)
    return attended.reshape(BLK, D)

def group_layer(pieces, weights):
    x_rows, time_rows, pos_rows, type_rows, mol_rows, pad_rows = pieces
    norm_gains, bias_rows, up_bias, input_weight, output_weight, up_weight, down_weight, kernel_means, kernel_widths, pair_scale, pair_shift, kernel_heads = weights
    stream = x_rows + time_embedding(time_rows, D)
    act_one = low(layer_norm(stream, norm_gains[0], bias_rows[0]))
    qkv_shift = jnp.concatenate([bias_rows[2], jnp.zeros_like(bias_rows[2]), bias_rows[3]])
    projected = low(low_back(jnp.dot(act_one, input_weight, precision=highest) + qkv_shift))
    per_group = x_rows.shape[0] // BLK
    split_shape = (per_group, BLK, HEADS, HEAD_SIZE)
    queries = projected[:, :D].reshape(split_shape)
    key_rows = projected[:, D:2 * D].reshape(split_shape)
    value_rows = projected[:, 2 * D:].reshape(split_shape)
    pos_blocks = jnp.transpose(pos_rows.reshape(3, per_group, BLK), (1, 0, 2))
    tables = (kernel_means, kernel_widths, pair_scale, pair_shift, kernel_heads)

    def run_block(block_pieces):
        return attend_block(block_pieces, tables)
    attended = lax.map(jax.checkpoint(run_block), (queries, key_rows, value_rows, pos_blocks, type_rows.reshape(per_group, BLK), mol_rows.reshape(per_group, BLK), pad_rows.reshape(per_group, BLK)))
    attended_low = low(low_back(attended.reshape(-1, D)))
    mid = stream + low_back(jnp.dot(attended_low, output_weight, precision=highest) + bias_rows[4])
    act_two = low(layer_norm(mid, norm_gains[1], bias_rows[1]))
    hidden = low(gelu_value(low_back(jnp.dot(act_two, up_weight, precision=highest) + up_bias)))
    return mid + low_back(jnp.dot(hidden, down_weight, precision=highest) + bias_rows[5])

def reference(inputs, times, positions, atom_types, molecule_ids, pad_mask, cotangent, norm_gains, bias_rows, up_bias, input_weight, output_weight, up_weight, down_weight, kernel_means, kernel_widths, pair_scale, pair_shift, kernel_heads):
    weights = tuple((item.astype(jnp.float32) for item in (norm_gains, bias_rows, up_bias, input_weight, output_weight, up_weight, down_weight, kernel_means, kernel_widths, pair_scale, pair_shift, kernel_heads)))
    group_rows = 8 * BLK
    group_count = ATOMS // group_rows

    def to_groups(array):
        return array.reshape((group_count, group_rows) + array.shape[1:])
    pos_groups = jnp.transpose(positions.reshape(3, group_count, group_rows), (1, 0, 2))
    fixed_pieces = (to_groups(times), pos_groups, to_groups(atom_types), to_groups(molecule_ids), to_groups(pad_mask))

    def forward(x_groups, params):

        def step(running, pieces):
            return (running, jax.checkpoint(group_layer)(pieces, params))
        return lax.scan(step, None, (x_groups,) + fixed_pieces)[1]
    final, pullback = jax.vjp(forward, to_groups(inputs.astype(jnp.float32)), weights)
    inputs_grad, grads = pullback(to_groups(cotangent.astype(jnp.float32)))
    rows = final.reshape(ATOMS, D).astype(jnp.bfloat16)
    return (rows, inputs_grad.reshape(ATOMS, D), grads[0], grads[1], grads[2], grads[3], grads[4], grads[5], grads[6], grads[7], grads[8], grads[9], grads[10], grads[11])
```

```python
from functools import partial
import math

import jax
import jax.numpy as jnp
from jax import lax
from jax.sharding import Mesh, PartitionSpec as P
import numpy as np

ATOM_TYPES = 64


epsilon = 1e-05
masked_score = -1000000000.0
time_scale = 1000.0
root_two_pi = math.sqrt(2.0 * math.pi)
highest = lax.Precision.HIGHEST


def time_embedding(times, model_width):
    half_width = model_width // 2
    counter = jnp.arange(half_width, dtype=jnp.float32)
    frequency = jnp.exp(counter * (-math.log(10000.0) / half_width))
    angles = (time_scale * times)[:, None] * frequency[None, :]
    return jnp.concatenate([jnp.sin(angles), jnp.cos(angles)], axis=1)


def layer_norm(values, gain_row, shift_row):
    center = values - jnp.mean(values, axis=1, keepdims=True)
    inv_std = lax.rsqrt(jnp.mean(center * center, axis=1, keepdims=True) + epsilon)
    normed = center * inv_std
    return (normed * gain_row + shift_row, normed, inv_std)


def norm_backward(grad_out, normed, inv_std, gain_row):
    grad_normed = grad_out * gain_row
    first_mean = jnp.mean(grad_normed, axis=1, keepdims=True)
    second_mean = jnp.mean(grad_normed * normed, axis=1, keepdims=True)
    grad_input = inv_std * (grad_normed - first_mean - normed * second_mean)
    return (grad_input, jnp.sum(grad_out * normed, axis=0), jnp.sum(grad_out, axis=0))


def gelu_value(values):
    return values * (0.5 + 0.5 * lax.erf(values * math.sqrt(0.5)))


def gelu_slope(values):
    return (
        0.5
        + 0.5 * lax.erf(values * math.sqrt(0.5))
        + values * jnp.exp(-0.5 * values * values) / root_two_pi
    )


def pair_terms(pos_rows, pos_cols, type_rows, type_cols, tables):
    kernel_means, kernel_widths, scale_table, shift_table = tables
    offsets = pos_rows[:, :, None] - pos_cols[:, None, :]
    distance = jnp.sqrt(jnp.sum(offsets * offsets, axis=0))
    type_range = jnp.arange(ATOM_TYPES, dtype=jnp.int32)
    hot_rows = (type_rows[:, None] == type_range[None, :]).astype(jnp.float32)
    hot_cols = (type_cols[:, None] == type_range[None, :]).astype(jnp.float32)
    scale_pair = jnp.dot(
        jnp.dot(hot_rows, scale_table, precision=highest), hot_cols.T, precision=highest
    )
    shift_pair = jnp.dot(
        jnp.dot(hot_rows, shift_table, precision=highest), hot_cols.T, precision=highest
    )
    stretched = scale_pair * distance + shift_pair
    kernel_gap = (stretched[:, :, None] - kernel_means) / kernel_widths
    kernels = jnp.exp(-0.5 * kernel_gap * kernel_gap) / (root_two_pi * kernel_widths)
    return (distance, hot_rows, hot_cols, kernel_gap, kernels)


def allowed_pairs(row_ids, col_ids, mol_rows, mol_cols, pad_cols):
    same_mol = mol_rows[:, None] == mol_cols[None, :]
    key_live = (pad_cols[None, :] == 1) | (row_ids[:, None] == col_ids[None, :])
    return same_mol & key_live


def tile_scores(q_tile, key_block, kernels_low, kernel_heads, allowed, score_scale):
    pair_bias = jnp.einsum(
        "ijk,kh->hij", kernels_low, kernel_heads, preferred_element_type=jnp.float32
    )
    raw_scores = jnp.einsum("ihd,jhd->hij", q_tile, key_block, preferred_element_type=jnp.float32)
    return jnp.where(allowed[None], raw_scores * score_scale + pair_bias, masked_score)


def block_forward(pieces, tables, kernel_heads, tile_rows):
    queries, key_block, value_block, positions, types, mols, pads = pieces
    block_rows = queries.shape[0]
    score_scale = 1.0 / math.sqrt(queries.shape[2])
    col_ids = jnp.arange(block_rows, dtype=jnp.int32)

    def one_tile(running, tile_index):
        first_row = tile_index * tile_rows
        row_ids = first_row + jnp.arange(tile_rows, dtype=jnp.int32)
        terms = pair_terms(positions, positions, types, types, tables)
        kernels_low = terms[4].astype(jnp.bfloat16)
        allowed = allowed_pairs(row_ids, col_ids, mols, mols, pads)
        scores = tile_scores(queries, key_block, kernels_low, kernel_heads, allowed, score_scale)
        row_max = jnp.max(scores, axis=2, keepdims=True)
        exponent = jnp.exp(scores - row_max)
        row_sum = jnp.sum(exponent, axis=2, keepdims=True)
        probs_low = (exponent / row_sum).astype(jnp.bfloat16)
        attended = jnp.einsum(
            "hij,jhd->ihd", probs_low, value_block, preferred_element_type=jnp.float32
        )
        return (running, (attended, (row_max + jnp.log(row_sum))[:, :, 0]))

    count = block_rows // tile_rows
    if count == 1:
        _, (attended, log_sums) = one_tile(None, 0)
        return (attended.reshape(block_rows, -1), log_sums)
    _, (attended, log_sums) = lax.scan(one_tile, None, jnp.arange(count, dtype=jnp.int32))
    attended = attended.reshape(block_rows, -1)
    log_sums = jnp.transpose(log_sums, (1, 0, 2)).reshape(log_sums.shape[1], block_rows)
    return (attended, log_sums)


def block_backward(running, pieces, tables, kernel_heads, tile_rows):
    queries, key_block, value_block, grad_attended, log_sums, positions, types, mols, pads = pieces
    kernel_widths = tables[1]
    block_rows = queries.shape[0]
    score_scale = 1.0 / math.sqrt(queries.shape[2])
    col_ids = jnp.arange(block_rows, dtype=jnp.int32)

    def one_tile(partial_sums, tile_index):
        keys_grad, values_grad, heads_grad, means_grad, widths_grad, scale_grad, shift_grad = (
            partial_sums
        )
        first_row = tile_index * tile_rows
        row_ids = first_row + jnp.arange(tile_rows, dtype=jnp.int32)
        distance, hot_rows, hot_cols, kernel_gap, kernels = pair_terms(
            positions, positions, types, types, tables
        )
        kernels_low = kernels.astype(jnp.bfloat16)
        allowed = allowed_pairs(row_ids, col_ids, mols, mols, pads)
        scores = tile_scores(queries, key_block, kernels_low, kernel_heads, allowed, score_scale)
        attn_probs = jnp.exp(scores - log_sums[:, :, None])
        grad_probs = jnp.einsum(
            "ihd,jhd->hij", grad_attended, value_block, preferred_element_type=jnp.float32
        )
        values_grad = values_grad + jnp.einsum(
            "hij,ihd->jhd",
            attn_probs.astype(jnp.bfloat16),
            grad_attended,
            preferred_element_type=jnp.float32,
        )
        probs_dot = jnp.sum(attn_probs * grad_probs, axis=2, keepdims=True)
        grad_scores = (attn_probs * (grad_probs - probs_dot)).astype(jnp.bfloat16)
        query_grad = (
            jnp.einsum("hij,jhd->ihd", grad_scores, key_block, preferred_element_type=jnp.float32)
            * score_scale
        )
        keys_grad = (
            keys_grad
            + jnp.einsum("hij,ihd->jhd", grad_scores, queries, preferred_element_type=jnp.float32)
            * score_scale
        )
        heads_grad = heads_grad + jnp.einsum(
            "ijk,hij->kh", kernels_low, grad_scores, preferred_element_type=jnp.float32
        )
        grad_kernels = jnp.einsum(
            "hij,kh->ijk", grad_scores, kernel_heads, preferred_element_type=jnp.float32
        )
        spread = grad_kernels * kernels
        mean_part = spread * kernel_gap / kernel_widths
        means_grad = means_grad + jnp.sum(mean_part, axis=(0, 1))
        widths_grad = widths_grad + jnp.sum(
            spread * (kernel_gap * kernel_gap - 1.0) / kernel_widths, axis=(0, 1)
        )
        grad_stretched = -jnp.sum(mean_part, axis=2)
        scale_grad = scale_grad + jnp.dot(
            jnp.dot(hot_rows.T, grad_stretched * distance, precision=highest),
            hot_cols,
            precision=highest,
        )
        shift_grad = shift_grad + jnp.dot(
            jnp.dot(hot_rows.T, grad_stretched, precision=highest), hot_cols, precision=highest
        )
        return (
            (keys_grad, values_grad, heads_grad, means_grad, widths_grad, scale_grad, shift_grad),
            query_grad,
        )

    zero_block = jnp.zeros(key_block.shape, jnp.float32)
    count = block_rows // tile_rows
    if count == 1:
        sums_out, query_grads = one_tile((zero_block, zero_block) + tuple(running), 0)
        return (sums_out[2:], (query_grads.reshape(key_block.shape), sums_out[0], sums_out[1]))
    sums_out, query_grads = lax.scan(
        one_tile, (zero_block, zero_block) + tuple(running), jnp.arange(count, dtype=jnp.int32)
    )
    query_grads = query_grads.reshape(key_block.shape)
    return (sums_out[2:], (query_grads, sums_out[0], sums_out[1]))


def snake_ring(chips_x, chips_other):
    if chips_x == 2 and chips_other >= 2:
        return [2 * z for z in range(chips_other)] + [
            2 * z + 1 for z in reversed(range(chips_other))
        ]
    return list(range(chips_x * chips_other))


class Ring:
    def __init__(self, order):
        self.order = order
        self.n = len(order)
        pos = np.zeros(self.n, np.int32)
        for i, c in enumerate(order):
            pos[c] = i
        self.pos = pos
        self.cw = [(order[i], order[(i + 1) % self.n]) for i in range(self.n)]
        self.ccw = [(order[i], order[(i - 1) % self.n]) for i in range(self.n)]

    def here(self):
        chip = lax.axis_index("chip")
        core = lax.axis_index("core")
        return chip, core, jnp.asarray(self.pos)[chip]

    def chip_at(self, position):
        return jnp.asarray(np.array(self.order, np.int32))[position % self.n]


SWAP = [(0, 1), (1, 0)]


def _halves(x, axis):
    size = x.shape[axis] // 2
    return (
        lax.slice_in_dim(x, 0, size, axis=axis),
        lax.slice_in_dim(x, size, 2 * size, axis=axis),
    )


def ring_gather(ring, pieces, chips):
    if ring is None:
        return [
            lax.all_gather(x, ("chip", "core"), axis=0, tiled=False).reshape((chips, 2) + x.shape)
            for x, _ in pieces
        ]
    chip, core, p = ring.here()
    n = ring.n
    bufs, fronts = [], []
    for x, axis in pieces:
        buf = jnp.zeros((n, 2) + x.shape, x.dtype)
        buf = lax.dynamic_update_slice(buf, x[None, None], (chip, core) + (0,) * x.ndim)
        bufs.append(buf)
        if axis is None:
            fronts.append([x, None])
        else:
            fronts.append(list(_halves(x, axis)))
    partner = lax.ppermute([x for x, _ in pieces], "core", SWAP)
    for i, x in enumerate(partner):
        bufs[i] = lax.dynamic_update_slice(
            bufs[i], x[None, None], (chip, 1 - core) + (0,) * x.ndim
        )
    for step in range(1, n):
        going = [f[0] for f in fronts]
        coming = [f[1] for f in fronts if f[1] is not None]
        going = lax.ppermute(going, "chip", ring.cw)
        coming = lax.ppermute(coming, "chip", ring.ccw) if coming else []
        from_cw = ring.chip_at(p - step)
        from_ccw = ring.chip_at(p + step)
        both = lax.ppermute([going, coming], "core", SWAP)
        j = 0
        for i, (x, axis) in enumerate(pieces):
            fronts[i][0] = going[i]
            parts = [(going[i], both[0][i], from_cw, 0)]
            if axis is not None:
                fronts[i][1] = coming[j]
                parts.append((coming[j], both[1][j], from_ccw, x.shape[axis] // 2))
                j += 1
            for mine, theirs, source, offset in parts:
                start = [0] * x.ndim
                if axis is not None:
                    start[axis] = offset
                bufs[i] = lax.dynamic_update_slice(
                    bufs[i], mine[None, None], (source, core) + tuple(start)
                )
                bufs[i] = lax.dynamic_update_slice(
                    bufs[i], theirs[None, None], (source, 1 - core) + tuple(start)
                )
    return bufs


def ring_reduce(ring, pieces, send=jnp.bfloat16):
    if ring is None:
        owned = []
        for g, _ in pieces:
            flat = g.reshape((-1,) + g.shape[3:])
            part = lax.psum_scatter(flat, ("chip", "core"), scatter_dimension=0, tiled=True)
            owned.append(lax.psum(part.astype(send), "rep").astype(jnp.float32))
        return owned
    chip, core, p = ring.here()
    n = ring.n
    mine, theirs = [], []
    for g, _ in pieces:
        mine.append(lax.dynamic_index_in_dim(g, core, axis=1, keepdims=False))
        theirs.append(lax.dynamic_index_in_dim(g, 1 - core, axis=1, keepdims=False).astype(send))
    got = lax.ppermute(theirs, "core", SWAP)
    sums = [m + t.astype(jnp.float32) for m, t in zip(mine, got)]
    cw_parts, ccw_parts = [], []
    for (g, axis), total in zip(pieces, sums):
        if axis is None:
            cw_parts.append(total)
            ccw_parts.append(None)
        else:
            a, b = _halves(total, axis + 1)
            cw_parts.append(a)
            ccw_parts.append(b)

    def block(parts, position):
        return lax.dynamic_index_in_dim(parts, ring.chip_at(position), axis=0, keepdims=False)

    acc_cw = [block(t, p - 1) for t in cw_parts]
    acc_ccw = [block(t, p + 1) for t in ccw_parts if t is not None]
    for step in range(1, n):
        acc_cw = lax.ppermute([a.astype(send) for a in acc_cw], "chip", ring.cw)
        acc_cw = [a.astype(jnp.float32) + block(t, p - 1 - step) for a, t in zip(acc_cw, cw_parts)]
        if acc_ccw:
            acc_ccw = lax.ppermute([a.astype(send) for a in acc_ccw], "chip", ring.ccw)
            live = [t for t in ccw_parts if t is not None]
            acc_ccw = [a.astype(jnp.float32) + block(t, p + 1 + step) for a, t in zip(acc_ccw, live)]
    owned, j = [], 0
    for (g, axis), a in zip(pieces, acc_cw):
        if axis is None:
            owned.append(a)
        else:
            owned.append(jnp.concatenate([a, acc_ccw[j]], axis=axis))
            j += 1
    other = lax.ppermute([o.astype(send) for o in owned], "rep", SWAP)
    return [o + t.astype(jnp.float32) for o, t in zip(owned, other)]


SMALL_ROWS, SMALL_LANES = 16, 768


def small_layout(fsdp):
    d = 768 // fsdp
    sizes = [2 * d, 6 * d, 3072 // fsdp, 128 // fsdp, 128 // fsdp, 4096 // fsdp, 4096 // fsdp, (128 // fsdp) * 32]
    offsets, at = [], 0
    for size in sizes:
        offsets.append((at, size))
        at += size
    assert at <= SMALL_ROWS * SMALL_LANES
    return offsets


def pack_small(parts):
    flat = jnp.concatenate([part.reshape(-1) for part in parts])
    flat = jnp.pad(flat, (0, SMALL_ROWS * SMALL_LANES - flat.shape[0]))
    return flat.reshape(SMALL_ROWS, SMALL_LANES)


def unpack_small_full(gathered, offsets, fsdp):
    flat = gathered.reshape(fsdp, -1).astype(jnp.float32)
    take = [flat[:, at : at + size] for at, size in offsets]
    d = 768 // fsdp
    return [
        take[0].reshape(fsdp, 2, d).transpose(1, 0, 2).reshape(2, -1),
        take[1].reshape(fsdp, 6, d).transpose(1, 0, 2).reshape(6, -1),
        take[2].reshape(-1),
        take[3].reshape(-1),
        take[4].reshape(-1),
        take[5].reshape(ATOM_TYPES, ATOM_TYPES),
        take[6].reshape(ATOM_TYPES, ATOM_TYPES),
        take[7].reshape(-1, 32),
    ]


def pack_small_grads(grads, fsdp, chips):
    d = 768 // fsdp
    blocks = [
        grads[0].reshape(2, fsdp, d).transpose(1, 0, 2),
        grads[1].reshape(6, fsdp, d).transpose(1, 0, 2),
    ] + [g.reshape(-1) for g in grads[2:]]
    flat = jnp.concatenate([blk.reshape(fsdp, -1) for blk in blocks], axis=1)
    flat = jnp.pad(flat, ((0, 0), (0, SMALL_ROWS * SMALL_LANES - flat.shape[1])))
    return flat.reshape(chips, 2, SMALL_ROWS, SMALL_LANES)


def unpack_small_owned(block, offsets):
    flat = block.reshape(-1)
    take = [flat[at : at + size] for at, size in offsets]
    return [
        take[0].reshape(2, -1),
        take[1].reshape(6, -1),
        take[2],
        take[3],
        take[4],
        take[5],
        take[6],
        take[7].reshape(-1, 32),
    ]


def make_body(ring, chips):
    fsdp = 2 * chips

    def body(
        inputs,
        times,
        positions,
        atom_types,
        molecule_ids,
        pad_mask,
        cotangent,
        norm_gains,
        bias_rows,
        up_bias,
        input_weight,
        output_weight,
        up_weight,
        down_weight,
        kernel_means,
        kernel_widths,
        pair_scale,
        pair_shift,
        kernel_heads,
    ):
        offsets = small_layout(fsdp)
        small = pack_small(
            [norm_gains, bias_rows, up_bias, kernel_means, kernel_widths, pair_scale, pair_shift, kernel_heads]
        )
        width = input_weight.shape[0]
        first = jnp.concatenate([small.reshape(-1, width), input_weight.T], axis=0)
        second = jnp.concatenate(
            [output_weight.T, up_weight.T, down_weight.T.reshape(-1, width)], axis=0
        )
        first_all = lax.all_gather(first, ("chip", "core"), axis=0, tiled=False)
        second_all = lax.all_gather(second, ("chip", "core"), axis=0, tiled=False)
        small_rows = small.size // width
        params = unpack_small_full(first_all[:, :small_rows], offsets, fsdp)
        in_t = first_all[:, small_rows:].reshape(-1, width)
        out_rows = output_weight.shape[1]
        up_rows = up_weight.shape[1]
        out_t = second_all[:, :out_rows].reshape(-1, width)
        up_t = second_all[:, out_rows : out_rows + up_rows].reshape(-1, width)
        down_t = (
            second_all[:, out_rows + up_rows :]
            .reshape(fsdp, down_weight.shape[1], -1)
            .reshape(-1, down_weight.shape[0])
        )
        gains_now, biases_now, up_shift = params[0], params[1], params[2]
        tables = (params[3], params[4], params[5], params[6])
        heads_full = params[7].astype(jnp.bfloat16)

        row_count = inputs.shape[0]
        model_width = inputs.shape[1]
        head_count = heads_full.shape[1]
        head_size = model_width // head_count
        block_rows = min(128, row_count)
        blocks = row_count // block_rows
        tile_rows = min(128, block_rows)
        nt = (((1,), (1,)), ((), ()))
        tn = (((0,), (0,)), ((), ()))

        stream = inputs.astype(jnp.float32) + time_embedding(times, model_width)
        normed_out, normed_one, inv_one = layer_norm(stream, gains_now[0], biases_now[0])
        act_one = normed_out.astype(jnp.bfloat16)
        qkv_shift = jnp.concatenate([biases_now[2], jnp.zeros_like(biases_now[2]), biases_now[3]])
        projected = (
            lax.dot_general(act_one, in_t, nt, preferred_element_type=jnp.float32) + qkv_shift
        ).astype(jnp.bfloat16)
        split_shape = (blocks, block_rows, head_count, head_size)
        queries = projected[:, :model_width].reshape(split_shape)
        key_rows = projected[:, model_width : 2 * model_width].reshape(split_shape)
        value_rows = projected[:, 2 * model_width :].reshape(split_shape)
        pos_blocks = jnp.transpose(positions.reshape(3, blocks, block_rows), (1, 0, 2))
        type_blocks = atom_types.reshape(blocks, block_rows)
        mol_blocks = molecule_ids.reshape(blocks, block_rows)
        pad_blocks = pad_mask.reshape(blocks, block_rows)
        fwd = [
            block_forward(
                (queries[b], key_rows[b], value_rows[b], pos_blocks[b], type_blocks[b], mol_blocks[b], pad_blocks[b]),
                tables=tables,
                kernel_heads=heads_full,
                tile_rows=tile_rows,
            )
            for b in range(blocks)
        ]
        attended = jnp.stack([f[0] for f in fwd])
        log_sums = [f[1] for f in fwd]
        attended_low = attended.reshape(row_count, model_width).astype(jnp.bfloat16)
        mid = stream + (
            lax.dot_general(attended_low, out_t, nt, preferred_element_type=jnp.float32)
            + biases_now[4]
        )
        normed_out_two, normed_two, inv_two = layer_norm(mid, gains_now[1], biases_now[1])
        act_two = normed_out_two.astype(jnp.bfloat16)
        hidden_pre = (
            lax.dot_general(act_two, up_t, nt, preferred_element_type=jnp.float32) + up_shift
        )
        hidden_low = gelu_value(hidden_pre).astype(jnp.bfloat16)
        final = mid + (
            lax.dot_general(hidden_low, down_t, nt, preferred_element_type=jnp.float32)
            + biases_now[5]
        )
        rows_out = final.astype(jnp.bfloat16)

        grad_final = cotangent.astype(jnp.float32)
        down_grad_t = lax.dot_general(cotangent, hidden_low, tn, preferred_element_type=jnp.float32)
        grad_hidden = jnp.dot(cotangent, down_t, preferred_element_type=jnp.float32) * gelu_slope(
            hidden_pre
        )
        grad_hidden_low = grad_hidden.astype(jnp.bfloat16)
        up_grad_t = lax.dot_general(grad_hidden_low, act_two, tn, preferred_element_type=jnp.float32)
        up_bias_grad = jnp.sum(grad_hidden_low.astype(jnp.float32), axis=0)
        grad_act_two = jnp.dot(grad_hidden_low, up_t, preferred_element_type=jnp.float32)
        grad_norm_two, gain_two_grad, shift_two_grad = norm_backward(
            grad_act_two, normed_two, inv_two, gains_now[1]
        )
        grad_mid = grad_final + grad_norm_two
        grad_branch_low = grad_mid.astype(jnp.bfloat16)
        out_grad_t = lax.dot_general(
            grad_branch_low, attended_low, tn, preferred_element_type=jnp.float32
        )
        late_packed = jnp.concatenate(
            [
                out_grad_t.reshape(chips, 2, -1, model_width),
                up_grad_t.reshape(chips, 2, -1, model_width),
                down_grad_t.reshape(chips, 2, -1, model_width),
            ],
            axis=2,
        )
        (late_owned,) = ring_reduce(ring, [(late_packed, 1)])
        grad_attended = jnp.dot(grad_branch_low, out_t, preferred_element_type=jnp.float32).astype(
            jnp.bfloat16
        )
        kernel_count = tables[0].shape[0]
        start_sums = (
            jnp.zeros((kernel_count, head_count), jnp.float32),
            jnp.zeros((kernel_count,), jnp.float32),
            jnp.zeros((kernel_count,), jnp.float32),
            jnp.zeros((ATOM_TYPES, ATOM_TYPES), jnp.float32),
            jnp.zeros((ATOM_TYPES, ATOM_TYPES), jnp.float32),
        )
        kernel_sums = start_sums
        q_grads, k_grads, v_grads = [], [], []
        grad_attended_blocks = grad_attended.reshape(split_shape)
        for b in range(blocks):
            kernel_sums, (qg, kg, vg) = block_backward(
                kernel_sums,
                (
                    queries[b],
                    key_rows[b],
                    value_rows[b],
                    grad_attended_blocks[b],
                    log_sums[b],
                    pos_blocks[b],
                    type_blocks[b],
                    mol_blocks[b],
                    pad_blocks[b],
                ),
                tables=tables,
                kernel_heads=heads_full,
                tile_rows=tile_rows,
            )
            q_grads.append(qg)
            k_grads.append(kg)
            v_grads.append(vg)
        queries_grad = jnp.stack(q_grads)
        keys_grad = jnp.stack(k_grads)
        values_grad = jnp.stack(v_grads)
        grad_projected = jnp.concatenate(
            [
                queries_grad.reshape(row_count, model_width),
                keys_grad.reshape(row_count, model_width),
                values_grad.reshape(row_count, model_width),
            ],
            axis=1,
        ).astype(jnp.bfloat16)
        in_grad_t = lax.dot_general(grad_projected, act_one, tn, preferred_element_type=jnp.float32)
        grad_act_one = jnp.dot(grad_projected, in_t, preferred_element_type=jnp.float32)
        grad_norm_one, gain_one_grad, shift_one_grad = norm_backward(
            grad_act_one, normed_one, inv_one, gains_now[0]
        )
        inputs_grad = grad_mid + grad_norm_one
        projected_sums = jnp.sum(grad_projected.astype(jnp.float32), axis=0)
        heads_grad, means_grad, widths_grad, scale_grad, shift_grad = kernel_sums
        small_grads = [
            jnp.stack([gain_one_grad, gain_two_grad]),
            jnp.stack(
                [
                    shift_one_grad,
                    shift_two_grad,
                    projected_sums[:model_width],
                    projected_sums[2 * model_width :],
                    jnp.sum(grad_branch_low.astype(jnp.float32), axis=0),
                    jnp.sum(grad_final, axis=0),
                ]
            ),
            up_bias_grad,
            means_grad,
            widths_grad,
            scale_grad,
            shift_grad,
            heads_grad,
        ]
        in_owned, small_owned = ring_reduce(
            ring,
            [
                (in_grad_t.reshape((chips, 2, -1) + in_grad_t.shape[1:]), 1),
                (pack_small_grads(small_grads, fsdp, chips), None),
            ],
        )
        out_owned = late_owned[: out_rows]
        up_owned = late_owned[out_rows : out_rows + up_rows]
        down_owned = late_owned[out_rows + up_rows :].reshape(down_weight.shape[1], -1)
        sg = unpack_small_owned(small_owned, offsets)
        return (
            rows_out,
            inputs_grad,
            sg[0],
            sg[1],
            sg[2],
            in_owned.T,
            out_owned.T,
            up_owned.T,
            down_owned.T,
            sg[3],
            sg[4],
            sg[5],
            sg[6],
            sg[7],
        )

    return body


def solution(mesh):
    reps, fsdp = mesh.devices.shape
    chips = fsdp // 2
    grid = Mesh(mesh.devices.reshape(reps, chips, 2), ("rep", "chip", "core"))
    chips_x = 1
    try:
        coords = [tuple(d.coords) for d in mesh.devices[0, ::2]]
        xs = sorted({c[0] for c in coords})
        chips_x = len(xs)
        flat_ok = all(
            coords[i][0] == xs[i % chips_x] for i in range(chips)
        )
        if not flat_ok:
            chips_x = 1
    except Exception:
        chips_x = 1
    ring = None
    if chips <= 8:
        ring = Ring(snake_ring(chips_x, chips // chips_x))
    atoms = ("rep", "chip", "core")
    cols = ("chip", "core")
    placed = (
        P(atoms, None),
        P(atoms),
        P(None, atoms),
        P(atoms),
        P(atoms),
        P(atoms),
        P(atoms, None),
        P(None, cols),
        P(None, cols),
        P(cols),
        P(None, cols),
        P(None, cols),
        P(None, cols),
        P(None, cols),
        P(cols),
        P(cols),
        P(cols),
        P(cols),
        P(cols, None),
    )
    return jax.shard_map(
        make_body(ring, chips),
        mesh=grid,
        in_specs=placed,
        out_specs=(
            P(atoms, None),
            P(atoms, None),
            P(None, cols),
            P(None, cols),
            P(cols),
            P(None, cols),
            P(None, cols),
            P(None, cols),
            P(None, cols),
            P(cols),
            P(cols),
            P(cols),
            P(cols),
            P(cols, None),
        ),
        check_vma=False,
    )
```

```python
from functools import partial
import math

import jax
import jax.numpy as jnp
from jax import lax
from jax.sharding import Mesh, PartitionSpec as P
import numpy as np

ATOM_TYPES = 64


epsilon = 1e-05
masked_score = -1000000000.0
time_scale = 1000.0
root_two_pi = math.sqrt(2.0 * math.pi)
highest = lax.Precision.HIGHEST


def time_embedding(times, model_width):
    half_width = model_width // 2
    counter = jnp.arange(half_width, dtype=jnp.float32)
    frequency = jnp.exp(counter * (-math.log(10000.0) / half_width))
    angles = (time_scale * times)[:, None] * frequency[None, :]
    return jnp.concatenate([jnp.sin(angles), jnp.cos(angles)], axis=1)


def layer_norm(values, gain_row, shift_row):
    center = values - jnp.mean(values, axis=1, keepdims=True)
    inv_std = lax.rsqrt(jnp.mean(center * center, axis=1, keepdims=True) + epsilon)
    normed = center * inv_std
    return (normed * gain_row + shift_row, normed, inv_std)


def norm_backward(grad_out, normed, inv_std, gain_row):
    grad_normed = grad_out * gain_row
    first_mean = jnp.mean(grad_normed, axis=1, keepdims=True)
    second_mean = jnp.mean(grad_normed * normed, axis=1, keepdims=True)
    grad_input = inv_std * (grad_normed - first_mean - normed * second_mean)
    return (grad_input, jnp.sum(grad_out * normed, axis=0), jnp.sum(grad_out, axis=0))


def gelu_value(values):
    return values * (0.5 + 0.5 * lax.erf(values * math.sqrt(0.5)))


def gelu_slope(values):
    return (
        0.5
        + 0.5 * lax.erf(values * math.sqrt(0.5))
        + values * jnp.exp(-0.5 * values * values) / root_two_pi
    )


def pair_terms(pos_rows, pos_cols, type_rows, type_cols, tables):
    kernel_means, kernel_widths, scale_table, shift_table = tables
    offsets = pos_rows[:, :, None] - pos_cols[:, None, :]
    distance = jnp.sqrt(jnp.sum(offsets * offsets, axis=0))
    type_range = jnp.arange(ATOM_TYPES, dtype=jnp.int32)
    hot_rows = (type_rows[:, None] == type_range[None, :]).astype(jnp.float32)
    hot_cols = (type_cols[:, None] == type_range[None, :]).astype(jnp.float32)
    scale_pair = jnp.dot(
        jnp.dot(hot_rows, scale_table, precision=highest), hot_cols.T, precision=highest
    )
    shift_pair = jnp.dot(
        jnp.dot(hot_rows, shift_table, precision=highest), hot_cols.T, precision=highest
    )
    stretched = scale_pair * distance + shift_pair
    kernel_gap = (stretched[:, :, None] - kernel_means) / kernel_widths
    kernels = jnp.exp(-0.5 * kernel_gap * kernel_gap) / (root_two_pi * kernel_widths)
    return (distance, hot_rows, hot_cols, kernel_gap, kernels)


def allowed_pairs(row_ids, col_ids, mol_rows, mol_cols, pad_cols):
    same_mol = mol_rows[:, None] == mol_cols[None, :]
    key_live = (pad_cols[None, :] == 1) | (row_ids[:, None] == col_ids[None, :])
    return same_mol & key_live


def tile_scores(q_tile, key_block, kernels_low, kernel_heads, allowed, score_scale):
    pair_bias = jnp.einsum(
        "ijk,kh->hij", kernels_low, kernel_heads, preferred_element_type=jnp.float32
    )
    raw_scores = jnp.einsum("ihd,jhd->hij", q_tile, key_block, preferred_element_type=jnp.float32)
    return jnp.where(allowed[None], raw_scores * score_scale + pair_bias, masked_score)


def block_forward(pieces, tables, kernel_heads, tile_rows):
    queries, key_block, value_block, positions, types, mols, pads = pieces
    block_rows = queries.shape[0]
    score_scale = 1.0 / math.sqrt(queries.shape[2])
    col_ids = jnp.arange(block_rows, dtype=jnp.int32)

    def one_tile(running, tile_index):
        first_row = tile_index * tile_rows
        row_ids = first_row + jnp.arange(tile_rows, dtype=jnp.int32)
        terms = pair_terms(positions, positions, types, types, tables)
        kernels_low = terms[4].astype(jnp.bfloat16)
        allowed = allowed_pairs(row_ids, col_ids, mols, mols, pads)
        scores = tile_scores(queries, key_block, kernels_low, kernel_heads, allowed, score_scale)
        row_max = jnp.max(scores, axis=2, keepdims=True)
        exponent = jnp.exp(scores - row_max)
        row_sum = jnp.sum(exponent, axis=2, keepdims=True)
        probs_low = (exponent / row_sum).astype(jnp.bfloat16)
        attended = jnp.einsum(
            "hij,jhd->ihd", probs_low, value_block, preferred_element_type=jnp.float32
        )
        return (running, (attended, (row_max + jnp.log(row_sum))[:, :, 0]))

    count = block_rows // tile_rows
    if count == 1:
        _, (attended, log_sums) = one_tile(None, 0)
        return (attended.reshape(block_rows, -1), log_sums)
    _, (attended, log_sums) = lax.scan(one_tile, None, jnp.arange(count, dtype=jnp.int32))
    attended = attended.reshape(block_rows, -1)
    log_sums = jnp.transpose(log_sums, (1, 0, 2)).reshape(log_sums.shape[1], block_rows)
    return (attended, log_sums)


def block_backward(running, pieces, tables, kernel_heads, tile_rows):
    queries, key_block, value_block, grad_attended, log_sums, positions, types, mols, pads = pieces
    kernel_widths = tables[1]
    block_rows = queries.shape[0]
    score_scale = 1.0 / math.sqrt(queries.shape[2])
    col_ids = jnp.arange(block_rows, dtype=jnp.int32)

    def one_tile(partial_sums, tile_index):
        keys_grad, values_grad, heads_grad, means_grad, widths_grad, scale_grad, shift_grad = (
            partial_sums
        )
        first_row = tile_index * tile_rows
        row_ids = first_row + jnp.arange(tile_rows, dtype=jnp.int32)
        distance, hot_rows, hot_cols, kernel_gap, kernels = pair_terms(
            positions, positions, types, types, tables
        )
        kernels_low = kernels.astype(jnp.bfloat16)
        allowed = allowed_pairs(row_ids, col_ids, mols, mols, pads)
        scores = tile_scores(queries, key_block, kernels_low, kernel_heads, allowed, score_scale)
        attn_probs = jnp.exp(scores - log_sums[:, :, None])
        grad_probs = jnp.einsum(
            "ihd,jhd->hij", grad_attended, value_block, preferred_element_type=jnp.float32
        )
        values_grad = values_grad + jnp.einsum(
            "hij,ihd->jhd",
            attn_probs.astype(jnp.bfloat16),
            grad_attended,
            preferred_element_type=jnp.float32,
        )
        probs_dot = jnp.sum(attn_probs * grad_probs, axis=2, keepdims=True)
        grad_scores = (attn_probs * (grad_probs - probs_dot)).astype(jnp.bfloat16)
        query_grad = (
            jnp.einsum("hij,jhd->ihd", grad_scores, key_block, preferred_element_type=jnp.float32)
            * score_scale
        )
        keys_grad = (
            keys_grad
            + jnp.einsum("hij,ihd->jhd", grad_scores, queries, preferred_element_type=jnp.float32)
            * score_scale
        )
        heads_grad = heads_grad + jnp.einsum(
            "ijk,hij->kh", kernels_low, grad_scores, preferred_element_type=jnp.float32
        )
        grad_kernels = jnp.einsum(
            "hij,kh->ijk", grad_scores, kernel_heads, preferred_element_type=jnp.float32
        )
        spread = grad_kernels * kernels
        mean_part = spread * kernel_gap / kernel_widths
        means_grad = means_grad + jnp.sum(mean_part, axis=(0, 1))
        widths_grad = widths_grad + jnp.sum(
            spread * (kernel_gap * kernel_gap - 1.0) / kernel_widths, axis=(0, 1)
        )
        grad_stretched = -jnp.sum(mean_part, axis=2)
        scale_grad = scale_grad + jnp.dot(
            jnp.dot(hot_rows.T, grad_stretched * distance, precision=highest),
            hot_cols,
            precision=highest,
        )
        shift_grad = shift_grad + jnp.dot(
            jnp.dot(hot_rows.T, grad_stretched, precision=highest), hot_cols, precision=highest
        )
        return (
            (keys_grad, values_grad, heads_grad, means_grad, widths_grad, scale_grad, shift_grad),
            query_grad,
        )

    zero_block = jnp.zeros(key_block.shape, jnp.float32)
    count = block_rows // tile_rows
    if count == 1:
        sums_out, query_grads = one_tile((zero_block, zero_block) + tuple(running), 0)
        return (sums_out[2:], (query_grads.reshape(key_block.shape), sums_out[0], sums_out[1]))
    sums_out, query_grads = lax.scan(
        one_tile, (zero_block, zero_block) + tuple(running), jnp.arange(count, dtype=jnp.int32)
    )
    query_grads = query_grads.reshape(key_block.shape)
    return (sums_out[2:], (query_grads, sums_out[0], sums_out[1]))


def snake_ring(chips_x, chips_other):
    if chips_x == 2 and chips_other >= 2:
        return [2 * z for z in range(chips_other)] + [
            2 * z + 1 for z in reversed(range(chips_other))
        ]
    return list(range(chips_x * chips_other))


class Ring:
    def __init__(self, order):
        self.order = order
        self.n = len(order)
        pos = np.zeros(self.n, np.int32)
        for i, c in enumerate(order):
            pos[c] = i
        self.pos = pos
        self.cw = [(order[i], order[(i + 1) % self.n]) for i in range(self.n)]
        self.ccw = [(order[i], order[(i - 1) % self.n]) for i in range(self.n)]

    def here(self):
        chip = lax.axis_index("chip")
        core = lax.axis_index("core")
        return chip, core, jnp.asarray(self.pos)[chip]

    def chip_at(self, position):
        return jnp.asarray(np.array(self.order, np.int32))[position % self.n]


SWAP = [(0, 1), (1, 0)]


def _halves(x, axis):
    size = x.shape[axis] // 2
    return (
        lax.slice_in_dim(x, 0, size, axis=axis),
        lax.slice_in_dim(x, size, 2 * size, axis=axis),
    )


def ring_gather(ring, pieces, chips):
    if ring is None:
        return [
            lax.all_gather(x, ("chip", "core"), axis=0, tiled=False).reshape((chips, 2) + x.shape)
            for x, _ in pieces
        ]
    chip, core, p = ring.here()
    n = ring.n
    bufs, fronts = [], []
    for x, axis in pieces:
        buf = jnp.zeros((n, 2) + x.shape, x.dtype)
        buf = lax.dynamic_update_slice(buf, x[None, None], (chip, core) + (0,) * x.ndim)
        bufs.append(buf)
        if axis is None:
            fronts.append([x, None])
        else:
            fronts.append(list(_halves(x, axis)))
    partner = lax.ppermute([x for x, _ in pieces], "core", SWAP)
    for i, x in enumerate(partner):
        bufs[i] = lax.dynamic_update_slice(
            bufs[i], x[None, None], (chip, 1 - core) + (0,) * x.ndim
        )
    for step in range(1, n):
        going = [f[0] for f in fronts]
        coming = [f[1] for f in fronts if f[1] is not None]
        going = lax.ppermute(going, "chip", ring.cw)
        coming = lax.ppermute(coming, "chip", ring.ccw) if coming else []
        from_cw = ring.chip_at(p - step)
        from_ccw = ring.chip_at(p + step)
        both = lax.ppermute([going, coming], "core", SWAP)
        j = 0
        for i, (x, axis) in enumerate(pieces):
            fronts[i][0] = going[i]
            parts = [(going[i], both[0][i], from_cw, 0)]
            if axis is not None:
                fronts[i][1] = coming[j]
                parts.append((coming[j], both[1][j], from_ccw, x.shape[axis] // 2))
                j += 1
            for mine, theirs, source, offset in parts:
                start = [0] * x.ndim
                if axis is not None:
                    start[axis] = offset
                bufs[i] = lax.dynamic_update_slice(
                    bufs[i], mine[None, None], (source, core) + tuple(start)
                )
                bufs[i] = lax.dynamic_update_slice(
                    bufs[i], theirs[None, None], (source, 1 - core) + tuple(start)
                )
    return bufs


def ring_reduce_steps(ring, pieces, send=jnp.bfloat16):
    if ring is None:
        owned = []
        for g, _ in pieces:
            flat = g.reshape((-1,) + g.shape[3:])
            part = lax.psum_scatter(flat, ("chip", "core"), scatter_dimension=0, tiled=True)
            owned.append(lax.psum(part.astype(send), "rep").astype(jnp.float32))
        yield owned
        return owned
    chip, core, p = ring.here()
    n = ring.n
    mine, theirs = [], []
    for g, _ in pieces:
        mine.append(lax.dynamic_index_in_dim(g, core, axis=1, keepdims=False))
        theirs.append(lax.dynamic_index_in_dim(g, 1 - core, axis=1, keepdims=False).astype(send))
    got = lax.ppermute(theirs, "core", SWAP)
    yield got
    flows = []
    for i, (g, way) in enumerate(pieces):
        if isinstance(way, tuple):
            axis = way[1] + 1
            for d, (m, t) in zip((1, -1), zip(_halves(mine[i], axis), _halves(got[i], axis))):
                flows.append((i, d, m, t))
        else:
            flows.append((i, way, mine[i], got[i]))

    def contribution(m, t, position):
        at = ring.chip_at(position)
        own = lax.dynamic_index_in_dim(m, at, axis=0, keepdims=False)
        other = lax.dynamic_index_in_dim(t, at, axis=0, keepdims=False)
        return own + other.astype(jnp.float32)

    acc = [contribution(m, t, p - d) for _, d, m, t in flows]
    for step in range(1, n):
        moved = []
        for d in (1, -1):
            chosen = [k for k, f in enumerate(flows) if f[1] == d]
            if chosen:
                out = lax.ppermute([acc[k].astype(send) for k in chosen], "chip", ring.cw if d == 1 else ring.ccw)
                for k, o in zip(chosen, out):
                    acc[k] = o
                moved.extend(out)
        yield moved
        acc = [
            a.astype(jnp.float32) + contribution(m, t, p - d * (1 + step))
            for a, (_, d, m, t) in zip(acc, flows)
        ]
    owned = []
    for i, (g, way) in enumerate(pieces):
        parts = [a for a, f in zip(acc, flows) if f[0] == i]
        owned.append(parts[0] if len(parts) == 1 else jnp.concatenate(parts, axis=way[1]))
    other = lax.ppermute([o.astype(send) for o in owned], "rep", SWAP)
    yield other
    return [o + t.astype(jnp.float32) for o, t in zip(owned, other)]


def run_steps(gen):
    while True:
        try:
            next(gen)
        except StopIteration as done:
            return done.value


SMALL_ROWS, SMALL_LANES = 16, 768


def small_layout(fsdp):
    d = 768 // fsdp
    sizes = [2 * d, 6 * d, 3072 // fsdp, 128 // fsdp, 128 // fsdp, 4096 // fsdp, 4096 // fsdp, (128 // fsdp) * 32]
    offsets, at = [], 0
    for size in sizes:
        offsets.append((at, size))
        at += size
    assert at <= SMALL_ROWS * SMALL_LANES
    return offsets


def pack_small(parts):
    flat = jnp.concatenate([part.reshape(-1) for part in parts])
    flat = jnp.pad(flat, (0, SMALL_ROWS * SMALL_LANES - flat.shape[0]))
    return flat.reshape(SMALL_ROWS, SMALL_LANES)


def unpack_small_full(gathered, offsets, fsdp):
    flat = gathered.reshape(fsdp, -1).astype(jnp.float32)
    take = [flat[:, at : at + size] for at, size in offsets]
    d = 768 // fsdp
    return [
        take[0].reshape(fsdp, 2, d).transpose(1, 0, 2).reshape(2, -1),
        take[1].reshape(fsdp, 6, d).transpose(1, 0, 2).reshape(6, -1),
        take[2].reshape(-1),
        take[3].reshape(-1),
        take[4].reshape(-1),
        take[5].reshape(ATOM_TYPES, ATOM_TYPES),
        take[6].reshape(ATOM_TYPES, ATOM_TYPES),
        take[7].reshape(-1, 32),
    ]


def pack_small_grads(grads, fsdp, chips):
    d = 768 // fsdp
    blocks = [
        grads[0].reshape(2, fsdp, d).transpose(1, 0, 2),
        grads[1].reshape(6, fsdp, d).transpose(1, 0, 2),
    ] + [g.reshape(-1) for g in grads[2:]]
    flat = jnp.concatenate([blk.reshape(fsdp, -1) for blk in blocks], axis=1)
    flat = jnp.pad(flat, ((0, 0), (0, SMALL_ROWS * SMALL_LANES - flat.shape[1])))
    return flat.reshape(chips, 2, SMALL_ROWS, SMALL_LANES)


def unpack_small_owned(block, offsets):
    flat = block.reshape(-1)
    take = [flat[at : at + size] for at, size in offsets]
    return [
        take[0].reshape(2, -1),
        take[1].reshape(6, -1),
        take[2],
        take[3],
        take[4],
        take[5],
        take[6],
        take[7].reshape(-1, 32),
    ]


def make_body(ring, chips):
    fsdp = 2 * chips

    def body(
        inputs,
        times,
        positions,
        atom_types,
        molecule_ids,
        pad_mask,
        cotangent,
        norm_gains,
        bias_rows,
        up_bias,
        input_weight,
        output_weight,
        up_weight,
        down_weight,
        kernel_means,
        kernel_widths,
        pair_scale,
        pair_shift,
        kernel_heads,
    ):
        offsets = small_layout(fsdp)
        small = pack_small(
            [norm_gains, bias_rows, up_bias, kernel_means, kernel_widths, pair_scale, pair_shift, kernel_heads]
        )
        width = input_weight.shape[0]
        first = jnp.concatenate([small.reshape(-1, width), input_weight.T], axis=0)
        second = jnp.concatenate(
            [output_weight.T, up_weight.T, down_weight.T.reshape(-1, width)], axis=0
        )
        first_all = lax.all_gather(first, ("chip", "core"), axis=0, tiled=False)
        second_all = lax.all_gather(second, ("chip", "core"), axis=0, tiled=False)
        small_rows = small.size // width
        params = unpack_small_full(first_all[:, :small_rows], offsets, fsdp)
        in_t = first_all[:, small_rows:].reshape(-1, width)
        out_rows = output_weight.shape[1]
        up_rows = up_weight.shape[1]
        out_t = second_all[:, :out_rows].reshape(-1, width)
        up_t = second_all[:, out_rows : out_rows + up_rows].reshape(-1, width)
        down_t = (
            second_all[:, out_rows + up_rows :]
            .reshape(fsdp, down_weight.shape[1], -1)
            .reshape(-1, down_weight.shape[0])
        )
        gains_now, biases_now, up_shift = params[0], params[1], params[2]
        tables = (params[3], params[4], params[5], params[6])
        heads_full = params[7].astype(jnp.bfloat16)

        row_count = inputs.shape[0]
        model_width = inputs.shape[1]
        head_count = heads_full.shape[1]
        head_size = model_width // head_count
        block_rows = min(128, row_count)
        blocks = row_count // block_rows
        tile_rows = min(128, block_rows)
        nt = (((1,), (1,)), ((), ()))
        tn = (((0,), (0,)), ((), ()))

        stream = inputs.astype(jnp.float32) + time_embedding(times, model_width)
        normed_out, normed_one, inv_one = layer_norm(stream, gains_now[0], biases_now[0])
        act_one = normed_out.astype(jnp.bfloat16)
        qkv_shift = jnp.concatenate([biases_now[2], jnp.zeros_like(biases_now[2]), biases_now[3]])
        projected = (
            lax.dot_general(act_one, in_t, nt, preferred_element_type=jnp.float32) + qkv_shift
        ).astype(jnp.bfloat16)
        split_shape = (blocks, block_rows, head_count, head_size)
        queries = projected[:, :model_width].reshape(split_shape)
        key_rows = projected[:, model_width : 2 * model_width].reshape(split_shape)
        value_rows = projected[:, 2 * model_width :].reshape(split_shape)
        pos_blocks = jnp.transpose(positions.reshape(3, blocks, block_rows), (1, 0, 2))
        type_blocks = atom_types.reshape(blocks, block_rows)
        mol_blocks = molecule_ids.reshape(blocks, block_rows)
        pad_blocks = pad_mask.reshape(blocks, block_rows)
        fwd = [
            block_forward(
                (queries[b], key_rows[b], value_rows[b], pos_blocks[b], type_blocks[b], mol_blocks[b], pad_blocks[b]),
                tables=tables,
                kernel_heads=heads_full,
                tile_rows=tile_rows,
            )
            for b in range(blocks)
        ]
        attended = jnp.stack([f[0] for f in fwd])
        log_sums = [f[1] for f in fwd]
        attended_low = attended.reshape(row_count, model_width).astype(jnp.bfloat16)
        mid = stream + (
            lax.dot_general(attended_low, out_t, nt, preferred_element_type=jnp.float32)
            + biases_now[4]
        )
        normed_out_two, normed_two, inv_two = layer_norm(mid, gains_now[1], biases_now[1])
        act_two = normed_out_two.astype(jnp.bfloat16)
        hidden_pre = (
            lax.dot_general(act_two, up_t, nt, preferred_element_type=jnp.float32) + up_shift
        )
        hidden_low = gelu_value(hidden_pre).astype(jnp.bfloat16)
        final = mid + (
            lax.dot_general(hidden_low, down_t, nt, preferred_element_type=jnp.float32)
            + biases_now[5]
        )
        rows_out = final.astype(jnp.bfloat16)

        grad_final = cotangent.astype(jnp.float32)
        down_grad_t = lax.dot_general(cotangent, hidden_low, tn, preferred_element_type=jnp.float32)
        grad_hidden = jnp.dot(cotangent, down_t, preferred_element_type=jnp.float32) * gelu_slope(
            hidden_pre
        )
        grad_hidden_low = grad_hidden.astype(jnp.bfloat16)
        up_grad_t = lax.dot_general(grad_hidden_low, act_two, tn, preferred_element_type=jnp.float32)
        up_bias_grad = jnp.sum(grad_hidden_low.astype(jnp.float32), axis=0)
        grad_act_two = jnp.dot(grad_hidden_low, up_t, preferred_element_type=jnp.float32)
        grad_norm_two, gain_two_grad, shift_two_grad = norm_backward(
            grad_act_two, normed_two, inv_two, gains_now[1]
        )
        grad_mid = grad_final + grad_norm_two
        grad_branch_low = grad_mid.astype(jnp.bfloat16)
        out_grad_t = lax.dot_general(
            grad_branch_low, attended_low, tn, preferred_element_type=jnp.float32
        )
        late_rows = jnp.concatenate(
            [
                out_grad_t.reshape(chips, 2, -1, model_width),
                up_grad_t.reshape(chips, 2, -1, model_width),
            ],
            axis=2,
        )
        late = ring_reduce_steps(
            ring, [(late_rows, 1), (down_grad_t.reshape((chips, 2, -1) + down_grad_t.shape[1:]), -1)]
        )
        grad_attended = jnp.dot(grad_branch_low, out_t, preferred_element_type=jnp.float32).astype(
            jnp.bfloat16
        )
        kernel_count = tables[0].shape[0]
        start_sums = (
            jnp.zeros((kernel_count, head_count), jnp.float32),
            jnp.zeros((kernel_count,), jnp.float32),
            jnp.zeros((kernel_count,), jnp.float32),
            jnp.zeros((ATOM_TYPES, ATOM_TYPES), jnp.float32),
            jnp.zeros((ATOM_TYPES, ATOM_TYPES), jnp.float32),
        )
        kernel_sums = start_sums
        q_grads, k_grads, v_grads = [], [], []
        grad_attended_blocks = grad_attended.reshape(split_shape)
        late_owned = None
        per_block = -(-(ring.n + 1 if ring is not None else 1) // blocks)
        for b in range(blocks):
            ready = []
            for _ in range(per_block if late_owned is None else 0):
                try:
                    ready.extend(next(late))
                except StopIteration as done:
                    late_owned = done.value
                    break
            gate = grad_attended_blocks[b]
            if ready:
                _, gate = lax.optimization_barrier((ready, gate))
            kernel_sums, (qg, kg, vg) = block_backward(
                kernel_sums,
                (
                    queries[b],
                    key_rows[b],
                    value_rows[b],
                    gate,
                    log_sums[b],
                    pos_blocks[b],
                    type_blocks[b],
                    mol_blocks[b],
                    pad_blocks[b],
                ),
                tables=tables,
                kernel_heads=heads_full,
                tile_rows=tile_rows,
            )
            q_grads.append(qg)
            k_grads.append(kg)
            v_grads.append(vg)
        queries_grad = jnp.stack(q_grads)
        keys_grad = jnp.stack(k_grads)
        values_grad = jnp.stack(v_grads)
        grad_projected = jnp.concatenate(
            [
                queries_grad.reshape(row_count, model_width),
                keys_grad.reshape(row_count, model_width),
                values_grad.reshape(row_count, model_width),
            ],
            axis=1,
        ).astype(jnp.bfloat16)
        in_grad_t = lax.dot_general(grad_projected, act_one, tn, preferred_element_type=jnp.float32)
        grad_act_one = jnp.dot(grad_projected, in_t, preferred_element_type=jnp.float32)
        grad_norm_one, gain_one_grad, shift_one_grad = norm_backward(
            grad_act_one, normed_one, inv_one, gains_now[0]
        )
        inputs_grad = grad_mid + grad_norm_one
        projected_sums = jnp.sum(grad_projected.astype(jnp.float32), axis=0)
        heads_grad, means_grad, widths_grad, scale_grad, shift_grad = kernel_sums
        small_grads = [
            jnp.stack([gain_one_grad, gain_two_grad]),
            jnp.stack(
                [
                    shift_one_grad,
                    shift_two_grad,
                    projected_sums[:model_width],
                    projected_sums[2 * model_width :],
                    jnp.sum(grad_branch_low.astype(jnp.float32), axis=0),
                    jnp.sum(grad_final, axis=0),
                ]
            ),
            up_bias_grad,
            means_grad,
            widths_grad,
            scale_grad,
            shift_grad,
            heads_grad,
        ]
        if late_owned is None:
            late_owned = run_steps(late)
        out_owned = late_owned[0][:out_rows]
        up_owned = late_owned[0][out_rows:]
        down_owned = late_owned[1]
        in_owned, small_owned = run_steps(ring_reduce_steps(
            ring,
            [
                (in_grad_t.reshape((chips, 2, -1) + in_grad_t.shape[1:]), ("split", 1)),
                (pack_small_grads(small_grads, fsdp, chips), 1),
            ],
        ))
        sg = unpack_small_owned(small_owned, offsets)
        return (
            rows_out,
            inputs_grad,
            sg[0],
            sg[1],
            sg[2],
            in_owned.T,
            out_owned.T,
            up_owned.T,
            down_owned.T,
            sg[3],
            sg[4],
            sg[5],
            sg[6],
            sg[7],
        )

    return body


def solution(mesh):
    reps, fsdp = mesh.devices.shape
    chips = fsdp // 2
    grid = Mesh(mesh.devices.reshape(reps, chips, 2), ("rep", "chip", "core"))
    chips_x = 1
    try:
        coords = [tuple(d.coords) for d in mesh.devices[0, ::2]]
        xs = sorted({c[0] for c in coords})
        chips_x = len(xs)
        flat_ok = all(
            coords[i][0] == xs[i % chips_x] for i in range(chips)
        )
        if not flat_ok:
            chips_x = 1
    except Exception:
        chips_x = 1
    ring = None
    if chips <= 8:
        ring = Ring(snake_ring(chips_x, chips // chips_x))
    atoms = ("rep", "chip", "core")
    cols = ("chip", "core")
    placed = (
        P(atoms, None),
        P(atoms),
        P(None, atoms),
        P(atoms),
        P(atoms),
        P(atoms),
        P(atoms, None),
        P(None, cols),
        P(None, cols),
        P(cols),
        P(None, cols),
        P(None, cols),
        P(None, cols),
        P(None, cols),
        P(cols),
        P(cols),
        P(cols),
        P(cols),
        P(cols, None),
    )
    return jax.shard_map(
        make_body(ring, chips),
        mesh=grid,
        in_specs=placed,
        out_specs=(
            P(atoms, None),
            P(atoms, None),
            P(None, cols),
            P(None, cols),
            P(cols),
            P(None, cols),
            P(None, cols),
            P(None, cols),
            P(None, cols),
            P(cols),
            P(cols),
            P(cols),
            P(cols),
            P(cols, None),
        ),
        check_vma=False,
    )
```

```python
from functools import partial
import math

import jax
import jax.numpy as jnp
from jax import lax
from jax.sharding import Mesh, PartitionSpec as P
import numpy as np

ATOM_TYPES = 64


epsilon = 1e-05
masked_score = -1000000000.0
time_scale = 1000.0
root_two_pi = math.sqrt(2.0 * math.pi)
highest = lax.Precision.HIGHEST


def time_embedding(times, model_width):
    half_width = model_width // 2
    counter = jnp.arange(half_width, dtype=jnp.float32)
    frequency = jnp.exp(counter * (-math.log(10000.0) / half_width))
    angles = (time_scale * times)[:, None] * frequency[None, :]
    return jnp.concatenate([jnp.sin(angles), jnp.cos(angles)], axis=1)


def layer_norm(values, gain_row, shift_row):
    center = values - jnp.mean(values, axis=1, keepdims=True)
    inv_std = lax.rsqrt(jnp.mean(center * center, axis=1, keepdims=True) + epsilon)
    normed = center * inv_std
    return (normed * gain_row + shift_row, normed, inv_std)


def norm_backward(grad_out, normed, inv_std, gain_row):
    grad_normed = grad_out * gain_row
    first_mean = jnp.mean(grad_normed, axis=1, keepdims=True)
    second_mean = jnp.mean(grad_normed * normed, axis=1, keepdims=True)
    grad_input = inv_std * (grad_normed - first_mean - normed * second_mean)
    return (grad_input, jnp.sum(grad_out * normed, axis=0), jnp.sum(grad_out, axis=0))


def gelu_value(values):
    return values * (0.5 + 0.5 * lax.erf(values * math.sqrt(0.5)))


def gelu_slope(values):
    return (
        0.5
        + 0.5 * lax.erf(values * math.sqrt(0.5))
        + values * jnp.exp(-0.5 * values * values) / root_two_pi
    )


def pair_terms(pos_rows, pos_cols, type_rows, type_cols, tables):
    kernel_means, kernel_widths, scale_table, shift_table = tables
    offsets = pos_rows[:, :, None] - pos_cols[:, None, :]
    distance = jnp.sqrt(jnp.sum(offsets * offsets, axis=0))
    type_range = jnp.arange(ATOM_TYPES, dtype=jnp.int32)
    hot_rows = (type_rows[:, None] == type_range[None, :]).astype(jnp.float32)
    hot_cols = (type_cols[:, None] == type_range[None, :]).astype(jnp.float32)
    scale_pair = jnp.dot(
        jnp.dot(hot_rows, scale_table, precision=highest), hot_cols.T, precision=highest
    )
    shift_pair = jnp.dot(
        jnp.dot(hot_rows, shift_table, precision=highest), hot_cols.T, precision=highest
    )
    stretched = scale_pair * distance + shift_pair
    kernel_gap = (stretched[:, :, None] - kernel_means) / kernel_widths
    kernels = jnp.exp(-0.5 * kernel_gap * kernel_gap) / (root_two_pi * kernel_widths)
    return (distance, hot_rows, hot_cols, kernel_gap, kernels)


def allowed_pairs(row_ids, col_ids, mol_rows, mol_cols, pad_cols):
    same_mol = mol_rows[:, None] == mol_cols[None, :]
    key_live = (pad_cols[None, :] == 1) | (row_ids[:, None] == col_ids[None, :])
    return same_mol & key_live


def tile_scores(q_tile, key_block, kernels_low, kernel_heads, allowed, score_scale):
    pair_bias = jnp.einsum(
        "ijk,kh->hij", kernels_low, kernel_heads, preferred_element_type=jnp.float32
    )
    raw_scores = jnp.einsum("ihd,jhd->hij", q_tile, key_block, preferred_element_type=jnp.float32)
    return jnp.where(allowed[None], raw_scores * score_scale + pair_bias, masked_score)


def block_forward(pieces, tables, kernel_heads, tile_rows):
    queries, key_block, value_block, positions, types, mols, pads = pieces
    block_rows = queries.shape[0]
    score_scale = 1.0 / math.sqrt(queries.shape[2])
    col_ids = jnp.arange(block_rows, dtype=jnp.int32)

    def one_tile(running, tile_index):
        first_row = tile_index * tile_rows
        row_ids = first_row + jnp.arange(tile_rows, dtype=jnp.int32)
        terms = pair_terms(positions, positions, types, types, tables)
        kernels_low = terms[4].astype(jnp.bfloat16)
        allowed = allowed_pairs(row_ids, col_ids, mols, mols, pads)
        scores = tile_scores(queries, key_block, kernels_low, kernel_heads, allowed, score_scale)
        row_max = jnp.max(scores, axis=2, keepdims=True)
        exponent = jnp.exp(scores - row_max)
        row_sum = jnp.sum(exponent, axis=2, keepdims=True)
        probs_low = (exponent / row_sum).astype(jnp.bfloat16)
        attended = jnp.einsum(
            "hij,jhd->ihd", probs_low, value_block, preferred_element_type=jnp.float32
        )
        return (running, (attended, (row_max + jnp.log(row_sum))[:, :, 0]))

    count = block_rows // tile_rows
    if count == 1:
        _, (attended, log_sums) = one_tile(None, 0)
        return (attended.reshape(block_rows, -1), log_sums)
    _, (attended, log_sums) = lax.scan(one_tile, None, jnp.arange(count, dtype=jnp.int32))
    attended = attended.reshape(block_rows, -1)
    log_sums = jnp.transpose(log_sums, (1, 0, 2)).reshape(log_sums.shape[1], block_rows)
    return (attended, log_sums)


def block_backward(running, pieces, tables, kernel_heads, tile_rows):
    queries, key_block, value_block, grad_attended, log_sums, positions, types, mols, pads = pieces
    kernel_widths = tables[1]
    block_rows = queries.shape[0]
    score_scale = 1.0 / math.sqrt(queries.shape[2])
    col_ids = jnp.arange(block_rows, dtype=jnp.int32)

    def one_tile(partial_sums, tile_index):
        keys_grad, values_grad, heads_grad, means_grad, widths_grad, scale_grad, shift_grad = (
            partial_sums
        )
        first_row = tile_index * tile_rows
        row_ids = first_row + jnp.arange(tile_rows, dtype=jnp.int32)
        distance, hot_rows, hot_cols, kernel_gap, kernels = pair_terms(
            positions, positions, types, types, tables
        )
        kernels_low = kernels.astype(jnp.bfloat16)
        allowed = allowed_pairs(row_ids, col_ids, mols, mols, pads)
        scores = tile_scores(queries, key_block, kernels_low, kernel_heads, allowed, score_scale)
        attn_probs = jnp.exp(scores - log_sums[:, :, None])
        grad_probs = jnp.einsum(
            "ihd,jhd->hij", grad_attended, value_block, preferred_element_type=jnp.float32
        )
        values_grad = values_grad + jnp.einsum(
            "hij,ihd->jhd",
            attn_probs.astype(jnp.bfloat16),
            grad_attended,
            preferred_element_type=jnp.float32,
        )
        probs_dot = jnp.sum(attn_probs * grad_probs, axis=2, keepdims=True)
        grad_scores = (attn_probs * (grad_probs - probs_dot)).astype(jnp.bfloat16)
        query_grad = (
            jnp.einsum("hij,jhd->ihd", grad_scores, key_block, preferred_element_type=jnp.float32)
            * score_scale
        )
        keys_grad = (
            keys_grad
            + jnp.einsum("hij,ihd->jhd", grad_scores, queries, preferred_element_type=jnp.float32)
            * score_scale
        )
        heads_grad = heads_grad + jnp.einsum(
            "ijk,hij->kh", kernels_low, grad_scores, preferred_element_type=jnp.float32
        )
        grad_kernels = jnp.einsum(
            "hij,kh->ijk", grad_scores, kernel_heads, preferred_element_type=jnp.float32
        )
        spread = grad_kernels * kernels
        mean_part = spread * kernel_gap / kernel_widths
        means_grad = means_grad + jnp.sum(mean_part, axis=(0, 1))
        widths_grad = widths_grad + jnp.sum(
            spread * (kernel_gap * kernel_gap - 1.0) / kernel_widths, axis=(0, 1)
        )
        grad_stretched = -jnp.sum(mean_part, axis=2)
        scale_grad = scale_grad + jnp.dot(
            jnp.dot(hot_rows.T, grad_stretched * distance, precision=highest),
            hot_cols,
            precision=highest,
        )
        shift_grad = shift_grad + jnp.dot(
            jnp.dot(hot_rows.T, grad_stretched, precision=highest), hot_cols, precision=highest
        )
        return (
            (keys_grad, values_grad, heads_grad, means_grad, widths_grad, scale_grad, shift_grad),
            query_grad,
        )

    zero_block = jnp.zeros(key_block.shape, jnp.float32)
    count = block_rows // tile_rows
    if count == 1:
        sums_out, query_grads = one_tile((zero_block, zero_block) + tuple(running), 0)
        return (sums_out[2:], (query_grads.reshape(key_block.shape), sums_out[0], sums_out[1]))
    sums_out, query_grads = lax.scan(
        one_tile, (zero_block, zero_block) + tuple(running), jnp.arange(count, dtype=jnp.int32)
    )
    query_grads = query_grads.reshape(key_block.shape)
    return (sums_out[2:], (query_grads, sums_out[0], sums_out[1]))


def snake_ring(chips_x, chips_other):
    if chips_x == 2 and chips_other >= 2:
        return [2 * z for z in range(chips_other)] + [
            2 * z + 1 for z in reversed(range(chips_other))
        ]
    return list(range(chips_x * chips_other))


class Ring:
    def __init__(self, order):
        self.order = order
        self.n = len(order)
        pos = np.zeros(self.n, np.int32)
        for i, c in enumerate(order):
            pos[c] = i
        self.pos = pos
        self.cw = [(order[i], order[(i + 1) % self.n]) for i in range(self.n)]
        self.ccw = [(order[i], order[(i - 1) % self.n]) for i in range(self.n)]

    def here(self):
        chip = lax.axis_index("chip")
        core = lax.axis_index("core")
        return chip, core, jnp.asarray(self.pos)[chip]

    def chip_at(self, position):
        return jnp.asarray(np.array(self.order, np.int32))[position % self.n]


SWAP = [(0, 1), (1, 0)]


def _halves(x, axis):
    size = x.shape[axis] // 2
    return (
        lax.slice_in_dim(x, 0, size, axis=axis),
        lax.slice_in_dim(x, size, 2 * size, axis=axis),
    )


def ring_gather(ring, pieces, chips):
    if ring is None:
        return [
            lax.all_gather(x, ("chip", "core"), axis=0, tiled=False).reshape((chips, 2) + x.shape)
            for x, _ in pieces
        ]
    chip, core, p = ring.here()
    n = ring.n
    bufs, fronts = [], []
    for x, axis in pieces:
        buf = jnp.zeros((n, 2) + x.shape, x.dtype)
        buf = lax.dynamic_update_slice(buf, x[None, None], (chip, core) + (0,) * x.ndim)
        bufs.append(buf)
        if axis is None:
            fronts.append([x, None])
        else:
            fronts.append(list(_halves(x, axis)))
    partner = lax.ppermute([x for x, _ in pieces], "core", SWAP)
    for i, x in enumerate(partner):
        bufs[i] = lax.dynamic_update_slice(
            bufs[i], x[None, None], (chip, 1 - core) + (0,) * x.ndim
        )
    for step in range(1, n):
        going = [f[0] for f in fronts]
        coming = [f[1] for f in fronts if f[1] is not None]
        going = lax.ppermute(going, "chip", ring.cw)
        coming = lax.ppermute(coming, "chip", ring.ccw) if coming else []
        from_cw = ring.chip_at(p - step)
        from_ccw = ring.chip_at(p + step)
        both = lax.ppermute([going, coming], "core", SWAP)
        j = 0
        for i, (x, axis) in enumerate(pieces):
            fronts[i][0] = going[i]
            parts = [(going[i], both[0][i], from_cw, 0)]
            if axis is not None:
                fronts[i][1] = coming[j]
                parts.append((coming[j], both[1][j], from_ccw, x.shape[axis] // 2))
                j += 1
            for mine, theirs, source, offset in parts:
                start = [0] * x.ndim
                if axis is not None:
                    start[axis] = offset
                bufs[i] = lax.dynamic_update_slice(
                    bufs[i], mine[None, None], (source, core) + tuple(start)
                )
                bufs[i] = lax.dynamic_update_slice(
                    bufs[i], theirs[None, None], (source, 1 - core) + tuple(start)
                )
    return bufs


def ring_reduce_steps(ring, pieces, send=jnp.bfloat16):
    if ring is None:
        owned = []
        for g, _ in pieces:
            flat = g.reshape((-1,) + g.shape[3:])
            part = lax.psum_scatter(flat, ("chip", "core"), scatter_dimension=0, tiled=True)
            owned.append(lax.psum(part.astype(send), "rep").astype(jnp.float32))
        yield owned
        return owned
    chip, core, p = ring.here()
    n = ring.n
    mine, theirs = [], []
    for g, _ in pieces:
        mine.append(lax.dynamic_index_in_dim(g, core, axis=1, keepdims=False))
        theirs.append(lax.dynamic_index_in_dim(g, 1 - core, axis=1, keepdims=False).astype(send))
    got = lax.ppermute(theirs, "core", SWAP)
    yield got
    flows = []
    for i, (g, way) in enumerate(pieces):
        if isinstance(way, tuple):
            axis = way[1] + 1
            for d, (m, t) in zip((1, -1), zip(_halves(mine[i], axis), _halves(got[i], axis))):
                flows.append((i, d, m, t))
        else:
            flows.append((i, way, mine[i], got[i]))

    def contribution(m, t, position):
        at = ring.chip_at(position)
        own = lax.dynamic_index_in_dim(m, at, axis=0, keepdims=False)
        other = lax.dynamic_index_in_dim(t, at, axis=0, keepdims=False)
        return own + other.astype(jnp.float32)

    acc = [contribution(m, t, p - d) for _, d, m, t in flows]
    for step in range(1, n):
        moved = []
        for d in (1, -1):
            chosen = [k for k, f in enumerate(flows) if f[1] == d]
            if chosen:
                out = lax.ppermute([acc[k].astype(send) for k in chosen], "chip", ring.cw if d == 1 else ring.ccw)
                for k, o in zip(chosen, out):
                    acc[k] = o
                moved.extend(out)
        yield moved
        acc = [
            a.astype(jnp.float32) + contribution(m, t, p - d * (1 + step))
            for a, (_, d, m, t) in zip(acc, flows)
        ]
    owned = []
    for i, (g, way) in enumerate(pieces):
        parts = [a for a, f in zip(acc, flows) if f[0] == i]
        owned.append(parts[0] if len(parts) == 1 else jnp.concatenate(parts, axis=way[1]))
    other = lax.ppermute([o.astype(send) for o in owned], "rep", SWAP)
    yield other
    return [o + t.astype(jnp.float32) for o, t in zip(owned, other)]


def run_steps(gen):
    while True:
        try:
            next(gen)
        except StopIteration as done:
            return done.value


SMALL_ROWS, SMALL_LANES = 16, 768


def small_layout(fsdp):
    d = 768 // fsdp
    sizes = [2 * d, 6 * d, 3072 // fsdp, 128 // fsdp, 128 // fsdp, 4096 // fsdp, 4096 // fsdp, (128 // fsdp) * 32]
    offsets, at = [], 0
    for size in sizes:
        offsets.append((at, size))
        at += size
    assert at <= SMALL_ROWS * SMALL_LANES
    return offsets


def pack_small(parts):
    flat = jnp.concatenate([part.reshape(-1) for part in parts])
    flat = jnp.pad(flat, (0, SMALL_ROWS * SMALL_LANES - flat.shape[0]))
    return flat.reshape(SMALL_ROWS, SMALL_LANES)


def unpack_small_full(gathered, offsets, fsdp):
    flat = gathered.reshape(fsdp, -1).astype(jnp.float32)
    take = [flat[:, at : at + size] for at, size in offsets]
    d = 768 // fsdp
    return [
        take[0].reshape(fsdp, 2, d).transpose(1, 0, 2).reshape(2, -1),
        take[1].reshape(fsdp, 6, d).transpose(1, 0, 2).reshape(6, -1),
        take[2].reshape(-1),
        take[3].reshape(-1),
        take[4].reshape(-1),
        take[5].reshape(ATOM_TYPES, ATOM_TYPES),
        take[6].reshape(ATOM_TYPES, ATOM_TYPES),
        take[7].reshape(-1, 32),
    ]


def pack_small_grads(grads, fsdp, chips):
    d = 768 // fsdp
    blocks = [
        grads[0].reshape(2, fsdp, d).transpose(1, 0, 2),
        grads[1].reshape(6, fsdp, d).transpose(1, 0, 2),
    ] + [g.reshape(-1) for g in grads[2:]]
    flat = jnp.concatenate([blk.reshape(fsdp, -1) for blk in blocks], axis=1)
    flat = jnp.pad(flat, ((0, 0), (0, SMALL_ROWS * SMALL_LANES - flat.shape[1])))
    return flat.reshape(chips, 2, SMALL_ROWS, SMALL_LANES)


def unpack_small_owned(block, offsets):
    flat = block.reshape(-1)
    take = [flat[at : at + size] for at, size in offsets]
    return [
        take[0].reshape(2, -1),
        take[1].reshape(6, -1),
        take[2],
        take[3],
        take[4],
        take[5],
        take[6],
        take[7].reshape(-1, 32),
    ]


def make_body(ring, chips):
    fsdp = 2 * chips

    def body(
        inputs,
        times,
        positions,
        atom_types,
        molecule_ids,
        pad_mask,
        cotangent,
        norm_gains,
        bias_rows,
        up_bias,
        input_weight,
        output_weight,
        up_weight,
        down_weight,
        kernel_means,
        kernel_widths,
        pair_scale,
        pair_shift,
        kernel_heads,
    ):
        offsets = small_layout(fsdp)
        small = pack_small(
            [norm_gains, bias_rows, up_bias, kernel_means, kernel_widths, pair_scale, pair_shift, kernel_heads]
        )
        width = input_weight.shape[0]
        first = jnp.concatenate([small.reshape(-1, width), input_weight.T], axis=0)
        second = jnp.concatenate(
            [output_weight.T, up_weight.T, down_weight.T.reshape(-1, width)], axis=0
        )
        first_all = lax.all_gather(first, ("chip", "core"), axis=0, tiled=False)
        second_all = lax.all_gather(second, ("chip", "core"), axis=0, tiled=False)
        small_rows = small.size // width
        params = unpack_small_full(first_all[:, :small_rows], offsets, fsdp)
        in_t = first_all[:, small_rows:].reshape(-1, width)
        out_rows = output_weight.shape[1]
        up_rows = up_weight.shape[1]
        out_t = second_all[:, :out_rows].reshape(-1, width)
        up_t = second_all[:, out_rows : out_rows + up_rows].reshape(-1, width)
        down_t = (
            second_all[:, out_rows + up_rows :]
            .reshape(fsdp, down_weight.shape[1], -1)
            .reshape(-1, down_weight.shape[0])
        )
        gains_now, biases_now, up_shift = params[0], params[1], params[2]
        tables = (params[3], params[4], params[5], params[6])
        heads_full = params[7].astype(jnp.bfloat16)

        row_count = inputs.shape[0]
        model_width = inputs.shape[1]
        head_count = heads_full.shape[1]
        head_size = model_width // head_count
        block_rows = min(128, row_count)
        blocks = row_count // block_rows
        tile_rows = min(128, block_rows)
        nt = (((1,), (1,)), ((), ()))
        tn = (((0,), (0,)), ((), ()))

        stream = inputs.astype(jnp.float32) + time_embedding(times, model_width)
        normed_out, normed_one, inv_one = layer_norm(stream, gains_now[0], biases_now[0])
        act_one = normed_out.astype(jnp.bfloat16)
        qkv_shift = jnp.concatenate([biases_now[2], jnp.zeros_like(biases_now[2]), biases_now[3]])
        projected = (
            lax.dot_general(act_one, in_t, nt, preferred_element_type=jnp.float32) + qkv_shift
        ).astype(jnp.bfloat16)
        split_shape = (blocks, block_rows, head_count, head_size)
        queries = projected[:, :model_width].reshape(split_shape)
        key_rows = projected[:, model_width : 2 * model_width].reshape(split_shape)
        value_rows = projected[:, 2 * model_width :].reshape(split_shape)
        pos_blocks = jnp.transpose(positions.reshape(3, blocks, block_rows), (1, 0, 2))
        type_blocks = atom_types.reshape(blocks, block_rows)
        mol_blocks = molecule_ids.reshape(blocks, block_rows)
        pad_blocks = pad_mask.reshape(blocks, block_rows)
        fwd = [
            block_forward(
                (queries[b], key_rows[b], value_rows[b], pos_blocks[b], type_blocks[b], mol_blocks[b], pad_blocks[b]),
                tables=tables,
                kernel_heads=heads_full,
                tile_rows=tile_rows,
            )
            for b in range(blocks)
        ]
        attended = jnp.stack([f[0] for f in fwd])
        log_sums = [f[1] for f in fwd]
        attended_low = attended.reshape(row_count, model_width).astype(jnp.bfloat16)
        mid = stream + (
            lax.dot_general(attended_low, out_t, nt, preferred_element_type=jnp.float32)
            + biases_now[4]
        )
        normed_out_two, normed_two, inv_two = layer_norm(mid, gains_now[1], biases_now[1])
        act_two = normed_out_two.astype(jnp.bfloat16)
        hidden_pre = (
            lax.dot_general(act_two, up_t, nt, preferred_element_type=jnp.float32) + up_shift
        )
        hidden_low = gelu_value(hidden_pre).astype(jnp.bfloat16)
        final = mid + (
            lax.dot_general(hidden_low, down_t, nt, preferred_element_type=jnp.float32)
            + biases_now[5]
        )
        rows_out = final.astype(jnp.bfloat16)

        grad_final = cotangent.astype(jnp.float32)
        down_grad_t = lax.dot_general(cotangent, hidden_low, tn, preferred_element_type=jnp.float32)
        grad_hidden = jnp.dot(cotangent, down_t, preferred_element_type=jnp.float32) * gelu_slope(
            hidden_pre
        )
        grad_hidden_low = grad_hidden.astype(jnp.bfloat16)
        up_grad_t = lax.dot_general(grad_hidden_low, act_two, tn, preferred_element_type=jnp.float32)
        up_bias_grad = jnp.sum(grad_hidden_low.astype(jnp.float32), axis=0)
        grad_act_two = jnp.dot(grad_hidden_low, up_t, preferred_element_type=jnp.float32)
        grad_norm_two, gain_two_grad, shift_two_grad = norm_backward(
            grad_act_two, normed_two, inv_two, gains_now[1]
        )
        grad_mid = grad_final + grad_norm_two
        grad_branch_low = grad_mid.astype(jnp.bfloat16)
        out_grad_t = lax.dot_general(
            grad_branch_low, attended_low, tn, preferred_element_type=jnp.float32
        )
        late_rows = jnp.concatenate(
            [
                out_grad_t.reshape(chips, 2, -1, model_width),
                up_grad_t.reshape(chips, 2, -1, model_width),
            ],
            axis=2,
        )
        late = ring_reduce_steps(
            ring, [(late_rows, 1), (down_grad_t.reshape((chips, 2, -1) + down_grad_t.shape[1:]), -1)]
        )
        grad_attended = jnp.dot(grad_branch_low, out_t, preferred_element_type=jnp.float32).astype(
            jnp.bfloat16
        )
        kernel_count = tables[0].shape[0]
        start_sums = (
            jnp.zeros((kernel_count, head_count), jnp.float32),
            jnp.zeros((kernel_count,), jnp.float32),
            jnp.zeros((kernel_count,), jnp.float32),
            jnp.zeros((ATOM_TYPES, ATOM_TYPES), jnp.float32),
            jnp.zeros((ATOM_TYPES, ATOM_TYPES), jnp.float32),
        )
        kernel_sums = start_sums
        q_grads, k_grads, v_grads = [], [], []
        grad_attended_blocks = grad_attended.reshape(split_shape)
        late_owned = None
        per_block = -(-(ring.n + 1 if ring is not None else 1) // blocks)
        for b in range(blocks):
            ready = []
            for _ in range(per_block if late_owned is None else 0):
                try:
                    ready.extend(next(late))
                except StopIteration as done:
                    late_owned = done.value
                    break
            gate = grad_attended_blocks[b]
            if ready:
                _, gate = lax.optimization_barrier((ready, gate))
            kernel_sums, (qg, kg, vg) = block_backward(
                kernel_sums,
                (
                    queries[b],
                    key_rows[b],
                    value_rows[b],
                    gate,
                    log_sums[b],
                    pos_blocks[b],
                    type_blocks[b],
                    mol_blocks[b],
                    pad_blocks[b],
                ),
                tables=tables,
                kernel_heads=heads_full,
                tile_rows=tile_rows,
            )
            q_grads.append(qg)
            k_grads.append(kg)
            v_grads.append(vg)
        queries_grad = jnp.stack(q_grads)
        keys_grad = jnp.stack(k_grads)
        values_grad = jnp.stack(v_grads)
        grad_projected = jnp.concatenate(
            [
                queries_grad.reshape(row_count, model_width),
                keys_grad.reshape(row_count, model_width),
                values_grad.reshape(row_count, model_width),
            ],
            axis=1,
        ).astype(jnp.bfloat16)
        in_grad_t = lax.dot_general(grad_projected, act_one, tn, preferred_element_type=jnp.float32)
        grad_act_one = jnp.dot(grad_projected, in_t, preferred_element_type=jnp.float32)
        grad_norm_one, gain_one_grad, shift_one_grad = norm_backward(
            grad_act_one, normed_one, inv_one, gains_now[0]
        )
        inputs_grad = grad_mid + grad_norm_one
        projected_sums = jnp.sum(grad_projected.astype(jnp.float32), axis=0)
        heads_grad, means_grad, widths_grad, scale_grad, shift_grad = kernel_sums
        small_grads = [
            jnp.stack([gain_one_grad, gain_two_grad]),
            jnp.stack(
                [
                    shift_one_grad,
                    shift_two_grad,
                    projected_sums[:model_width],
                    projected_sums[2 * model_width :],
                    jnp.sum(grad_branch_low.astype(jnp.float32), axis=0),
                    jnp.sum(grad_final, axis=0),
                ]
            ),
            up_bias_grad,
            means_grad,
            widths_grad,
            scale_grad,
            shift_grad,
            heads_grad,
        ]
        if late_owned is None:
            late_owned = run_steps(late)
        out_owned = late_owned[0][:out_rows]
        up_owned = late_owned[0][out_rows:]
        down_owned = late_owned[1]
        last = jnp.concatenate(
            [
                in_grad_t.reshape((chips, 2, -1) + in_grad_t.shape[1:]),
                pack_small_grads(small_grads, fsdp, chips),
            ],
            axis=2,
        )
        (last_owned,) = run_steps(ring_reduce_steps(ring, [(last, ("split", 1))]))
        in_rows = in_grad_t.shape[0] // fsdp
        in_owned = last_owned[:in_rows]
        small_owned = last_owned[in_rows:]
        sg = unpack_small_owned(small_owned, offsets)
        return (
            rows_out,
            inputs_grad,
            sg[0],
            sg[1],
            sg[2],
            in_owned.T,
            out_owned.T,
            up_owned.T,
            down_owned.T,
            sg[3],
            sg[4],
            sg[5],
            sg[6],
            sg[7],
        )

    return body


def solution(mesh):
    reps, fsdp = mesh.devices.shape
    chips = fsdp // 2
    grid = Mesh(mesh.devices.reshape(reps, chips, 2), ("rep", "chip", "core"))
    chips_x = 1
    try:
        coords = [tuple(d.coords) for d in mesh.devices[0, ::2]]
        xs = sorted({c[0] for c in coords})
        chips_x = len(xs)
        flat_ok = all(
            coords[i][0] == xs[i % chips_x] for i in range(chips)
        )
        if not flat_ok:
            chips_x = 1
    except Exception:
        chips_x = 1
    ring = None
    if chips <= 8:
        ring = Ring(snake_ring(chips_x, chips // chips_x))
    atoms = ("rep", "chip", "core")
    cols = ("chip", "core")
    placed = (
        P(atoms, None),
        P(atoms),
        P(None, atoms),
        P(atoms),
        P(atoms),
        P(atoms),
        P(atoms, None),
        P(None, cols),
        P(None, cols),
        P(cols),
        P(None, cols),
        P(None, cols),
        P(None, cols),
        P(None, cols),
        P(cols),
        P(cols),
        P(cols),
        P(cols),
        P(cols, None),
    )
    return jax.shard_map(
        make_body(ring, chips),
        mesh=grid,
        in_specs=placed,
        out_specs=(
            P(atoms, None),
            P(atoms, None),
            P(None, cols),
            P(None, cols),
            P(cols),
            P(None, cols),
            P(None, cols),
            P(None, cols),
            P(None, cols),
            P(cols),
            P(cols),
            P(cols),
            P(cols),
            P(cols, None),
        ),
        check_vma=False,
    )
```

```python
from functools import partial
import math

import jax
import jax.numpy as jnp
from jax import lax
from jax.sharding import Mesh, PartitionSpec as P
import numpy as np

ATOM_TYPES = 64


epsilon = 1e-05
masked_score = -1000000000.0
time_scale = 1000.0
root_two_pi = math.sqrt(2.0 * math.pi)
highest = lax.Precision.HIGHEST


def time_embedding(times, model_width):
    half_width = model_width // 2
    counter = jnp.arange(half_width, dtype=jnp.float32)
    frequency = jnp.exp(counter * (-math.log(10000.0) / half_width))
    angles = (time_scale * times)[:, None] * frequency[None, :]
    return jnp.concatenate([jnp.sin(angles), jnp.cos(angles)], axis=1)


def layer_norm(values, gain_row, shift_row):
    center = values - jnp.mean(values, axis=1, keepdims=True)
    inv_std = lax.rsqrt(jnp.mean(center * center, axis=1, keepdims=True) + epsilon)
    normed = center * inv_std
    return (normed * gain_row + shift_row, normed, inv_std)


def norm_backward(grad_out, normed, inv_std, gain_row):
    grad_normed = grad_out * gain_row
    first_mean = jnp.mean(grad_normed, axis=1, keepdims=True)
    second_mean = jnp.mean(grad_normed * normed, axis=1, keepdims=True)
    grad_input = inv_std * (grad_normed - first_mean - normed * second_mean)
    return (grad_input, jnp.sum(grad_out * normed, axis=0), jnp.sum(grad_out, axis=0))


def gelu_value(values):
    return values * (0.5 + 0.5 * lax.erf(values * math.sqrt(0.5)))


def gelu_slope(values):
    return (
        0.5
        + 0.5 * lax.erf(values * math.sqrt(0.5))
        + values * jnp.exp(-0.5 * values * values) / root_two_pi
    )


def pair_terms(pos_rows, pos_cols, type_rows, type_cols, tables):
    kernel_means, kernel_widths, scale_table, shift_table = tables
    offsets = pos_rows[:, :, None] - pos_cols[:, None, :]
    distance = jnp.sqrt(jnp.sum(offsets * offsets, axis=0))
    type_range = jnp.arange(ATOM_TYPES, dtype=jnp.int32)
    hot_rows = (type_rows[:, None] == type_range[None, :]).astype(jnp.float32)
    hot_cols = (type_cols[:, None] == type_range[None, :]).astype(jnp.float32)
    scale_pair = jnp.dot(
        jnp.dot(hot_rows, scale_table, precision=highest), hot_cols.T, precision=highest
    )
    shift_pair = jnp.dot(
        jnp.dot(hot_rows, shift_table, precision=highest), hot_cols.T, precision=highest
    )
    stretched = scale_pair * distance + shift_pair
    kernel_gap = (stretched[:, :, None] - kernel_means) / kernel_widths
    kernels = jnp.exp(-0.5 * kernel_gap * kernel_gap) / (root_two_pi * kernel_widths)
    return (distance, hot_rows, hot_cols, kernel_gap, kernels)


def allowed_pairs(row_ids, col_ids, mol_rows, mol_cols, pad_cols):
    same_mol = mol_rows[:, None] == mol_cols[None, :]
    key_live = (pad_cols[None, :] == 1) | (row_ids[:, None] == col_ids[None, :])
    return same_mol & key_live


def tile_scores(q_tile, key_block, kernels_low, kernel_heads, allowed, score_scale):
    pair_bias = jnp.einsum(
        "ijk,kh->hij", kernels_low, kernel_heads, preferred_element_type=jnp.float32
    )
    raw_scores = jnp.einsum("ihd,jhd->hij", q_tile, key_block, preferred_element_type=jnp.float32)
    return jnp.where(allowed[None], raw_scores * score_scale + pair_bias, masked_score)


def block_forward(pieces, tables, kernel_heads, tile_rows):
    queries, key_block, value_block, positions, types, mols, pads = pieces
    block_rows = queries.shape[0]
    score_scale = 1.0 / math.sqrt(queries.shape[2])
    col_ids = jnp.arange(block_rows, dtype=jnp.int32)

    def one_tile(running, tile_index):
        first_row = tile_index * tile_rows
        row_ids = first_row + jnp.arange(tile_rows, dtype=jnp.int32)
        terms = pair_terms(positions, positions, types, types, tables)
        kernels_low = terms[4].astype(jnp.bfloat16)
        allowed = allowed_pairs(row_ids, col_ids, mols, mols, pads)
        scores = tile_scores(queries, key_block, kernels_low, kernel_heads, allowed, score_scale)
        row_max = jnp.max(scores, axis=2, keepdims=True)
        exponent = jnp.exp(scores - row_max)
        row_sum = jnp.sum(exponent, axis=2, keepdims=True)
        probs_low = (exponent / row_sum).astype(jnp.bfloat16)
        attended = jnp.einsum(
            "hij,jhd->ihd", probs_low, value_block, preferred_element_type=jnp.float32
        )
        return (running, (attended, (row_max + jnp.log(row_sum))[:, :, 0]))

    count = block_rows // tile_rows
    if count == 1:
        _, (attended, log_sums) = one_tile(None, 0)
        return (attended.reshape(block_rows, -1), log_sums)
    _, (attended, log_sums) = lax.scan(one_tile, None, jnp.arange(count, dtype=jnp.int32))
    attended = attended.reshape(block_rows, -1)
    log_sums = jnp.transpose(log_sums, (1, 0, 2)).reshape(log_sums.shape[1], block_rows)
    return (attended, log_sums)


def block_backward(running, pieces, tables, kernel_heads, tile_rows, hook=None):
    queries, key_block, value_block, grad_attended, log_sums, positions, types, mols, pads = pieces
    kernel_widths = tables[1]
    block_rows = queries.shape[0]
    score_scale = 1.0 / math.sqrt(queries.shape[2])
    col_ids = jnp.arange(block_rows, dtype=jnp.int32)

    def one_tile(partial_sums, tile_index):
        keys_grad, values_grad, heads_grad, means_grad, widths_grad, scale_grad, shift_grad = (
            partial_sums
        )
        first_row = tile_index * tile_rows
        row_ids = first_row + jnp.arange(tile_rows, dtype=jnp.int32)
        distance, hot_rows, hot_cols, kernel_gap, kernels = pair_terms(
            positions, positions, types, types, tables
        )
        kernels_low = kernels.astype(jnp.bfloat16)
        allowed = allowed_pairs(row_ids, col_ids, mols, mols, pads)
        scores = tile_scores(queries, key_block, kernels_low, kernel_heads, allowed, score_scale)
        attn_probs = jnp.exp(scores - log_sums[:, :, None])
        grad_probs = jnp.einsum(
            "ihd,jhd->hij", grad_attended, value_block, preferred_element_type=jnp.float32
        )
        values_grad = values_grad + jnp.einsum(
            "hij,ihd->jhd",
            attn_probs.astype(jnp.bfloat16),
            grad_attended,
            preferred_element_type=jnp.float32,
        )
        probs_dot = jnp.sum(attn_probs * grad_probs, axis=2, keepdims=True)
        grad_scores = (attn_probs * (grad_probs - probs_dot)).astype(jnp.bfloat16)
        if hook is not None:
            grad_scores = hook(grad_scores)
        query_grad = (
            jnp.einsum("hij,jhd->ihd", grad_scores, key_block, preferred_element_type=jnp.float32)
            * score_scale
        )
        keys_grad = (
            keys_grad
            + jnp.einsum("hij,ihd->jhd", grad_scores, queries, preferred_element_type=jnp.float32)
            * score_scale
        )
        heads_grad = heads_grad + jnp.einsum(
            "ijk,hij->kh", kernels_low, grad_scores, preferred_element_type=jnp.float32
        )
        grad_kernels = jnp.einsum(
            "hij,kh->ijk", grad_scores, kernel_heads, preferred_element_type=jnp.float32
        )
        spread = grad_kernels * kernels
        mean_part = spread * kernel_gap / kernel_widths
        means_grad = means_grad + jnp.sum(mean_part, axis=(0, 1))
        widths_grad = widths_grad + jnp.sum(
            spread * (kernel_gap * kernel_gap - 1.0) / kernel_widths, axis=(0, 1)
        )
        grad_stretched = -jnp.sum(mean_part, axis=2)
        scale_grad = scale_grad + jnp.dot(
            jnp.dot(hot_rows.T, grad_stretched * distance, precision=highest),
            hot_cols,
            precision=highest,
        )
        shift_grad = shift_grad + jnp.dot(
            jnp.dot(hot_rows.T, grad_stretched, precision=highest), hot_cols, precision=highest
        )
        return (
            (keys_grad, values_grad, heads_grad, means_grad, widths_grad, scale_grad, shift_grad),
            query_grad,
        )

    zero_block = jnp.zeros(key_block.shape, jnp.float32)
    count = block_rows // tile_rows
    if count == 1:
        sums_out, query_grads = one_tile((zero_block, zero_block) + tuple(running), 0)
        return (sums_out[2:], (query_grads.reshape(key_block.shape), sums_out[0], sums_out[1]))
    sums_out, query_grads = lax.scan(
        one_tile, (zero_block, zero_block) + tuple(running), jnp.arange(count, dtype=jnp.int32)
    )
    query_grads = query_grads.reshape(key_block.shape)
    return (sums_out[2:], (query_grads, sums_out[0], sums_out[1]))


def snake_ring(chips_x, chips_other):
    if chips_x == 2 and chips_other >= 2:
        return [2 * z for z in range(chips_other)] + [
            2 * z + 1 for z in reversed(range(chips_other))
        ]
    return list(range(chips_x * chips_other))


class Ring:
    def __init__(self, order):
        self.order = order
        self.n = len(order)
        pos = np.zeros(self.n, np.int32)
        for i, c in enumerate(order):
            pos[c] = i
        self.pos = pos
        self.cw = [(order[i], order[(i + 1) % self.n]) for i in range(self.n)]
        self.ccw = [(order[i], order[(i - 1) % self.n]) for i in range(self.n)]

    def here(self):
        chip = lax.axis_index("chip")
        core = lax.axis_index("core")
        return chip, core, jnp.asarray(self.pos)[chip]

    def chip_at(self, position):
        return jnp.asarray(np.array(self.order, np.int32))[position % self.n]


SWAP = [(0, 1), (1, 0)]


def _halves(x, axis):
    size = x.shape[axis] // 2
    return (
        lax.slice_in_dim(x, 0, size, axis=axis),
        lax.slice_in_dim(x, size, 2 * size, axis=axis),
    )


def ring_gather(ring, pieces, chips):
    if ring is None:
        return [
            lax.all_gather(x, ("chip", "core"), axis=0, tiled=False).reshape((chips, 2) + x.shape)
            for x, _ in pieces
        ]
    chip, core, p = ring.here()
    n = ring.n
    bufs, fronts = [], []
    for x, axis in pieces:
        buf = jnp.zeros((n, 2) + x.shape, x.dtype)
        buf = lax.dynamic_update_slice(buf, x[None, None], (chip, core) + (0,) * x.ndim)
        bufs.append(buf)
        if axis is None:
            fronts.append([x, None])
        else:
            fronts.append(list(_halves(x, axis)))
    partner = lax.ppermute([x for x, _ in pieces], "core", SWAP)
    for i, x in enumerate(partner):
        bufs[i] = lax.dynamic_update_slice(
            bufs[i], x[None, None], (chip, 1 - core) + (0,) * x.ndim
        )
    for step in range(1, n):
        going = [f[0] for f in fronts]
        coming = [f[1] for f in fronts if f[1] is not None]
        going = lax.ppermute(going, "chip", ring.cw)
        coming = lax.ppermute(coming, "chip", ring.ccw) if coming else []
        from_cw = ring.chip_at(p - step)
        from_ccw = ring.chip_at(p + step)
        both = lax.ppermute([going, coming], "core", SWAP)
        j = 0
        for i, (x, axis) in enumerate(pieces):
            fronts[i][0] = going[i]
            parts = [(going[i], both[0][i], from_cw, 0)]
            if axis is not None:
                fronts[i][1] = coming[j]
                parts.append((coming[j], both[1][j], from_ccw, x.shape[axis] // 2))
                j += 1
            for mine, theirs, source, offset in parts:
                start = [0] * x.ndim
                if axis is not None:
                    start[axis] = offset
                bufs[i] = lax.dynamic_update_slice(
                    bufs[i], mine[None, None], (source, core) + tuple(start)
                )
                bufs[i] = lax.dynamic_update_slice(
                    bufs[i], theirs[None, None], (source, 1 - core) + tuple(start)
                )
    return bufs


def ring_reduce_steps(ring, pieces, send=jnp.bfloat16):
    if ring is None:
        owned = []
        for g, _ in pieces:
            flat = g.reshape((-1,) + g.shape[3:])
            part = lax.psum_scatter(flat, ("chip", "core"), scatter_dimension=0, tiled=True)
            owned.append(lax.psum(part.astype(send), "rep").astype(jnp.float32))
        yield owned
        return owned
    chip, core, p = ring.here()
    n = ring.n
    mine, theirs = [], []
    for g, _ in pieces:
        mine.append(lax.dynamic_index_in_dim(g, core, axis=1, keepdims=False))
        theirs.append(lax.dynamic_index_in_dim(g, 1 - core, axis=1, keepdims=False).astype(send))
    got = lax.ppermute(theirs, "core", SWAP)
    yield got
    flows = []
    for i, (g, way) in enumerate(pieces):
        if isinstance(way, tuple):
            axis = way[1] + 1
            for d, (m, t) in zip((1, -1), zip(_halves(mine[i], axis), _halves(got[i], axis))):
                flows.append((i, d, m, t))
        else:
            flows.append((i, way, mine[i], got[i]))

    def contribution(m, t, position):
        at = ring.chip_at(position)
        own = lax.dynamic_index_in_dim(m, at, axis=0, keepdims=False)
        other = lax.dynamic_index_in_dim(t, at, axis=0, keepdims=False)
        return own + other.astype(jnp.float32)

    acc = [contribution(m, t, p - d) for _, d, m, t in flows]
    for step in range(1, n):
        moved = []
        for d in (1, -1):
            chosen = [k for k, f in enumerate(flows) if f[1] == d]
            if chosen:
                out = lax.ppermute([acc[k].astype(send) for k in chosen], "chip", ring.cw if d == 1 else ring.ccw)
                for k, o in zip(chosen, out):
                    acc[k] = o
                moved.extend(out)
        yield moved
        acc = [
            a.astype(jnp.float32) + contribution(m, t, p - d * (1 + step))
            for a, (_, d, m, t) in zip(acc, flows)
        ]
    owned = []
    for i, (g, way) in enumerate(pieces):
        parts = [a for a, f in zip(acc, flows) if f[0] == i]
        owned.append(parts[0] if len(parts) == 1 else jnp.concatenate(parts, axis=way[1]))
    other = lax.ppermute([o.astype(send) for o in owned], "rep", SWAP)
    yield other
    return [o + t.astype(jnp.float32) for o, t in zip(owned, other)]


class Stepper:
    def __init__(self, gen):
        self.gen = gen
        self.result = None
        self.over = False

    def tie(self, value):
        if self.over:
            return value
        try:
            ready = next(self.gen)
        except StopIteration as done:
            self.result, self.over = done.value, True
            return value
        _, value = lax.optimization_barrier((ready, value))
        return value

    def finish(self):
        if not self.over:
            self.result, self.over = run_steps(self.gen), True
        return self.result


def run_steps(gen):
    while True:
        try:
            next(gen)
        except StopIteration as done:
            return done.value


SMALL_ROWS, SMALL_LANES = 16, 768


def small_layout(fsdp):
    d = 768 // fsdp
    sizes = [2 * d, 6 * d, 3072 // fsdp, 128 // fsdp, 128 // fsdp, 4096 // fsdp, 4096 // fsdp, (128 // fsdp) * 32]
    offsets, at = [], 0
    for size in sizes:
        offsets.append((at, size))
        at += size
    assert at <= SMALL_ROWS * SMALL_LANES
    return offsets


def pack_small(parts):
    flat = jnp.concatenate([part.reshape(-1) for part in parts])
    flat = jnp.pad(flat, (0, SMALL_ROWS * SMALL_LANES - flat.shape[0]))
    return flat.reshape(SMALL_ROWS, SMALL_LANES)


def unpack_small_full(gathered, offsets, fsdp):
    flat = gathered.reshape(fsdp, -1).astype(jnp.float32)
    take = [flat[:, at : at + size] for at, size in offsets]
    d = 768 // fsdp
    return [
        take[0].reshape(fsdp, 2, d).transpose(1, 0, 2).reshape(2, -1),
        take[1].reshape(fsdp, 6, d).transpose(1, 0, 2).reshape(6, -1),
        take[2].reshape(-1),
        take[3].reshape(-1),
        take[4].reshape(-1),
        take[5].reshape(ATOM_TYPES, ATOM_TYPES),
        take[6].reshape(ATOM_TYPES, ATOM_TYPES),
        take[7].reshape(-1, 32),
    ]


def pack_small_grads(grads, fsdp, chips):
    d = 768 // fsdp
    blocks = [
        grads[0].reshape(2, fsdp, d).transpose(1, 0, 2),
        grads[1].reshape(6, fsdp, d).transpose(1, 0, 2),
    ] + [g.reshape(-1) for g in grads[2:]]
    flat = jnp.concatenate([blk.reshape(fsdp, -1) for blk in blocks], axis=1)
    flat = jnp.pad(flat, ((0, 0), (0, SMALL_ROWS * SMALL_LANES - flat.shape[1])))
    return flat.reshape(chips, 2, SMALL_ROWS, SMALL_LANES)


def unpack_small_owned(block, offsets):
    flat = block.reshape(-1)
    take = [flat[at : at + size] for at, size in offsets]
    return [
        take[0].reshape(2, -1),
        take[1].reshape(6, -1),
        take[2],
        take[3],
        take[4],
        take[5],
        take[6],
        take[7].reshape(-1, 32),
    ]


def make_body(ring, chips):
    fsdp = 2 * chips

    def body(
        inputs,
        times,
        positions,
        atom_types,
        molecule_ids,
        pad_mask,
        cotangent,
        norm_gains,
        bias_rows,
        up_bias,
        input_weight,
        output_weight,
        up_weight,
        down_weight,
        kernel_means,
        kernel_widths,
        pair_scale,
        pair_shift,
        kernel_heads,
    ):
        offsets = small_layout(fsdp)
        small = pack_small(
            [norm_gains, bias_rows, up_bias, kernel_means, kernel_widths, pair_scale, pair_shift, kernel_heads]
        )
        width = input_weight.shape[0]
        first = jnp.concatenate([small.reshape(-1, width), input_weight.T], axis=0)
        second = jnp.concatenate(
            [output_weight.T, up_weight.T, down_weight.T.reshape(-1, width)], axis=0
        )
        first_all = lax.all_gather(first, ("chip", "core"), axis=0, tiled=False)
        second_all = lax.all_gather(second, ("chip", "core"), axis=0, tiled=False)
        small_rows = small.size // width
        params = unpack_small_full(first_all[:, :small_rows], offsets, fsdp)
        in_t = first_all[:, small_rows:].reshape(-1, width)
        out_rows = output_weight.shape[1]
        up_rows = up_weight.shape[1]
        out_t = second_all[:, :out_rows].reshape(-1, width)
        up_t = second_all[:, out_rows : out_rows + up_rows].reshape(-1, width)
        down_t = (
            second_all[:, out_rows + up_rows :]
            .reshape(fsdp, down_weight.shape[1], -1)
            .reshape(-1, down_weight.shape[0])
        )
        gains_now, biases_now, up_shift = params[0], params[1], params[2]
        tables = (params[3], params[4], params[5], params[6])
        heads_full = params[7].astype(jnp.bfloat16)

        row_count = inputs.shape[0]
        model_width = inputs.shape[1]
        head_count = heads_full.shape[1]
        head_size = model_width // head_count
        block_rows = min(128, row_count)
        blocks = row_count // block_rows
        tile_rows = min(128, block_rows)
        nt = (((1,), (1,)), ((), ()))
        tn = (((0,), (0,)), ((), ()))

        stream = inputs.astype(jnp.float32) + time_embedding(times, model_width)
        normed_out, normed_one, inv_one = layer_norm(stream, gains_now[0], biases_now[0])
        act_one = normed_out.astype(jnp.bfloat16)
        qkv_shift = jnp.concatenate([biases_now[2], jnp.zeros_like(biases_now[2]), biases_now[3]])
        projected = (
            lax.dot_general(act_one, in_t, nt, preferred_element_type=jnp.float32) + qkv_shift
        ).astype(jnp.bfloat16)
        split_shape = (blocks, block_rows, head_count, head_size)
        queries = projected[:, :model_width].reshape(split_shape)
        key_rows = projected[:, model_width : 2 * model_width].reshape(split_shape)
        value_rows = projected[:, 2 * model_width :].reshape(split_shape)
        pos_blocks = jnp.transpose(positions.reshape(3, blocks, block_rows), (1, 0, 2))
        type_blocks = atom_types.reshape(blocks, block_rows)
        mol_blocks = molecule_ids.reshape(blocks, block_rows)
        pad_blocks = pad_mask.reshape(blocks, block_rows)
        fwd = [
            block_forward(
                (queries[b], key_rows[b], value_rows[b], pos_blocks[b], type_blocks[b], mol_blocks[b], pad_blocks[b]),
                tables=tables,
                kernel_heads=heads_full,
                tile_rows=tile_rows,
            )
            for b in range(blocks)
        ]
        attended = jnp.stack([f[0] for f in fwd])
        log_sums = [f[1] for f in fwd]
        attended_low = attended.reshape(row_count, model_width).astype(jnp.bfloat16)
        mid = stream + (
            lax.dot_general(attended_low, out_t, nt, preferred_element_type=jnp.float32)
            + biases_now[4]
        )
        normed_out_two, normed_two, inv_two = layer_norm(mid, gains_now[1], biases_now[1])
        act_two = normed_out_two.astype(jnp.bfloat16)
        hidden_pre = (
            lax.dot_general(act_two, up_t, nt, preferred_element_type=jnp.float32) + up_shift
        )
        hidden_low = gelu_value(hidden_pre).astype(jnp.bfloat16)
        final = mid + (
            lax.dot_general(hidden_low, down_t, nt, preferred_element_type=jnp.float32)
            + biases_now[5]
        )
        rows_out = final.astype(jnp.bfloat16)

        grad_final = cotangent.astype(jnp.float32)
        down_grad_t = lax.dot_general(cotangent, hidden_low, tn, preferred_element_type=jnp.float32)
        grad_hidden = jnp.dot(cotangent, down_t, preferred_element_type=jnp.float32) * gelu_slope(
            hidden_pre
        )
        grad_hidden_low = grad_hidden.astype(jnp.bfloat16)
        up_grad_t = lax.dot_general(grad_hidden_low, act_two, tn, preferred_element_type=jnp.float32)
        up_bias_grad = jnp.sum(grad_hidden_low.astype(jnp.float32), axis=0)
        grad_act_two = jnp.dot(grad_hidden_low, up_t, preferred_element_type=jnp.float32)
        grad_norm_two, gain_two_grad, shift_two_grad = norm_backward(
            grad_act_two, normed_two, inv_two, gains_now[1]
        )
        grad_mid = grad_final + grad_norm_two
        grad_branch_low = grad_mid.astype(jnp.bfloat16)
        out_grad_t = lax.dot_general(
            grad_branch_low, attended_low, tn, preferred_element_type=jnp.float32
        )
        late_rows = jnp.concatenate(
            [
                out_grad_t.reshape(chips, 2, -1, model_width),
                up_grad_t.reshape(chips, 2, -1, model_width),
            ],
            axis=2,
        )
        late = ring_reduce_steps(
            ring, [(late_rows, 1), (down_grad_t.reshape((chips, 2, -1) + down_grad_t.shape[1:]), -1)]
        )
        grad_attended = jnp.dot(grad_branch_low, out_t, preferred_element_type=jnp.float32).astype(
            jnp.bfloat16
        )
        kernel_count = tables[0].shape[0]
        start_sums = (
            jnp.zeros((kernel_count, head_count), jnp.float32),
            jnp.zeros((kernel_count,), jnp.float32),
            jnp.zeros((kernel_count,), jnp.float32),
            jnp.zeros((ATOM_TYPES, ATOM_TYPES), jnp.float32),
            jnp.zeros((ATOM_TYPES, ATOM_TYPES), jnp.float32),
        )
        kernel_sums = start_sums
        q_grads, k_grads, v_grads = [], [], []
        grad_attended_blocks = grad_attended.reshape(split_shape)
        stepper = Stepper(late)
        for b in range(blocks):
            gate = grad_attended_blocks[b]
            if b > 0:
                gate = stepper.tie(gate)
            kernel_sums, (qg, kg, vg) = block_backward(
                kernel_sums,
                (
                    queries[b],
                    key_rows[b],
                    value_rows[b],
                    gate,
                    log_sums[b],
                    pos_blocks[b],
                    type_blocks[b],
                    mol_blocks[b],
                    pad_blocks[b],
                ),
                tables=tables,
                kernel_heads=heads_full,
                tile_rows=tile_rows,
                hook=stepper.tie,
            )
            q_grads.append(qg)
            k_grads.append(kg)
            v_grads.append(vg)
        queries_grad = jnp.stack(q_grads)
        keys_grad = jnp.stack(k_grads)
        values_grad = jnp.stack(v_grads)
        grad_projected = jnp.concatenate(
            [
                queries_grad.reshape(row_count, model_width),
                keys_grad.reshape(row_count, model_width),
                values_grad.reshape(row_count, model_width),
            ],
            axis=1,
        ).astype(jnp.bfloat16)
        in_grad_t = lax.dot_general(grad_projected, act_one, tn, preferred_element_type=jnp.float32)
        grad_act_one = jnp.dot(grad_projected, in_t, preferred_element_type=jnp.float32)
        grad_norm_one, gain_one_grad, shift_one_grad = norm_backward(
            grad_act_one, normed_one, inv_one, gains_now[0]
        )
        inputs_grad = grad_mid + grad_norm_one
        projected_sums = jnp.sum(grad_projected.astype(jnp.float32), axis=0)
        heads_grad, means_grad, widths_grad, scale_grad, shift_grad = kernel_sums
        small_grads = [
            jnp.stack([gain_one_grad, gain_two_grad]),
            jnp.stack(
                [
                    shift_one_grad,
                    shift_two_grad,
                    projected_sums[:model_width],
                    projected_sums[2 * model_width :],
                    jnp.sum(grad_branch_low.astype(jnp.float32), axis=0),
                    jnp.sum(grad_final, axis=0),
                ]
            ),
            up_bias_grad,
            means_grad,
            widths_grad,
            scale_grad,
            shift_grad,
            heads_grad,
        ]
        late_owned = stepper.finish()
        out_owned = late_owned[0][:out_rows]
        up_owned = late_owned[0][out_rows:]
        down_owned = late_owned[1]
        last = jnp.concatenate(
            [
                in_grad_t.reshape((chips, 2, -1) + in_grad_t.shape[1:]),
                pack_small_grads(small_grads, fsdp, chips),
            ],
            axis=2,
        )
        (last_owned,) = run_steps(ring_reduce_steps(ring, [(last, ("split", 1))]))
        in_rows = in_grad_t.shape[0] // fsdp
        in_owned = last_owned[:in_rows]
        small_owned = last_owned[in_rows:]
        sg = unpack_small_owned(small_owned, offsets)
        return (
            rows_out,
            inputs_grad,
            sg[0],
            sg[1],
            sg[2],
            in_owned.T,
            out_owned.T,
            up_owned.T,
            down_owned.T,
            sg[3],
            sg[4],
            sg[5],
            sg[6],
            sg[7],
        )

    return body


def solution(mesh):
    reps, fsdp = mesh.devices.shape
    chips = fsdp // 2
    grid = Mesh(mesh.devices.reshape(reps, chips, 2), ("rep", "chip", "core"))
    chips_x = 1
    try:
        coords = [tuple(d.coords) for d in mesh.devices[0, ::2]]
        xs = sorted({c[0] for c in coords})
        chips_x = len(xs)
        flat_ok = all(
            coords[i][0] == xs[i % chips_x] for i in range(chips)
        )
        if not flat_ok:
            chips_x = 1
    except Exception:
        chips_x = 1
    ring = None
    if chips <= 8:
        ring = Ring(snake_ring(chips_x, chips // chips_x))
    atoms = ("rep", "chip", "core")
    cols = ("chip", "core")
    placed = (
        P(atoms, None),
        P(atoms),
        P(None, atoms),
        P(atoms),
        P(atoms),
        P(atoms),
        P(atoms, None),
        P(None, cols),
        P(None, cols),
        P(cols),
        P(None, cols),
        P(None, cols),
        P(None, cols),
        P(None, cols),
        P(cols),
        P(cols),
        P(cols),
        P(cols),
        P(cols, None),
    )
    return jax.shard_map(
        make_body(ring, chips),
        mesh=grid,
        in_specs=placed,
        out_specs=(
            P(atoms, None),
            P(atoms, None),
            P(None, cols),
            P(None, cols),
            P(cols),
            P(None, cols),
            P(None, cols),
            P(None, cols),
            P(None, cols),
            P(cols),
            P(cols),
            P(cols),
            P(cols),
            P(cols, None),
        ),
        check_vma=False,
    )
```

```python
from functools import partial
import math

import jax
import jax.numpy as jnp
from jax import lax
from jax.sharding import Mesh, PartitionSpec as P
import numpy as np

ATOM_TYPES = 64


epsilon = 1e-05
masked_score = -1000000000.0
time_scale = 1000.0
root_two_pi = math.sqrt(2.0 * math.pi)
highest = lax.Precision.HIGHEST


def time_embedding(times, model_width):
    half_width = model_width // 2
    counter = jnp.arange(half_width, dtype=jnp.float32)
    frequency = jnp.exp(counter * (-math.log(10000.0) / half_width))
    angles = (time_scale * times)[:, None] * frequency[None, :]
    return jnp.concatenate([jnp.sin(angles), jnp.cos(angles)], axis=1)


def layer_norm(values, gain_row, shift_row):
    center = values - jnp.mean(values, axis=1, keepdims=True)
    inv_std = lax.rsqrt(jnp.mean(center * center, axis=1, keepdims=True) + epsilon)
    normed = center * inv_std
    return (normed * gain_row + shift_row, normed, inv_std)


def norm_backward(grad_out, normed, inv_std, gain_row):
    grad_normed = grad_out * gain_row
    first_mean = jnp.mean(grad_normed, axis=1, keepdims=True)
    second_mean = jnp.mean(grad_normed * normed, axis=1, keepdims=True)
    grad_input = inv_std * (grad_normed - first_mean - normed * second_mean)
    return (grad_input, jnp.sum(grad_out * normed, axis=0), jnp.sum(grad_out, axis=0))


def gelu_value(values):
    return values * (0.5 + 0.5 * lax.erf(values * math.sqrt(0.5)))


def gelu_slope(values):
    return (
        0.5
        + 0.5 * lax.erf(values * math.sqrt(0.5))
        + values * jnp.exp(-0.5 * values * values) / root_two_pi
    )


def pair_terms(pos_rows, pos_cols, type_rows, type_cols, tables):
    kernel_means, kernel_widths, scale_table, shift_table = tables
    offsets = pos_rows[:, :, None] - pos_cols[:, None, :]
    distance = jnp.sqrt(jnp.sum(offsets * offsets, axis=0))
    type_range = jnp.arange(ATOM_TYPES, dtype=jnp.int32)
    hot_rows = (type_rows[:, None] == type_range[None, :]).astype(jnp.float32)
    hot_cols = (type_cols[:, None] == type_range[None, :]).astype(jnp.float32)
    scale_pair = jnp.dot(
        jnp.dot(hot_rows, scale_table, precision=highest), hot_cols.T, precision=highest
    )
    shift_pair = jnp.dot(
        jnp.dot(hot_rows, shift_table, precision=highest), hot_cols.T, precision=highest
    )
    stretched = scale_pair * distance + shift_pair
    kernel_gap = (stretched[:, :, None] - kernel_means) / kernel_widths
    kernels = jnp.exp(-0.5 * kernel_gap * kernel_gap) / (root_two_pi * kernel_widths)
    return (distance, hot_rows, hot_cols, kernel_gap, kernels)


def allowed_pairs(row_ids, col_ids, mol_rows, mol_cols, pad_cols):
    same_mol = mol_rows[:, None] == mol_cols[None, :]
    key_live = (pad_cols[None, :] == 1) | (row_ids[:, None] == col_ids[None, :])
    return same_mol & key_live


def tile_scores(q_tile, key_block, kernels_low, kernel_heads, allowed, score_scale):
    pair_bias = jnp.einsum(
        "ijk,kh->hij", kernels_low, kernel_heads, preferred_element_type=jnp.float32
    )
    raw_scores = jnp.einsum("ihd,jhd->hij", q_tile, key_block, preferred_element_type=jnp.float32)
    return jnp.where(allowed[None], raw_scores * score_scale + pair_bias, masked_score)


def block_forward(pieces, tables, kernel_heads, tile_rows):
    queries, key_block, value_block, positions, types, mols, pads = pieces
    block_rows = queries.shape[0]
    score_scale = 1.0 / math.sqrt(queries.shape[2])
    col_ids = jnp.arange(block_rows, dtype=jnp.int32)

    def one_tile(running, tile_index):
        first_row = tile_index * tile_rows
        row_ids = first_row + jnp.arange(tile_rows, dtype=jnp.int32)
        terms = pair_terms(positions, positions, types, types, tables)
        kernels_low = terms[4].astype(jnp.bfloat16)
        allowed = allowed_pairs(row_ids, col_ids, mols, mols, pads)
        scores = tile_scores(queries, key_block, kernels_low, kernel_heads, allowed, score_scale)
        row_max = jnp.max(scores, axis=2, keepdims=True)
        exponent = jnp.exp(scores - row_max)
        row_sum = jnp.sum(exponent, axis=2, keepdims=True)
        probs_low = (exponent / row_sum).astype(jnp.bfloat16)
        attended = jnp.einsum(
            "hij,jhd->ihd", probs_low, value_block, preferred_element_type=jnp.float32
        )
        return (running, (attended, (row_max + jnp.log(row_sum))[:, :, 0]))

    count = block_rows // tile_rows
    if count == 1:
        _, (attended, log_sums) = one_tile(None, 0)
        return (attended.reshape(block_rows, -1), log_sums)
    _, (attended, log_sums) = lax.scan(one_tile, None, jnp.arange(count, dtype=jnp.int32))
    attended = attended.reshape(block_rows, -1)
    log_sums = jnp.transpose(log_sums, (1, 0, 2)).reshape(log_sums.shape[1], block_rows)
    return (attended, log_sums)


def block_backward(running, pieces, tables, kernel_heads, tile_rows, hook=None):
    queries, key_block, value_block, grad_attended, log_sums, positions, types, mols, pads = pieces
    kernel_widths = tables[1]
    block_rows = queries.shape[0]
    score_scale = 1.0 / math.sqrt(queries.shape[2])
    col_ids = jnp.arange(block_rows, dtype=jnp.int32)

    def one_tile(partial_sums, tile_index):
        keys_grad, values_grad, heads_grad, means_grad, widths_grad, scale_grad, shift_grad = (
            partial_sums
        )
        first_row = tile_index * tile_rows
        row_ids = first_row + jnp.arange(tile_rows, dtype=jnp.int32)
        distance, hot_rows, hot_cols, kernel_gap, kernels = pair_terms(
            positions, positions, types, types, tables
        )
        kernels_low = kernels.astype(jnp.bfloat16)
        allowed = allowed_pairs(row_ids, col_ids, mols, mols, pads)
        scores = tile_scores(queries, key_block, kernels_low, kernel_heads, allowed, score_scale)
        attn_probs = jnp.exp(scores - log_sums[:, :, None])
        grad_probs = jnp.einsum(
            "ihd,jhd->hij", grad_attended, value_block, preferred_element_type=jnp.float32
        )
        values_grad = values_grad + jnp.einsum(
            "hij,ihd->jhd",
            attn_probs.astype(jnp.bfloat16),
            grad_attended,
            preferred_element_type=jnp.float32,
        )
        probs_dot = jnp.sum(attn_probs * grad_probs, axis=2, keepdims=True)
        grad_scores = (attn_probs * (grad_probs - probs_dot)).astype(jnp.bfloat16)
        if hook is not None:
            grad_scores = hook(grad_scores)
        query_grad = (
            jnp.einsum("hij,jhd->ihd", grad_scores, key_block, preferred_element_type=jnp.float32)
            * score_scale
        )
        keys_grad = (
            keys_grad
            + jnp.einsum("hij,ihd->jhd", grad_scores, queries, preferred_element_type=jnp.float32)
            * score_scale
        )
        heads_grad = heads_grad + jnp.einsum(
            "ijk,hij->kh", kernels_low, grad_scores, preferred_element_type=jnp.float32
        )
        grad_kernels = jnp.einsum(
            "hij,kh->ijk", grad_scores, kernel_heads, preferred_element_type=jnp.float32
        )
        spread = grad_kernels * kernels
        mean_part = spread * kernel_gap / kernel_widths
        means_grad = means_grad + jnp.sum(mean_part, axis=(0, 1))
        widths_grad = widths_grad + jnp.sum(
            spread * (kernel_gap * kernel_gap - 1.0) / kernel_widths, axis=(0, 1)
        )
        grad_stretched = -jnp.sum(mean_part, axis=2)
        scale_grad = scale_grad + jnp.dot(
            jnp.dot(hot_rows.T, grad_stretched * distance, precision=highest),
            hot_cols,
            precision=highest,
        )
        shift_grad = shift_grad + jnp.dot(
            jnp.dot(hot_rows.T, grad_stretched, precision=highest), hot_cols, precision=highest
        )
        return (
            (keys_grad, values_grad, heads_grad, means_grad, widths_grad, scale_grad, shift_grad),
            query_grad,
        )

    zero_block = jnp.zeros(key_block.shape, jnp.float32)
    count = block_rows // tile_rows
    if count == 1:
        sums_out, query_grads = one_tile((zero_block, zero_block) + tuple(running), 0)
        return (sums_out[2:], (query_grads.reshape(key_block.shape), sums_out[0], sums_out[1]))
    sums_out, query_grads = lax.scan(
        one_tile, (zero_block, zero_block) + tuple(running), jnp.arange(count, dtype=jnp.int32)
    )
    query_grads = query_grads.reshape(key_block.shape)
    return (sums_out[2:], (query_grads, sums_out[0], sums_out[1]))


def snake_ring(chips_x, chips_other):
    if chips_x == 2 and chips_other >= 2:
        return [2 * z for z in range(chips_other)] + [
            2 * z + 1 for z in reversed(range(chips_other))
        ]
    return list(range(chips_x * chips_other))


class Ring:
    def __init__(self, order):
        self.order = order
        self.n = len(order)
        pos = np.zeros(self.n, np.int32)
        for i, c in enumerate(order):
            pos[c] = i
        self.pos = pos
        self.cw = [(order[i], order[(i + 1) % self.n]) for i in range(self.n)]
        self.ccw = [(order[i], order[(i - 1) % self.n]) for i in range(self.n)]

    def here(self):
        chip = lax.axis_index("chip")
        core = lax.axis_index("core")
        return chip, core, jnp.asarray(self.pos)[chip]

    def chip_at(self, position):
        return jnp.asarray(np.array(self.order, np.int32))[position % self.n]


SWAP = [(0, 1), (1, 0)]


def _halves(x, axis):
    size = x.shape[axis] // 2
    return (
        lax.slice_in_dim(x, 0, size, axis=axis),
        lax.slice_in_dim(x, size, 2 * size, axis=axis),
    )


def ring_gather(ring, pieces, chips):
    if ring is None:
        return [
            lax.all_gather(x, ("chip", "core"), axis=0, tiled=False).reshape((chips, 2) + x.shape)
            for x, _ in pieces
        ]
    chip, core, p = ring.here()
    n = ring.n
    bufs, fronts = [], []
    for x, axis in pieces:
        buf = jnp.zeros((n, 2) + x.shape, x.dtype)
        buf = lax.dynamic_update_slice(buf, x[None, None], (chip, core) + (0,) * x.ndim)
        bufs.append(buf)
        if axis is None:
            fronts.append([x, None])
        else:
            fronts.append(list(_halves(x, axis)))
    partner = lax.ppermute([x for x, _ in pieces], "core", SWAP)
    for i, x in enumerate(partner):
        bufs[i] = lax.dynamic_update_slice(
            bufs[i], x[None, None], (chip, 1 - core) + (0,) * x.ndim
        )
    for step in range(1, n):
        going = [f[0] for f in fronts]
        coming = [f[1] for f in fronts if f[1] is not None]
        going = lax.ppermute(going, "chip", ring.cw)
        coming = lax.ppermute(coming, "chip", ring.ccw) if coming else []
        from_cw = ring.chip_at(p - step)
        from_ccw = ring.chip_at(p + step)
        both = lax.ppermute([going, coming], "core", SWAP)
        j = 0
        for i, (x, axis) in enumerate(pieces):
            fronts[i][0] = going[i]
            parts = [(going[i], both[0][i], from_cw, 0)]
            if axis is not None:
                fronts[i][1] = coming[j]
                parts.append((coming[j], both[1][j], from_ccw, x.shape[axis] // 2))
                j += 1
            for mine, theirs, source, offset in parts:
                start = [0] * x.ndim
                if axis is not None:
                    start[axis] = offset
                bufs[i] = lax.dynamic_update_slice(
                    bufs[i], mine[None, None], (source, core) + tuple(start)
                )
                bufs[i] = lax.dynamic_update_slice(
                    bufs[i], theirs[None, None], (source, 1 - core) + tuple(start)
                )
    return bufs


def ring_reduce_steps(ring, pieces, send=jnp.bfloat16):
    if ring is None:
        owned = []
        for g, _ in pieces:
            flat = g.reshape((-1,) + g.shape[3:])
            part = lax.psum_scatter(flat, ("chip", "core"), scatter_dimension=0, tiled=True)
            owned.append(lax.psum(part.astype(send), "rep").astype(jnp.float32))
        yield owned
        return owned
    chip, core, p = ring.here()
    n = ring.n
    mine, theirs = [], []
    for g, _ in pieces:
        mine.append(lax.dynamic_index_in_dim(g, core, axis=1, keepdims=False))
        theirs.append(lax.dynamic_index_in_dim(g, 1 - core, axis=1, keepdims=False).astype(send))
    got = lax.ppermute(theirs, "core", SWAP)
    yield got
    flows = []
    for i, (g, way) in enumerate(pieces):
        if isinstance(way, tuple):
            axis = way[1] + 1
            for d, (m, t) in zip((1, -1), zip(_halves(mine[i], axis), _halves(got[i], axis))):
                flows.append((i, d, m, t))
        else:
            flows.append((i, way, mine[i], got[i]))

    def contribution(m, t, position):
        at = ring.chip_at(position)
        own = lax.dynamic_index_in_dim(m, at, axis=0, keepdims=False)
        other = lax.dynamic_index_in_dim(t, at, axis=0, keepdims=False)
        return own + other.astype(jnp.float32)

    acc = [contribution(m, t, p - d) for _, d, m, t in flows]
    for step in range(1, n):
        moved = []
        for d in (1, -1):
            chosen = [k for k, f in enumerate(flows) if f[1] == d]
            if chosen:
                out = lax.ppermute([acc[k].astype(send) for k in chosen], "chip", ring.cw if d == 1 else ring.ccw)
                for k, o in zip(chosen, out):
                    acc[k] = o
                moved.extend(out)
        yield moved
        acc = [
            a.astype(jnp.float32) + contribution(m, t, p - d * (1 + step))
            for a, (_, d, m, t) in zip(acc, flows)
        ]
    owned = []
    for i, (g, way) in enumerate(pieces):
        parts = [a for a, f in zip(acc, flows) if f[0] == i]
        owned.append(parts[0] if len(parts) == 1 else jnp.concatenate(parts, axis=way[1]))
    other = lax.ppermute([o.astype(send) for o in owned], "rep", SWAP)
    yield other
    return [o + t.astype(jnp.float32) for o, t in zip(owned, other)]


class Stepper:
    def __init__(self, gen):
        self.gen = gen
        self.result = None
        self.over = False

    def tie(self, value):
        if self.over:
            return value
        try:
            ready = next(self.gen)
        except StopIteration as done:
            self.result, self.over = done.value, True
            return value
        _, value = lax.optimization_barrier((ready, value))
        return value

    def finish(self):
        if not self.over:
            self.result, self.over = run_steps(self.gen), True
        return self.result


def run_steps(gen):
    while True:
        try:
            next(gen)
        except StopIteration as done:
            return done.value


SMALL_ROWS, SMALL_LANES = 16, 768


def small_layout(fsdp):
    d = 768 // fsdp
    sizes = [2 * d, 6 * d, 3072 // fsdp, 128 // fsdp, 128 // fsdp, 4096 // fsdp, 4096 // fsdp, (128 // fsdp) * 32]
    offsets, at = [], 0
    for size in sizes:
        offsets.append((at, size))
        at += size
    assert at <= SMALL_ROWS * SMALL_LANES
    return offsets


def pack_small(parts):
    flat = jnp.concatenate([part.reshape(-1) for part in parts])
    flat = jnp.pad(flat, (0, SMALL_ROWS * SMALL_LANES - flat.shape[0]))
    return flat.reshape(SMALL_ROWS, SMALL_LANES)


def unpack_small_full(gathered, offsets, fsdp):
    flat = gathered.reshape(fsdp, -1).astype(jnp.float32)
    take = [flat[:, at : at + size] for at, size in offsets]
    d = 768 // fsdp
    return [
        take[0].reshape(fsdp, 2, d).transpose(1, 0, 2).reshape(2, -1),
        take[1].reshape(fsdp, 6, d).transpose(1, 0, 2).reshape(6, -1),
        take[2].reshape(-1),
        take[3].reshape(-1),
        take[4].reshape(-1),
        take[5].reshape(ATOM_TYPES, ATOM_TYPES),
        take[6].reshape(ATOM_TYPES, ATOM_TYPES),
        take[7].reshape(-1, 32),
    ]


def pack_small_grads(grads, fsdp, chips):
    d = 768 // fsdp
    blocks = [
        grads[0].reshape(2, fsdp, d).transpose(1, 0, 2),
        grads[1].reshape(6, fsdp, d).transpose(1, 0, 2),
    ] + [g.reshape(-1) for g in grads[2:]]
    flat = jnp.concatenate([blk.reshape(fsdp, -1) for blk in blocks], axis=1)
    flat = jnp.pad(flat, ((0, 0), (0, SMALL_ROWS * SMALL_LANES - flat.shape[1])))
    return flat.reshape(chips, 2, SMALL_ROWS, SMALL_LANES)


def unpack_small_owned(block, offsets):
    flat = block.reshape(-1)
    take = [flat[at : at + size] for at, size in offsets]
    return [
        take[0].reshape(2, -1),
        take[1].reshape(6, -1),
        take[2],
        take[3],
        take[4],
        take[5],
        take[6],
        take[7].reshape(-1, 32),
    ]


def make_body(ring, chips):
    fsdp = 2 * chips

    def body(
        inputs,
        times,
        positions,
        atom_types,
        molecule_ids,
        pad_mask,
        cotangent,
        norm_gains,
        bias_rows,
        up_bias,
        input_weight,
        output_weight,
        up_weight,
        down_weight,
        kernel_means,
        kernel_widths,
        pair_scale,
        pair_shift,
        kernel_heads,
    ):
        offsets = small_layout(fsdp)
        small = pack_small(
            [norm_gains, bias_rows, up_bias, kernel_means, kernel_widths, pair_scale, pair_shift, kernel_heads]
        )
        width = input_weight.shape[0]
        first = jnp.concatenate([small.reshape(-1, width), input_weight.T], axis=0)
        second = jnp.concatenate(
            [output_weight.T, up_weight.T, down_weight.T.reshape(-1, width)], axis=0
        )
        first_all = lax.all_gather(first, ("chip", "core"), axis=0, tiled=False)
        second_all = lax.all_gather(second, ("chip", "core"), axis=0, tiled=False)
        small_rows = small.size // width
        params = unpack_small_full(first_all[:, :small_rows], offsets, fsdp)
        in_t = first_all[:, small_rows:].reshape(-1, width)
        out_rows = output_weight.shape[1]
        up_rows = up_weight.shape[1]
        out_t = second_all[:, :out_rows].reshape(-1, width)
        up_t = second_all[:, out_rows : out_rows + up_rows].reshape(-1, width)
        down_t = (
            second_all[:, out_rows + up_rows :]
            .reshape(fsdp, down_weight.shape[1], -1)
            .reshape(-1, down_weight.shape[0])
        )
        gains_now, biases_now, up_shift = params[0], params[1], params[2]
        tables = (params[3], params[4], params[5], params[6])
        heads_full = params[7].astype(jnp.bfloat16)

        row_count = inputs.shape[0]
        model_width = inputs.shape[1]
        head_count = heads_full.shape[1]
        head_size = model_width // head_count
        block_rows = min(128, row_count)
        blocks = row_count // block_rows
        tile_rows = min(128, block_rows)
        nt = (((1,), (1,)), ((), ()))
        tn = (((0,), (0,)), ((), ()))

        stream = inputs.astype(jnp.float32) + time_embedding(times, model_width)
        normed_out, normed_one, inv_one = layer_norm(stream, gains_now[0], biases_now[0])
        act_one = normed_out.astype(jnp.bfloat16)
        qkv_shift = jnp.concatenate([biases_now[2], jnp.zeros_like(biases_now[2]), biases_now[3]])
        projected = (
            lax.dot_general(act_one, in_t, nt, preferred_element_type=jnp.float32) + qkv_shift
        ).astype(jnp.bfloat16)
        split_shape = (blocks, block_rows, head_count, head_size)
        queries = projected[:, :model_width].reshape(split_shape)
        key_rows = projected[:, model_width : 2 * model_width].reshape(split_shape)
        value_rows = projected[:, 2 * model_width :].reshape(split_shape)
        pos_blocks = jnp.transpose(positions.reshape(3, blocks, block_rows), (1, 0, 2))
        type_blocks = atom_types.reshape(blocks, block_rows)
        mol_blocks = molecule_ids.reshape(blocks, block_rows)
        pad_blocks = pad_mask.reshape(blocks, block_rows)
        fwd = [
            block_forward(
                (queries[b], key_rows[b], value_rows[b], pos_blocks[b], type_blocks[b], mol_blocks[b], pad_blocks[b]),
                tables=tables,
                kernel_heads=heads_full,
                tile_rows=tile_rows,
            )
            for b in range(blocks)
        ]
        attended = jnp.stack([f[0] for f in fwd])
        log_sums = [f[1] for f in fwd]
        attended_low = attended.reshape(row_count, model_width).astype(jnp.bfloat16)
        mid = stream + (
            lax.dot_general(attended_low, out_t, nt, preferred_element_type=jnp.float32)
            + biases_now[4]
        )
        normed_out_two, normed_two, inv_two = layer_norm(mid, gains_now[1], biases_now[1])
        act_two = normed_out_two.astype(jnp.bfloat16)
        hidden_pre = (
            lax.dot_general(act_two, up_t, nt, preferred_element_type=jnp.float32) + up_shift
        )
        hidden_low = gelu_value(hidden_pre).astype(jnp.bfloat16)
        final = mid + (
            lax.dot_general(hidden_low, down_t, nt, preferred_element_type=jnp.float32)
            + biases_now[5]
        )
        rows_out = final.astype(jnp.bfloat16)

        grad_final = cotangent.astype(jnp.float32)
        down_grad_t = lax.dot_general(cotangent, hidden_low, tn, preferred_element_type=jnp.float32)
        grad_hidden = jnp.dot(cotangent, down_t, preferred_element_type=jnp.float32) * gelu_slope(
            hidden_pre
        )
        grad_hidden_low = grad_hidden.astype(jnp.bfloat16)
        up_grad_t = lax.dot_general(grad_hidden_low, act_two, tn, preferred_element_type=jnp.float32)
        up_bias_grad = jnp.sum(grad_hidden_low.astype(jnp.float32), axis=0)
        grad_act_two = jnp.dot(grad_hidden_low, up_t, preferred_element_type=jnp.float32)
        grad_norm_two, gain_two_grad, shift_two_grad = norm_backward(
            grad_act_two, normed_two, inv_two, gains_now[1]
        )
        grad_mid = grad_final + grad_norm_two
        grad_branch_low = grad_mid.astype(jnp.bfloat16)
        out_grad_t = lax.dot_general(
            grad_branch_low, attended_low, tn, preferred_element_type=jnp.float32
        )
        late_rows = jnp.concatenate(
            [
                out_grad_t.reshape(chips, 2, -1, model_width),
                up_grad_t.reshape(chips, 2, -1, model_width),
            ],
            axis=2,
        )
        late = ring_reduce_steps(
            ring, [(late_rows, 1), (down_grad_t.reshape((chips, 2, -1) + down_grad_t.shape[1:]), -1)]
        )
        grad_attended = jnp.dot(grad_branch_low, out_t, preferred_element_type=jnp.float32).astype(
            jnp.bfloat16
        )
        kernel_count = tables[0].shape[0]
        start_sums = (
            jnp.zeros((kernel_count, head_count), jnp.float32),
            jnp.zeros((kernel_count,), jnp.float32),
            jnp.zeros((kernel_count,), jnp.float32),
            jnp.zeros((ATOM_TYPES, ATOM_TYPES), jnp.float32),
            jnp.zeros((ATOM_TYPES, ATOM_TYPES), jnp.float32),
        )
        kernel_sums = start_sums
        q_grads, k_grads, v_grads = [], [], []
        grad_attended_blocks = grad_attended.reshape(split_shape)
        stepper = Stepper(late)
        for b in range(blocks):
            gate = stepper.tie(grad_attended_blocks[b])
            kernel_sums, (qg, kg, vg) = block_backward(
                kernel_sums,
                (
                    queries[b],
                    key_rows[b],
                    value_rows[b],
                    gate,
                    log_sums[b],
                    pos_blocks[b],
                    type_blocks[b],
                    mol_blocks[b],
                    pad_blocks[b],
                ),
                tables=tables,
                kernel_heads=heads_full,
                tile_rows=tile_rows,
                hook=stepper.tie,
            )
            q_grads.append(qg)
            k_grads.append(kg)
            v_grads.append(vg)
        queries_grad = jnp.stack(q_grads)
        keys_grad = jnp.stack(k_grads)
        values_grad = jnp.stack(v_grads)
        grad_projected = jnp.concatenate(
            [
                queries_grad.reshape(row_count, model_width),
                keys_grad.reshape(row_count, model_width),
                values_grad.reshape(row_count, model_width),
            ],
            axis=1,
        ).astype(jnp.bfloat16)
        in_grad_t = lax.dot_general(grad_projected, act_one, tn, preferred_element_type=jnp.float32)
        grad_act_one = jnp.dot(grad_projected, in_t, preferred_element_type=jnp.float32)
        grad_norm_one, gain_one_grad, shift_one_grad = norm_backward(
            grad_act_one, normed_one, inv_one, gains_now[0]
        )
        inputs_grad = grad_mid + grad_norm_one
        projected_sums = jnp.sum(grad_projected.astype(jnp.float32), axis=0)
        heads_grad, means_grad, widths_grad, scale_grad, shift_grad = kernel_sums
        small_grads = [
            jnp.stack([gain_one_grad, gain_two_grad]),
            jnp.stack(
                [
                    shift_one_grad,
                    shift_two_grad,
                    projected_sums[:model_width],
                    projected_sums[2 * model_width :],
                    jnp.sum(grad_branch_low.astype(jnp.float32), axis=0),
                    jnp.sum(grad_final, axis=0),
                ]
            ),
            up_bias_grad,
            means_grad,
            widths_grad,
            scale_grad,
            shift_grad,
            heads_grad,
        ]
        late_owned = stepper.finish()
        out_owned = late_owned[0][:out_rows]
        up_owned = late_owned[0][out_rows:]
        down_owned = late_owned[1]
        last = jnp.concatenate(
            [
                in_grad_t.reshape((chips, 2, -1) + in_grad_t.shape[1:]),
                pack_small_grads(small_grads, fsdp, chips),
            ],
            axis=2,
        )
        (last_owned,) = run_steps(ring_reduce_steps(ring, [(last, ("split", 1))]))
        in_rows = in_grad_t.shape[0] // fsdp
        in_owned = last_owned[:in_rows]
        small_owned = last_owned[in_rows:]
        sg = unpack_small_owned(small_owned, offsets)
        return (
            rows_out,
            inputs_grad,
            sg[0],
            sg[1],
            sg[2],
            in_owned.T,
            out_owned.T,
            up_owned.T,
            down_owned.T,
            sg[3],
            sg[4],
            sg[5],
            sg[6],
            sg[7],
        )

    return body


def solution(mesh):
    reps, fsdp = mesh.devices.shape
    chips = fsdp // 2
    grid = Mesh(mesh.devices.reshape(reps, chips, 2), ("rep", "chip", "core"))
    chips_x = 1
    try:
        coords = [tuple(d.coords) for d in mesh.devices[0, ::2]]
        xs = sorted({c[0] for c in coords})
        chips_x = len(xs)
        flat_ok = all(
            coords[i][0] == xs[i % chips_x] for i in range(chips)
        )
        if not flat_ok:
            chips_x = 1
    except Exception:
        chips_x = 1
    ring = None
    if chips <= 8:
        ring = Ring(snake_ring(chips_x, chips // chips_x))
    atoms = ("rep", "chip", "core")
    cols = ("chip", "core")
    placed = (
        P(atoms, None),
        P(atoms),
        P(None, atoms),
        P(atoms),
        P(atoms),
        P(atoms),
        P(atoms, None),
        P(None, cols),
        P(None, cols),
        P(cols),
        P(None, cols),
        P(None, cols),
        P(None, cols),
        P(None, cols),
        P(cols),
        P(cols),
        P(cols),
        P(cols),
        P(cols, None),
    )
    return jax.shard_map(
        make_body(ring, chips),
        mesh=grid,
        in_specs=placed,
        out_specs=(
            P(atoms, None),
            P(atoms, None),
            P(None, cols),
            P(None, cols),
            P(cols),
            P(None, cols),
            P(None, cols),
            P(None, cols),
            P(None, cols),
            P(cols),
            P(cols),
            P(cols),
            P(cols),
            P(cols, None),
        ),
        check_vma=False,
    )
```

```python
from functools import partial
import math

import jax
import jax.numpy as jnp
from jax import lax
from jax.sharding import Mesh, PartitionSpec as P
import numpy as np

ATOM_TYPES = 64


epsilon = 1e-05
masked_score = -1000000000.0
time_scale = 1000.0
root_two_pi = math.sqrt(2.0 * math.pi)
highest = lax.Precision.HIGHEST


def time_embedding(times, model_width):
    half_width = model_width // 2
    counter = jnp.arange(half_width, dtype=jnp.float32)
    frequency = jnp.exp(counter * (-math.log(10000.0) / half_width))
    angles = (time_scale * times)[:, None] * frequency[None, :]
    return jnp.concatenate([jnp.sin(angles), jnp.cos(angles)], axis=1)


def layer_norm(values, gain_row, shift_row):
    center = values - jnp.mean(values, axis=1, keepdims=True)
    inv_std = lax.rsqrt(jnp.mean(center * center, axis=1, keepdims=True) + epsilon)
    normed = center * inv_std
    return (normed * gain_row + shift_row, normed, inv_std)


def norm_backward(grad_out, normed, inv_std, gain_row):
    grad_normed = grad_out * gain_row
    first_mean = jnp.mean(grad_normed, axis=1, keepdims=True)
    second_mean = jnp.mean(grad_normed * normed, axis=1, keepdims=True)
    grad_input = inv_std * (grad_normed - first_mean - normed * second_mean)
    return (grad_input, jnp.sum(grad_out * normed, axis=0), jnp.sum(grad_out, axis=0))


def gelu_value(values):
    return values * (0.5 + 0.5 * lax.erf(values * math.sqrt(0.5)))


def gelu_slope(values):
    return (
        0.5
        + 0.5 * lax.erf(values * math.sqrt(0.5))
        + values * jnp.exp(-0.5 * values * values) / root_two_pi
    )


def pair_terms(pos_rows, pos_cols, type_rows, type_cols, tables):
    kernel_means, kernel_widths, scale_table, shift_table = tables
    offsets = pos_rows[:, :, None] - pos_cols[:, None, :]
    distance = jnp.sqrt(jnp.sum(offsets * offsets, axis=0))
    type_range = jnp.arange(ATOM_TYPES, dtype=jnp.int32)
    hot_rows = (type_rows[:, None] == type_range[None, :]).astype(jnp.float32)
    hot_cols = (type_cols[:, None] == type_range[None, :]).astype(jnp.float32)
    scale_pair = jnp.dot(
        jnp.dot(hot_rows, scale_table, precision=highest), hot_cols.T, precision=highest
    )
    shift_pair = jnp.dot(
        jnp.dot(hot_rows, shift_table, precision=highest), hot_cols.T, precision=highest
    )
    stretched = scale_pair * distance + shift_pair
    kernel_gap = (stretched[:, :, None] - kernel_means) / kernel_widths
    kernels = jnp.exp(-0.5 * kernel_gap * kernel_gap) / (root_two_pi * kernel_widths)
    return (distance, hot_rows, hot_cols, kernel_gap, kernels)


def allowed_pairs(row_ids, col_ids, mol_rows, mol_cols, pad_cols):
    same_mol = mol_rows[:, None] == mol_cols[None, :]
    key_live = (pad_cols[None, :] == 1) | (row_ids[:, None] == col_ids[None, :])
    return same_mol & key_live


def tile_scores(q_tile, key_block, kernels_low, kernel_heads, allowed, score_scale):
    pair_bias = jnp.einsum(
        "ijk,kh->hij", kernels_low, kernel_heads, preferred_element_type=jnp.float32
    )
    raw_scores = jnp.einsum("ihd,jhd->hij", q_tile, key_block, preferred_element_type=jnp.float32)
    return jnp.where(allowed[None], raw_scores * score_scale + pair_bias, masked_score)


def block_forward(pieces, tables, kernel_heads, tile_rows):
    queries, key_block, value_block, positions, types, mols, pads = pieces
    block_rows = queries.shape[0]
    score_scale = 1.0 / math.sqrt(queries.shape[2])
    col_ids = jnp.arange(block_rows, dtype=jnp.int32)

    def one_tile(running, tile_index):
        first_row = tile_index * tile_rows
        row_ids = first_row + jnp.arange(tile_rows, dtype=jnp.int32)
        terms = pair_terms(positions, positions, types, types, tables)
        kernels_low = terms[4].astype(jnp.bfloat16)
        allowed = allowed_pairs(row_ids, col_ids, mols, mols, pads)
        scores = tile_scores(queries, key_block, kernels_low, kernel_heads, allowed, score_scale)
        row_max = jnp.max(scores, axis=2, keepdims=True)
        exponent = jnp.exp(scores - row_max)
        row_sum = jnp.sum(exponent, axis=2, keepdims=True)
        probs_low = (exponent / row_sum).astype(jnp.bfloat16)
        attended = jnp.einsum(
            "hij,jhd->ihd", probs_low, value_block, preferred_element_type=jnp.float32
        )
        return (running, (attended, (row_max + jnp.log(row_sum))[:, :, 0]))

    count = block_rows // tile_rows
    if count == 1:
        _, (attended, log_sums) = one_tile(None, 0)
        return (attended.reshape(block_rows, -1), log_sums)
    _, (attended, log_sums) = lax.scan(one_tile, None, jnp.arange(count, dtype=jnp.int32))
    attended = attended.reshape(block_rows, -1)
    log_sums = jnp.transpose(log_sums, (1, 0, 2)).reshape(log_sums.shape[1], block_rows)
    return (attended, log_sums)


def block_backward(running, pieces, tables, kernel_heads, tile_rows, hook=None):
    queries, key_block, value_block, grad_attended, log_sums, positions, types, mols, pads = pieces
    kernel_widths = tables[1]
    block_rows = queries.shape[0]
    score_scale = 1.0 / math.sqrt(queries.shape[2])
    col_ids = jnp.arange(block_rows, dtype=jnp.int32)

    def one_tile(partial_sums, tile_index):
        keys_grad, values_grad, heads_grad, means_grad, widths_grad, scale_grad, shift_grad = (
            partial_sums
        )
        first_row = tile_index * tile_rows
        row_ids = first_row + jnp.arange(tile_rows, dtype=jnp.int32)
        distance, hot_rows, hot_cols, kernel_gap, kernels = pair_terms(
            positions, positions, types, types, tables
        )
        kernels_low = kernels.astype(jnp.bfloat16)
        allowed = allowed_pairs(row_ids, col_ids, mols, mols, pads)
        scores = tile_scores(queries, key_block, kernels_low, kernel_heads, allowed, score_scale)
        attn_probs = jnp.exp(scores - log_sums[:, :, None])
        grad_probs = jnp.einsum(
            "ihd,jhd->hij", grad_attended, value_block, preferred_element_type=jnp.float32
        )
        values_grad = values_grad + jnp.einsum(
            "hij,ihd->jhd",
            attn_probs.astype(jnp.bfloat16),
            grad_attended,
            preferred_element_type=jnp.float32,
        )
        probs_dot = jnp.sum(attn_probs * grad_probs, axis=2, keepdims=True)
        grad_scores = (attn_probs * (grad_probs - probs_dot)).astype(jnp.bfloat16)
        if hook is not None:
            grad_scores = hook(grad_scores)
        query_grad = (
            jnp.einsum("hij,jhd->ihd", grad_scores, key_block, preferred_element_type=jnp.float32)
            * score_scale
        )
        keys_grad = (
            keys_grad
            + jnp.einsum("hij,ihd->jhd", grad_scores, queries, preferred_element_type=jnp.float32)
            * score_scale
        )
        heads_grad = heads_grad + jnp.einsum(
            "ijk,hij->kh", kernels_low, grad_scores, preferred_element_type=jnp.float32
        )
        grad_kernels = jnp.einsum(
            "hij,kh->ijk", grad_scores, kernel_heads, preferred_element_type=jnp.float32
        )
        spread = grad_kernels * kernels
        mean_part = spread * kernel_gap / kernel_widths
        means_grad = means_grad + jnp.sum(mean_part, axis=(0, 1))
        widths_grad = widths_grad + jnp.sum(
            spread * (kernel_gap * kernel_gap - 1.0) / kernel_widths, axis=(0, 1)
        )
        grad_stretched = -jnp.sum(mean_part, axis=2)
        scale_grad = scale_grad + jnp.dot(
            jnp.dot(hot_rows.T, grad_stretched * distance, precision=highest),
            hot_cols,
            precision=highest,
        )
        shift_grad = shift_grad + jnp.dot(
            jnp.dot(hot_rows.T, grad_stretched, precision=highest), hot_cols, precision=highest
        )
        return (
            (keys_grad, values_grad, heads_grad, means_grad, widths_grad, scale_grad, shift_grad),
            query_grad,
        )

    zero_block = jnp.zeros(key_block.shape, jnp.float32)
    count = block_rows // tile_rows
    if count == 1:
        sums_out, query_grads = one_tile((zero_block, zero_block) + tuple(running), 0)
        return (sums_out[2:], (query_grads.reshape(key_block.shape), sums_out[0], sums_out[1]))
    sums_out, query_grads = lax.scan(
        one_tile, (zero_block, zero_block) + tuple(running), jnp.arange(count, dtype=jnp.int32)
    )
    query_grads = query_grads.reshape(key_block.shape)
    return (sums_out[2:], (query_grads, sums_out[0], sums_out[1]))


def snake_ring(chips_x, chips_other):
    if chips_x == 2 and chips_other >= 2:
        return [2 * z for z in range(chips_other)] + [
            2 * z + 1 for z in reversed(range(chips_other))
        ]
    return list(range(chips_x * chips_other))


class Ring:
    def __init__(self, order):
        self.order = order
        self.n = len(order)
        pos = np.zeros(self.n, np.int32)
        for i, c in enumerate(order):
            pos[c] = i
        self.pos = pos
        self.cw = [(order[i], order[(i + 1) % self.n]) for i in range(self.n)]
        self.ccw = [(order[i], order[(i - 1) % self.n]) for i in range(self.n)]

    def here(self):
        chip = lax.axis_index("chip")
        core = lax.axis_index("core")
        return chip, core, jnp.asarray(self.pos)[chip]

    def chip_at(self, position):
        return jnp.asarray(np.array(self.order, np.int32))[position % self.n]


SWAP = [(0, 1), (1, 0)]


def _halves(x, axis):
    size = x.shape[axis] // 2
    return (
        lax.slice_in_dim(x, 0, size, axis=axis),
        lax.slice_in_dim(x, size, 2 * size, axis=axis),
    )


def ring_gather(ring, pieces, chips):
    if ring is None:
        return [
            lax.all_gather(x, ("chip", "core"), axis=0, tiled=False).reshape((chips, 2) + x.shape)
            for x, _ in pieces
        ]
    chip, core, p = ring.here()
    n = ring.n
    bufs, fronts = [], []
    for x, axis in pieces:
        buf = jnp.zeros((n, 2) + x.shape, x.dtype)
        buf = lax.dynamic_update_slice(buf, x[None, None], (chip, core) + (0,) * x.ndim)
        bufs.append(buf)
        if axis is None:
            fronts.append([x, None])
        else:
            fronts.append(list(_halves(x, axis)))
    partner = lax.ppermute([x for x, _ in pieces], "core", SWAP)
    for i, x in enumerate(partner):
        bufs[i] = lax.dynamic_update_slice(
            bufs[i], x[None, None], (chip, 1 - core) + (0,) * x.ndim
        )
    for step in range(1, n):
        going = [f[0] for f in fronts]
        coming = [f[1] for f in fronts if f[1] is not None]
        going = lax.ppermute(going, "chip", ring.cw)
        coming = lax.ppermute(coming, "chip", ring.ccw) if coming else []
        from_cw = ring.chip_at(p - step)
        from_ccw = ring.chip_at(p + step)
        both = lax.ppermute([going, coming], "core", SWAP)
        j = 0
        for i, (x, axis) in enumerate(pieces):
            fronts[i][0] = going[i]
            parts = [(going[i], both[0][i], from_cw, 0)]
            if axis is not None:
                fronts[i][1] = coming[j]
                parts.append((coming[j], both[1][j], from_ccw, x.shape[axis] // 2))
                j += 1
            for mine, theirs, source, offset in parts:
                start = [0] * x.ndim
                if axis is not None:
                    start[axis] = offset
                bufs[i] = lax.dynamic_update_slice(
                    bufs[i], mine[None, None], (source, core) + tuple(start)
                )
                bufs[i] = lax.dynamic_update_slice(
                    bufs[i], theirs[None, None], (source, 1 - core) + tuple(start)
                )
    return bufs


def ring_reduce_steps(ring, pieces, send=jnp.bfloat16):
    if ring is None:
        owned = []
        for g, _ in pieces:
            flat = g.reshape((-1,) + g.shape[3:])
            part = lax.psum_scatter(flat, ("chip", "core"), scatter_dimension=0, tiled=True)
            owned.append(lax.psum(part.astype(send), "rep").astype(jnp.float32))
        yield owned
        return owned
    chip, core, p = ring.here()
    n = ring.n
    mine, theirs = [], []
    for g, _ in pieces:
        mine.append(lax.dynamic_index_in_dim(g, core, axis=1, keepdims=False))
        theirs.append(lax.dynamic_index_in_dim(g, 1 - core, axis=1, keepdims=False).astype(send))
    got = lax.ppermute(theirs, "core", SWAP)
    yield got
    flows = []
    for i, (g, way) in enumerate(pieces):
        if way == "both":
            flows.append((i, 1, n // 2, mine[i], got[i]))
            flows.append((i, -1, (n - 1) // 2, mine[i], got[i]))
        elif isinstance(way, tuple):
            axis = way[1] + 1
            for d, (m, t) in zip((1, -1), zip(_halves(mine[i], axis), _halves(got[i], axis))):
                flows.append((i, d, n - 1, m, t))
        else:
            flows.append((i, way, n - 1, mine[i], got[i]))

    def contribution(m, t, position):
        at = ring.chip_at(position)
        own = lax.dynamic_index_in_dim(m, at, axis=0, keepdims=False)
        other = lax.dynamic_index_in_dim(t, at, axis=0, keepdims=False)
        return own + other.astype(jnp.float32)

    acc = [contribution(m, t, p + d * hops) for _, d, hops, m, t in flows]
    for step in range(1, max(f[2] for f in flows) + 1):
        moved = []
        for d in (1, -1):
            chosen = [k for k, f in enumerate(flows) if f[1] == d and f[2] >= step]
            if chosen:
                out = lax.ppermute([acc[k].astype(send) for k in chosen], "chip", ring.cw if d == 1 else ring.ccw)
                for k, o in zip(chosen, out):
                    acc[k] = o.astype(jnp.float32)
                moved.extend(out)
        yield moved
        for k, (_, d, hops, m, t) in enumerate(flows):
            if hops > step:
                acc[k] = acc[k] + contribution(m, t, p + d * (hops - step))
    owned = []
    for i, (g, way) in enumerate(pieces):
        parts = [(a, f) for a, f in zip(acc, flows) if f[0] == i]
        if way == "both":
            total = contribution(parts[0][1][3], parts[0][1][4], p) + parts[0][0] + parts[1][0]
        else:
            total = [a + contribution(f[3], f[4], p) for a, f in parts]
            total = total[0] if len(total) == 1 else jnp.concatenate(total, axis=way[1])
        owned.append(total)
    other = lax.ppermute([o.astype(send) for o in owned], "rep", SWAP)
    yield other
    return [o + t.astype(jnp.float32) for o, t in zip(owned, other)]


class Stepper:
    def __init__(self, gen):
        self.gen = gen
        self.result = None
        self.over = False

    def tie(self, value):
        if self.over:
            return value
        try:
            ready = next(self.gen)
        except StopIteration as done:
            self.result, self.over = done.value, True
            return value
        _, value = lax.optimization_barrier((ready, value))
        return value

    def finish(self):
        if not self.over:
            self.result, self.over = run_steps(self.gen), True
        return self.result


def run_steps(gen):
    while True:
        try:
            next(gen)
        except StopIteration as done:
            return done.value


SMALL_ROWS, SMALL_LANES = 16, 768


def small_layout(fsdp):
    d = 768 // fsdp
    sizes = [2 * d, 6 * d, 3072 // fsdp, 128 // fsdp, 128 // fsdp, 4096 // fsdp, 4096 // fsdp, (128 // fsdp) * 32]
    offsets, at = [], 0
    for size in sizes:
        offsets.append((at, size))
        at += size
    assert at <= SMALL_ROWS * SMALL_LANES
    return offsets


def pack_small(parts):
    flat = jnp.concatenate([part.reshape(-1) for part in parts])
    flat = jnp.pad(flat, (0, SMALL_ROWS * SMALL_LANES - flat.shape[0]))
    return flat.reshape(SMALL_ROWS, SMALL_LANES)


def unpack_small_full(gathered, offsets, fsdp):
    flat = gathered.reshape(fsdp, -1).astype(jnp.float32)
    take = [flat[:, at : at + size] for at, size in offsets]
    d = 768 // fsdp
    return [
        take[0].reshape(fsdp, 2, d).transpose(1, 0, 2).reshape(2, -1),
        take[1].reshape(fsdp, 6, d).transpose(1, 0, 2).reshape(6, -1),
        take[2].reshape(-1),
        take[3].reshape(-1),
        take[4].reshape(-1),
        take[5].reshape(ATOM_TYPES, ATOM_TYPES),
        take[6].reshape(ATOM_TYPES, ATOM_TYPES),
        take[7].reshape(-1, 32),
    ]


def pack_small_grads(grads, fsdp, chips):
    d = 768 // fsdp
    blocks = [
        grads[0].reshape(2, fsdp, d).transpose(1, 0, 2),
        grads[1].reshape(6, fsdp, d).transpose(1, 0, 2),
    ] + [g.reshape(-1) for g in grads[2:]]
    flat = jnp.concatenate([blk.reshape(fsdp, -1) for blk in blocks], axis=1)
    flat = jnp.pad(flat, ((0, 0), (0, SMALL_ROWS * SMALL_LANES - flat.shape[1])))
    return flat.reshape(chips, 2, SMALL_ROWS, SMALL_LANES)


def unpack_small_owned(block, offsets):
    flat = block.reshape(-1)
    take = [flat[at : at + size] for at, size in offsets]
    return [
        take[0].reshape(2, -1),
        take[1].reshape(6, -1),
        take[2],
        take[3],
        take[4],
        take[5],
        take[6],
        take[7].reshape(-1, 32),
    ]


def make_body(ring, chips):
    fsdp = 2 * chips

    def body(
        inputs,
        times,
        positions,
        atom_types,
        molecule_ids,
        pad_mask,
        cotangent,
        norm_gains,
        bias_rows,
        up_bias,
        input_weight,
        output_weight,
        up_weight,
        down_weight,
        kernel_means,
        kernel_widths,
        pair_scale,
        pair_shift,
        kernel_heads,
    ):
        offsets = small_layout(fsdp)
        small = pack_small(
            [norm_gains, bias_rows, up_bias, kernel_means, kernel_widths, pair_scale, pair_shift, kernel_heads]
        )
        width = input_weight.shape[0]
        first = jnp.concatenate([small.reshape(-1, width), input_weight.T], axis=0)
        second = jnp.concatenate(
            [output_weight.T, up_weight.T, down_weight.T.reshape(-1, width)], axis=0
        )
        first_all = lax.all_gather(first, ("chip", "core"), axis=0, tiled=False)
        second_all = lax.all_gather(second, ("chip", "core"), axis=0, tiled=False)
        small_rows = small.size // width
        params = unpack_small_full(first_all[:, :small_rows], offsets, fsdp)
        in_t = first_all[:, small_rows:].reshape(-1, width)
        out_rows = output_weight.shape[1]
        up_rows = up_weight.shape[1]
        out_t = second_all[:, :out_rows].reshape(-1, width)
        up_t = second_all[:, out_rows : out_rows + up_rows].reshape(-1, width)
        down_t = (
            second_all[:, out_rows + up_rows :]
            .reshape(fsdp, down_weight.shape[1], -1)
            .reshape(-1, down_weight.shape[0])
        )
        gains_now, biases_now, up_shift = params[0], params[1], params[2]
        tables = (params[3], params[4], params[5], params[6])
        heads_full = params[7].astype(jnp.bfloat16)

        row_count = inputs.shape[0]
        model_width = inputs.shape[1]
        head_count = heads_full.shape[1]
        head_size = model_width // head_count
        block_rows = min(128, row_count)
        blocks = row_count // block_rows
        tile_rows = min(128, block_rows)
        nt = (((1,), (1,)), ((), ()))
        tn = (((0,), (0,)), ((), ()))

        stream = inputs.astype(jnp.float32) + time_embedding(times, model_width)
        normed_out, normed_one, inv_one = layer_norm(stream, gains_now[0], biases_now[0])
        act_one = normed_out.astype(jnp.bfloat16)
        qkv_shift = jnp.concatenate([biases_now[2], jnp.zeros_like(biases_now[2]), biases_now[3]])
        projected = (
            lax.dot_general(act_one, in_t, nt, preferred_element_type=jnp.float32) + qkv_shift
        ).astype(jnp.bfloat16)
        split_shape = (blocks, block_rows, head_count, head_size)
        queries = projected[:, :model_width].reshape(split_shape)
        key_rows = projected[:, model_width : 2 * model_width].reshape(split_shape)
        value_rows = projected[:, 2 * model_width :].reshape(split_shape)
        pos_blocks = jnp.transpose(positions.reshape(3, blocks, block_rows), (1, 0, 2))
        type_blocks = atom_types.reshape(blocks, block_rows)
        mol_blocks = molecule_ids.reshape(blocks, block_rows)
        pad_blocks = pad_mask.reshape(blocks, block_rows)
        fwd = [
            block_forward(
                (queries[b], key_rows[b], value_rows[b], pos_blocks[b], type_blocks[b], mol_blocks[b], pad_blocks[b]),
                tables=tables,
                kernel_heads=heads_full,
                tile_rows=tile_rows,
            )
            for b in range(blocks)
        ]
        attended = jnp.stack([f[0] for f in fwd])
        log_sums = [f[1] for f in fwd]
        attended_low = attended.reshape(row_count, model_width).astype(jnp.bfloat16)
        mid = stream + (
            lax.dot_general(attended_low, out_t, nt, preferred_element_type=jnp.float32)
            + biases_now[4]
        )
        normed_out_two, normed_two, inv_two = layer_norm(mid, gains_now[1], biases_now[1])
        act_two = normed_out_two.astype(jnp.bfloat16)
        hidden_pre = (
            lax.dot_general(act_two, up_t, nt, preferred_element_type=jnp.float32) + up_shift
        )
        hidden_low = gelu_value(hidden_pre).astype(jnp.bfloat16)
        final = mid + (
            lax.dot_general(hidden_low, down_t, nt, preferred_element_type=jnp.float32)
            + biases_now[5]
        )
        rows_out = final.astype(jnp.bfloat16)

        grad_final = cotangent.astype(jnp.float32)
        down_grad_t = lax.dot_general(cotangent, hidden_low, tn, preferred_element_type=jnp.float32)
        grad_hidden = jnp.dot(cotangent, down_t, preferred_element_type=jnp.float32) * gelu_slope(
            hidden_pre
        )
        grad_hidden_low = grad_hidden.astype(jnp.bfloat16)
        up_grad_t = lax.dot_general(grad_hidden_low, act_two, tn, preferred_element_type=jnp.float32)
        up_bias_grad = jnp.sum(grad_hidden_low.astype(jnp.float32), axis=0)
        grad_act_two = jnp.dot(grad_hidden_low, up_t, preferred_element_type=jnp.float32)
        grad_norm_two, gain_two_grad, shift_two_grad = norm_backward(
            grad_act_two, normed_two, inv_two, gains_now[1]
        )
        grad_mid = grad_final + grad_norm_two
        grad_branch_low = grad_mid.astype(jnp.bfloat16)
        out_grad_t = lax.dot_general(
            grad_branch_low, attended_low, tn, preferred_element_type=jnp.float32
        )
        late_rows = jnp.concatenate(
            [
                out_grad_t.reshape(chips, 2, -1, model_width),
                up_grad_t.reshape(chips, 2, -1, model_width),
            ],
            axis=2,
        )
        late = ring_reduce_steps(
            ring, [(late_rows, "both"), (down_grad_t.reshape((chips, 2, -1) + down_grad_t.shape[1:]), "both")]
        )
        grad_attended = jnp.dot(grad_branch_low, out_t, preferred_element_type=jnp.float32).astype(
            jnp.bfloat16
        )
        kernel_count = tables[0].shape[0]
        start_sums = (
            jnp.zeros((kernel_count, head_count), jnp.float32),
            jnp.zeros((kernel_count,), jnp.float32),
            jnp.zeros((kernel_count,), jnp.float32),
            jnp.zeros((ATOM_TYPES, ATOM_TYPES), jnp.float32),
            jnp.zeros((ATOM_TYPES, ATOM_TYPES), jnp.float32),
        )
        kernel_sums = start_sums
        q_grads, k_grads, v_grads = [], [], []
        grad_attended_blocks = grad_attended.reshape(split_shape)
        stepper = Stepper(late)
        for b in range(blocks):
            gate = stepper.tie(grad_attended_blocks[b])
            kernel_sums, (qg, kg, vg) = block_backward(
                kernel_sums,
                (
                    queries[b],
                    key_rows[b],
                    value_rows[b],
                    gate,
                    log_sums[b],
                    pos_blocks[b],
                    type_blocks[b],
                    mol_blocks[b],
                    pad_blocks[b],
                ),
                tables=tables,
                kernel_heads=heads_full,
                tile_rows=tile_rows,
                hook=stepper.tie,
            )
            q_grads.append(qg)
            k_grads.append(kg)
            v_grads.append(vg)
        queries_grad = jnp.stack(q_grads)
        keys_grad = jnp.stack(k_grads)
        values_grad = jnp.stack(v_grads)
        grad_projected = jnp.concatenate(
            [
                queries_grad.reshape(row_count, model_width),
                keys_grad.reshape(row_count, model_width),
                values_grad.reshape(row_count, model_width),
            ],
            axis=1,
        ).astype(jnp.bfloat16)
        in_grad_t = lax.dot_general(grad_projected, act_one, tn, preferred_element_type=jnp.float32)
        grad_act_one = jnp.dot(grad_projected, in_t, preferred_element_type=jnp.float32)
        grad_norm_one, gain_one_grad, shift_one_grad = norm_backward(
            grad_act_one, normed_one, inv_one, gains_now[0]
        )
        inputs_grad = grad_mid + grad_norm_one
        projected_sums = jnp.sum(grad_projected.astype(jnp.float32), axis=0)
        heads_grad, means_grad, widths_grad, scale_grad, shift_grad = kernel_sums
        small_grads = [
            jnp.stack([gain_one_grad, gain_two_grad]),
            jnp.stack(
                [
                    shift_one_grad,
                    shift_two_grad,
                    projected_sums[:model_width],
                    projected_sums[2 * model_width :],
                    jnp.sum(grad_branch_low.astype(jnp.float32), axis=0),
                    jnp.sum(grad_final, axis=0),
                ]
            ),
            up_bias_grad,
            means_grad,
            widths_grad,
            scale_grad,
            shift_grad,
            heads_grad,
        ]
        late_owned = stepper.finish()
        out_owned = late_owned[0][:out_rows]
        up_owned = late_owned[0][out_rows:]
        down_owned = late_owned[1]
        last = jnp.concatenate(
            [
                in_grad_t.reshape((chips, 2, -1) + in_grad_t.shape[1:]),
                pack_small_grads(small_grads, fsdp, chips),
            ],
            axis=2,
        )
        (last_owned,) = run_steps(ring_reduce_steps(ring, [(last, "both")]))
        in_rows = in_grad_t.shape[0] // fsdp
        in_owned = last_owned[:in_rows]
        small_owned = last_owned[in_rows:]
        sg = unpack_small_owned(small_owned, offsets)
        return (
            rows_out,
            inputs_grad,
            sg[0],
            sg[1],
            sg[2],
            in_owned.T,
            out_owned.T,
            up_owned.T,
            down_owned.T,
            sg[3],
            sg[4],
            sg[5],
            sg[6],
            sg[7],
        )

    return body


def solution(mesh):
    reps, fsdp = mesh.devices.shape
    chips = fsdp // 2
    grid = Mesh(mesh.devices.reshape(reps, chips, 2), ("rep", "chip", "core"))
    chips_x = 1
    try:
        coords = [tuple(d.coords) for d in mesh.devices[0, ::2]]
        xs = sorted({c[0] for c in coords})
        chips_x = len(xs)
        flat_ok = all(
            coords[i][0] == xs[i % chips_x] for i in range(chips)
        )
        if not flat_ok:
            chips_x = 1
    except Exception:
        chips_x = 1
    ring = None
    if chips <= 8:
        ring = Ring(snake_ring(chips_x, chips // chips_x))
    atoms = ("rep", "chip", "core")
    cols = ("chip", "core")
    placed = (
        P(atoms, None),
        P(atoms),
        P(None, atoms),
        P(atoms),
        P(atoms),
        P(atoms),
        P(atoms, None),
        P(None, cols),
        P(None, cols),
        P(cols),
        P(None, cols),
        P(None, cols),
        P(None, cols),
        P(None, cols),
        P(cols),
        P(cols),
        P(cols),
        P(cols),
        P(cols, None),
    )
    return jax.shard_map(
        make_body(ring, chips),
        mesh=grid,
        in_specs=placed,
        out_specs=(
            P(atoms, None),
            P(atoms, None),
            P(None, cols),
            P(None, cols),
            P(cols),
            P(None, cols),
            P(None, cols),
            P(None, cols),
            P(None, cols),
            P(cols),
            P(cols),
            P(cols),
            P(cols),
            P(cols, None),
        ),
        check_vma=False,
    )
```

```python
from functools import partial
import math

import jax
import jax.numpy as jnp
from jax import lax
from jax.experimental import pallas as pl
from jax.experimental.pallas import tpu as pltpu
from jax.sharding import Mesh, PartitionSpec as P
import numpy as np

ATOM_TYPES = 64


epsilon = 1e-05
masked_score = -1000000000.0
time_scale = 1000.0
root_two_pi = math.sqrt(2.0 * math.pi)
highest = lax.Precision.HIGHEST


def time_embedding(times, model_width):
    half_width = model_width // 2
    counter = jnp.arange(half_width, dtype=jnp.float32)
    frequency = jnp.exp(counter * (-math.log(10000.0) / half_width))
    angles = (time_scale * times)[:, None] * frequency[None, :]
    return jnp.concatenate([jnp.sin(angles), jnp.cos(angles)], axis=1)


def layer_norm(values, gain_row, shift_row):
    center = values - jnp.mean(values, axis=1, keepdims=True)
    inv_std = lax.rsqrt(jnp.mean(center * center, axis=1, keepdims=True) + epsilon)
    normed = center * inv_std
    return (normed * gain_row + shift_row, normed, inv_std)


def norm_backward(grad_out, normed, inv_std, gain_row):
    grad_normed = grad_out * gain_row
    first_mean = jnp.mean(grad_normed, axis=1, keepdims=True)
    second_mean = jnp.mean(grad_normed * normed, axis=1, keepdims=True)
    grad_input = inv_std * (grad_normed - first_mean - normed * second_mean)
    return (grad_input, jnp.sum(grad_out * normed, axis=0), jnp.sum(grad_out, axis=0))


def gelu_value(values):
    return values * (0.5 + 0.5 * lax.erf(values * math.sqrt(0.5)))


def gelu_slope(values):
    return (
        0.5
        + 0.5 * lax.erf(values * math.sqrt(0.5))
        + values * jnp.exp(-0.5 * values * values) / root_two_pi
    )


def pair_terms(pos_rows, pos_cols, type_rows, type_cols, tables):
    kernel_means, kernel_widths, scale_table, shift_table = tables
    offsets = pos_rows[:, :, None] - pos_cols[:, None, :]
    distance = jnp.sqrt(jnp.sum(offsets * offsets, axis=0))
    type_range = jnp.arange(ATOM_TYPES, dtype=jnp.int32)
    hot_rows = (type_rows[:, None] == type_range[None, :]).astype(jnp.float32)
    hot_cols = (type_cols[:, None] == type_range[None, :]).astype(jnp.float32)
    scale_pair = jnp.dot(
        jnp.dot(hot_rows, scale_table, precision=highest), hot_cols.T, precision=highest
    )
    shift_pair = jnp.dot(
        jnp.dot(hot_rows, shift_table, precision=highest), hot_cols.T, precision=highest
    )
    stretched = scale_pair * distance + shift_pair
    kernel_gap = (stretched[:, :, None] - kernel_means) / kernel_widths
    kernels = jnp.exp(-0.5 * kernel_gap * kernel_gap) / (root_two_pi * kernel_widths)
    return (distance, hot_rows, hot_cols, kernel_gap, kernels)


def allowed_pairs(row_ids, col_ids, mol_rows, mol_cols, pad_cols):
    same_mol = mol_rows[:, None] == mol_cols[None, :]
    key_live = (pad_cols[None, :] == 1) | (row_ids[:, None] == col_ids[None, :])
    return same_mol & key_live


def tile_scores(q_tile, key_block, kernels_low, kernel_heads, allowed, score_scale):
    pair_bias = jnp.einsum(
        "ijk,kh->hij", kernels_low, kernel_heads, preferred_element_type=jnp.float32
    )
    raw_scores = jnp.einsum("ihd,jhd->hij", q_tile, key_block, preferred_element_type=jnp.float32)
    return jnp.where(allowed[None], raw_scores * score_scale + pair_bias, masked_score)


def block_forward(pieces, tables, kernel_heads, tile_rows):
    queries, key_block, value_block, positions, types, mols, pads = pieces
    block_rows = queries.shape[0]
    score_scale = 1.0 / math.sqrt(queries.shape[2])
    col_ids = jnp.arange(block_rows, dtype=jnp.int32)

    def one_tile(running, tile_index):
        first_row = tile_index * tile_rows
        row_ids = first_row + jnp.arange(tile_rows, dtype=jnp.int32)
        terms = pair_terms(positions, positions, types, types, tables)
        kernels_low = terms[4].astype(jnp.bfloat16)
        allowed = allowed_pairs(row_ids, col_ids, mols, mols, pads)
        scores = tile_scores(queries, key_block, kernels_low, kernel_heads, allowed, score_scale)
        row_max = jnp.max(scores, axis=2, keepdims=True)
        exponent = jnp.exp(scores - row_max)
        row_sum = jnp.sum(exponent, axis=2, keepdims=True)
        probs_low = (exponent / row_sum).astype(jnp.bfloat16)
        attended = jnp.einsum(
            "hij,jhd->ihd", probs_low, value_block, preferred_element_type=jnp.float32
        )
        return (running, (attended, (row_max + jnp.log(row_sum))[:, :, 0]))

    count = block_rows // tile_rows
    if count == 1:
        _, (attended, log_sums) = one_tile(None, 0)
        return (attended.reshape(block_rows, -1), log_sums)
    _, (attended, log_sums) = lax.scan(one_tile, None, jnp.arange(count, dtype=jnp.int32))
    attended = attended.reshape(block_rows, -1)
    log_sums = jnp.transpose(log_sums, (1, 0, 2)).reshape(log_sums.shape[1], block_rows)
    return (attended, log_sums)


def block_backward(running, pieces, tables, kernel_heads, tile_rows, hook=None):
    queries, key_block, value_block, grad_attended, log_sums, positions, types, mols, pads = pieces
    kernel_widths = tables[1]
    block_rows = queries.shape[0]
    score_scale = 1.0 / math.sqrt(queries.shape[2])
    col_ids = jnp.arange(block_rows, dtype=jnp.int32)

    def one_tile(partial_sums, tile_index):
        keys_grad, values_grad, heads_grad, means_grad, widths_grad, scale_grad, shift_grad = (
            partial_sums
        )
        first_row = tile_index * tile_rows
        row_ids = first_row + jnp.arange(tile_rows, dtype=jnp.int32)
        distance, hot_rows, hot_cols, kernel_gap, kernels = pair_terms(
            positions, positions, types, types, tables
        )
        kernels_low = kernels.astype(jnp.bfloat16)
        allowed = allowed_pairs(row_ids, col_ids, mols, mols, pads)
        scores = tile_scores(queries, key_block, kernels_low, kernel_heads, allowed, score_scale)
        attn_probs = jnp.exp(scores - log_sums[:, :, None])
        grad_probs = jnp.einsum(
            "ihd,jhd->hij", grad_attended, value_block, preferred_element_type=jnp.float32
        )
        values_grad = values_grad + jnp.einsum(
            "hij,ihd->jhd",
            attn_probs.astype(jnp.bfloat16),
            grad_attended,
            preferred_element_type=jnp.float32,
        )
        probs_dot = jnp.sum(attn_probs * grad_probs, axis=2, keepdims=True)
        grad_scores = (attn_probs * (grad_probs - probs_dot)).astype(jnp.bfloat16)
        if hook is not None:
            grad_scores = hook(grad_scores)
        query_grad = (
            jnp.einsum("hij,jhd->ihd", grad_scores, key_block, preferred_element_type=jnp.float32)
            * score_scale
        )
        keys_grad = (
            keys_grad
            + jnp.einsum("hij,ihd->jhd", grad_scores, queries, preferred_element_type=jnp.float32)
            * score_scale
        )
        heads_grad = heads_grad + jnp.einsum(
            "ijk,hij->kh", kernels_low, grad_scores, preferred_element_type=jnp.float32
        )
        grad_kernels = jnp.einsum(
            "hij,kh->ijk", grad_scores, kernel_heads, preferred_element_type=jnp.float32
        )
        spread = grad_kernels * kernels
        mean_part = spread * kernel_gap / kernel_widths
        means_grad = means_grad + jnp.sum(mean_part, axis=(0, 1))
        widths_grad = widths_grad + jnp.sum(
            spread * (kernel_gap * kernel_gap - 1.0) / kernel_widths, axis=(0, 1)
        )
        grad_stretched = -jnp.sum(mean_part, axis=2)
        scale_grad = scale_grad + jnp.dot(
            jnp.dot(hot_rows.T, grad_stretched * distance, precision=highest),
            hot_cols,
            precision=highest,
        )
        shift_grad = shift_grad + jnp.dot(
            jnp.dot(hot_rows.T, grad_stretched, precision=highest), hot_cols, precision=highest
        )
        return (
            (keys_grad, values_grad, heads_grad, means_grad, widths_grad, scale_grad, shift_grad),
            query_grad,
        )

    zero_block = jnp.zeros(key_block.shape, jnp.float32)
    count = block_rows // tile_rows
    if count == 1:
        sums_out, query_grads = one_tile((zero_block, zero_block) + tuple(running), 0)
        return (sums_out[2:], (query_grads.reshape(key_block.shape), sums_out[0], sums_out[1]))
    sums_out, query_grads = lax.scan(
        one_tile, (zero_block, zero_block) + tuple(running), jnp.arange(count, dtype=jnp.int32)
    )
    query_grads = query_grads.reshape(key_block.shape)
    return (sums_out[2:], (query_grads, sums_out[0], sums_out[1]))


def _bias_kernel(s_ref, ht_ref, m_ref, iw_ref, c_ref, out_ref):
    rows = s_ref.shape[0]

    def body(i, carry):
        s = s_ref[pl.ds(i, 1), :]
        gap = (s - m_ref[...]) * iw_ref[...]
        kv = jnp.exp(-0.5 * gap * gap) * c_ref[...]
        out_ref[i] = jnp.dot(ht_ref[...], kv.astype(jnp.bfloat16), preferred_element_type=jnp.float32)
        return carry

    lax.fori_loop(0, rows, body, 0)


def pair_bias_call(stretched, heads_t, means_col, inv_col, coef_col):
    rows, cols = stretched.shape
    heads = heads_t.shape[0]
    kernels = heads_t.shape[1]
    vmem = pl.BlockSpec(memory_space=pltpu.VMEM)
    return pl.pallas_call(
        _bias_kernel,
        out_shape=jax.ShapeDtypeStruct((rows, heads, cols), jnp.float32),
        in_specs=[vmem] * 5,
        out_specs=vmem,
        cost_estimate=pl.CostEstimate(
            flops=2 * rows * cols * kernels * heads + 8 * rows * cols * kernels,
            transcendentals=rows * cols * kernels,
            bytes_accessed=rows * cols * 4 + rows * heads * cols * 4,
        ),
    )(stretched, heads_t, means_col, inv_col, coef_col)


def _grad_kernel(s_ref, g_ref, h_ref, m_ref, iw_ref, c_ref, gs_ref, ma_ref, wa_ref, hg_ref):
    rows = s_ref.shape[0]
    ma_ref[...] = jnp.zeros_like(ma_ref)
    wa_ref[...] = jnp.zeros_like(wa_ref)
    hg_ref[...] = jnp.zeros_like(hg_ref)

    def body(i, carry):
        s = s_ref[pl.ds(i, 1), :]
        iw = iw_ref[...]
        gap = (s - m_ref[...]) * iw
        g2 = gap * gap
        kv = jnp.exp(-0.5 * g2) * c_ref[...]
        gi = g_ref[i]
        gk = jnp.dot(h_ref[...], gi, preferred_element_type=jnp.float32)
        spread = gk * kv
        mp = spread * gap * iw
        ma_ref[...] += mp
        wa_ref[...] += spread * (g2 - 1.0) * iw
        gs_ref[pl.ds(i, 1), :] = -jnp.sum(mp, axis=0, keepdims=True)
        hg_ref[...] += lax.dot_general(
            kv.astype(jnp.bfloat16), gi, (((1,), (1,)), ((), ())), preferred_element_type=jnp.float32
        )
        return carry

    lax.fori_loop(0, rows, body, 0)


def kernel_grads_call(stretched, grad_scores_ihj, heads, means_col, inv_col, coef_col):
    rows, cols = stretched.shape
    kernels, nheads = heads.shape
    vmem = pl.BlockSpec(memory_space=pltpu.VMEM)
    return pl.pallas_call(
        _grad_kernel,
        out_shape=(
            jax.ShapeDtypeStruct((rows, cols), jnp.float32),
            jax.ShapeDtypeStruct((kernels, cols), jnp.float32),
            jax.ShapeDtypeStruct((kernels, cols), jnp.float32),
            jax.ShapeDtypeStruct((kernels, nheads), jnp.float32),
        ),
        in_specs=[vmem] * 6,
        out_specs=(vmem, vmem, vmem, vmem),
        cost_estimate=pl.CostEstimate(
            flops=4 * rows * cols * kernels * nheads + 16 * rows * cols * kernels,
            transcendentals=rows * cols * kernels,
            bytes_accessed=rows * cols * 8 + rows * nheads * cols * 2,
        ),
    )(stretched, grad_scores_ihj, heads, means_col, inv_col, coef_col)


def stretch_terms(positions, types, tables):
    kernel_means, kernel_widths, scale_table, shift_table = tables
    offsets = positions[:, :, None] - positions[:, None, :]
    distance = jnp.sqrt(jnp.sum(offsets * offsets, axis=0))
    type_range = jnp.arange(ATOM_TYPES, dtype=jnp.int32)
    hot = (types[:, None] == type_range[None, :]).astype(jnp.float32)
    scale_pair = jnp.dot(jnp.dot(hot, scale_table, precision=highest), hot.T, precision=highest)
    shift_pair = jnp.dot(jnp.dot(hot, shift_table, precision=highest), hot.T, precision=highest)
    return distance, hot, scale_pair * distance + shift_pair


def kernel_columns(tables):
    kernel_means, kernel_widths = tables[0], tables[1]
    return (
        kernel_means[:, None],
        (1.0 / kernel_widths)[:, None],
        (1.0 / (root_two_pi * kernel_widths))[:, None],
    )


def block_forward_fast(pieces, tables, kernel_heads):
    queries, key_block, value_block, positions, types, mols, pads = pieces
    block_rows = queries.shape[0]
    score_scale = 1.0 / math.sqrt(queries.shape[2])
    ids = jnp.arange(block_rows, dtype=jnp.int32)
    _, _, stretched = stretch_terms(positions, types, tables)
    bias = pair_bias_call(stretched, kernel_heads.T, *kernel_columns(tables))
    pair_bias = jnp.transpose(bias, (1, 0, 2))
    raw_scores = jnp.einsum("ihd,jhd->hij", queries, key_block, preferred_element_type=jnp.float32)
    allowed = allowed_pairs(ids, ids, mols, mols, pads)
    scores = jnp.where(allowed[None], raw_scores * score_scale + pair_bias, masked_score)
    row_max = jnp.max(scores, axis=2, keepdims=True)
    exponent = jnp.exp(scores - row_max)
    probs = exponent / jnp.sum(exponent, axis=2, keepdims=True)
    attended = jnp.einsum(
        "hij,jhd->ihd", probs.astype(jnp.bfloat16), value_block, preferred_element_type=jnp.float32
    )
    return attended.reshape(block_rows, -1), probs


def block_backward_fast(running, pieces, tables, kernel_heads, hook=None):
    queries, key_block, value_block, grad_attended, probs, positions, types, mols, pads = pieces
    heads_grad, means_grad, widths_grad, scale_grad, shift_grad = running
    score_scale = 1.0 / math.sqrt(queries.shape[2])
    distance, hot, stretched = stretch_terms(positions, types, tables)
    grad_probs = jnp.einsum(
        "ihd,jhd->hij", grad_attended, value_block, preferred_element_type=jnp.float32
    )
    values_grad = jnp.einsum(
        "hij,ihd->jhd", probs.astype(jnp.bfloat16), grad_attended, preferred_element_type=jnp.float32
    )
    probs_dot = jnp.sum(probs * grad_probs, axis=2, keepdims=True)
    grad_scores = (probs * (grad_probs - probs_dot)).astype(jnp.bfloat16)
    if hook is not None:
        grad_scores = hook(grad_scores)
    query_grad = (
        jnp.einsum("hij,jhd->ihd", grad_scores, key_block, preferred_element_type=jnp.float32)
        * score_scale
    )
    keys_grad = (
        jnp.einsum("hij,ihd->jhd", grad_scores, queries, preferred_element_type=jnp.float32)
        * score_scale
    )
    grad_stretched, mean_parts, width_parts, heads_part = kernel_grads_call(
        stretched, jnp.transpose(grad_scores, (1, 0, 2)), kernel_heads, *kernel_columns(tables)
    )
    running = (
        heads_grad + heads_part,
        means_grad + jnp.sum(mean_parts, axis=1),
        widths_grad + jnp.sum(width_parts, axis=1),
        scale_grad
        + jnp.dot(jnp.dot(hot.T, grad_stretched * distance, precision=highest), hot, precision=highest),
        shift_grad + jnp.dot(jnp.dot(hot.T, grad_stretched, precision=highest), hot, precision=highest),
    )
    return running, (query_grad, keys_grad, values_grad)


def snake_ring(chips_x, chips_other):
    if chips_x == 2 and chips_other >= 2:
        return [2 * z for z in range(chips_other)] + [
            2 * z + 1 for z in reversed(range(chips_other))
        ]
    return list(range(chips_x * chips_other))


class Ring:
    def __init__(self, order):
        self.order = order
        self.n = len(order)
        pos = np.zeros(self.n, np.int32)
        for i, c in enumerate(order):
            pos[c] = i
        self.pos = pos
        self.cw = [(order[i], order[(i + 1) % self.n]) for i in range(self.n)]
        self.ccw = [(order[i], order[(i - 1) % self.n]) for i in range(self.n)]

    def here(self):
        chip = lax.axis_index("chip")
        core = lax.axis_index("core")
        return chip, core, jnp.asarray(self.pos)[chip]

    def chip_at(self, position):
        return jnp.asarray(np.array(self.order, np.int32))[position % self.n]


SWAP = [(0, 1), (1, 0)]


def _halves(x, axis):
    size = x.shape[axis] // 2
    return (
        lax.slice_in_dim(x, 0, size, axis=axis),
        lax.slice_in_dim(x, size, 2 * size, axis=axis),
    )


def ring_gather(ring, pieces, chips):
    if ring is None:
        return [
            lax.all_gather(x, ("chip", "core"), axis=0, tiled=False).reshape((chips, 2) + x.shape)
            for x, _ in pieces
        ]
    chip, core, p = ring.here()
    n = ring.n
    bufs, fronts = [], []
    for x, axis in pieces:
        buf = jnp.zeros((n, 2) + x.shape, x.dtype)
        buf = lax.dynamic_update_slice(buf, x[None, None], (chip, core) + (0,) * x.ndim)
        bufs.append(buf)
        if axis is None:
            fronts.append([x, None])
        else:
            fronts.append(list(_halves(x, axis)))
    partner = lax.ppermute([x for x, _ in pieces], "core", SWAP)
    for i, x in enumerate(partner):
        bufs[i] = lax.dynamic_update_slice(
            bufs[i], x[None, None], (chip, 1 - core) + (0,) * x.ndim
        )
    for step in range(1, n):
        going = [f[0] for f in fronts]
        coming = [f[1] for f in fronts if f[1] is not None]
        going = lax.ppermute(going, "chip", ring.cw)
        coming = lax.ppermute(coming, "chip", ring.ccw) if coming else []
        from_cw = ring.chip_at(p - step)
        from_ccw = ring.chip_at(p + step)
        both = lax.ppermute([going, coming], "core", SWAP)
        j = 0
        for i, (x, axis) in enumerate(pieces):
            fronts[i][0] = going[i]
            parts = [(going[i], both[0][i], from_cw, 0)]
            if axis is not None:
                fronts[i][1] = coming[j]
                parts.append((coming[j], both[1][j], from_ccw, x.shape[axis] // 2))
                j += 1
            for mine, theirs, source, offset in parts:
                start = [0] * x.ndim
                if axis is not None:
                    start[axis] = offset
                bufs[i] = lax.dynamic_update_slice(
                    bufs[i], mine[None, None], (source, core) + tuple(start)
                )
                bufs[i] = lax.dynamic_update_slice(
                    bufs[i], theirs[None, None], (source, 1 - core) + tuple(start)
                )
    return bufs


def ring_reduce_steps(ring, pieces, send=jnp.bfloat16):
    if ring is None:
        owned = []
        for g, _ in pieces:
            flat = g.reshape((-1,) + g.shape[3:])
            part = lax.psum_scatter(flat, ("chip", "core"), scatter_dimension=0, tiled=True)
            owned.append(lax.psum(part.astype(send), "rep").astype(jnp.float32))
        yield owned
        return owned
    chip, core, p = ring.here()
    n = ring.n
    mine, theirs = [], []
    for g, _ in pieces:
        mine.append(lax.dynamic_index_in_dim(g, core, axis=1, keepdims=False))
        theirs.append(lax.dynamic_index_in_dim(g, 1 - core, axis=1, keepdims=False).astype(send))
    got = lax.ppermute(theirs, "core", SWAP)
    yield got
    flows = []
    for i, (g, way) in enumerate(pieces):
        if way == "both":
            flows.append((i, 1, n // 2, mine[i], got[i]))
            flows.append((i, -1, (n - 1) // 2, mine[i], got[i]))
        elif isinstance(way, tuple):
            axis = way[1] + 1
            for d, (m, t) in zip((1, -1), zip(_halves(mine[i], axis), _halves(got[i], axis))):
                flows.append((i, d, n - 1, m, t))
        else:
            flows.append((i, way, n - 1, mine[i], got[i]))

    def contribution(m, t, position):
        at = ring.chip_at(position)
        own = lax.dynamic_index_in_dim(m, at, axis=0, keepdims=False)
        other = lax.dynamic_index_in_dim(t, at, axis=0, keepdims=False)
        return own + other.astype(jnp.float32)

    acc = [contribution(m, t, p + d * hops) for _, d, hops, m, t in flows]
    for step in range(1, max(f[2] for f in flows) + 1):
        moved = []
        for d in (1, -1):
            chosen = [k for k, f in enumerate(flows) if f[1] == d and f[2] >= step]
            if chosen:
                out = lax.ppermute([acc[k].astype(send) for k in chosen], "chip", ring.cw if d == 1 else ring.ccw)
                for k, o in zip(chosen, out):
                    acc[k] = o.astype(jnp.float32)
                moved.extend(out)
        yield moved
        for k, (_, d, hops, m, t) in enumerate(flows):
            if hops > step:
                acc[k] = acc[k] + contribution(m, t, p + d * (hops - step))
    owned = []
    for i, (g, way) in enumerate(pieces):
        parts = [(a, f) for a, f in zip(acc, flows) if f[0] == i]
        if way == "both":
            total = contribution(parts[0][1][3], parts[0][1][4], p) + parts[0][0] + parts[1][0]
        else:
            total = [a + contribution(f[3], f[4], p) for a, f in parts]
            total = total[0] if len(total) == 1 else jnp.concatenate(total, axis=way[1])
        owned.append(total)
    other = lax.ppermute([o.astype(send) for o in owned], "rep", SWAP)
    yield other
    return [o + t.astype(jnp.float32) for o, t in zip(owned, other)]


class Stepper:
    def __init__(self, gen):
        self.gen = gen
        self.result = None
        self.over = False

    def tie(self, value):
        if self.over:
            return value
        try:
            ready = next(self.gen)
        except StopIteration as done:
            self.result, self.over = done.value, True
            return value
        _, value = lax.optimization_barrier((ready, value))
        return value

    def finish(self):
        if not self.over:
            self.result, self.over = run_steps(self.gen), True
        return self.result


def run_steps(gen):
    while True:
        try:
            next(gen)
        except StopIteration as done:
            return done.value


SMALL_ROWS, SMALL_LANES = 16, 768


def small_layout(fsdp):
    d = 768 // fsdp
    sizes = [2 * d, 6 * d, 3072 // fsdp, 128 // fsdp, 128 // fsdp, 4096 // fsdp, 4096 // fsdp, (128 // fsdp) * 32]
    offsets, at = [], 0
    for size in sizes:
        offsets.append((at, size))
        at += size
    assert at <= SMALL_ROWS * SMALL_LANES
    return offsets


def pack_small(parts):
    flat = jnp.concatenate([part.reshape(-1) for part in parts])
    flat = jnp.pad(flat, (0, SMALL_ROWS * SMALL_LANES - flat.shape[0]))
    return flat.reshape(SMALL_ROWS, SMALL_LANES)


def unpack_small_full(gathered, offsets, fsdp):
    flat = gathered.reshape(fsdp, -1).astype(jnp.float32)
    take = [flat[:, at : at + size] for at, size in offsets]
    d = 768 // fsdp
    return [
        take[0].reshape(fsdp, 2, d).transpose(1, 0, 2).reshape(2, -1),
        take[1].reshape(fsdp, 6, d).transpose(1, 0, 2).reshape(6, -1),
        take[2].reshape(-1),
        take[3].reshape(-1),
        take[4].reshape(-1),
        take[5].reshape(ATOM_TYPES, ATOM_TYPES),
        take[6].reshape(ATOM_TYPES, ATOM_TYPES),
        take[7].reshape(-1, 32),
    ]


def pack_small_grads(grads, fsdp, chips):
    d = 768 // fsdp
    blocks = [
        grads[0].reshape(2, fsdp, d).transpose(1, 0, 2),
        grads[1].reshape(6, fsdp, d).transpose(1, 0, 2),
    ] + [g.reshape(-1) for g in grads[2:]]
    flat = jnp.concatenate([blk.reshape(fsdp, -1) for blk in blocks], axis=1)
    flat = jnp.pad(flat, ((0, 0), (0, SMALL_ROWS * SMALL_LANES - flat.shape[1])))
    return flat.reshape(chips, 2, SMALL_ROWS, SMALL_LANES)


def unpack_small_owned(block, offsets):
    flat = block.reshape(-1)
    take = [flat[at : at + size] for at, size in offsets]
    return [
        take[0].reshape(2, -1),
        take[1].reshape(6, -1),
        take[2],
        take[3],
        take[4],
        take[5],
        take[6],
        take[7].reshape(-1, 32),
    ]


def make_body(ring, chips):
    fsdp = 2 * chips

    def body(
        inputs,
        times,
        positions,
        atom_types,
        molecule_ids,
        pad_mask,
        cotangent,
        norm_gains,
        bias_rows,
        up_bias,
        input_weight,
        output_weight,
        up_weight,
        down_weight,
        kernel_means,
        kernel_widths,
        pair_scale,
        pair_shift,
        kernel_heads,
    ):
        offsets = small_layout(fsdp)
        small = pack_small(
            [norm_gains, bias_rows, up_bias, kernel_means, kernel_widths, pair_scale, pair_shift, kernel_heads]
        )
        width = input_weight.shape[0]
        first = jnp.concatenate([small.reshape(-1, width), input_weight.T], axis=0)
        second = jnp.concatenate(
            [output_weight.T, up_weight.T, down_weight.T.reshape(-1, width)], axis=0
        )
        first_all = lax.all_gather(first, ("chip", "core"), axis=0, tiled=False)
        second_all = lax.all_gather(second, ("chip", "core"), axis=0, tiled=False)
        small_rows = small.size // width
        params = unpack_small_full(first_all[:, :small_rows], offsets, fsdp)
        in_t = first_all[:, small_rows:].reshape(-1, width)
        out_rows = output_weight.shape[1]
        up_rows = up_weight.shape[1]
        out_t = second_all[:, :out_rows].reshape(-1, width)
        up_t = second_all[:, out_rows : out_rows + up_rows].reshape(-1, width)
        down_t = (
            second_all[:, out_rows + up_rows :]
            .reshape(fsdp, down_weight.shape[1], -1)
            .reshape(-1, down_weight.shape[0])
        )
        gains_now, biases_now, up_shift = params[0], params[1], params[2]
        tables = (params[3], params[4], params[5], params[6])
        heads_full = params[7].astype(jnp.bfloat16)

        row_count = inputs.shape[0]
        model_width = inputs.shape[1]
        head_count = heads_full.shape[1]
        head_size = model_width // head_count
        block_rows = min(128, row_count)
        blocks = row_count // block_rows
        tile_rows = min(128, block_rows)
        nt = (((1,), (1,)), ((), ()))
        tn = (((0,), (0,)), ((), ()))

        stream = inputs.astype(jnp.float32) + time_embedding(times, model_width)
        normed_out, normed_one, inv_one = layer_norm(stream, gains_now[0], biases_now[0])
        act_one = normed_out.astype(jnp.bfloat16)
        qkv_shift = jnp.concatenate([biases_now[2], jnp.zeros_like(biases_now[2]), biases_now[3]])
        projected = (
            lax.dot_general(act_one, in_t, nt, preferred_element_type=jnp.float32) + qkv_shift
        ).astype(jnp.bfloat16)
        split_shape = (blocks, block_rows, head_count, head_size)
        queries = projected[:, :model_width].reshape(split_shape)
        key_rows = projected[:, model_width : 2 * model_width].reshape(split_shape)
        value_rows = projected[:, 2 * model_width :].reshape(split_shape)
        pos_blocks = jnp.transpose(positions.reshape(3, blocks, block_rows), (1, 0, 2))
        type_blocks = atom_types.reshape(blocks, block_rows)
        mol_blocks = molecule_ids.reshape(blocks, block_rows)
        pad_blocks = pad_mask.reshape(blocks, block_rows)
        fwd = [
            block_forward_fast(
                (queries[b], key_rows[b], value_rows[b], pos_blocks[b], type_blocks[b], mol_blocks[b], pad_blocks[b]),
                tables,
                heads_full,
            )
            for b in range(blocks)
        ]
        attended = jnp.stack([f[0] for f in fwd])
        log_sums = [f[1] for f in fwd]
        attended_low = attended.reshape(row_count, model_width).astype(jnp.bfloat16)
        mid = stream + (
            lax.dot_general(attended_low, out_t, nt, preferred_element_type=jnp.float32)
            + biases_now[4]
        )
        normed_out_two, normed_two, inv_two = layer_norm(mid, gains_now[1], biases_now[1])
        act_two = normed_out_two.astype(jnp.bfloat16)
        hidden_pre = (
            lax.dot_general(act_two, up_t, nt, preferred_element_type=jnp.float32) + up_shift
        )
        hidden_low = gelu_value(hidden_pre).astype(jnp.bfloat16)
        final = mid + (
            lax.dot_general(hidden_low, down_t, nt, preferred_element_type=jnp.float32)
            + biases_now[5]
        )
        rows_out = final.astype(jnp.bfloat16)

        grad_final = cotangent.astype(jnp.float32)
        down_grad_t = lax.dot_general(cotangent, hidden_low, tn, preferred_element_type=jnp.float32)
        grad_hidden = jnp.dot(cotangent, down_t, preferred_element_type=jnp.float32) * gelu_slope(
            hidden_pre
        )
        grad_hidden_low = grad_hidden.astype(jnp.bfloat16)
        up_grad_t = lax.dot_general(grad_hidden_low, act_two, tn, preferred_element_type=jnp.float32)
        up_bias_grad = jnp.sum(grad_hidden_low.astype(jnp.float32), axis=0)
        grad_act_two = jnp.dot(grad_hidden_low, up_t, preferred_element_type=jnp.float32)
        grad_norm_two, gain_two_grad, shift_two_grad = norm_backward(
            grad_act_two, normed_two, inv_two, gains_now[1]
        )
        grad_mid = grad_final + grad_norm_two
        grad_branch_low = grad_mid.astype(jnp.bfloat16)
        out_grad_t = lax.dot_general(
            grad_branch_low, attended_low, tn, preferred_element_type=jnp.float32
        )
        late_rows = jnp.concatenate(
            [
                out_grad_t.reshape(chips, 2, -1, model_width),
                up_grad_t.reshape(chips, 2, -1, model_width),
            ],
            axis=2,
        )
        late = ring_reduce_steps(
            ring, [(late_rows, "both"), (down_grad_t.reshape((chips, 2, -1) + down_grad_t.shape[1:]), "both")]
        )
        grad_attended = jnp.dot(grad_branch_low, out_t, preferred_element_type=jnp.float32).astype(
            jnp.bfloat16
        )
        kernel_count = tables[0].shape[0]
        start_sums = (
            jnp.zeros((kernel_count, head_count), jnp.float32),
            jnp.zeros((kernel_count,), jnp.float32),
            jnp.zeros((kernel_count,), jnp.float32),
            jnp.zeros((ATOM_TYPES, ATOM_TYPES), jnp.float32),
            jnp.zeros((ATOM_TYPES, ATOM_TYPES), jnp.float32),
        )
        kernel_sums = start_sums
        q_grads, k_grads, v_grads = [], [], []
        grad_attended_blocks = grad_attended.reshape(split_shape)
        stepper = Stepper(late)
        for b in range(blocks):
            gate = stepper.tie(grad_attended_blocks[b])
            kernel_sums, (qg, kg, vg) = block_backward_fast(
                kernel_sums,
                (
                    queries[b],
                    key_rows[b],
                    value_rows[b],
                    gate,
                    log_sums[b],
                    pos_blocks[b],
                    type_blocks[b],
                    mol_blocks[b],
                    pad_blocks[b],
                ),
                tables,
                heads_full,
                hook=stepper.tie,
            )
            q_grads.append(qg)
            k_grads.append(kg)
            v_grads.append(vg)
        queries_grad = jnp.stack(q_grads)
        keys_grad = jnp.stack(k_grads)
        values_grad = jnp.stack(v_grads)
        grad_projected = jnp.concatenate(
            [
                queries_grad.reshape(row_count, model_width),
                keys_grad.reshape(row_count, model_width),
                values_grad.reshape(row_count, model_width),
            ],
            axis=1,
        ).astype(jnp.bfloat16)
        in_grad_t = lax.dot_general(grad_projected, act_one, tn, preferred_element_type=jnp.float32)
        grad_act_one = jnp.dot(grad_projected, in_t, preferred_element_type=jnp.float32)
        grad_norm_one, gain_one_grad, shift_one_grad = norm_backward(
            grad_act_one, normed_one, inv_one, gains_now[0]
        )
        inputs_grad = grad_mid + grad_norm_one
        projected_sums = jnp.sum(grad_projected.astype(jnp.float32), axis=0)
        heads_grad, means_grad, widths_grad, scale_grad, shift_grad = kernel_sums
        small_grads = [
            jnp.stack([gain_one_grad, gain_two_grad]),
            jnp.stack(
                [
                    shift_one_grad,
                    shift_two_grad,
                    projected_sums[:model_width],
                    projected_sums[2 * model_width :],
                    jnp.sum(grad_branch_low.astype(jnp.float32), axis=0),
                    jnp.sum(grad_final, axis=0),
                ]
            ),
            up_bias_grad,
            means_grad,
            widths_grad,
            scale_grad,
            shift_grad,
            heads_grad,
        ]
        late_owned = stepper.finish()
        out_owned = late_owned[0][:out_rows]
        up_owned = late_owned[0][out_rows:]
        down_owned = late_owned[1]
        last = jnp.concatenate(
            [
                in_grad_t.reshape((chips, 2, -1) + in_grad_t.shape[1:]),
                pack_small_grads(small_grads, fsdp, chips),
            ],
            axis=2,
        )
        (last_owned,) = run_steps(ring_reduce_steps(ring, [(last, "both")]))
        in_rows = in_grad_t.shape[0] // fsdp
        in_owned = last_owned[:in_rows]
        small_owned = last_owned[in_rows:]
        sg = unpack_small_owned(small_owned, offsets)
        return (
            rows_out,
            inputs_grad,
            sg[0],
            sg[1],
            sg[2],
            in_owned.T,
            out_owned.T,
            up_owned.T,
            down_owned.T,
            sg[3],
            sg[4],
            sg[5],
            sg[6],
            sg[7],
        )

    return body


def solution(mesh):
    reps, fsdp = mesh.devices.shape
    chips = fsdp // 2
    grid = Mesh(mesh.devices.reshape(reps, chips, 2), ("rep", "chip", "core"))
    chips_x = 1
    try:
        coords = [tuple(d.coords) for d in mesh.devices[0, ::2]]
        xs = sorted({c[0] for c in coords})
        chips_x = len(xs)
        flat_ok = all(
            coords[i][0] == xs[i % chips_x] for i in range(chips)
        )
        if not flat_ok:
            chips_x = 1
    except Exception:
        chips_x = 1
    ring = None
    if chips <= 8:
        ring = Ring(snake_ring(chips_x, chips // chips_x))
    atoms = ("rep", "chip", "core")
    cols = ("chip", "core")
    placed = (
        P(atoms, None),
        P(atoms),
        P(None, atoms),
        P(atoms),
        P(atoms),
        P(atoms),
        P(atoms, None),
        P(None, cols),
        P(None, cols),
        P(cols),
        P(None, cols),
        P(None, cols),
        P(None, cols),
        P(None, cols),
        P(cols),
        P(cols),
        P(cols),
        P(cols),
        P(cols, None),
    )
    return jax.shard_map(
        make_body(ring, chips),
        mesh=grid,
        in_specs=placed,
        out_specs=(
            P(atoms, None),
            P(atoms, None),
            P(None, cols),
            P(None, cols),
            P(cols),
            P(None, cols),
            P(None, cols),
            P(None, cols),
            P(None, cols),
            P(cols),
            P(cols),
            P(cols),
            P(cols),
            P(cols, None),
        ),
        check_vma=False,
    )
```

```python
from functools import partial
import math

import jax
import jax.numpy as jnp
from jax import lax
from jax.sharding import Mesh, PartitionSpec as P
import numpy as np

ATOM_TYPES = 64


epsilon = 1e-05
masked_score = -1000000000.0
time_scale = 1000.0
root_two_pi = math.sqrt(2.0 * math.pi)
highest = lax.Precision.HIGHEST


def time_embedding(times, model_width):
    half_width = model_width // 2
    counter = jnp.arange(half_width, dtype=jnp.float32)
    frequency = jnp.exp(counter * (-math.log(10000.0) / half_width))
    angles = (time_scale * times)[:, None] * frequency[None, :]
    return jnp.concatenate([jnp.sin(angles), jnp.cos(angles)], axis=1)


def layer_norm(values, gain_row, shift_row):
    center = values - jnp.mean(values, axis=1, keepdims=True)
    inv_std = lax.rsqrt(jnp.mean(center * center, axis=1, keepdims=True) + epsilon)
    normed = center * inv_std
    return (normed * gain_row + shift_row, normed, inv_std)


def norm_backward(grad_out, normed, inv_std, gain_row):
    grad_normed = grad_out * gain_row
    first_mean = jnp.mean(grad_normed, axis=1, keepdims=True)
    second_mean = jnp.mean(grad_normed * normed, axis=1, keepdims=True)
    grad_input = inv_std * (grad_normed - first_mean - normed * second_mean)
    return (grad_input, jnp.sum(grad_out * normed, axis=0), jnp.sum(grad_out, axis=0))


def gelu_value(values):
    return values * (0.5 + 0.5 * lax.erf(values * math.sqrt(0.5)))


def gelu_slope(values):
    return (
        0.5
        + 0.5 * lax.erf(values * math.sqrt(0.5))
        + values * jnp.exp(-0.5 * values * values) / root_two_pi
    )


def pair_terms(pos_rows, pos_cols, type_rows, type_cols, tables):
    kernel_means, kernel_widths, scale_table, shift_table = tables
    offsets = pos_rows[:, :, None] - pos_cols[:, None, :]
    distance = jnp.sqrt(jnp.sum(offsets * offsets, axis=0))
    type_range = jnp.arange(ATOM_TYPES, dtype=jnp.int32)
    hot_rows = (type_rows[:, None] == type_range[None, :]).astype(jnp.float32)
    hot_cols = (type_cols[:, None] == type_range[None, :]).astype(jnp.float32)
    scale_pair = jnp.dot(
        jnp.dot(hot_rows, scale_table, precision=highest), hot_cols.T, precision=highest
    )
    shift_pair = jnp.dot(
        jnp.dot(hot_rows, shift_table, precision=highest), hot_cols.T, precision=highest
    )
    stretched = scale_pair * distance + shift_pair
    kernel_gap = (stretched[:, :, None] - kernel_means) / kernel_widths
    kernels = jnp.exp(-0.5 * kernel_gap * kernel_gap) / (root_two_pi * kernel_widths)
    return (distance, hot_rows, hot_cols, kernel_gap, kernels)


def allowed_pairs(row_ids, col_ids, mol_rows, mol_cols, pad_cols):
    same_mol = mol_rows[:, None] == mol_cols[None, :]
    key_live = (pad_cols[None, :] == 1) | (row_ids[:, None] == col_ids[None, :])
    return same_mol & key_live


def tile_scores(q_tile, key_block, kernels_low, kernel_heads, allowed, score_scale):
    pair_bias = jnp.einsum(
        "ijk,kh->hij", kernels_low, kernel_heads, preferred_element_type=jnp.float32
    )
    raw_scores = jnp.einsum("ihd,jhd->hij", q_tile, key_block, preferred_element_type=jnp.float32)
    return jnp.where(allowed[None], raw_scores * score_scale + pair_bias, masked_score)


def block_forward(pieces, tables, kernel_heads, tile_rows):
    queries, key_block, value_block, positions, types, mols, pads = pieces
    block_rows = queries.shape[0]
    score_scale = 1.0 / math.sqrt(queries.shape[2])
    col_ids = jnp.arange(block_rows, dtype=jnp.int32)

    def one_tile(running, tile_index):
        first_row = tile_index * tile_rows
        row_ids = first_row + jnp.arange(tile_rows, dtype=jnp.int32)
        terms = pair_terms(positions, positions, types, types, tables)
        kernels_low = terms[4].astype(jnp.bfloat16)
        allowed = allowed_pairs(row_ids, col_ids, mols, mols, pads)
        scores = tile_scores(queries, key_block, kernels_low, kernel_heads, allowed, score_scale)
        row_max = jnp.max(scores, axis=2, keepdims=True)
        exponent = jnp.exp(scores - row_max)
        row_sum = jnp.sum(exponent, axis=2, keepdims=True)
        probs_low = (exponent / row_sum).astype(jnp.bfloat16)
        attended = jnp.einsum(
            "hij,jhd->ihd", probs_low, value_block, preferred_element_type=jnp.float32
        )
        return (running, (attended, (row_max + jnp.log(row_sum))[:, :, 0]))

    count = block_rows // tile_rows
    if count == 1:
        _, (attended, log_sums) = one_tile(None, 0)
        return (attended.reshape(block_rows, -1), log_sums)
    _, (attended, log_sums) = lax.scan(one_tile, None, jnp.arange(count, dtype=jnp.int32))
    attended = attended.reshape(block_rows, -1)
    log_sums = jnp.transpose(log_sums, (1, 0, 2)).reshape(log_sums.shape[1], block_rows)
    return (attended, log_sums)


def block_backward(running, pieces, tables, kernel_heads, tile_rows, hook=None):
    queries, key_block, value_block, grad_attended, log_sums, positions, types, mols, pads = pieces
    kernel_widths = tables[1]
    block_rows = queries.shape[0]
    score_scale = 1.0 / math.sqrt(queries.shape[2])
    col_ids = jnp.arange(block_rows, dtype=jnp.int32)

    def one_tile(partial_sums, tile_index):
        keys_grad, values_grad, heads_grad, means_grad, widths_grad, scale_grad, shift_grad = (
            partial_sums
        )
        first_row = tile_index * tile_rows
        row_ids = first_row + jnp.arange(tile_rows, dtype=jnp.int32)
        distance, hot_rows, hot_cols, kernel_gap, kernels = pair_terms(
            positions, positions, types, types, tables
        )
        kernels_low = kernels.astype(jnp.bfloat16)
        allowed = allowed_pairs(row_ids, col_ids, mols, mols, pads)
        scores = tile_scores(queries, key_block, kernels_low, kernel_heads, allowed, score_scale)
        attn_probs = jnp.exp(scores - log_sums[:, :, None])
        grad_probs = jnp.einsum(
            "ihd,jhd->hij", grad_attended, value_block, preferred_element_type=jnp.float32
        )
        values_grad = values_grad + jnp.einsum(
            "hij,ihd->jhd",
            attn_probs.astype(jnp.bfloat16),
            grad_attended,
            preferred_element_type=jnp.float32,
        )
        probs_dot = jnp.sum(attn_probs * grad_probs, axis=2, keepdims=True)
        grad_scores = (attn_probs * (grad_probs - probs_dot)).astype(jnp.bfloat16)
        if hook is not None:
            grad_scores = hook(grad_scores)
        query_grad = (
            jnp.einsum("hij,jhd->ihd", grad_scores, key_block, preferred_element_type=jnp.float32)
            * score_scale
        )
        keys_grad = (
            keys_grad
            + jnp.einsum("hij,ihd->jhd", grad_scores, queries, preferred_element_type=jnp.float32)
            * score_scale
        )
        heads_grad = heads_grad + jnp.einsum(
            "ijk,hij->kh", kernels_low, grad_scores, preferred_element_type=jnp.float32
        )
        heads_f = kernel_heads.astype(jnp.float32)
        scores_f = grad_scores.astype(jnp.float32)
        slope_mean = kernels * kernel_gap / kernel_widths
        slope_width = kernels * (kernel_gap * kernel_gap - 1.0) / kernel_widths
        mean_heads = jnp.einsum("hij,ijk->hk", scores_f, slope_mean, precision=highest)
        width_heads = jnp.einsum("hij,ijk->hk", scores_f, slope_width, precision=highest)
        means_grad = means_grad + jnp.einsum("kh,hk->k", heads_f, mean_heads, precision=highest)
        widths_grad = widths_grad + jnp.einsum("kh,hk->k", heads_f, width_heads, precision=highest)
        per_head = jnp.einsum("ijk,kh->hij", slope_mean, heads_f, precision=highest)
        grad_stretched = -jnp.sum(scores_f * per_head, axis=0)
        scale_grad = scale_grad + jnp.dot(
            jnp.dot(hot_rows.T, grad_stretched * distance, precision=highest),
            hot_cols,
            precision=highest,
        )
        shift_grad = shift_grad + jnp.dot(
            jnp.dot(hot_rows.T, grad_stretched, precision=highest), hot_cols, precision=highest
        )
        return (
            (keys_grad, values_grad, heads_grad, means_grad, widths_grad, scale_grad, shift_grad),
            query_grad,
        )

    zero_block = jnp.zeros(key_block.shape, jnp.float32)
    count = block_rows // tile_rows
    if count == 1:
        sums_out, query_grads = one_tile((zero_block, zero_block) + tuple(running), 0)
        return (sums_out[2:], (query_grads.reshape(key_block.shape), sums_out[0], sums_out[1]))
    sums_out, query_grads = lax.scan(
        one_tile, (zero_block, zero_block) + tuple(running), jnp.arange(count, dtype=jnp.int32)
    )
    query_grads = query_grads.reshape(key_block.shape)
    return (sums_out[2:], (query_grads, sums_out[0], sums_out[1]))


def snake_ring(chips_x, chips_other):
    if chips_x == 2 and chips_other >= 2:
        return [2 * z for z in range(chips_other)] + [
            2 * z + 1 for z in reversed(range(chips_other))
        ]
    return list(range(chips_x * chips_other))


class Ring:
    def __init__(self, order):
        self.order = order
        self.n = len(order)
        pos = np.zeros(self.n, np.int32)
        for i, c in enumerate(order):
            pos[c] = i
        self.pos = pos
        self.cw = [(order[i], order[(i + 1) % self.n]) for i in range(self.n)]
        self.ccw = [(order[i], order[(i - 1) % self.n]) for i in range(self.n)]

    def here(self):
        chip = lax.axis_index("chip")
        core = lax.axis_index("core")
        return chip, core, jnp.asarray(self.pos)[chip]

    def chip_at(self, position):
        return jnp.asarray(np.array(self.order, np.int32))[position % self.n]


SWAP = [(0, 1), (1, 0)]


def _halves(x, axis):
    size = x.shape[axis] // 2
    return (
        lax.slice_in_dim(x, 0, size, axis=axis),
        lax.slice_in_dim(x, size, 2 * size, axis=axis),
    )


def ring_gather(ring, pieces, chips):
    if ring is None:
        return [
            lax.all_gather(x, ("chip", "core"), axis=0, tiled=False).reshape((chips, 2) + x.shape)
            for x, _ in pieces
        ]
    chip, core, p = ring.here()
    n = ring.n
    bufs, fronts = [], []
    for x, axis in pieces:
        buf = jnp.zeros((n, 2) + x.shape, x.dtype)
        buf = lax.dynamic_update_slice(buf, x[None, None], (chip, core) + (0,) * x.ndim)
        bufs.append(buf)
        if axis is None:
            fronts.append([x, None])
        else:
            fronts.append(list(_halves(x, axis)))
    partner = lax.ppermute([x for x, _ in pieces], "core", SWAP)
    for i, x in enumerate(partner):
        bufs[i] = lax.dynamic_update_slice(
            bufs[i], x[None, None], (chip, 1 - core) + (0,) * x.ndim
        )
    for step in range(1, n):
        going = [f[0] for f in fronts]
        coming = [f[1] for f in fronts if f[1] is not None]
        going = lax.ppermute(going, "chip", ring.cw)
        coming = lax.ppermute(coming, "chip", ring.ccw) if coming else []
        from_cw = ring.chip_at(p - step)
        from_ccw = ring.chip_at(p + step)
        both = lax.ppermute([going, coming], "core", SWAP)
        j = 0
        for i, (x, axis) in enumerate(pieces):
            fronts[i][0] = going[i]
            parts = [(going[i], both[0][i], from_cw, 0)]
            if axis is not None:
                fronts[i][1] = coming[j]
                parts.append((coming[j], both[1][j], from_ccw, x.shape[axis] // 2))
                j += 1
            for mine, theirs, source, offset in parts:
                start = [0] * x.ndim
                if axis is not None:
                    start[axis] = offset
                bufs[i] = lax.dynamic_update_slice(
                    bufs[i], mine[None, None], (source, core) + tuple(start)
                )
                bufs[i] = lax.dynamic_update_slice(
                    bufs[i], theirs[None, None], (source, 1 - core) + tuple(start)
                )
    return bufs


def ring_reduce_steps(ring, pieces, send=jnp.bfloat16):
    if ring is None:
        owned = []
        for g, _ in pieces:
            flat = g.reshape((-1,) + g.shape[3:])
            part = lax.psum_scatter(flat, ("chip", "core"), scatter_dimension=0, tiled=True)
            owned.append(lax.psum(part.astype(send), "rep").astype(jnp.float32))
        yield owned
        return owned
    chip, core, p = ring.here()
    n = ring.n
    mine, theirs = [], []
    for g, _ in pieces:
        mine.append(lax.dynamic_index_in_dim(g, core, axis=1, keepdims=False))
        theirs.append(lax.dynamic_index_in_dim(g, 1 - core, axis=1, keepdims=False).astype(send))
    got = lax.ppermute(theirs, "core", SWAP)
    yield got
    flows = []
    for i, (g, way) in enumerate(pieces):
        if way == "both":
            flows.append((i, 1, n // 2, mine[i], got[i]))
            flows.append((i, -1, (n - 1) // 2, mine[i], got[i]))
        elif isinstance(way, tuple):
            axis = way[1] + 1
            for d, (m, t) in zip((1, -1), zip(_halves(mine[i], axis), _halves(got[i], axis))):
                flows.append((i, d, n - 1, m, t))
        else:
            flows.append((i, way, n - 1, mine[i], got[i]))

    def contribution(m, t, position):
        at = ring.chip_at(position)
        own = lax.dynamic_index_in_dim(m, at, axis=0, keepdims=False)
        other = lax.dynamic_index_in_dim(t, at, axis=0, keepdims=False)
        return own + other.astype(jnp.float32)

    acc = [contribution(m, t, p + d * hops) for _, d, hops, m, t in flows]
    for step in range(1, max(f[2] for f in flows) + 1):
        moved = []
        for d in (1, -1):
            chosen = [k for k, f in enumerate(flows) if f[1] == d and f[2] >= step]
            if chosen:
                out = lax.ppermute([acc[k].astype(send) for k in chosen], "chip", ring.cw if d == 1 else ring.ccw)
                for k, o in zip(chosen, out):
                    acc[k] = o.astype(jnp.float32)
                moved.extend(out)
        yield moved
        for k, (_, d, hops, m, t) in enumerate(flows):
            if hops > step:
                acc[k] = acc[k] + contribution(m, t, p + d * (hops - step))
    owned = []
    for i, (g, way) in enumerate(pieces):
        parts = [(a, f) for a, f in zip(acc, flows) if f[0] == i]
        if way == "both":
            total = contribution(parts[0][1][3], parts[0][1][4], p) + parts[0][0] + parts[1][0]
        else:
            total = [a + contribution(f[3], f[4], p) for a, f in parts]
            total = total[0] if len(total) == 1 else jnp.concatenate(total, axis=way[1])
        owned.append(total)
    other = lax.ppermute([o.astype(send) for o in owned], "rep", SWAP)
    yield other
    return [o + t.astype(jnp.float32) for o, t in zip(owned, other)]


class Stepper:
    def __init__(self, gen):
        self.gen = gen
        self.result = None
        self.over = False

    def tie(self, value):
        if self.over:
            return value
        try:
            ready = next(self.gen)
        except StopIteration as done:
            self.result, self.over = done.value, True
            return value
        _, value = lax.optimization_barrier((ready, value))
        return value

    def finish(self):
        if not self.over:
            self.result, self.over = run_steps(self.gen), True
        return self.result


def run_steps(gen):
    while True:
        try:
            next(gen)
        except StopIteration as done:
            return done.value


SMALL_ROWS, SMALL_LANES = 16, 768
GRAD_ROWS = 8


def small_layout(fsdp):
    d = 768 // fsdp
    sizes = [2 * d, 6 * d, 3072 // fsdp, 128 // fsdp, 128 // fsdp, 4096 // fsdp, 4096 // fsdp, (128 // fsdp) * 32]
    offsets, at = [], 0
    for size in sizes:
        offsets.append((at, size))
        at += size
    assert at <= SMALL_ROWS * SMALL_LANES
    return offsets


def pack_small(parts):
    flat = jnp.concatenate([part.reshape(-1) for part in parts])
    flat = jnp.pad(flat, (0, SMALL_ROWS * SMALL_LANES - flat.shape[0]))
    return flat.reshape(SMALL_ROWS, SMALL_LANES)


def unpack_small_full(gathered, offsets, fsdp):
    flat = gathered.reshape(fsdp, -1).astype(jnp.float32)
    take = [flat[:, at : at + size] for at, size in offsets]
    d = 768 // fsdp
    return [
        take[0].reshape(fsdp, 2, d).transpose(1, 0, 2).reshape(2, -1),
        take[1].reshape(fsdp, 6, d).transpose(1, 0, 2).reshape(6, -1),
        take[2].reshape(-1),
        take[3].reshape(-1),
        take[4].reshape(-1),
        take[5].reshape(ATOM_TYPES, ATOM_TYPES),
        take[6].reshape(ATOM_TYPES, ATOM_TYPES),
        take[7].reshape(-1, 32),
    ]


def pack_small_grads(grads, fsdp, chips):
    d = 768 // fsdp
    blocks = [
        grads[0].reshape(2, fsdp, d).transpose(1, 0, 2),
        grads[1].reshape(6, fsdp, d).transpose(1, 0, 2),
    ] + [g.reshape(-1) for g in grads[2:]]
    flat = jnp.concatenate([blk.reshape(fsdp, -1) for blk in blocks], axis=1)
    flat = jnp.pad(flat, ((0, 0), (0, GRAD_ROWS * SMALL_LANES - flat.shape[1])))
    return flat.reshape(chips, 2, GRAD_ROWS, SMALL_LANES)


def unpack_small_owned(block, offsets):
    flat = block.reshape(-1)
    take = [flat[at : at + size] for at, size in offsets]
    return [
        take[0].reshape(2, -1),
        take[1].reshape(6, -1),
        take[2],
        take[3],
        take[4],
        take[5],
        take[6],
        take[7].reshape(-1, 32),
    ]


def make_body(ring, chips):
    fsdp = 2 * chips

    def body(
        inputs,
        times,
        positions,
        atom_types,
        molecule_ids,
        pad_mask,
        cotangent,
        norm_gains,
        bias_rows,
        up_bias,
        input_weight,
        output_weight,
        up_weight,
        down_weight,
        kernel_means,
        kernel_widths,
        pair_scale,
        pair_shift,
        kernel_heads,
    ):
        offsets = small_layout(fsdp)
        small = pack_small(
            [norm_gains, bias_rows, up_bias, kernel_means, kernel_widths, pair_scale, pair_shift, kernel_heads]
        )
        width = input_weight.shape[0]
        first = jnp.concatenate([small.reshape(-1, width), input_weight.T], axis=0)
        second = jnp.concatenate(
            [output_weight.T, up_weight.T, down_weight.T.reshape(-1, width)], axis=0
        )
        first_all = lax.all_gather(first, ("chip", "core"), axis=0, tiled=False)
        second_all = lax.all_gather(second, ("chip", "core"), axis=0, tiled=False)
        small_rows = small.size // width
        params = unpack_small_full(first_all[:, :small_rows], offsets, fsdp)
        in_t = first_all[:, small_rows:].reshape(-1, width)
        out_rows = output_weight.shape[1]
        up_rows = up_weight.shape[1]
        out_t = second_all[:, :out_rows].reshape(-1, width)
        up_t = second_all[:, out_rows : out_rows + up_rows].reshape(-1, width)
        down_t = (
            second_all[:, out_rows + up_rows :]
            .reshape(fsdp, down_weight.shape[1], -1)
            .reshape(-1, down_weight.shape[0])
        )
        gains_now, biases_now, up_shift = params[0], params[1], params[2]
        tables = (params[3], params[4], params[5], params[6])
        heads_full = params[7].astype(jnp.bfloat16)

        row_count = inputs.shape[0]
        model_width = inputs.shape[1]
        head_count = heads_full.shape[1]
        head_size = model_width // head_count
        block_rows = min(128, row_count)
        blocks = row_count // block_rows
        tile_rows = min(128, block_rows)
        nt = (((1,), (1,)), ((), ()))
        tn = (((0,), (0,)), ((), ()))

        stream = inputs.astype(jnp.float32) + time_embedding(times, model_width)
        normed_out, normed_one, inv_one = layer_norm(stream, gains_now[0], biases_now[0])
        act_one = normed_out.astype(jnp.bfloat16)
        qkv_shift = jnp.concatenate([biases_now[2], jnp.zeros_like(biases_now[2]), biases_now[3]])
        projected = (
            lax.dot_general(act_one, in_t, nt, preferred_element_type=jnp.float32) + qkv_shift
        ).astype(jnp.bfloat16)
        split_shape = (blocks, block_rows, head_count, head_size)
        queries = projected[:, :model_width].reshape(split_shape)
        key_rows = projected[:, model_width : 2 * model_width].reshape(split_shape)
        value_rows = projected[:, 2 * model_width :].reshape(split_shape)
        pos_blocks = jnp.transpose(positions.reshape(3, blocks, block_rows), (1, 0, 2))
        type_blocks = atom_types.reshape(blocks, block_rows)
        mol_blocks = molecule_ids.reshape(blocks, block_rows)
        pad_blocks = pad_mask.reshape(blocks, block_rows)
        fwd = [
            block_forward(
                (queries[b], key_rows[b], value_rows[b], pos_blocks[b], type_blocks[b], mol_blocks[b], pad_blocks[b]),
                tables=tables,
                kernel_heads=heads_full,
                tile_rows=tile_rows,
            )
            for b in range(blocks)
        ]
        attended = jnp.stack([f[0] for f in fwd])
        log_sums = [f[1] for f in fwd]
        attended_low = attended.reshape(row_count, model_width).astype(jnp.bfloat16)
        mid = stream + (
            lax.dot_general(attended_low, out_t, nt, preferred_element_type=jnp.float32)
            + biases_now[4]
        )
        normed_out_two, normed_two, inv_two = layer_norm(mid, gains_now[1], biases_now[1])
        act_two = normed_out_two.astype(jnp.bfloat16)
        hidden_pre = (
            lax.dot_general(act_two, up_t, nt, preferred_element_type=jnp.float32) + up_shift
        )
        hidden_low = gelu_value(hidden_pre).astype(jnp.bfloat16)
        final = mid + (
            lax.dot_general(hidden_low, down_t, nt, preferred_element_type=jnp.float32)
            + biases_now[5]
        )
        rows_out = final.astype(jnp.bfloat16)

        grad_final = cotangent.astype(jnp.float32)
        down_grad_t = lax.dot_general(cotangent, hidden_low, tn, preferred_element_type=jnp.float32)
        grad_hidden = jnp.dot(cotangent, down_t, preferred_element_type=jnp.float32) * gelu_slope(
            hidden_pre
        )
        grad_hidden_low = grad_hidden.astype(jnp.bfloat16)
        up_grad_t = lax.dot_general(grad_hidden_low, act_two, tn, preferred_element_type=jnp.float32)
        up_bias_grad = jnp.sum(grad_hidden_low.astype(jnp.float32), axis=0)
        grad_act_two = jnp.dot(grad_hidden_low, up_t, preferred_element_type=jnp.float32)
        grad_norm_two, gain_two_grad, shift_two_grad = norm_backward(
            grad_act_two, normed_two, inv_two, gains_now[1]
        )
        grad_mid = grad_final + grad_norm_two
        grad_branch_low = grad_mid.astype(jnp.bfloat16)
        out_grad_t = lax.dot_general(
            grad_branch_low, attended_low, tn, preferred_element_type=jnp.float32
        )
        late_rows = jnp.concatenate(
            [
                out_grad_t.reshape(chips, 2, -1, model_width),
                up_grad_t.reshape(chips, 2, -1, model_width),
            ],
            axis=2,
        )
        late = ring_reduce_steps(
            ring, [(late_rows, "both"), (down_grad_t.reshape((chips, 2, -1) + down_grad_t.shape[1:]), "both")]
        )
        grad_attended = jnp.dot(grad_branch_low, out_t, preferred_element_type=jnp.float32).astype(
            jnp.bfloat16
        )
        kernel_count = tables[0].shape[0]
        start_sums = (
            jnp.zeros((kernel_count, head_count), jnp.float32),
            jnp.zeros((kernel_count,), jnp.float32),
            jnp.zeros((kernel_count,), jnp.float32),
            jnp.zeros((ATOM_TYPES, ATOM_TYPES), jnp.float32),
            jnp.zeros((ATOM_TYPES, ATOM_TYPES), jnp.float32),
        )
        kernel_sums = start_sums
        q_grads, k_grads, v_grads = [], [], []
        grad_attended_blocks = grad_attended.reshape(split_shape)
        stepper = Stepper(late)
        for b in range(blocks):
            gate = stepper.tie(grad_attended_blocks[b])
            kernel_sums, (qg, kg, vg) = block_backward(
                kernel_sums,
                (
                    queries[b],
                    key_rows[b],
                    value_rows[b],
                    gate,
                    log_sums[b],
                    pos_blocks[b],
                    type_blocks[b],
                    mol_blocks[b],
                    pad_blocks[b],
                ),
                tables=tables,
                kernel_heads=heads_full,
                tile_rows=tile_rows,
                hook=stepper.tie,
            )
            q_grads.append(qg)
            k_grads.append(kg)
            v_grads.append(vg)
        queries_grad = jnp.stack(q_grads)
        keys_grad = jnp.stack(k_grads)
        values_grad = jnp.stack(v_grads)
        grad_projected = jnp.concatenate(
            [
                queries_grad.reshape(row_count, model_width),
                keys_grad.reshape(row_count, model_width),
                values_grad.reshape(row_count, model_width),
            ],
            axis=1,
        ).astype(jnp.bfloat16)
        in_grad_t = lax.dot_general(grad_projected, act_one, tn, preferred_element_type=jnp.float32)
        grad_act_one = jnp.dot(grad_projected, in_t, preferred_element_type=jnp.float32)
        grad_norm_one, gain_one_grad, shift_one_grad = norm_backward(
            grad_act_one, normed_one, inv_one, gains_now[0]
        )
        inputs_grad = grad_mid + grad_norm_one
        projected_sums = jnp.sum(grad_projected.astype(jnp.float32), axis=0)
        heads_grad, means_grad, widths_grad, scale_grad, shift_grad = kernel_sums
        small_grads = [
            jnp.stack([gain_one_grad, gain_two_grad]),
            jnp.stack(
                [
                    shift_one_grad,
                    shift_two_grad,
                    projected_sums[:model_width],
                    projected_sums[2 * model_width :],
                    jnp.sum(grad_branch_low.astype(jnp.float32), axis=0),
                    jnp.sum(grad_final, axis=0),
                ]
            ),
            up_bias_grad,
            means_grad,
            widths_grad,
            scale_grad,
            shift_grad,
            heads_grad,
        ]
        late_owned = stepper.finish()
        out_owned = late_owned[0][:out_rows]
        up_owned = late_owned[0][out_rows:]
        down_owned = late_owned[1]
        last = jnp.concatenate(
            [
                in_grad_t.reshape((chips, 2, -1) + in_grad_t.shape[1:]),
                pack_small_grads(small_grads, fsdp, chips),
            ],
            axis=2,
        )
        (last_owned,) = run_steps(ring_reduce_steps(ring, [(last, "both")]))
        in_rows = in_grad_t.shape[0] // fsdp
        in_owned = last_owned[:in_rows]
        small_owned = last_owned[in_rows:]
        sg = unpack_small_owned(small_owned, offsets)
        return (
            rows_out,
            inputs_grad,
            sg[0],
            sg[1],
            sg[2],
            in_owned.T,
            out_owned.T,
            up_owned.T,
            down_owned.T,
            sg[3],
            sg[4],
            sg[5],
            sg[6],
            sg[7],
        )

    return body


def solution(mesh):
    reps, fsdp = mesh.devices.shape
    chips = fsdp // 2
    grid = Mesh(mesh.devices.reshape(reps, chips, 2), ("rep", "chip", "core"))
    chips_x = 1
    try:
        coords = [tuple(d.coords) for d in mesh.devices[0, ::2]]
        xs = sorted({c[0] for c in coords})
        chips_x = len(xs)
        flat_ok = all(
            coords[i][0] == xs[i % chips_x] for i in range(chips)
        )
        if not flat_ok:
            chips_x = 1
    except Exception:
        chips_x = 1
    ring = None
    if chips <= 8:
        ring = Ring(snake_ring(chips_x, chips // chips_x))
    atoms = ("rep", "chip", "core")
    cols = ("chip", "core")
    placed = (
        P(atoms, None),
        P(atoms),
        P(None, atoms),
        P(atoms),
        P(atoms),
        P(atoms),
        P(atoms, None),
        P(None, cols),
        P(None, cols),
        P(cols),
        P(None, cols),
        P(None, cols),
        P(None, cols),
        P(None, cols),
        P(cols),
        P(cols),
        P(cols),
        P(cols),
        P(cols, None),
    )
    return jax.shard_map(
        make_body(ring, chips),
        mesh=grid,
        in_specs=placed,
        out_specs=(
            P(atoms, None),
            P(atoms, None),
            P(None, cols),
            P(None, cols),
            P(cols),
            P(None, cols),
            P(None, cols),
            P(None, cols),
            P(None, cols),
            P(cols),
            P(cols),
            P(cols),
            P(cols),
            P(cols, None),
        ),
        check_vma=False,
    )
```

```python
from functools import partial
import math

import jax
import jax.numpy as jnp
from jax import lax
from jax.sharding import Mesh, PartitionSpec as P
import numpy as np

ATOM_TYPES = 64


epsilon = 1e-05
masked_score = -1000000000.0
time_scale = 1000.0
root_two_pi = math.sqrt(2.0 * math.pi)
highest = lax.Precision.HIGHEST


def time_embedding(times, model_width):
    half_width = model_width // 2
    counter = jnp.arange(half_width, dtype=jnp.float32)
    frequency = jnp.exp(counter * (-math.log(10000.0) / half_width))
    angles = (time_scale * times)[:, None] * frequency[None, :]
    return jnp.concatenate([jnp.sin(angles), jnp.cos(angles)], axis=1)


def layer_norm(values, gain_row, shift_row):
    center = values - jnp.mean(values, axis=1, keepdims=True)
    inv_std = lax.rsqrt(jnp.mean(center * center, axis=1, keepdims=True) + epsilon)
    normed = center * inv_std
    return (normed * gain_row + shift_row, normed, inv_std)


def norm_backward(grad_out, normed, inv_std, gain_row):
    grad_normed = grad_out * gain_row
    first_mean = jnp.mean(grad_normed, axis=1, keepdims=True)
    second_mean = jnp.mean(grad_normed * normed, axis=1, keepdims=True)
    grad_input = inv_std * (grad_normed - first_mean - normed * second_mean)
    return (grad_input, jnp.sum(grad_out * normed, axis=0), jnp.sum(grad_out, axis=0))


def gelu_value(values):
    return values * (0.5 + 0.5 * lax.erf(values * math.sqrt(0.5)))


def gelu_slope(values):
    return (
        0.5
        + 0.5 * lax.erf(values * math.sqrt(0.5))
        + values * jnp.exp(-0.5 * values * values) / root_two_pi
    )


def pair_terms(pos_rows, pos_cols, type_rows, type_cols, tables):
    kernel_means, kernel_widths, scale_table, shift_table = tables
    offsets = pos_rows[:, :, None] - pos_cols[:, None, :]
    distance = jnp.sqrt(jnp.sum(offsets * offsets, axis=0))
    type_range = jnp.arange(ATOM_TYPES, dtype=jnp.int32)
    hot_rows = (type_rows[:, None] == type_range[None, :]).astype(jnp.float32)
    hot_cols = (type_cols[:, None] == type_range[None, :]).astype(jnp.float32)
    scale_pair = jnp.dot(
        jnp.dot(hot_rows, scale_table, precision=highest), hot_cols.T, precision=highest
    )
    shift_pair = jnp.dot(
        jnp.dot(hot_rows, shift_table, precision=highest), hot_cols.T, precision=highest
    )
    stretched = scale_pair * distance + shift_pair
    kernel_gap = (stretched[:, :, None] - kernel_means) / kernel_widths
    kernels = jnp.exp(-0.5 * kernel_gap * kernel_gap) / (root_two_pi * kernel_widths)
    return (distance, hot_rows, hot_cols, kernel_gap, kernels)


def allowed_pairs(row_ids, col_ids, mol_rows, mol_cols, pad_cols):
    same_mol = mol_rows[:, None] == mol_cols[None, :]
    key_live = (pad_cols[None, :] == 1) | (row_ids[:, None] == col_ids[None, :])
    return same_mol & key_live


def tile_scores(q_tile, key_block, kernels_low, kernel_heads, allowed, score_scale):
    pair_bias = jnp.einsum(
        "ijk,kh->hij", kernels_low, kernel_heads, preferred_element_type=jnp.float32
    )
    raw_scores = jnp.einsum("ihd,jhd->hij", q_tile, key_block, preferred_element_type=jnp.float32)
    return jnp.where(allowed[None], raw_scores * score_scale + pair_bias, masked_score)


def block_forward(pieces, tables, kernel_heads, tile_rows):
    queries, key_block, value_block, positions, types, mols, pads = pieces
    block_rows = queries.shape[0]
    score_scale = 1.0 / math.sqrt(queries.shape[2])
    col_ids = jnp.arange(block_rows, dtype=jnp.int32)

    def one_tile(running, tile_index):
        first_row = tile_index * tile_rows
        row_ids = first_row + jnp.arange(tile_rows, dtype=jnp.int32)
        terms = pair_terms(positions, positions, types, types, tables)
        kernels_low = terms[4].astype(jnp.bfloat16)
        allowed = allowed_pairs(row_ids, col_ids, mols, mols, pads)
        scores = tile_scores(queries, key_block, kernels_low, kernel_heads, allowed, score_scale)
        row_max = jnp.max(scores, axis=2, keepdims=True)
        exponent = jnp.exp(scores - row_max)
        row_sum = jnp.sum(exponent, axis=2, keepdims=True)
        probs_low = (exponent / row_sum).astype(jnp.bfloat16)
        attended = jnp.einsum(
            "hij,jhd->ihd", probs_low, value_block, preferred_element_type=jnp.float32
        )
        return (running, (attended, (row_max + jnp.log(row_sum))[:, :, 0]))

    count = block_rows // tile_rows
    if count == 1:
        _, (attended, log_sums) = one_tile(None, 0)
        return (attended.reshape(block_rows, -1), log_sums)
    _, (attended, log_sums) = lax.scan(one_tile, None, jnp.arange(count, dtype=jnp.int32))
    attended = attended.reshape(block_rows, -1)
    log_sums = jnp.transpose(log_sums, (1, 0, 2)).reshape(log_sums.shape[1], block_rows)
    return (attended, log_sums)


def block_backward(running, pieces, tables, kernel_heads, tile_rows, hook=None):
    queries, key_block, value_block, grad_attended, log_sums, positions, types, mols, pads = pieces
    kernel_widths = tables[1]
    block_rows = queries.shape[0]
    score_scale = 1.0 / math.sqrt(queries.shape[2])
    col_ids = jnp.arange(block_rows, dtype=jnp.int32)

    def one_tile(partial_sums, tile_index):
        keys_grad, values_grad, heads_grad, means_grad, widths_grad, scale_grad, shift_grad = (
            partial_sums
        )
        first_row = tile_index * tile_rows
        row_ids = first_row + jnp.arange(tile_rows, dtype=jnp.int32)
        distance, hot_rows, hot_cols, kernel_gap, kernels = pair_terms(
            positions, positions, types, types, tables
        )
        kernels_low = kernels.astype(jnp.bfloat16)
        allowed = allowed_pairs(row_ids, col_ids, mols, mols, pads)
        scores = tile_scores(queries, key_block, kernels_low, kernel_heads, allowed, score_scale)
        attn_probs = jnp.exp(scores - log_sums[:, :, None])
        grad_probs = jnp.einsum(
            "ihd,jhd->hij", grad_attended, value_block, preferred_element_type=jnp.float32
        )
        values_grad = values_grad + jnp.einsum(
            "hij,ihd->jhd",
            attn_probs.astype(jnp.bfloat16),
            grad_attended,
            preferred_element_type=jnp.float32,
        )
        probs_dot = jnp.sum(attn_probs * grad_probs, axis=2, keepdims=True)
        grad_scores = (attn_probs * (grad_probs - probs_dot)).astype(jnp.bfloat16)
        if hook is not None:
            grad_scores = hook(grad_scores)
        query_grad = (
            jnp.einsum("hij,jhd->ihd", grad_scores, key_block, preferred_element_type=jnp.float32)
            * score_scale
        )
        keys_grad = (
            keys_grad
            + jnp.einsum("hij,ihd->jhd", grad_scores, queries, preferred_element_type=jnp.float32)
            * score_scale
        )
        heads_grad = heads_grad + jnp.einsum(
            "ijk,hij->kh", kernels_low, grad_scores, preferred_element_type=jnp.float32
        )
        grad_kernels = jnp.einsum(
            "hij,kh->ijk", grad_scores, kernel_heads, preferred_element_type=jnp.float32
        )
        spread = grad_kernels * kernels
        mean_part = spread * kernel_gap / kernel_widths
        means_grad = means_grad + jnp.sum(mean_part, axis=(0, 1))
        widths_grad = widths_grad + jnp.sum(
            spread * (kernel_gap * kernel_gap - 1.0) / kernel_widths, axis=(0, 1)
        )
        grad_stretched = -jnp.sum(mean_part, axis=2)
        scale_grad = scale_grad + jnp.dot(
            jnp.dot(hot_rows.T, grad_stretched * distance, precision=highest),
            hot_cols,
            precision=highest,
        )
        shift_grad = shift_grad + jnp.dot(
            jnp.dot(hot_rows.T, grad_stretched, precision=highest), hot_cols, precision=highest
        )
        return (
            (keys_grad, values_grad, heads_grad, means_grad, widths_grad, scale_grad, shift_grad),
            query_grad,
        )

    zero_block = jnp.zeros(key_block.shape, jnp.float32)
    count = block_rows // tile_rows
    if count == 1:
        sums_out, query_grads = one_tile((zero_block, zero_block) + tuple(running), 0)
        return (sums_out[2:], (query_grads.reshape(key_block.shape), sums_out[0], sums_out[1]))
    sums_out, query_grads = lax.scan(
        one_tile, (zero_block, zero_block) + tuple(running), jnp.arange(count, dtype=jnp.int32)
    )
    query_grads = query_grads.reshape(key_block.shape)
    return (sums_out[2:], (query_grads, sums_out[0], sums_out[1]))


def attention_grads(pieces, tables, kernel_heads, hook=None):
    queries, key_block, value_block, grad_attended, log_sums, positions, types, mols, pads = pieces
    block_rows = queries.shape[0]
    score_scale = 1.0 / math.sqrt(queries.shape[2])
    ids = jnp.arange(block_rows, dtype=jnp.int32)
    _, _, _, _, kernels = pair_terms(positions, positions, types, types, tables)
    allowed = allowed_pairs(ids, ids, mols, mols, pads)
    scores = tile_scores(
        queries, key_block, kernels.astype(jnp.bfloat16), kernel_heads, allowed, score_scale
    )
    attn_probs = jnp.exp(scores - log_sums[:, :, None])
    grad_probs = jnp.einsum(
        "ihd,jhd->hij", grad_attended, value_block, preferred_element_type=jnp.float32
    )
    values_grad = jnp.einsum(
        "hij,ihd->jhd", attn_probs.astype(jnp.bfloat16), grad_attended, preferred_element_type=jnp.float32
    )
    probs_dot = jnp.sum(attn_probs * grad_probs, axis=2, keepdims=True)
    grad_scores = (attn_probs * (grad_probs - probs_dot)).astype(jnp.bfloat16)
    if hook is not None:
        grad_scores = hook(grad_scores)
    query_grad = (
        jnp.einsum("hij,jhd->ihd", grad_scores, key_block, preferred_element_type=jnp.float32)
        * score_scale
    )
    keys_grad = (
        jnp.einsum("hij,ihd->jhd", grad_scores, queries, preferred_element_type=jnp.float32)
        * score_scale
    )
    return query_grad, keys_grad, values_grad, grad_scores


def kernel_grads(running, grad_scores, positions, types, tables, kernel_heads):
    heads_grad, means_grad, widths_grad, scale_grad, shift_grad = running
    kernel_widths = tables[1]
    distance, hot_rows, hot_cols, kernel_gap, kernels = pair_terms(
        positions, positions, types, types, tables
    )
    heads_grad = heads_grad + jnp.einsum(
        "ijk,hij->kh", kernels.astype(jnp.bfloat16), grad_scores, preferred_element_type=jnp.float32
    )
    grad_kernels = jnp.einsum(
        "hij,kh->ijk", grad_scores, kernel_heads, preferred_element_type=jnp.float32
    )
    spread = grad_kernels * kernels
    mean_part = spread * kernel_gap / kernel_widths
    means_grad = means_grad + jnp.sum(mean_part, axis=(0, 1))
    widths_grad = widths_grad + jnp.sum(
        spread * (kernel_gap * kernel_gap - 1.0) / kernel_widths, axis=(0, 1)
    )
    grad_stretched = -jnp.sum(mean_part, axis=2)
    scale_grad = scale_grad + jnp.dot(
        jnp.dot(hot_rows.T, grad_stretched * distance, precision=highest), hot_cols, precision=highest
    )
    shift_grad = shift_grad + jnp.dot(
        jnp.dot(hot_rows.T, grad_stretched, precision=highest), hot_cols, precision=highest
    )
    return heads_grad, means_grad, widths_grad, scale_grad, shift_grad


def snake_ring(chips_x, chips_other):
    if chips_x == 2 and chips_other >= 2:
        return [2 * z for z in range(chips_other)] + [
            2 * z + 1 for z in reversed(range(chips_other))
        ]
    return list(range(chips_x * chips_other))


class Ring:
    def __init__(self, order):
        self.order = order
        self.n = len(order)
        pos = np.zeros(self.n, np.int32)
        for i, c in enumerate(order):
            pos[c] = i
        self.pos = pos
        self.cw = [(order[i], order[(i + 1) % self.n]) for i in range(self.n)]
        self.ccw = [(order[i], order[(i - 1) % self.n]) for i in range(self.n)]

    def here(self):
        chip = lax.axis_index("chip")
        core = lax.axis_index("core")
        return chip, core, jnp.asarray(self.pos)[chip]

    def chip_at(self, position):
        return jnp.asarray(np.array(self.order, np.int32))[position % self.n]


SWAP = [(0, 1), (1, 0)]


def _halves(x, axis):
    size = x.shape[axis] // 2
    return (
        lax.slice_in_dim(x, 0, size, axis=axis),
        lax.slice_in_dim(x, size, 2 * size, axis=axis),
    )


def ring_gather(ring, pieces, chips):
    if ring is None:
        return [
            lax.all_gather(x, ("chip", "core"), axis=0, tiled=False).reshape((chips, 2) + x.shape)
            for x, _ in pieces
        ]
    chip, core, p = ring.here()
    n = ring.n
    bufs, fronts = [], []
    for x, axis in pieces:
        buf = jnp.zeros((n, 2) + x.shape, x.dtype)
        buf = lax.dynamic_update_slice(buf, x[None, None], (chip, core) + (0,) * x.ndim)
        bufs.append(buf)
        if axis is None:
            fronts.append([x, None])
        else:
            fronts.append(list(_halves(x, axis)))
    partner = lax.ppermute([x for x, _ in pieces], "core", SWAP)
    for i, x in enumerate(partner):
        bufs[i] = lax.dynamic_update_slice(
            bufs[i], x[None, None], (chip, 1 - core) + (0,) * x.ndim
        )
    for step in range(1, n):
        going = [f[0] for f in fronts]
        coming = [f[1] for f in fronts if f[1] is not None]
        going = lax.ppermute(going, "chip", ring.cw)
        coming = lax.ppermute(coming, "chip", ring.ccw) if coming else []
        from_cw = ring.chip_at(p - step)
        from_ccw = ring.chip_at(p + step)
        both = lax.ppermute([going, coming], "core", SWAP)
        j = 0
        for i, (x, axis) in enumerate(pieces):
            fronts[i][0] = going[i]
            parts = [(going[i], both[0][i], from_cw, 0)]
            if axis is not None:
                fronts[i][1] = coming[j]
                parts.append((coming[j], both[1][j], from_ccw, x.shape[axis] // 2))
                j += 1
            for mine, theirs, source, offset in parts:
                start = [0] * x.ndim
                if axis is not None:
                    start[axis] = offset
                bufs[i] = lax.dynamic_update_slice(
                    bufs[i], mine[None, None], (source, core) + tuple(start)
                )
                bufs[i] = lax.dynamic_update_slice(
                    bufs[i], theirs[None, None], (source, 1 - core) + tuple(start)
                )
    return bufs


def ring_reduce_steps(ring, pieces, send=jnp.bfloat16):
    if ring is None:
        owned = []
        for g, _ in pieces:
            flat = g.reshape((-1,) + g.shape[3:])
            part = lax.psum_scatter(flat, ("chip", "core"), scatter_dimension=0, tiled=True)
            owned.append(lax.psum(part.astype(send), "rep").astype(jnp.float32))
        yield owned
        return owned
    chip, core, p = ring.here()
    n = ring.n
    mine, theirs = [], []
    for g, _ in pieces:
        mine.append(lax.dynamic_index_in_dim(g, core, axis=1, keepdims=False))
        theirs.append(lax.dynamic_index_in_dim(g, 1 - core, axis=1, keepdims=False).astype(send))
    got = lax.ppermute(theirs, "core", SWAP)
    yield got
    flows = []
    for i, (g, way) in enumerate(pieces):
        if way == "both":
            flows.append((i, 1, n // 2, mine[i], got[i]))
            flows.append((i, -1, (n - 1) // 2, mine[i], got[i]))
        elif isinstance(way, tuple):
            axis = way[1] + 1
            for d, (m, t) in zip((1, -1), zip(_halves(mine[i], axis), _halves(got[i], axis))):
                flows.append((i, d, n - 1, m, t))
        else:
            flows.append((i, way, n - 1, mine[i], got[i]))

    def contribution(m, t, position):
        at = ring.chip_at(position)
        own = lax.dynamic_index_in_dim(m, at, axis=0, keepdims=False)
        other = lax.dynamic_index_in_dim(t, at, axis=0, keepdims=False)
        return own + other.astype(jnp.float32)

    acc = [contribution(m, t, p + d * hops) for _, d, hops, m, t in flows]
    for step in range(1, max(f[2] for f in flows) + 1):
        moved = []
        for d in (1, -1):
            chosen = [k for k, f in enumerate(flows) if f[1] == d and f[2] >= step]
            if chosen:
                out = lax.ppermute([acc[k].astype(send) for k in chosen], "chip", ring.cw if d == 1 else ring.ccw)
                for k, o in zip(chosen, out):
                    acc[k] = o.astype(jnp.float32)
                moved.extend(out)
        yield moved
        for k, (_, d, hops, m, t) in enumerate(flows):
            if hops > step:
                acc[k] = acc[k] + contribution(m, t, p + d * (hops - step))
    owned = []
    for i, (g, way) in enumerate(pieces):
        parts = [(a, f) for a, f in zip(acc, flows) if f[0] == i]
        if way == "both":
            total = contribution(parts[0][1][3], parts[0][1][4], p) + parts[0][0] + parts[1][0]
        else:
            total = [a + contribution(f[3], f[4], p) for a, f in parts]
            total = total[0] if len(total) == 1 else jnp.concatenate(total, axis=way[1])
        owned.append(total)
    other = lax.ppermute([o.astype(send) for o in owned], "rep", SWAP)
    yield other
    return [o + t.astype(jnp.float32) for o, t in zip(owned, other)]


class Stepper:
    def __init__(self, gen):
        self.gen = gen
        self.result = None
        self.over = False

    def tie(self, value):
        if self.over:
            return value
        try:
            ready = next(self.gen)
        except StopIteration as done:
            self.result, self.over = done.value, True
            return value
        _, value = lax.optimization_barrier((ready, value))
        return value

    def finish(self):
        if not self.over:
            self.result, self.over = run_steps(self.gen), True
        return self.result


def run_steps(gen):
    while True:
        try:
            next(gen)
        except StopIteration as done:
            return done.value


SMALL_ROWS, SMALL_LANES = 16, 768


def small_layout(fsdp):
    d = 768 // fsdp
    sizes = [2 * d, 6 * d, 3072 // fsdp, 128 // fsdp, 128 // fsdp, 4096 // fsdp, 4096 // fsdp, (128 // fsdp) * 32]
    offsets, at = [], 0
    for size in sizes:
        offsets.append((at, size))
        at += size
    assert at <= SMALL_ROWS * SMALL_LANES
    return offsets


def pack_small(parts):
    flat = jnp.concatenate([part.reshape(-1) for part in parts])
    flat = jnp.pad(flat, (0, SMALL_ROWS * SMALL_LANES - flat.shape[0]))
    return flat.reshape(SMALL_ROWS, SMALL_LANES)


def unpack_small_full(gathered, offsets, fsdp):
    flat = gathered.reshape(fsdp, -1).astype(jnp.float32)
    take = [flat[:, at : at + size] for at, size in offsets]
    d = 768 // fsdp
    return [
        take[0].reshape(fsdp, 2, d).transpose(1, 0, 2).reshape(2, -1),
        take[1].reshape(fsdp, 6, d).transpose(1, 0, 2).reshape(6, -1),
        take[2].reshape(-1),
        take[3].reshape(-1),
        take[4].reshape(-1),
        take[5].reshape(ATOM_TYPES, ATOM_TYPES),
        take[6].reshape(ATOM_TYPES, ATOM_TYPES),
        take[7].reshape(-1, 32),
    ]


def pack_small_grads(grads, fsdp, chips):
    d = 768 // fsdp
    blocks = [
        grads[0].reshape(2, fsdp, d).transpose(1, 0, 2),
        grads[1].reshape(6, fsdp, d).transpose(1, 0, 2),
    ] + [g.reshape(-1) for g in grads[2:]]
    flat = jnp.concatenate([blk.reshape(fsdp, -1) for blk in blocks], axis=1)
    flat = jnp.pad(flat, ((0, 0), (0, SMALL_ROWS * SMALL_LANES - flat.shape[1])))
    return flat.reshape(chips, 2, SMALL_ROWS, SMALL_LANES)


def unpack_small_owned(block, offsets):
    flat = block.reshape(-1)
    take = [flat[at : at + size] for at, size in offsets]
    return [
        take[0].reshape(2, -1),
        take[1].reshape(6, -1),
        take[2],
        take[3],
        take[4],
        take[5],
        take[6],
        take[7].reshape(-1, 32),
    ]


def make_body(ring, chips):
    fsdp = 2 * chips

    def body(
        inputs,
        times,
        positions,
        atom_types,
        molecule_ids,
        pad_mask,
        cotangent,
        norm_gains,
        bias_rows,
        up_bias,
        input_weight,
        output_weight,
        up_weight,
        down_weight,
        kernel_means,
        kernel_widths,
        pair_scale,
        pair_shift,
        kernel_heads,
    ):
        offsets = small_layout(fsdp)
        small = pack_small(
            [norm_gains, bias_rows, up_bias, kernel_means, kernel_widths, pair_scale, pair_shift, kernel_heads]
        )
        width = input_weight.shape[0]
        first = jnp.concatenate([small.reshape(-1, width), input_weight.T], axis=0)
        second = jnp.concatenate(
            [output_weight.T, up_weight.T, down_weight.T.reshape(-1, width)], axis=0
        )
        first_all = lax.all_gather(first, ("chip", "core"), axis=0, tiled=False)
        second_all = lax.all_gather(second, ("chip", "core"), axis=0, tiled=False)
        small_rows = small.size // width
        params = unpack_small_full(first_all[:, :small_rows], offsets, fsdp)
        in_t = first_all[:, small_rows:].reshape(-1, width)
        out_rows = output_weight.shape[1]
        up_rows = up_weight.shape[1]
        out_t = second_all[:, :out_rows].reshape(-1, width)
        up_t = second_all[:, out_rows : out_rows + up_rows].reshape(-1, width)
        down_t = (
            second_all[:, out_rows + up_rows :]
            .reshape(fsdp, down_weight.shape[1], -1)
            .reshape(-1, down_weight.shape[0])
        )
        gains_now, biases_now, up_shift = params[0], params[1], params[2]
        tables = (params[3], params[4], params[5], params[6])
        heads_full = params[7].astype(jnp.bfloat16)

        row_count = inputs.shape[0]
        model_width = inputs.shape[1]
        head_count = heads_full.shape[1]
        head_size = model_width // head_count
        block_rows = min(128, row_count)
        blocks = row_count // block_rows
        tile_rows = min(128, block_rows)
        nt = (((1,), (1,)), ((), ()))
        tn = (((0,), (0,)), ((), ()))

        stream = inputs.astype(jnp.float32) + time_embedding(times, model_width)
        normed_out, normed_one, inv_one = layer_norm(stream, gains_now[0], biases_now[0])
        act_one = normed_out.astype(jnp.bfloat16)
        qkv_shift = jnp.concatenate([biases_now[2], jnp.zeros_like(biases_now[2]), biases_now[3]])
        projected = (
            lax.dot_general(act_one, in_t, nt, preferred_element_type=jnp.float32) + qkv_shift
        ).astype(jnp.bfloat16)
        split_shape = (blocks, block_rows, head_count, head_size)
        queries = projected[:, :model_width].reshape(split_shape)
        key_rows = projected[:, model_width : 2 * model_width].reshape(split_shape)
        value_rows = projected[:, 2 * model_width :].reshape(split_shape)
        pos_blocks = jnp.transpose(positions.reshape(3, blocks, block_rows), (1, 0, 2))
        type_blocks = atom_types.reshape(blocks, block_rows)
        mol_blocks = molecule_ids.reshape(blocks, block_rows)
        pad_blocks = pad_mask.reshape(blocks, block_rows)
        fwd = [
            block_forward(
                (queries[b], key_rows[b], value_rows[b], pos_blocks[b], type_blocks[b], mol_blocks[b], pad_blocks[b]),
                tables=tables,
                kernel_heads=heads_full,
                tile_rows=tile_rows,
            )
            for b in range(blocks)
        ]
        attended = jnp.stack([f[0] for f in fwd])
        log_sums = [f[1] for f in fwd]
        attended_low = attended.reshape(row_count, model_width).astype(jnp.bfloat16)
        mid = stream + (
            lax.dot_general(attended_low, out_t, nt, preferred_element_type=jnp.float32)
            + biases_now[4]
        )
        normed_out_two, normed_two, inv_two = layer_norm(mid, gains_now[1], biases_now[1])
        act_two = normed_out_two.astype(jnp.bfloat16)
        hidden_pre = (
            lax.dot_general(act_two, up_t, nt, preferred_element_type=jnp.float32) + up_shift
        )
        hidden_low = gelu_value(hidden_pre).astype(jnp.bfloat16)
        final = mid + (
            lax.dot_general(hidden_low, down_t, nt, preferred_element_type=jnp.float32)
            + biases_now[5]
        )
        rows_out = final.astype(jnp.bfloat16)

        grad_final = cotangent.astype(jnp.float32)
        down_grad_t = lax.dot_general(cotangent, hidden_low, tn, preferred_element_type=jnp.float32)
        grad_hidden = jnp.dot(cotangent, down_t, preferred_element_type=jnp.float32) * gelu_slope(
            hidden_pre
        )
        grad_hidden_low = grad_hidden.astype(jnp.bfloat16)
        up_grad_t = lax.dot_general(grad_hidden_low, act_two, tn, preferred_element_type=jnp.float32)
        up_bias_grad = jnp.sum(grad_hidden_low.astype(jnp.float32), axis=0)
        grad_act_two = jnp.dot(grad_hidden_low, up_t, preferred_element_type=jnp.float32)
        grad_norm_two, gain_two_grad, shift_two_grad = norm_backward(
            grad_act_two, normed_two, inv_two, gains_now[1]
        )
        grad_mid = grad_final + grad_norm_two
        grad_branch_low = grad_mid.astype(jnp.bfloat16)
        out_grad_t = lax.dot_general(
            grad_branch_low, attended_low, tn, preferred_element_type=jnp.float32
        )
        late_rows = jnp.concatenate(
            [
                out_grad_t.reshape(chips, 2, -1, model_width),
                up_grad_t.reshape(chips, 2, -1, model_width),
            ],
            axis=2,
        )
        late = ring_reduce_steps(
            ring, [(late_rows, "both"), (down_grad_t.reshape((chips, 2, -1) + down_grad_t.shape[1:]), "both")]
        )
        grad_attended = jnp.dot(grad_branch_low, out_t, preferred_element_type=jnp.float32).astype(
            jnp.bfloat16
        )
        kernel_count = tables[0].shape[0]
        start_sums = (
            jnp.zeros((kernel_count, head_count), jnp.float32),
            jnp.zeros((kernel_count,), jnp.float32),
            jnp.zeros((kernel_count,), jnp.float32),
            jnp.zeros((ATOM_TYPES, ATOM_TYPES), jnp.float32),
            jnp.zeros((ATOM_TYPES, ATOM_TYPES), jnp.float32),
        )
        kernel_sums = start_sums
        q_grads, k_grads, v_grads = [], [], []
        grad_attended_blocks = grad_attended.reshape(split_shape)
        stepper = Stepper(late)
        q_grads, k_grads, v_grads, score_grads = [], [], [], []
        for b in range(blocks):
            gate = stepper.tie(grad_attended_blocks[b])
            qg, kg, vg, sg_b = attention_grads(
                (
                    queries[b],
                    key_rows[b],
                    value_rows[b],
                    gate,
                    log_sums[b],
                    pos_blocks[b],
                    type_blocks[b],
                    mol_blocks[b],
                    pad_blocks[b],
                ),
                tables,
                heads_full,
                hook=stepper.tie,
            )
            q_grads.append(qg)
            k_grads.append(kg)
            v_grads.append(vg)
            score_grads.append(sg_b)
        queries_grad = jnp.stack(q_grads)
        keys_grad = jnp.stack(k_grads)
        values_grad = jnp.stack(v_grads)
        grad_projected = jnp.concatenate(
            [
                queries_grad.reshape(row_count, model_width),
                keys_grad.reshape(row_count, model_width),
                values_grad.reshape(row_count, model_width),
            ],
            axis=1,
        ).astype(jnp.bfloat16)
        in_grad_t = lax.dot_general(grad_projected, act_one, tn, preferred_element_type=jnp.float32)
        in_stepper = Stepper(
            ring_reduce_steps(ring, [(in_grad_t.reshape((chips, 2, -1) + in_grad_t.shape[1:]), "both")])
        )
        kernel_sums = start_sums
        for b in range(blocks):
            kernel_sums = kernel_grads(
                kernel_sums,
                in_stepper.tie(score_grads[b]),
                pos_blocks[b],
                type_blocks[b],
                tables,
                heads_full,
            )
        grad_act_one = jnp.dot(grad_projected, in_t, preferred_element_type=jnp.float32)
        grad_norm_one, gain_one_grad, shift_one_grad = norm_backward(
            grad_act_one, normed_one, inv_one, gains_now[0]
        )
        inputs_grad = grad_mid + grad_norm_one
        projected_sums = jnp.sum(grad_projected.astype(jnp.float32), axis=0)
        heads_grad, means_grad, widths_grad, scale_grad, shift_grad = kernel_sums
        small_grads = [
            jnp.stack([gain_one_grad, gain_two_grad]),
            jnp.stack(
                [
                    shift_one_grad,
                    shift_two_grad,
                    projected_sums[:model_width],
                    projected_sums[2 * model_width :],
                    jnp.sum(grad_branch_low.astype(jnp.float32), axis=0),
                    jnp.sum(grad_final, axis=0),
                ]
            ),
            up_bias_grad,
            means_grad,
            widths_grad,
            scale_grad,
            shift_grad,
            heads_grad,
        ]
        late_owned = stepper.finish()
        out_owned = late_owned[0][:out_rows]
        up_owned = late_owned[0][out_rows:]
        down_owned = late_owned[1]
        (small_owned,) = run_steps(
            ring_reduce_steps(ring, [(pack_small_grads(small_grads, fsdp, chips), "both")])
        )
        (in_owned,) = in_stepper.finish()
        sg = unpack_small_owned(small_owned, offsets)
        return (
            rows_out,
            inputs_grad,
            sg[0],
            sg[1],
            sg[2],
            in_owned.T,
            out_owned.T,
            up_owned.T,
            down_owned.T,
            sg[3],
            sg[4],
            sg[5],
            sg[6],
            sg[7],
        )

    return body


def solution(mesh):
    reps, fsdp = mesh.devices.shape
    chips = fsdp // 2
    grid = Mesh(mesh.devices.reshape(reps, chips, 2), ("rep", "chip", "core"))
    chips_x = 1
    try:
        coords = [tuple(d.coords) for d in mesh.devices[0, ::2]]
        xs = sorted({c[0] for c in coords})
        chips_x = len(xs)
        flat_ok = all(
            coords[i][0] == xs[i % chips_x] for i in range(chips)
        )
        if not flat_ok:
            chips_x = 1
    except Exception:
        chips_x = 1
    ring = None
    if chips <= 8:
        ring = Ring(snake_ring(chips_x, chips // chips_x))
    atoms = ("rep", "chip", "core")
    cols = ("chip", "core")
    placed = (
        P(atoms, None),
        P(atoms),
        P(None, atoms),
        P(atoms),
        P(atoms),
        P(atoms),
        P(atoms, None),
        P(None, cols),
        P(None, cols),
        P(cols),
        P(None, cols),
        P(None, cols),
        P(None, cols),
        P(None, cols),
        P(cols),
        P(cols),
        P(cols),
        P(cols),
        P(cols, None),
    )
    return jax.shard_map(
        make_body(ring, chips),
        mesh=grid,
        in_specs=placed,
        out_specs=(
            P(atoms, None),
            P(atoms, None),
            P(None, cols),
            P(None, cols),
            P(cols),
            P(None, cols),
            P(None, cols),
            P(None, cols),
            P(None, cols),
            P(cols),
            P(cols),
            P(cols),
            P(cols),
            P(cols, None),
        ),
        check_vma=False,
    )
```

```python
from functools import partial
import math

import jax
import jax.numpy as jnp
from jax import lax
from jax.sharding import Mesh, PartitionSpec as P
import numpy as np

ATOM_TYPES = 64


epsilon = 1e-05
masked_score = -1000000000.0
time_scale = 1000.0
root_two_pi = math.sqrt(2.0 * math.pi)
highest = lax.Precision.HIGHEST


def time_embedding(times, model_width):
    half_width = model_width // 2
    counter = jnp.arange(half_width, dtype=jnp.float32)
    frequency = jnp.exp(counter * (-math.log(10000.0) / half_width))
    angles = (time_scale * times)[:, None] * frequency[None, :]
    return jnp.concatenate([jnp.sin(angles), jnp.cos(angles)], axis=1)


def layer_norm(values, gain_row, shift_row):
    center = values - jnp.mean(values, axis=1, keepdims=True)
    inv_std = lax.rsqrt(jnp.mean(center * center, axis=1, keepdims=True) + epsilon)
    normed = center * inv_std
    return (normed * gain_row + shift_row, normed, inv_std)


def norm_backward(grad_out, normed, inv_std, gain_row):
    grad_normed = grad_out * gain_row
    first_mean = jnp.mean(grad_normed, axis=1, keepdims=True)
    second_mean = jnp.mean(grad_normed * normed, axis=1, keepdims=True)
    grad_input = inv_std * (grad_normed - first_mean - normed * second_mean)
    return (grad_input, jnp.sum(grad_out * normed, axis=0), jnp.sum(grad_out, axis=0))


def gelu_value(values):
    return values * (0.5 + 0.5 * lax.erf(values * math.sqrt(0.5)))


def gelu_slope(values):
    return (
        0.5
        + 0.5 * lax.erf(values * math.sqrt(0.5))
        + values * jnp.exp(-0.5 * values * values) / root_two_pi
    )


def pair_terms(pos_rows, pos_cols, type_rows, type_cols, tables):
    kernel_means, kernel_widths, scale_table, shift_table = tables
    offsets = pos_rows[:, :, None] - pos_cols[:, None, :]
    distance = jnp.sqrt(jnp.sum(offsets * offsets, axis=0))
    type_range = jnp.arange(ATOM_TYPES, dtype=jnp.int32)
    hot_rows = (type_rows[:, None] == type_range[None, :]).astype(jnp.float32)
    hot_cols = (type_cols[:, None] == type_range[None, :]).astype(jnp.float32)
    scale_pair = jnp.dot(
        jnp.dot(hot_rows, scale_table, precision=highest), hot_cols.T, precision=highest
    )
    shift_pair = jnp.dot(
        jnp.dot(hot_rows, shift_table, precision=highest), hot_cols.T, precision=highest
    )
    stretched = scale_pair * distance + shift_pair
    kernel_gap = (stretched[:, :, None] - kernel_means) / kernel_widths
    kernels = jnp.exp(-0.5 * kernel_gap * kernel_gap) / (root_two_pi * kernel_widths)
    return (distance, hot_rows, hot_cols, kernel_gap, kernels)


def allowed_pairs(row_ids, col_ids, mol_rows, mol_cols, pad_cols):
    same_mol = mol_rows[:, None] == mol_cols[None, :]
    key_live = (pad_cols[None, :] == 1) | (row_ids[:, None] == col_ids[None, :])
    return same_mol & key_live


def tile_scores(q_tile, key_block, kernels_low, kernel_heads, allowed, score_scale):
    pair_bias = jnp.einsum(
        "ijk,kh->hij", kernels_low, kernel_heads, preferred_element_type=jnp.float32
    )
    raw_scores = jnp.einsum("ihd,jhd->hij", q_tile, key_block, preferred_element_type=jnp.float32)
    return jnp.where(allowed[None], raw_scores * score_scale + pair_bias, masked_score)


def block_forward(pieces, tables, kernel_heads, tile_rows):
    queries, key_block, value_block, positions, types, mols, pads = pieces
    block_rows = queries.shape[0]
    score_scale = 1.0 / math.sqrt(queries.shape[2])
    col_ids = jnp.arange(block_rows, dtype=jnp.int32)

    def one_tile(running, tile_index):
        first_row = tile_index * tile_rows
        row_ids = first_row + jnp.arange(tile_rows, dtype=jnp.int32)
        terms = pair_terms(positions, positions, types, types, tables)
        kernels_low = terms[4].astype(jnp.bfloat16)
        allowed = allowed_pairs(row_ids, col_ids, mols, mols, pads)
        scores = tile_scores(queries, key_block, kernels_low, kernel_heads, allowed, score_scale)
        row_max = jnp.max(scores, axis=2, keepdims=True)
        exponent = jnp.exp(scores - row_max)
        row_sum = jnp.sum(exponent, axis=2, keepdims=True)
        probs = exponent / row_sum
        attended = jnp.einsum(
            "hij,jhd->ihd", probs.astype(jnp.bfloat16), value_block, preferred_element_type=jnp.float32
        )
        return (running, (attended, probs))

    count = block_rows // tile_rows
    if count == 1:
        _, (attended, probs) = one_tile(None, 0)
        return (attended.reshape(block_rows, -1), probs)
    _, (attended, log_sums) = lax.scan(one_tile, None, jnp.arange(count, dtype=jnp.int32))
    attended = attended.reshape(block_rows, -1)
    log_sums = jnp.transpose(log_sums, (1, 0, 2)).reshape(log_sums.shape[1], block_rows)
    return (attended, log_sums)


def block_backward(running, pieces, tables, kernel_heads, tile_rows, hook=None):
    queries, key_block, value_block, grad_attended, log_sums, positions, types, mols, pads = pieces
    kernel_widths = tables[1]
    block_rows = queries.shape[0]
    score_scale = 1.0 / math.sqrt(queries.shape[2])
    col_ids = jnp.arange(block_rows, dtype=jnp.int32)

    def one_tile(partial_sums, tile_index):
        keys_grad, values_grad, heads_grad, means_grad, widths_grad, scale_grad, shift_grad = (
            partial_sums
        )
        first_row = tile_index * tile_rows
        row_ids = first_row + jnp.arange(tile_rows, dtype=jnp.int32)
        distance, hot_rows, hot_cols, kernel_gap, kernels = pair_terms(
            positions, positions, types, types, tables
        )
        kernels_low = kernels.astype(jnp.bfloat16)
        attn_probs = log_sums
        grad_probs = jnp.einsum(
            "ihd,jhd->hij", grad_attended, value_block, preferred_element_type=jnp.float32
        )
        values_grad = values_grad + jnp.einsum(
            "hij,ihd->jhd",
            attn_probs.astype(jnp.bfloat16),
            grad_attended,
            preferred_element_type=jnp.float32,
        )
        probs_dot = jnp.sum(attn_probs * grad_probs, axis=2, keepdims=True)
        grad_scores = (attn_probs * (grad_probs - probs_dot)).astype(jnp.bfloat16)
        if hook is not None:
            grad_scores = hook(grad_scores)
        query_grad = (
            jnp.einsum("hij,jhd->ihd", grad_scores, key_block, preferred_element_type=jnp.float32)
            * score_scale
        )
        keys_grad = (
            keys_grad
            + jnp.einsum("hij,ihd->jhd", grad_scores, queries, preferred_element_type=jnp.float32)
            * score_scale
        )
        heads_grad = heads_grad + jnp.einsum(
            "ijk,hij->kh", kernels_low, grad_scores, preferred_element_type=jnp.float32
        )
        grad_kernels = jnp.einsum(
            "hij,kh->ijk", grad_scores, kernel_heads, preferred_element_type=jnp.float32
        )
        spread = grad_kernels * kernels
        mean_part = spread * kernel_gap / kernel_widths
        means_grad = means_grad + jnp.sum(mean_part, axis=(0, 1))
        widths_grad = widths_grad + jnp.sum(
            spread * (kernel_gap * kernel_gap - 1.0) / kernel_widths, axis=(0, 1)
        )
        grad_stretched = -jnp.sum(mean_part, axis=2)
        scale_grad = scale_grad + jnp.dot(
            jnp.dot(hot_rows.T, grad_stretched * distance, precision=highest),
            hot_cols,
            precision=highest,
        )
        shift_grad = shift_grad + jnp.dot(
            jnp.dot(hot_rows.T, grad_stretched, precision=highest), hot_cols, precision=highest
        )
        return (
            (keys_grad, values_grad, heads_grad, means_grad, widths_grad, scale_grad, shift_grad),
            query_grad,
        )

    zero_block = jnp.zeros(key_block.shape, jnp.float32)
    count = block_rows // tile_rows
    if count == 1:
        sums_out, query_grads = one_tile((zero_block, zero_block) + tuple(running), 0)
        return (sums_out[2:], (query_grads.reshape(key_block.shape), sums_out[0], sums_out[1]))
    sums_out, query_grads = lax.scan(
        one_tile, (zero_block, zero_block) + tuple(running), jnp.arange(count, dtype=jnp.int32)
    )
    query_grads = query_grads.reshape(key_block.shape)
    return (sums_out[2:], (query_grads, sums_out[0], sums_out[1]))


def snake_ring(chips_x, chips_other):
    if chips_x == 2 and chips_other >= 2:
        return [2 * z for z in range(chips_other)] + [
            2 * z + 1 for z in reversed(range(chips_other))
        ]
    return list(range(chips_x * chips_other))


class Ring:
    def __init__(self, order):
        self.order = order
        self.n = len(order)
        pos = np.zeros(self.n, np.int32)
        for i, c in enumerate(order):
            pos[c] = i
        self.pos = pos
        self.cw = [(order[i], order[(i + 1) % self.n]) for i in range(self.n)]
        self.ccw = [(order[i], order[(i - 1) % self.n]) for i in range(self.n)]

    def here(self):
        chip = lax.axis_index("chip")
        core = lax.axis_index("core")
        return chip, core, jnp.asarray(self.pos)[chip]

    def chip_at(self, position):
        return jnp.asarray(np.array(self.order, np.int32))[position % self.n]


SWAP = [(0, 1), (1, 0)]


def _halves(x, axis):
    size = x.shape[axis] // 2
    return (
        lax.slice_in_dim(x, 0, size, axis=axis),
        lax.slice_in_dim(x, size, 2 * size, axis=axis),
    )


def ring_gather(ring, pieces, chips):
    if ring is None:
        return [
            lax.all_gather(x, ("chip", "core"), axis=0, tiled=False).reshape((chips, 2) + x.shape)
            for x, _ in pieces
        ]
    chip, core, p = ring.here()
    n = ring.n
    bufs, fronts = [], []
    for x, axis in pieces:
        buf = jnp.zeros((n, 2) + x.shape, x.dtype)
        buf = lax.dynamic_update_slice(buf, x[None, None], (chip, core) + (0,) * x.ndim)
        bufs.append(buf)
        if axis is None:
            fronts.append([x, None])
        else:
            fronts.append(list(_halves(x, axis)))
    partner = lax.ppermute([x for x, _ in pieces], "core", SWAP)
    for i, x in enumerate(partner):
        bufs[i] = lax.dynamic_update_slice(
            bufs[i], x[None, None], (chip, 1 - core) + (0,) * x.ndim
        )
    for step in range(1, n):
        going = [f[0] for f in fronts]
        coming = [f[1] for f in fronts if f[1] is not None]
        going = lax.ppermute(going, "chip", ring.cw)
        coming = lax.ppermute(coming, "chip", ring.ccw) if coming else []
        from_cw = ring.chip_at(p - step)
        from_ccw = ring.chip_at(p + step)
        both = lax.ppermute([going, coming], "core", SWAP)
        j = 0
        for i, (x, axis) in enumerate(pieces):
            fronts[i][0] = going[i]
            parts = [(going[i], both[0][i], from_cw, 0)]
            if axis is not None:
                fronts[i][1] = coming[j]
                parts.append((coming[j], both[1][j], from_ccw, x.shape[axis] // 2))
                j += 1
            for mine, theirs, source, offset in parts:
                start = [0] * x.ndim
                if axis is not None:
                    start[axis] = offset
                bufs[i] = lax.dynamic_update_slice(
                    bufs[i], mine[None, None], (source, core) + tuple(start)
                )
                bufs[i] = lax.dynamic_update_slice(
                    bufs[i], theirs[None, None], (source, 1 - core) + tuple(start)
                )
    return bufs


def ring_reduce_steps(ring, pieces, send=jnp.bfloat16):
    if ring is None:
        owned = []
        for g, _ in pieces:
            flat = g.reshape((-1,) + g.shape[3:])
            part = lax.psum_scatter(flat, ("chip", "core"), scatter_dimension=0, tiled=True)
            owned.append(lax.psum(part.astype(send), "rep").astype(jnp.float32))
        yield owned
        return owned
    chip, core, p = ring.here()
    n = ring.n
    mine, theirs = [], []
    for g, _ in pieces:
        mine.append(lax.dynamic_index_in_dim(g, core, axis=1, keepdims=False))
        theirs.append(lax.dynamic_index_in_dim(g, 1 - core, axis=1, keepdims=False).astype(send))
    got = lax.ppermute(theirs, "core", SWAP)
    yield got
    flows = []
    for i, (g, way) in enumerate(pieces):
        if way == "both":
            flows.append((i, 1, n // 2, mine[i], got[i]))
            flows.append((i, -1, (n - 1) // 2, mine[i], got[i]))
        elif isinstance(way, tuple):
            axis = way[1] + 1
            for d, (m, t) in zip((1, -1), zip(_halves(mine[i], axis), _halves(got[i], axis))):
                flows.append((i, d, n - 1, m, t))
        else:
            flows.append((i, way, n - 1, mine[i], got[i]))

    def contribution(m, t, position):
        at = ring.chip_at(position)
        own = lax.dynamic_index_in_dim(m, at, axis=0, keepdims=False)
        other = lax.dynamic_index_in_dim(t, at, axis=0, keepdims=False)
        return own + other.astype(jnp.float32)

    acc = [contribution(m, t, p + d * hops) for _, d, hops, m, t in flows]
    for step in range(1, max(f[2] for f in flows) + 1):
        moved = []
        for d in (1, -1):
            chosen = [k for k, f in enumerate(flows) if f[1] == d and f[2] >= step]
            if chosen:
                out = lax.ppermute([acc[k].astype(send) for k in chosen], "chip", ring.cw if d == 1 else ring.ccw)
                for k, o in zip(chosen, out):
                    acc[k] = o.astype(jnp.float32)
                moved.extend(out)
        yield moved
        for k, (_, d, hops, m, t) in enumerate(flows):
            if hops > step:
                acc[k] = acc[k] + contribution(m, t, p + d * (hops - step))
    owned = []
    for i, (g, way) in enumerate(pieces):
        parts = [(a, f) for a, f in zip(acc, flows) if f[0] == i]
        if way == "both":
            total = contribution(parts[0][1][3], parts[0][1][4], p) + parts[0][0] + parts[1][0]
        else:
            total = [a + contribution(f[3], f[4], p) for a, f in parts]
            total = total[0] if len(total) == 1 else jnp.concatenate(total, axis=way[1])
        owned.append(total)
    other = lax.ppermute([o.astype(send) for o in owned], "rep", SWAP)
    yield other
    return [o + t.astype(jnp.float32) for o, t in zip(owned, other)]


class Stepper:
    def __init__(self, gen):
        self.gen = gen
        self.result = None
        self.over = False

    def tie(self, value):
        if self.over:
            return value
        try:
            ready = next(self.gen)
        except StopIteration as done:
            self.result, self.over = done.value, True
            return value
        _, value = lax.optimization_barrier((ready, value))
        return value

    def finish(self):
        if not self.over:
            self.result, self.over = run_steps(self.gen), True
        return self.result


def run_steps(gen):
    while True:
        try:
            next(gen)
        except StopIteration as done:
            return done.value


SMALL_ROWS, SMALL_LANES = 16, 768


def small_layout(fsdp):
    d = 768 // fsdp
    sizes = [2 * d, 6 * d, 3072 // fsdp, 128 // fsdp, 128 // fsdp, 4096 // fsdp, 4096 // fsdp, (128 // fsdp) * 32]
    offsets, at = [], 0
    for size in sizes:
        offsets.append((at, size))
        at += size
    assert at <= SMALL_ROWS * SMALL_LANES
    return offsets


def pack_small(parts):
    flat = jnp.concatenate([part.reshape(-1) for part in parts])
    flat = jnp.pad(flat, (0, SMALL_ROWS * SMALL_LANES - flat.shape[0]))
    return flat.reshape(SMALL_ROWS, SMALL_LANES)


def unpack_small_full(gathered, offsets, fsdp):
    flat = gathered.reshape(fsdp, -1).astype(jnp.float32)
    take = [flat[:, at : at + size] for at, size in offsets]
    d = 768 // fsdp
    return [
        take[0].reshape(fsdp, 2, d).transpose(1, 0, 2).reshape(2, -1),
        take[1].reshape(fsdp, 6, d).transpose(1, 0, 2).reshape(6, -1),
        take[2].reshape(-1),
        take[3].reshape(-1),
        take[4].reshape(-1),
        take[5].reshape(ATOM_TYPES, ATOM_TYPES),
        take[6].reshape(ATOM_TYPES, ATOM_TYPES),
        take[7].reshape(-1, 32),
    ]


def pack_small_grads(grads, fsdp, chips):
    d = 768 // fsdp
    blocks = [
        grads[0].reshape(2, fsdp, d).transpose(1, 0, 2),
        grads[1].reshape(6, fsdp, d).transpose(1, 0, 2),
    ] + [g.reshape(-1) for g in grads[2:]]
    flat = jnp.concatenate([blk.reshape(fsdp, -1) for blk in blocks], axis=1)
    flat = jnp.pad(flat, ((0, 0), (0, SMALL_ROWS * SMALL_LANES - flat.shape[1])))
    return flat.reshape(chips, 2, SMALL_ROWS, SMALL_LANES)


def unpack_small_owned(block, offsets):
    flat = block.reshape(-1)
    take = [flat[at : at + size] for at, size in offsets]
    return [
        take[0].reshape(2, -1),
        take[1].reshape(6, -1),
        take[2],
        take[3],
        take[4],
        take[5],
        take[6],
        take[7].reshape(-1, 32),
    ]


def make_body(ring, chips):
    fsdp = 2 * chips

    def body(
        inputs,
        times,
        positions,
        atom_types,
        molecule_ids,
        pad_mask,
        cotangent,
        norm_gains,
        bias_rows,
        up_bias,
        input_weight,
        output_weight,
        up_weight,
        down_weight,
        kernel_means,
        kernel_widths,
        pair_scale,
        pair_shift,
        kernel_heads,
    ):
        offsets = small_layout(fsdp)
        small = pack_small(
            [norm_gains, bias_rows, up_bias, kernel_means, kernel_widths, pair_scale, pair_shift, kernel_heads]
        )
        width = input_weight.shape[0]
        first = jnp.concatenate([small.reshape(-1, width), input_weight.T], axis=0)
        second = jnp.concatenate(
            [output_weight.T, up_weight.T, down_weight.T.reshape(-1, width)], axis=0
        )
        first_all = lax.all_gather(first, ("chip", "core"), axis=0, tiled=False)
        second_all = lax.all_gather(second, ("chip", "core"), axis=0, tiled=False)
        small_rows = small.size // width
        params = unpack_small_full(first_all[:, :small_rows], offsets, fsdp)
        in_t = first_all[:, small_rows:].reshape(-1, width)
        out_rows = output_weight.shape[1]
        up_rows = up_weight.shape[1]
        out_t = second_all[:, :out_rows].reshape(-1, width)
        up_t = second_all[:, out_rows : out_rows + up_rows].reshape(-1, width)
        down_t = (
            second_all[:, out_rows + up_rows :]
            .reshape(fsdp, down_weight.shape[1], -1)
            .reshape(-1, down_weight.shape[0])
        )
        gains_now, biases_now, up_shift = params[0], params[1], params[2]
        tables = (params[3], params[4], params[5], params[6])
        heads_full = params[7].astype(jnp.bfloat16)

        row_count = inputs.shape[0]
        model_width = inputs.shape[1]
        head_count = heads_full.shape[1]
        head_size = model_width // head_count
        block_rows = min(128, row_count)
        blocks = row_count // block_rows
        tile_rows = min(128, block_rows)
        nt = (((1,), (1,)), ((), ()))
        tn = (((0,), (0,)), ((), ()))

        stream = inputs.astype(jnp.float32) + time_embedding(times, model_width)
        normed_out, normed_one, inv_one = layer_norm(stream, gains_now[0], biases_now[0])
        act_one = normed_out.astype(jnp.bfloat16)
        qkv_shift = jnp.concatenate([biases_now[2], jnp.zeros_like(biases_now[2]), biases_now[3]])
        projected = (
            lax.dot_general(act_one, in_t, nt, preferred_element_type=jnp.float32) + qkv_shift
        ).astype(jnp.bfloat16)
        split_shape = (blocks, block_rows, head_count, head_size)
        queries = projected[:, :model_width].reshape(split_shape)
        key_rows = projected[:, model_width : 2 * model_width].reshape(split_shape)
        value_rows = projected[:, 2 * model_width :].reshape(split_shape)
        pos_blocks = jnp.transpose(positions.reshape(3, blocks, block_rows), (1, 0, 2))
        type_blocks = atom_types.reshape(blocks, block_rows)
        mol_blocks = molecule_ids.reshape(blocks, block_rows)
        pad_blocks = pad_mask.reshape(blocks, block_rows)
        fwd = [
            block_forward(
                (queries[b], key_rows[b], value_rows[b], pos_blocks[b], type_blocks[b], mol_blocks[b], pad_blocks[b]),
                tables=tables,
                kernel_heads=heads_full,
                tile_rows=tile_rows,
            )
            for b in range(blocks)
        ]
        attended = jnp.stack([f[0] for f in fwd])
        log_sums = [f[1] for f in fwd]
        attended_low = attended.reshape(row_count, model_width).astype(jnp.bfloat16)
        mid = stream + (
            lax.dot_general(attended_low, out_t, nt, preferred_element_type=jnp.float32)
            + biases_now[4]
        )
        normed_out_two, normed_two, inv_two = layer_norm(mid, gains_now[1], biases_now[1])
        act_two = normed_out_two.astype(jnp.bfloat16)
        hidden_pre = (
            lax.dot_general(act_two, up_t, nt, preferred_element_type=jnp.float32) + up_shift
        )
        hidden_low = gelu_value(hidden_pre).astype(jnp.bfloat16)
        final = mid + (
            lax.dot_general(hidden_low, down_t, nt, preferred_element_type=jnp.float32)
            + biases_now[5]
        )
        rows_out = final.astype(jnp.bfloat16)

        grad_final = cotangent.astype(jnp.float32)
        down_grad_t = lax.dot_general(cotangent, hidden_low, tn, preferred_element_type=jnp.float32)
        grad_hidden = jnp.dot(cotangent, down_t, preferred_element_type=jnp.float32) * gelu_slope(
            hidden_pre
        )
        grad_hidden_low = grad_hidden.astype(jnp.bfloat16)
        up_grad_t = lax.dot_general(grad_hidden_low, act_two, tn, preferred_element_type=jnp.float32)
        up_bias_grad = jnp.sum(grad_hidden_low.astype(jnp.float32), axis=0)
        grad_act_two = jnp.dot(grad_hidden_low, up_t, preferred_element_type=jnp.float32)
        grad_norm_two, gain_two_grad, shift_two_grad = norm_backward(
            grad_act_two, normed_two, inv_two, gains_now[1]
        )
        grad_mid = grad_final + grad_norm_two
        grad_branch_low = grad_mid.astype(jnp.bfloat16)
        out_grad_t = lax.dot_general(
            grad_branch_low, attended_low, tn, preferred_element_type=jnp.float32
        )
        late_rows = jnp.concatenate(
            [
                out_grad_t.reshape(chips, 2, -1, model_width),
                up_grad_t.reshape(chips, 2, -1, model_width),
            ],
            axis=2,
        )
        late = ring_reduce_steps(
            ring, [(late_rows, "both"), (down_grad_t.reshape((chips, 2, -1) + down_grad_t.shape[1:]), "both")]
        )
        grad_attended = jnp.dot(grad_branch_low, out_t, preferred_element_type=jnp.float32).astype(
            jnp.bfloat16
        )
        kernel_count = tables[0].shape[0]
        start_sums = (
            jnp.zeros((kernel_count, head_count), jnp.float32),
            jnp.zeros((kernel_count,), jnp.float32),
            jnp.zeros((kernel_count,), jnp.float32),
            jnp.zeros((ATOM_TYPES, ATOM_TYPES), jnp.float32),
            jnp.zeros((ATOM_TYPES, ATOM_TYPES), jnp.float32),
        )
        kernel_sums = start_sums
        q_grads, k_grads, v_grads = [], [], []
        grad_attended_blocks = grad_attended.reshape(split_shape)
        stepper = Stepper(late)
        for b in range(blocks):
            gate = stepper.tie(grad_attended_blocks[b])
            kernel_sums, (qg, kg, vg) = block_backward(
                kernel_sums,
                (
                    queries[b],
                    key_rows[b],
                    value_rows[b],
                    gate,
                    log_sums[b],
                    pos_blocks[b],
                    type_blocks[b],
                    mol_blocks[b],
                    pad_blocks[b],
                ),
                tables=tables,
                kernel_heads=heads_full,
                tile_rows=tile_rows,
                hook=stepper.tie,
            )
            q_grads.append(qg)
            k_grads.append(kg)
            v_grads.append(vg)
        queries_grad = jnp.stack(q_grads)
        keys_grad = jnp.stack(k_grads)
        values_grad = jnp.stack(v_grads)
        grad_projected = jnp.concatenate(
            [
                queries_grad.reshape(row_count, model_width),
                keys_grad.reshape(row_count, model_width),
                values_grad.reshape(row_count, model_width),
            ],
            axis=1,
        ).astype(jnp.bfloat16)
        in_grad_t = lax.dot_general(grad_projected, act_one, tn, preferred_element_type=jnp.float32)
        grad_act_one = jnp.dot(grad_projected, in_t, preferred_element_type=jnp.float32)
        grad_norm_one, gain_one_grad, shift_one_grad = norm_backward(
            grad_act_one, normed_one, inv_one, gains_now[0]
        )
        inputs_grad = grad_mid + grad_norm_one
        projected_sums = jnp.sum(grad_projected.astype(jnp.float32), axis=0)
        heads_grad, means_grad, widths_grad, scale_grad, shift_grad = kernel_sums
        small_grads = [
            jnp.stack([gain_one_grad, gain_two_grad]),
            jnp.stack(
                [
                    shift_one_grad,
                    shift_two_grad,
                    projected_sums[:model_width],
                    projected_sums[2 * model_width :],
                    jnp.sum(grad_branch_low.astype(jnp.float32), axis=0),
                    jnp.sum(grad_final, axis=0),
                ]
            ),
            up_bias_grad,
            means_grad,
            widths_grad,
            scale_grad,
            shift_grad,
            heads_grad,
        ]
        late_owned = stepper.finish()
        out_owned = late_owned[0][:out_rows]
        up_owned = late_owned[0][out_rows:]
        down_owned = late_owned[1]
        last = jnp.concatenate(
            [
                in_grad_t.reshape((chips, 2, -1) + in_grad_t.shape[1:]),
                pack_small_grads(small_grads, fsdp, chips),
            ],
            axis=2,
        )
        (last_owned,) = run_steps(ring_reduce_steps(ring, [(last, "both")]))
        in_rows = in_grad_t.shape[0] // fsdp
        in_owned = last_owned[:in_rows]
        small_owned = last_owned[in_rows:]
        sg = unpack_small_owned(small_owned, offsets)
        return (
            rows_out,
            inputs_grad,
            sg[0],
            sg[1],
            sg[2],
            in_owned.T,
            out_owned.T,
            up_owned.T,
            down_owned.T,
            sg[3],
            sg[4],
            sg[5],
            sg[6],
            sg[7],
        )

    return body


def solution(mesh):
    reps, fsdp = mesh.devices.shape
    chips = fsdp // 2
    grid = Mesh(mesh.devices.reshape(reps, chips, 2), ("rep", "chip", "core"))
    chips_x = 1
    try:
        coords = [tuple(d.coords) for d in mesh.devices[0, ::2]]
        xs = sorted({c[0] for c in coords})
        chips_x = len(xs)
        flat_ok = all(
            coords[i][0] == xs[i % chips_x] for i in range(chips)
        )
        if not flat_ok:
            chips_x = 1
    except Exception:
        chips_x = 1
    ring = None
    if chips <= 8:
        ring = Ring(snake_ring(chips_x, chips // chips_x))
    atoms = ("rep", "chip", "core")
    cols = ("chip", "core")
    placed = (
        P(atoms, None),
        P(atoms),
        P(None, atoms),
        P(atoms),
        P(atoms),
        P(atoms),
        P(atoms, None),
        P(None, cols),
        P(None, cols),
        P(cols),
        P(None, cols),
        P(None, cols),
        P(None, cols),
        P(None, cols),
        P(cols),
        P(cols),
        P(cols),
        P(cols),
        P(cols, None),
    )
    return jax.shard_map(
        make_body(ring, chips),
        mesh=grid,
        in_specs=placed,
        out_specs=(
            P(atoms, None),
            P(atoms, None),
            P(None, cols),
            P(None, cols),
            P(cols),
            P(None, cols),
            P(None, cols),
            P(None, cols),
            P(None, cols),
            P(cols),
            P(cols),
            P(cols),
            P(cols),
            P(cols, None),
        ),
        check_vma=False,
    )
```

```python
from functools import partial
import math

import jax
import jax.numpy as jnp
from jax import lax
from jax.sharding import Mesh, PartitionSpec as P
import numpy as np

ATOM_TYPES = 64


epsilon = 1e-05
masked_score = -1000000000.0
time_scale = 1000.0
root_two_pi = math.sqrt(2.0 * math.pi)
highest = lax.Precision.HIGHEST


def time_embedding(times, model_width):
    half_width = model_width // 2
    counter = jnp.arange(half_width, dtype=jnp.float32)
    frequency = jnp.exp(counter * (-math.log(10000.0) / half_width))
    angles = (time_scale * times)[:, None] * frequency[None, :]
    return jnp.concatenate([jnp.sin(angles), jnp.cos(angles)], axis=1)


def layer_norm(values, gain_row, shift_row):
    center = values - jnp.mean(values, axis=1, keepdims=True)
    inv_std = lax.rsqrt(jnp.mean(center * center, axis=1, keepdims=True) + epsilon)
    normed = center * inv_std
    return (normed * gain_row + shift_row, normed, inv_std)


def norm_backward(grad_out, normed, inv_std, gain_row):
    grad_normed = grad_out * gain_row
    first_mean = jnp.mean(grad_normed, axis=1, keepdims=True)
    second_mean = jnp.mean(grad_normed * normed, axis=1, keepdims=True)
    grad_input = inv_std * (grad_normed - first_mean - normed * second_mean)
    return (grad_input, jnp.sum(grad_out * normed, axis=0), jnp.sum(grad_out, axis=0))


def gelu_value(values):
    return values * (0.5 + 0.5 * lax.erf(values * math.sqrt(0.5)))


def gelu_slope(values):
    return (
        0.5
        + 0.5 * lax.erf(values * math.sqrt(0.5))
        + values * jnp.exp(-0.5 * values * values) / root_two_pi
    )


def pair_terms(pos_rows, pos_cols, type_rows, type_cols, tables):
    kernel_means, kernel_widths, scale_table, shift_table = tables
    offsets = pos_rows[:, :, None] - pos_cols[:, None, :]
    distance = jnp.sqrt(jnp.sum(offsets * offsets, axis=0))
    type_range = jnp.arange(ATOM_TYPES, dtype=jnp.int32)
    hot_rows = (type_rows[:, None] == type_range[None, :]).astype(jnp.float32)
    hot_cols = (type_cols[:, None] == type_range[None, :]).astype(jnp.float32)
    scale_pair = jnp.dot(
        jnp.dot(hot_rows, scale_table, precision=highest), hot_cols.T, precision=highest
    )
    shift_pair = jnp.dot(
        jnp.dot(hot_rows, shift_table, precision=highest), hot_cols.T, precision=highest
    )
    stretched = scale_pair * distance + shift_pair
    kernel_gap = (stretched[:, :, None] - kernel_means) / kernel_widths
    kernels = jnp.exp(-0.5 * kernel_gap * kernel_gap) / (root_two_pi * kernel_widths)
    return (distance, hot_rows, hot_cols, kernel_gap, kernels)


def allowed_pairs(row_ids, col_ids, mol_rows, mol_cols, pad_cols):
    same_mol = mol_rows[:, None] == mol_cols[None, :]
    key_live = (pad_cols[None, :] == 1) | (row_ids[:, None] == col_ids[None, :])
    return same_mol & key_live


def tile_scores(q_tile, key_block, kernels_low, kernel_heads, allowed, score_scale):
    pair_bias = jnp.einsum(
        "ijk,kh->hij", kernels_low, kernel_heads, preferred_element_type=jnp.float32
    )
    raw_scores = jnp.einsum("ihd,jhd->hij", q_tile, key_block, preferred_element_type=jnp.float32)
    return jnp.where(allowed[None], raw_scores * score_scale + pair_bias, masked_score)


def block_forward(pieces, tables, kernel_heads, tile_rows):
    queries, key_block, value_block, positions, types, mols, pads = pieces
    block_rows = queries.shape[0]
    score_scale = 1.0 / math.sqrt(queries.shape[2])
    col_ids = jnp.arange(block_rows, dtype=jnp.int32)

    def one_tile(running, tile_index):
        first_row = tile_index * tile_rows
        row_ids = first_row + jnp.arange(tile_rows, dtype=jnp.int32)
        terms = pair_terms(positions, positions, types, types, tables)
        kernels_low = terms[4].astype(jnp.bfloat16)
        allowed = allowed_pairs(row_ids, col_ids, mols, mols, pads)
        scores = tile_scores(queries, key_block, kernels_low, kernel_heads, allowed, score_scale)
        row_max = jnp.max(scores, axis=2, keepdims=True)
        exponent = jnp.exp(scores - row_max)
        row_sum = jnp.sum(exponent, axis=2, keepdims=True)
        probs_low = (exponent / row_sum).astype(jnp.bfloat16)
        attended = jnp.einsum(
            "hij,jhd->ihd", probs_low, value_block, preferred_element_type=jnp.float32
        )
        return (running, (attended, (row_max + jnp.log(row_sum))[:, :, 0]))

    count = block_rows // tile_rows
    if count == 1:
        _, (attended, log_sums) = one_tile(None, 0)
        return (attended.reshape(block_rows, -1), log_sums)
    _, (attended, log_sums) = lax.scan(one_tile, None, jnp.arange(count, dtype=jnp.int32))
    attended = attended.reshape(block_rows, -1)
    log_sums = jnp.transpose(log_sums, (1, 0, 2)).reshape(log_sums.shape[1], block_rows)
    return (attended, log_sums)


def block_backward(running, pieces, tables, kernel_heads, tile_rows, hook=None):
    queries, key_block, value_block, grad_attended, log_sums, positions, types, mols, pads = pieces
    kernel_widths = tables[1]
    block_rows = queries.shape[0]
    score_scale = 1.0 / math.sqrt(queries.shape[2])
    col_ids = jnp.arange(block_rows, dtype=jnp.int32)

    def one_tile(partial_sums, tile_index):
        keys_grad, values_grad, heads_grad, means_grad, widths_grad, scale_grad, shift_grad = (
            partial_sums
        )
        first_row = tile_index * tile_rows
        row_ids = first_row + jnp.arange(tile_rows, dtype=jnp.int32)
        distance, hot_rows, hot_cols, kernel_gap, kernels = pair_terms(
            positions, positions, types, types, tables
        )
        kernels_low = kernels.astype(jnp.bfloat16)
        allowed = allowed_pairs(row_ids, col_ids, mols, mols, pads)
        scores = tile_scores(queries, key_block, kernels_low, kernel_heads, allowed, score_scale)
        attn_probs = jnp.exp(scores - log_sums[:, :, None])
        grad_probs = jnp.einsum(
            "ihd,jhd->hij", grad_attended, value_block, preferred_element_type=jnp.float32
        )
        values_grad = values_grad + jnp.einsum(
            "hij,ihd->jhd",
            attn_probs.astype(jnp.bfloat16),
            grad_attended,
            preferred_element_type=jnp.float32,
        )
        probs_dot = jnp.sum(attn_probs * grad_probs, axis=2, keepdims=True)
        grad_scores = (attn_probs * (grad_probs - probs_dot)).astype(jnp.bfloat16)
        if hook is not None:
            grad_scores = hook(grad_scores)
        query_grad = (
            jnp.einsum("hij,jhd->ihd", grad_scores, key_block, preferred_element_type=jnp.float32)
            * score_scale
        )
        keys_grad = (
            keys_grad
            + jnp.einsum("hij,ihd->jhd", grad_scores, queries, preferred_element_type=jnp.float32)
            * score_scale
        )
        heads_grad = heads_grad + jnp.einsum(
            "ijk,hij->kh", kernels_low, grad_scores, preferred_element_type=jnp.float32
        )
        grad_kernels = jnp.einsum(
            "hij,kh->ijk", grad_scores, kernel_heads, preferred_element_type=jnp.float32
        )
        spread = grad_kernels * kernels
        mean_part = spread * kernel_gap / kernel_widths
        means_grad = means_grad + jnp.sum(mean_part, axis=(0, 1))
        widths_grad = widths_grad + jnp.sum(
            spread * (kernel_gap * kernel_gap - 1.0) / kernel_widths, axis=(0, 1)
        )
        grad_stretched = -jnp.sum(mean_part, axis=2)
        scale_grad = scale_grad + jnp.dot(
            jnp.dot(hot_rows.T, grad_stretched * distance, precision=highest),
            hot_cols,
            precision=highest,
        )
        shift_grad = shift_grad + jnp.dot(
            jnp.dot(hot_rows.T, grad_stretched, precision=highest), hot_cols, precision=highest
        )
        return (
            (keys_grad, values_grad, heads_grad, means_grad, widths_grad, scale_grad, shift_grad),
            query_grad,
        )

    zero_block = jnp.zeros(key_block.shape, jnp.float32)
    count = block_rows // tile_rows
    if count == 1:
        sums_out, query_grads = one_tile((zero_block, zero_block) + tuple(running), 0)
        return (sums_out[2:], (query_grads.reshape(key_block.shape), sums_out[0], sums_out[1]))
    sums_out, query_grads = lax.scan(
        one_tile, (zero_block, zero_block) + tuple(running), jnp.arange(count, dtype=jnp.int32)
    )
    query_grads = query_grads.reshape(key_block.shape)
    return (sums_out[2:], (query_grads, sums_out[0], sums_out[1]))


def snake_ring(chips_x, chips_other):
    if chips_x == 2 and chips_other >= 2:
        return [2 * z for z in range(chips_other)] + [
            2 * z + 1 for z in reversed(range(chips_other))
        ]
    return list(range(chips_x * chips_other))


class Ring:
    def __init__(self, order):
        self.order = order
        self.n = len(order)
        pos = np.zeros(self.n, np.int32)
        for i, c in enumerate(order):
            pos[c] = i
        self.pos = pos
        self.cw = [(order[i], order[(i + 1) % self.n]) for i in range(self.n)]
        self.ccw = [(order[i], order[(i - 1) % self.n]) for i in range(self.n)]

    def here(self):
        chip = lax.axis_index("chip")
        core = lax.axis_index("core")
        return chip, core, jnp.asarray(self.pos)[chip]

    def chip_at(self, position):
        return jnp.asarray(np.array(self.order, np.int32))[position % self.n]


SWAP = [(0, 1), (1, 0)]


def _halves(x, axis):
    size = x.shape[axis] // 2
    return (
        lax.slice_in_dim(x, 0, size, axis=axis),
        lax.slice_in_dim(x, size, 2 * size, axis=axis),
    )


def ring_gather(ring, pieces, chips):
    if ring is None:
        return [
            lax.all_gather(x, ("chip", "core"), axis=0, tiled=False).reshape((chips, 2) + x.shape)
            for x, _ in pieces
        ]
    chip, core, p = ring.here()
    n = ring.n
    bufs, fronts = [], []
    for x, axis in pieces:
        buf = jnp.zeros((n, 2) + x.shape, x.dtype)
        buf = lax.dynamic_update_slice(buf, x[None, None], (chip, core) + (0,) * x.ndim)
        bufs.append(buf)
        if axis is None:
            fronts.append([x, None])
        else:
            fronts.append(list(_halves(x, axis)))
    partner = lax.ppermute([x for x, _ in pieces], "core", SWAP)
    for i, x in enumerate(partner):
        bufs[i] = lax.dynamic_update_slice(
            bufs[i], x[None, None], (chip, 1 - core) + (0,) * x.ndim
        )
    for step in range(1, n):
        going = [f[0] for f in fronts]
        coming = [f[1] for f in fronts if f[1] is not None]
        going = lax.ppermute(going, "chip", ring.cw)
        coming = lax.ppermute(coming, "chip", ring.ccw) if coming else []
        from_cw = ring.chip_at(p - step)
        from_ccw = ring.chip_at(p + step)
        both = lax.ppermute([going, coming], "core", SWAP)
        j = 0
        for i, (x, axis) in enumerate(pieces):
            fronts[i][0] = going[i]
            parts = [(going[i], both[0][i], from_cw, 0)]
            if axis is not None:
                fronts[i][1] = coming[j]
                parts.append((coming[j], both[1][j], from_ccw, x.shape[axis] // 2))
                j += 1
            for mine, theirs, source, offset in parts:
                start = [0] * x.ndim
                if axis is not None:
                    start[axis] = offset
                bufs[i] = lax.dynamic_update_slice(
                    bufs[i], mine[None, None], (source, core) + tuple(start)
                )
                bufs[i] = lax.dynamic_update_slice(
                    bufs[i], theirs[None, None], (source, 1 - core) + tuple(start)
                )
    return bufs


def ring_reduce_steps(ring, pieces, send=jnp.bfloat16):
    if ring is None:
        owned = []
        for g, _ in pieces:
            flat = g.reshape((-1,) + g.shape[3:])
            part = lax.psum_scatter(flat, ("chip", "core"), scatter_dimension=0, tiled=True)
            owned.append(lax.psum(part.astype(send), "rep").astype(jnp.float32))
        yield owned
        return owned
    chip, core, p = ring.here()
    n = ring.n
    mine, theirs = [], []
    for g, _ in pieces:
        mine.append(lax.dynamic_index_in_dim(g, core, axis=1, keepdims=False))
        theirs.append(lax.dynamic_index_in_dim(g, 1 - core, axis=1, keepdims=False).astype(send))
    got = lax.ppermute(theirs, "core", SWAP)
    yield got
    flows = []
    for i, (g, way) in enumerate(pieces):
        if way == "both":
            flows.append((i, 1, n // 2, mine[i], got[i]))
            flows.append((i, -1, (n - 1) // 2, mine[i], got[i]))
        elif isinstance(way, tuple):
            axis = way[1] + 1
            for d, (m, t) in zip((1, -1), zip(_halves(mine[i], axis), _halves(got[i], axis))):
                flows.append((i, d, n - 1, m, t))
        else:
            flows.append((i, way, n - 1, mine[i], got[i]))

    def contribution(m, t, position):
        at = ring.chip_at(position)
        own = lax.dynamic_index_in_dim(m, at, axis=0, keepdims=False)
        other = lax.dynamic_index_in_dim(t, at, axis=0, keepdims=False)
        return own + other.astype(jnp.float32)

    acc = [contribution(m, t, p + d * hops) for _, d, hops, m, t in flows]
    for step in range(1, max(f[2] for f in flows) + 1):
        moved = []
        for d in (1, -1):
            chosen = [k for k, f in enumerate(flows) if f[1] == d and f[2] >= step]
            if chosen:
                out = lax.ppermute([acc[k].astype(send) for k in chosen], "chip", ring.cw if d == 1 else ring.ccw)
                for k, o in zip(chosen, out):
                    acc[k] = o.astype(jnp.float32)
                moved.extend(out)
        yield moved
        for k, (_, d, hops, m, t) in enumerate(flows):
            if hops > step:
                acc[k] = acc[k] + contribution(m, t, p + d * (hops - step))
    owned = []
    for i, (g, way) in enumerate(pieces):
        parts = [(a, f) for a, f in zip(acc, flows) if f[0] == i]
        if way == "both":
            total = contribution(parts[0][1][3], parts[0][1][4], p) + parts[0][0] + parts[1][0]
        else:
            total = [a + contribution(f[3], f[4], p) for a, f in parts]
            total = total[0] if len(total) == 1 else jnp.concatenate(total, axis=way[1])
        owned.append(total)
    other = lax.ppermute([o.astype(send) for o in owned], "rep", SWAP)
    yield other
    return [o + t.astype(jnp.float32) for o, t in zip(owned, other)]


class Stepper:
    def __init__(self, gen):
        self.gen = gen
        self.result = None
        self.over = False

    def tie(self, value):
        if self.over:
            return value
        try:
            ready = next(self.gen)
        except StopIteration as done:
            self.result, self.over = done.value, True
            return value
        _, value = lax.optimization_barrier((ready, value))
        return value

    def finish(self):
        if not self.over:
            self.result, self.over = run_steps(self.gen), True
        return self.result


def run_steps(gen):
    while True:
        try:
            next(gen)
        except StopIteration as done:
            return done.value


SMALL_ROWS, SMALL_LANES = 16, 768


def small_layout(fsdp):
    d = 768 // fsdp
    sizes = [2 * d, 6 * d, 3072 // fsdp, 128 // fsdp, 128 // fsdp, 4096 // fsdp, 4096 // fsdp, (128 // fsdp) * 32]
    offsets, at = [], 0
    for size in sizes:
        offsets.append((at, size))
        at += size
    assert at <= SMALL_ROWS * SMALL_LANES
    return offsets


def pack_small(parts):
    flat = jnp.concatenate([part.reshape(-1) for part in parts])
    flat = jnp.pad(flat, (0, SMALL_ROWS * SMALL_LANES - flat.shape[0]))
    return flat.reshape(SMALL_ROWS, SMALL_LANES)


def unpack_small_full(gathered, offsets, fsdp):
    flat = gathered.reshape(fsdp, -1).astype(jnp.float32)
    take = [flat[:, at : at + size] for at, size in offsets]
    d = 768 // fsdp
    return [
        take[0].reshape(fsdp, 2, d).transpose(1, 0, 2).reshape(2, -1),
        take[1].reshape(fsdp, 6, d).transpose(1, 0, 2).reshape(6, -1),
        take[2].reshape(-1),
        take[3].reshape(-1),
        take[4].reshape(-1),
        take[5].reshape(ATOM_TYPES, ATOM_TYPES),
        take[6].reshape(ATOM_TYPES, ATOM_TYPES),
        take[7].reshape(-1, 32),
    ]


def pack_small_grads(grads, fsdp, chips):
    d = 768 // fsdp
    blocks = [
        grads[0].reshape(2, fsdp, d).transpose(1, 0, 2),
        grads[1].reshape(6, fsdp, d).transpose(1, 0, 2),
    ] + [g.reshape(-1) for g in grads[2:]]
    flat = jnp.concatenate([blk.reshape(fsdp, -1) for blk in blocks], axis=1)
    flat = jnp.pad(flat, ((0, 0), (0, SMALL_ROWS * SMALL_LANES - flat.shape[1])))
    return flat.reshape(chips, 2, SMALL_ROWS, SMALL_LANES)


def unpack_small_owned(block, offsets):
    flat = block.reshape(-1)
    take = [flat[at : at + size] for at, size in offsets]
    return [
        take[0].reshape(2, -1),
        take[1].reshape(6, -1),
        take[2],
        take[3],
        take[4],
        take[5],
        take[6],
        take[7].reshape(-1, 32),
    ]


def make_body(ring, chips):
    fsdp = 2 * chips

    def body(
        inputs,
        times,
        positions,
        atom_types,
        molecule_ids,
        pad_mask,
        cotangent,
        norm_gains,
        bias_rows,
        up_bias,
        input_weight,
        output_weight,
        up_weight,
        down_weight,
        kernel_means,
        kernel_widths,
        pair_scale,
        pair_shift,
        kernel_heads,
    ):
        offsets = small_layout(fsdp)
        small = pack_small(
            [norm_gains, bias_rows, up_bias, kernel_means, kernel_widths, pair_scale, pair_shift, kernel_heads]
        )
        width = input_weight.shape[0]
        first = jnp.concatenate([small.reshape(-1, width), input_weight.T], axis=0)
        second = jnp.concatenate(
            [output_weight.T, up_weight.T, down_weight.T.reshape(-1, width)], axis=0
        )
        first_all = lax.all_gather(first, ("chip", "core"), axis=0, tiled=False)
        second_all = lax.all_gather(second, ("chip", "core"), axis=0, tiled=False)
        small_rows = small.size // width
        params = unpack_small_full(first_all[:, :small_rows], offsets, fsdp)
        in_t = first_all[:, small_rows:].reshape(-1, width)
        out_rows = output_weight.shape[1]
        up_rows = up_weight.shape[1]
        out_t = second_all[:, :out_rows].reshape(-1, width)
        up_t = second_all[:, out_rows : out_rows + up_rows].reshape(-1, width)
        down_t = (
            second_all[:, out_rows + up_rows :]
            .reshape(fsdp, down_weight.shape[1], -1)
            .reshape(-1, down_weight.shape[0])
        )
        gains_now, biases_now, up_shift = params[0], params[1], params[2]
        tables = (params[3], params[4], params[5], params[6])
        heads_full = params[7].astype(jnp.bfloat16)

        row_count = inputs.shape[0]
        model_width = inputs.shape[1]
        head_count = heads_full.shape[1]
        head_size = model_width // head_count
        block_rows = min(128, row_count)
        blocks = row_count // block_rows
        tile_rows = min(128, block_rows)
        nt = (((1,), (1,)), ((), ()))
        tn = (((0,), (0,)), ((), ()))

        stream = inputs.astype(jnp.float32) + time_embedding(times, model_width)
        normed_out, normed_one, inv_one = layer_norm(stream, gains_now[0], biases_now[0])
        act_one = normed_out.astype(jnp.bfloat16)
        qkv_shift = jnp.concatenate([biases_now[2], jnp.zeros_like(biases_now[2]), biases_now[3]])
        projected = (
            lax.dot_general(act_one, in_t, nt, preferred_element_type=jnp.float32) + qkv_shift
        ).astype(jnp.bfloat16)
        split_shape = (blocks, block_rows, head_count, head_size)
        queries = projected[:, :model_width].reshape(split_shape)
        key_rows = projected[:, model_width : 2 * model_width].reshape(split_shape)
        value_rows = projected[:, 2 * model_width :].reshape(split_shape)
        pos_blocks = jnp.transpose(positions.reshape(3, blocks, block_rows), (1, 0, 2))
        type_blocks = atom_types.reshape(blocks, block_rows)
        mol_blocks = molecule_ids.reshape(blocks, block_rows)
        pad_blocks = pad_mask.reshape(blocks, block_rows)
        fwd = [
            block_forward(
                (queries[b], key_rows[b], value_rows[b], pos_blocks[b], type_blocks[b], mol_blocks[b], pad_blocks[b]),
                tables=tables,
                kernel_heads=heads_full,
                tile_rows=tile_rows,
            )
            for b in range(blocks)
        ]
        attended = jnp.stack([f[0] for f in fwd])
        log_sums = [f[1] for f in fwd]
        attended_low = attended.reshape(row_count, model_width).astype(jnp.bfloat16)
        mid = stream + (
            lax.dot_general(attended_low, out_t, nt, preferred_element_type=jnp.float32)
            + biases_now[4]
        )
        normed_out_two, normed_two, inv_two = layer_norm(mid, gains_now[1], biases_now[1])
        act_two = normed_out_two.astype(jnp.bfloat16)
        hidden_pre = (
            lax.dot_general(act_two, up_t, nt, preferred_element_type=jnp.float32) + up_shift
        )
        hidden_low = gelu_value(hidden_pre).astype(jnp.bfloat16)
        final = mid + (
            lax.dot_general(hidden_low, down_t, nt, preferred_element_type=jnp.float32)
            + biases_now[5]
        )
        rows_out = final.astype(jnp.bfloat16)

        grad_final = cotangent.astype(jnp.float32)
        down_grad_t = lax.dot_general(cotangent, hidden_low, tn, preferred_element_type=jnp.float32)
        grad_hidden = jnp.dot(cotangent, down_t, preferred_element_type=jnp.float32) * gelu_slope(
            hidden_pre
        )
        grad_hidden_low = grad_hidden.astype(jnp.bfloat16)
        up_grad_t = lax.dot_general(grad_hidden_low, act_two, tn, preferred_element_type=jnp.float32)
        up_bias_grad = jnp.sum(grad_hidden_low.astype(jnp.float32), axis=0)
        grad_act_two = jnp.dot(grad_hidden_low, up_t, preferred_element_type=jnp.float32)
        grad_norm_two, gain_two_grad, shift_two_grad = norm_backward(
            grad_act_two, normed_two, inv_two, gains_now[1]
        )
        grad_mid = grad_final + grad_norm_two
        grad_branch_low = grad_mid.astype(jnp.bfloat16)
        out_grad_t = lax.dot_general(
            grad_branch_low, attended_low, tn, preferred_element_type=jnp.float32
        )
        late_rows = jnp.concatenate(
            [
                out_grad_t.reshape(chips, 2, -1, model_width),
                up_grad_t.reshape(chips, 2, -1, model_width),
            ],
            axis=2,
        )
        late = ring_reduce_steps(
            ring, [(late_rows, "both"), (down_grad_t.reshape((chips, 2, -1) + down_grad_t.shape[1:]), "both")]
        )
        grad_attended = jnp.dot(grad_branch_low, out_t, preferred_element_type=jnp.float32).astype(
            jnp.bfloat16
        )
        kernel_count = tables[0].shape[0]
        start_sums = (
            jnp.zeros((kernel_count, head_count), jnp.float32),
            jnp.zeros((kernel_count,), jnp.float32),
            jnp.zeros((kernel_count,), jnp.float32),
            jnp.zeros((ATOM_TYPES, ATOM_TYPES), jnp.float32),
            jnp.zeros((ATOM_TYPES, ATOM_TYPES), jnp.float32),
        )
        kernel_sums = start_sums
        q_grads, k_grads, v_grads = [], [], []
        grad_attended_blocks = grad_attended.reshape(split_shape)
        stepper = Stepper(late)
        for b in range(blocks):
            gate = grad_attended_blocks[b]
            if b > 0:
                gate = stepper.tie(gate)
            kernel_sums, (qg, kg, vg) = block_backward(
                kernel_sums,
                (
                    queries[b],
                    key_rows[b],
                    value_rows[b],
                    gate,
                    log_sums[b],
                    pos_blocks[b],
                    type_blocks[b],
                    mol_blocks[b],
                    pad_blocks[b],
                ),
                tables=tables,
                kernel_heads=heads_full,
                tile_rows=tile_rows,
                hook=stepper.tie,
            )
            q_grads.append(qg)
            k_grads.append(kg)
            v_grads.append(vg)
        queries_grad = jnp.stack(q_grads)
        keys_grad = jnp.stack(k_grads)
        values_grad = jnp.stack(v_grads)
        grad_projected = jnp.concatenate(
            [
                queries_grad.reshape(row_count, model_width),
                keys_grad.reshape(row_count, model_width),
                values_grad.reshape(row_count, model_width),
            ],
            axis=1,
        ).astype(jnp.bfloat16)
        in_grad_t = lax.dot_general(grad_projected, act_one, tn, preferred_element_type=jnp.float32)
        grad_act_one = jnp.dot(grad_projected, in_t, preferred_element_type=jnp.float32)
        grad_norm_one, gain_one_grad, shift_one_grad = norm_backward(
            grad_act_one, normed_one, inv_one, gains_now[0]
        )
        inputs_grad = grad_mid + grad_norm_one
        projected_sums = jnp.sum(grad_projected.astype(jnp.float32), axis=0)
        heads_grad, means_grad, widths_grad, scale_grad, shift_grad = kernel_sums
        small_grads = [
            jnp.stack([gain_one_grad, gain_two_grad]),
            jnp.stack(
                [
                    shift_one_grad,
                    shift_two_grad,
                    projected_sums[:model_width],
                    projected_sums[2 * model_width :],
                    jnp.sum(grad_branch_low.astype(jnp.float32), axis=0),
                    jnp.sum(grad_final, axis=0),
                ]
            ),
            up_bias_grad,
            means_grad,
            widths_grad,
            scale_grad,
            shift_grad,
            heads_grad,
        ]
        late_owned = stepper.finish()
        out_owned = late_owned[0][:out_rows]
        up_owned = late_owned[0][out_rows:]
        down_owned = late_owned[1]
        last = jnp.concatenate(
            [
                in_grad_t.reshape((chips, 2, -1) + in_grad_t.shape[1:]),
                pack_small_grads(small_grads, fsdp, chips),
            ],
            axis=2,
        )
        (last_owned,) = run_steps(ring_reduce_steps(ring, [(last, "both")]))
        in_rows = in_grad_t.shape[0] // fsdp
        in_owned = last_owned[:in_rows]
        small_owned = last_owned[in_rows:]
        sg = unpack_small_owned(small_owned, offsets)
        return (
            rows_out,
            inputs_grad,
            sg[0],
            sg[1],
            sg[2],
            in_owned.T,
            out_owned.T,
            up_owned.T,
            down_owned.T,
            sg[3],
            sg[4],
            sg[5],
            sg[6],
            sg[7],
        )

    return body


def solution(mesh):
    reps, fsdp = mesh.devices.shape
    chips = fsdp // 2
    grid = Mesh(mesh.devices.reshape(reps, chips, 2), ("rep", "chip", "core"))
    chips_x = 1
    try:
        coords = [tuple(d.coords) for d in mesh.devices[0, ::2]]
        xs = sorted({c[0] for c in coords})
        chips_x = len(xs)
        flat_ok = all(
            coords[i][0] == xs[i % chips_x] for i in range(chips)
        )
        if not flat_ok:
            chips_x = 1
    except Exception:
        chips_x = 1
    ring = None
    if chips <= 8:
        ring = Ring(snake_ring(chips_x, chips // chips_x))
    atoms = ("rep", "chip", "core")
    cols = ("chip", "core")
    placed = (
        P(atoms, None),
        P(atoms),
        P(None, atoms),
        P(atoms),
        P(atoms),
        P(atoms),
        P(atoms, None),
        P(None, cols),
        P(None, cols),
        P(cols),
        P(None, cols),
        P(None, cols),
        P(None, cols),
        P(None, cols),
        P(cols),
        P(cols),
        P(cols),
        P(cols),
        P(cols, None),
    )
    return jax.shard_map(
        make_body(ring, chips),
        mesh=grid,
        in_specs=placed,
        out_specs=(
            P(atoms, None),
            P(atoms, None),
            P(None, cols),
            P(None, cols),
            P(cols),
            P(None, cols),
            P(None, cols),
            P(None, cols),
            P(None, cols),
            P(cols),
            P(cols),
            P(cols),
            P(cols),
            P(cols, None),
        ),
        check_vma=False,
    )
```

```python
from functools import partial
import math

import jax
import jax.numpy as jnp
from jax import lax
from jax.sharding import Mesh, PartitionSpec as P
import numpy as np

ATOM_TYPES = 64


epsilon = 1e-05
masked_score = -1000000000.0
time_scale = 1000.0
root_two_pi = math.sqrt(2.0 * math.pi)
highest = lax.Precision.HIGHEST


def time_embedding(times, model_width):
    half_width = model_width // 2
    counter = jnp.arange(half_width, dtype=jnp.float32)
    frequency = jnp.exp(counter * (-math.log(10000.0) / half_width))
    angles = (time_scale * times)[:, None] * frequency[None, :]
    return jnp.concatenate([jnp.sin(angles), jnp.cos(angles)], axis=1)


def layer_norm(values, gain_row, shift_row):
    center = values - jnp.mean(values, axis=1, keepdims=True)
    inv_std = lax.rsqrt(jnp.mean(center * center, axis=1, keepdims=True) + epsilon)
    normed = center * inv_std
    return (normed * gain_row + shift_row, normed, inv_std)


def norm_backward(grad_out, normed, inv_std, gain_row):
    grad_normed = grad_out * gain_row
    first_mean = jnp.mean(grad_normed, axis=1, keepdims=True)
    second_mean = jnp.mean(grad_normed * normed, axis=1, keepdims=True)
    grad_input = inv_std * (grad_normed - first_mean - normed * second_mean)
    return (grad_input, jnp.sum(grad_out * normed, axis=0), jnp.sum(grad_out, axis=0))


def gelu_value(values):
    return values * (0.5 + 0.5 * lax.erf(values * math.sqrt(0.5)))


def gelu_slope(values):
    return (
        0.5
        + 0.5 * lax.erf(values * math.sqrt(0.5))
        + values * jnp.exp(-0.5 * values * values) / root_two_pi
    )


def pair_terms(pos_rows, pos_cols, type_rows, type_cols, tables):
    kernel_means, kernel_widths, scale_table, shift_table = tables
    offsets = pos_rows[:, :, None] - pos_cols[:, None, :]
    distance = jnp.sqrt(jnp.sum(offsets * offsets, axis=0))
    type_range = jnp.arange(ATOM_TYPES, dtype=jnp.int32)
    hot_rows = (type_rows[:, None] == type_range[None, :]).astype(jnp.float32)
    hot_cols = (type_cols[:, None] == type_range[None, :]).astype(jnp.float32)
    scale_pair = jnp.dot(
        jnp.dot(hot_rows, scale_table, precision=highest), hot_cols.T, precision=highest
    )
    shift_pair = jnp.dot(
        jnp.dot(hot_rows, shift_table, precision=highest), hot_cols.T, precision=highest
    )
    stretched = scale_pair * distance + shift_pair
    kernel_gap = (stretched[:, :, None] - kernel_means) / kernel_widths
    kernels = jnp.exp(-0.5 * kernel_gap * kernel_gap) / (root_two_pi * kernel_widths)
    return (distance, hot_rows, hot_cols, kernel_gap, kernels)


def allowed_pairs(row_ids, col_ids, mol_rows, mol_cols, pad_cols):
    same_mol = mol_rows[:, None] == mol_cols[None, :]
    key_live = (pad_cols[None, :] == 1) | (row_ids[:, None] == col_ids[None, :])
    return same_mol & key_live


def tile_scores(q_tile, key_block, kernels_low, kernel_heads, allowed, score_scale):
    pair_bias = jnp.einsum(
        "ijk,kh->hij", kernels_low, kernel_heads, preferred_element_type=jnp.float32
    )
    raw_scores = jnp.einsum("ihd,jhd->hij", q_tile, key_block, preferred_element_type=jnp.float32)
    return jnp.where(allowed[None], raw_scores * score_scale + pair_bias, masked_score)


def block_forward(pieces, tables, kernel_heads, tile_rows):
    queries, key_block, value_block, positions, types, mols, pads = pieces
    block_rows = queries.shape[0]
    score_scale = 1.0 / math.sqrt(queries.shape[2])
    col_ids = jnp.arange(block_rows, dtype=jnp.int32)

    def one_tile(running, tile_index):
        first_row = tile_index * tile_rows
        row_ids = first_row + jnp.arange(tile_rows, dtype=jnp.int32)
        terms = pair_terms(positions, positions, types, types, tables)
        kernels_low = terms[4].astype(jnp.bfloat16)
        allowed = allowed_pairs(row_ids, col_ids, mols, mols, pads)
        scores = tile_scores(queries, key_block, kernels_low, kernel_heads, allowed, score_scale)
        row_max = jnp.max(scores, axis=2, keepdims=True)
        exponent = jnp.exp(scores - row_max)
        row_sum = jnp.sum(exponent, axis=2, keepdims=True)
        probs_low = (exponent / row_sum).astype(jnp.bfloat16)
        attended = jnp.einsum(
            "hij,jhd->ihd", probs_low, value_block, preferred_element_type=jnp.float32
        )
        return (running, (attended, (row_max + jnp.log(row_sum))[:, :, 0]))

    count = block_rows // tile_rows
    if count == 1:
        _, (attended, log_sums) = one_tile(None, 0)
        return (attended.reshape(block_rows, -1), log_sums)
    _, (attended, log_sums) = lax.scan(one_tile, None, jnp.arange(count, dtype=jnp.int32))
    attended = attended.reshape(block_rows, -1)
    log_sums = jnp.transpose(log_sums, (1, 0, 2)).reshape(log_sums.shape[1], block_rows)
    return (attended, log_sums)


def block_backward(running, pieces, tables, kernel_heads, tile_rows, hook=None):
    queries, key_block, value_block, grad_attended, log_sums, positions, types, mols, pads = pieces
    kernel_widths = tables[1]
    block_rows = queries.shape[0]
    score_scale = 1.0 / math.sqrt(queries.shape[2])
    col_ids = jnp.arange(block_rows, dtype=jnp.int32)

    def one_tile(partial_sums, tile_index):
        keys_grad, values_grad, heads_grad, means_grad, widths_grad, scale_grad, shift_grad = (
            partial_sums
        )
        first_row = tile_index * tile_rows
        row_ids = first_row + jnp.arange(tile_rows, dtype=jnp.int32)
        distance, hot_rows, hot_cols, kernel_gap, kernels = pair_terms(
            positions, positions, types, types, tables
        )
        kernels_low = kernels.astype(jnp.bfloat16)
        allowed = allowed_pairs(row_ids, col_ids, mols, mols, pads)
        scores = tile_scores(queries, key_block, kernels_low, kernel_heads, allowed, score_scale)
        attn_probs = jnp.exp(scores - log_sums[:, :, None])
        grad_probs = jnp.einsum(
            "ihd,jhd->hij", grad_attended, value_block, preferred_element_type=jnp.float32
        )
        values_grad = values_grad + jnp.einsum(
            "hij,ihd->jhd",
            attn_probs.astype(jnp.bfloat16),
            grad_attended,
            preferred_element_type=jnp.float32,
        )
        probs_dot = jnp.sum(attn_probs * grad_probs, axis=2, keepdims=True)
        grad_scores = (attn_probs * (grad_probs - probs_dot)).astype(jnp.bfloat16)
        if hook is not None:
            grad_scores = hook(grad_scores)
        query_grad = (
            jnp.einsum("hij,jhd->ihd", grad_scores, key_block, preferred_element_type=jnp.float32)
            * score_scale
        )
        keys_grad = (
            keys_grad
            + jnp.einsum("hij,ihd->jhd", grad_scores, queries, preferred_element_type=jnp.float32)
            * score_scale
        )
        heads_grad = heads_grad + jnp.einsum(
            "ijk,hij->kh", kernels_low, grad_scores, preferred_element_type=jnp.float32
        )
        grad_kernels = jnp.einsum(
            "hij,kh->ijk", grad_scores, kernel_heads, preferred_element_type=jnp.float32
        )
        spread = grad_kernels * kernels
        mean_part = spread * kernel_gap / kernel_widths
        means_grad = means_grad + jnp.sum(mean_part, axis=(0, 1))
        widths_grad = widths_grad + jnp.sum(
            spread * (kernel_gap * kernel_gap - 1.0) / kernel_widths, axis=(0, 1)
        )
        grad_stretched = -jnp.sum(mean_part, axis=2)
        scale_grad = scale_grad + jnp.dot(
            jnp.dot(hot_rows.T, grad_stretched * distance, precision=highest),
            hot_cols,
            precision=highest,
        )
        shift_grad = shift_grad + jnp.dot(
            jnp.dot(hot_rows.T, grad_stretched, precision=highest), hot_cols, precision=highest
        )
        return (
            (keys_grad, values_grad, heads_grad, means_grad, widths_grad, scale_grad, shift_grad),
            query_grad,
        )

    zero_block = jnp.zeros(key_block.shape, jnp.float32)
    count = block_rows // tile_rows
    if count == 1:
        sums_out, query_grads = one_tile((zero_block, zero_block) + tuple(running), 0)
        return (sums_out[2:], (query_grads.reshape(key_block.shape), sums_out[0], sums_out[1]))
    sums_out, query_grads = lax.scan(
        one_tile, (zero_block, zero_block) + tuple(running), jnp.arange(count, dtype=jnp.int32)
    )
    query_grads = query_grads.reshape(key_block.shape)
    return (sums_out[2:], (query_grads, sums_out[0], sums_out[1]))


def snake_ring(chips_x, chips_other):
    if chips_x == 2 and chips_other >= 2:
        return [2 * z for z in range(chips_other)] + [
            2 * z + 1 for z in reversed(range(chips_other))
        ]
    return list(range(chips_x * chips_other))


class Ring:
    def __init__(self, order):
        self.order = order
        self.n = len(order)
        pos = np.zeros(self.n, np.int32)
        for i, c in enumerate(order):
            pos[c] = i
        self.pos = pos
        self.cw = [(order[i], order[(i + 1) % self.n]) for i in range(self.n)]
        self.ccw = [(order[i], order[(i - 1) % self.n]) for i in range(self.n)]

    def here(self):
        chip = lax.axis_index("chip")
        core = lax.axis_index("core")
        return chip, core, jnp.asarray(self.pos)[chip]

    def chip_at(self, position):
        return jnp.asarray(np.array(self.order, np.int32))[position % self.n]


SWAP = [(0, 1), (1, 0)]


def _halves(x, axis):
    size = x.shape[axis] // 2
    return (
        lax.slice_in_dim(x, 0, size, axis=axis),
        lax.slice_in_dim(x, size, 2 * size, axis=axis),
    )


def ring_gather(ring, pieces, chips):
    if ring is None:
        return [
            lax.all_gather(x, ("chip", "core"), axis=0, tiled=False).reshape((chips, 2) + x.shape)
            for x, _ in pieces
        ]
    chip, core, p = ring.here()
    n = ring.n
    bufs, fronts = [], []
    for x, axis in pieces:
        buf = jnp.zeros((n, 2) + x.shape, x.dtype)
        buf = lax.dynamic_update_slice(buf, x[None, None], (chip, core) + (0,) * x.ndim)
        bufs.append(buf)
        if axis is None:
            fronts.append([x, None])
        else:
            fronts.append(list(_halves(x, axis)))
    partner = lax.ppermute([x for x, _ in pieces], "core", SWAP)
    for i, x in enumerate(partner):
        bufs[i] = lax.dynamic_update_slice(
            bufs[i], x[None, None], (chip, 1 - core) + (0,) * x.ndim
        )
    for step in range(1, n):
        going = [f[0] for f in fronts]
        coming = [f[1] for f in fronts if f[1] is not None]
        going = lax.ppermute(going, "chip", ring.cw)
        coming = lax.ppermute(coming, "chip", ring.ccw) if coming else []
        from_cw = ring.chip_at(p - step)
        from_ccw = ring.chip_at(p + step)
        both = lax.ppermute([going, coming], "core", SWAP)
        j = 0
        for i, (x, axis) in enumerate(pieces):
            fronts[i][0] = going[i]
            parts = [(going[i], both[0][i], from_cw, 0)]
            if axis is not None:
                fronts[i][1] = coming[j]
                parts.append((coming[j], both[1][j], from_ccw, x.shape[axis] // 2))
                j += 1
            for mine, theirs, source, offset in parts:
                start = [0] * x.ndim
                if axis is not None:
                    start[axis] = offset
                bufs[i] = lax.dynamic_update_slice(
                    bufs[i], mine[None, None], (source, core) + tuple(start)
                )
                bufs[i] = lax.dynamic_update_slice(
                    bufs[i], theirs[None, None], (source, 1 - core) + tuple(start)
                )
    return bufs


def ring_reduce_steps(ring, pieces, send=jnp.bfloat16):
    if ring is None:
        owned = []
        for g, _ in pieces:
            flat = g.reshape((-1,) + g.shape[3:])
            part = lax.psum_scatter(flat, ("chip", "core"), scatter_dimension=0, tiled=True)
            owned.append(lax.psum(part.astype(send), "rep").astype(jnp.float32))
        yield owned
        return owned
    chip, core, p = ring.here()
    n = ring.n
    mine, theirs = [], []
    for g, _ in pieces:
        mine.append(lax.dynamic_index_in_dim(g, core, axis=1, keepdims=False))
        theirs.append(lax.dynamic_index_in_dim(g, 1 - core, axis=1, keepdims=False).astype(send))
    got = lax.ppermute(theirs, "core", SWAP)
    yield got
    flows = []
    for i, (g, way) in enumerate(pieces):
        if way == "both":
            flows.append((i, 1, n // 2, mine[i], got[i]))
            flows.append((i, -1, (n - 1) // 2, mine[i], got[i]))
        elif isinstance(way, tuple):
            axis = way[1] + 1
            for d, (m, t) in zip((1, -1), zip(_halves(mine[i], axis), _halves(got[i], axis))):
                flows.append((i, d, n - 1, m, t))
        else:
            flows.append((i, way, n - 1, mine[i], got[i]))

    def contribution(m, t, position):
        at = ring.chip_at(position)
        own = lax.dynamic_index_in_dim(m, at, axis=0, keepdims=False)
        other = lax.dynamic_index_in_dim(t, at, axis=0, keepdims=False)
        return own + other.astype(jnp.float32)

    acc = [contribution(m, t, p + d * hops) for _, d, hops, m, t in flows]
    for step in range(1, max(f[2] for f in flows) + 1):
        moved = []
        for d in (1, -1):
            chosen = [k for k, f in enumerate(flows) if f[1] == d and f[2] >= step]
            if chosen:
                out = lax.ppermute([acc[k].astype(send) for k in chosen], "chip", ring.cw if d == 1 else ring.ccw)
                for k, o in zip(chosen, out):
                    acc[k] = o.astype(jnp.float32)
                moved.extend(out)
        yield moved
        for k, (_, d, hops, m, t) in enumerate(flows):
            if hops > step:
                acc[k] = acc[k] + contribution(m, t, p + d * (hops - step))
    owned = []
    for i, (g, way) in enumerate(pieces):
        parts = [(a, f) for a, f in zip(acc, flows) if f[0] == i]
        if way == "both":
            total = contribution(parts[0][1][3], parts[0][1][4], p) + parts[0][0] + parts[1][0]
        else:
            total = [a + contribution(f[3], f[4], p) for a, f in parts]
            total = total[0] if len(total) == 1 else jnp.concatenate(total, axis=way[1])
        owned.append(total)
    other = lax.ppermute([o.astype(send) for o in owned], "rep", SWAP)
    yield other
    return [o + t.astype(jnp.float32) for o, t in zip(owned, other)]


class Stepper:
    def __init__(self, gen):
        self.gen = gen
        self.result = None
        self.over = False

    def tie(self, value):
        if self.over:
            return value
        try:
            ready = next(self.gen)
        except StopIteration as done:
            self.result, self.over = done.value, True
            return value
        _, value = lax.optimization_barrier((ready, value))
        return value

    def finish(self):
        if not self.over:
            self.result, self.over = run_steps(self.gen), True
        return self.result


def run_steps(gen):
    while True:
        try:
            next(gen)
        except StopIteration as done:
            return done.value


SMALL_ROWS, SMALL_LANES = 16, 768


def small_layout(fsdp):
    d = 768 // fsdp
    sizes = [2 * d, 6 * d, 3072 // fsdp, 128 // fsdp, 128 // fsdp, 4096 // fsdp, 4096 // fsdp, (128 // fsdp) * 32]
    offsets, at = [], 0
    for size in sizes:
        offsets.append((at, size))
        at += size
    assert at <= SMALL_ROWS * SMALL_LANES
    return offsets


def pack_small(parts):
    flat = jnp.concatenate([part.reshape(-1) for part in parts])
    flat = jnp.pad(flat, (0, SMALL_ROWS * SMALL_LANES - flat.shape[0]))
    return flat.reshape(SMALL_ROWS, SMALL_LANES)


def unpack_small_full(gathered, offsets, fsdp):
    flat = gathered.reshape(fsdp, -1).astype(jnp.float32)
    take = [flat[:, at : at + size] for at, size in offsets]
    d = 768 // fsdp
    return [
        take[0].reshape(fsdp, 2, d).transpose(1, 0, 2).reshape(2, -1),
        take[1].reshape(fsdp, 6, d).transpose(1, 0, 2).reshape(6, -1),
        take[2].reshape(-1),
        take[3].reshape(-1),
        take[4].reshape(-1),
        take[5].reshape(ATOM_TYPES, ATOM_TYPES),
        take[6].reshape(ATOM_TYPES, ATOM_TYPES),
        take[7].reshape(-1, 32),
    ]


def pack_small_grads(grads, fsdp, chips):
    d = 768 // fsdp
    blocks = [
        grads[0].reshape(2, fsdp, d).transpose(1, 0, 2),
        grads[1].reshape(6, fsdp, d).transpose(1, 0, 2),
    ] + [g.reshape(-1) for g in grads[2:]]
    flat = jnp.concatenate([blk.reshape(fsdp, -1) for blk in blocks], axis=1)
    flat = jnp.pad(flat, ((0, 0), (0, SMALL_ROWS * SMALL_LANES - flat.shape[1])))
    return flat.reshape(chips, 2, SMALL_ROWS, SMALL_LANES)


def unpack_small_owned(block, offsets):
    flat = block.reshape(-1)
    take = [flat[at : at + size] for at, size in offsets]
    return [
        take[0].reshape(2, -1),
        take[1].reshape(6, -1),
        take[2],
        take[3],
        take[4],
        take[5],
        take[6],
        take[7].reshape(-1, 32),
    ]


def make_body(ring, chips):
    fsdp = 2 * chips

    def body(
        inputs,
        times,
        positions,
        atom_types,
        molecule_ids,
        pad_mask,
        cotangent,
        norm_gains,
        bias_rows,
        up_bias,
        input_weight,
        output_weight,
        up_weight,
        down_weight,
        kernel_means,
        kernel_widths,
        pair_scale,
        pair_shift,
        kernel_heads,
    ):
        offsets = small_layout(fsdp)
        small = jnp.concatenate(
            [
                part.reshape(-1)
                for part in (norm_gains, bias_rows, up_bias, kernel_means, kernel_widths, pair_scale, pair_shift, kernel_heads)
            ]
        )
        small = jnp.pad(small, (0, -small.shape[0] % 128))
        width = input_weight.shape[0]
        small_all = lax.all_gather(small, ("chip", "core"), axis=0, tiled=False)
        in_t = lax.all_gather(input_weight.T, ("chip", "core"), axis=0, tiled=True)
        second = jnp.concatenate(
            [output_weight.T, up_weight.T, down_weight.T.reshape(-1, width)], axis=0
        )
        second_all = lax.all_gather(second, ("chip", "core"), axis=0, tiled=False)
        params = unpack_small_full(small_all, offsets, fsdp)
        out_rows = output_weight.shape[1]
        up_rows = up_weight.shape[1]
        out_t = second_all[:, :out_rows].reshape(-1, width)
        up_t = second_all[:, out_rows : out_rows + up_rows].reshape(-1, width)
        down_t = (
            second_all[:, out_rows + up_rows :]
            .reshape(fsdp, down_weight.shape[1], -1)
            .reshape(-1, down_weight.shape[0])
        )
        gains_now, biases_now, up_shift = params[0], params[1], params[2]
        tables = (params[3], params[4], params[5], params[6])
        heads_full = params[7].astype(jnp.bfloat16)

        row_count = inputs.shape[0]
        model_width = inputs.shape[1]
        head_count = heads_full.shape[1]
        head_size = model_width // head_count
        block_rows = min(128, row_count)
        blocks = row_count // block_rows
        tile_rows = min(128, block_rows)
        nt = (((1,), (1,)), ((), ()))
        tn = (((0,), (0,)), ((), ()))

        stream = inputs.astype(jnp.float32) + time_embedding(times, model_width)
        normed_out, normed_one, inv_one = layer_norm(stream, gains_now[0], biases_now[0])
        act_one = normed_out.astype(jnp.bfloat16)
        qkv_shift = jnp.concatenate([biases_now[2], jnp.zeros_like(biases_now[2]), biases_now[3]])
        projected = (
            lax.dot_general(act_one, in_t, nt, preferred_element_type=jnp.float32) + qkv_shift
        ).astype(jnp.bfloat16)
        split_shape = (blocks, block_rows, head_count, head_size)
        queries = projected[:, :model_width].reshape(split_shape)
        key_rows = projected[:, model_width : 2 * model_width].reshape(split_shape)
        value_rows = projected[:, 2 * model_width :].reshape(split_shape)
        pos_blocks = jnp.transpose(positions.reshape(3, blocks, block_rows), (1, 0, 2))
        type_blocks = atom_types.reshape(blocks, block_rows)
        mol_blocks = molecule_ids.reshape(blocks, block_rows)
        pad_blocks = pad_mask.reshape(blocks, block_rows)
        fwd = [
            block_forward(
                (queries[b], key_rows[b], value_rows[b], pos_blocks[b], type_blocks[b], mol_blocks[b], pad_blocks[b]),
                tables=tables,
                kernel_heads=heads_full,
                tile_rows=tile_rows,
            )
            for b in range(blocks)
        ]
        attended = jnp.stack([f[0] for f in fwd])
        log_sums = [f[1] for f in fwd]
        attended_low = attended.reshape(row_count, model_width).astype(jnp.bfloat16)
        mid = stream + (
            lax.dot_general(attended_low, out_t, nt, preferred_element_type=jnp.float32)
            + biases_now[4]
        )
        normed_out_two, normed_two, inv_two = layer_norm(mid, gains_now[1], biases_now[1])
        act_two = normed_out_two.astype(jnp.bfloat16)
        hidden_pre = (
            lax.dot_general(act_two, up_t, nt, preferred_element_type=jnp.float32) + up_shift
        )
        hidden_low = gelu_value(hidden_pre).astype(jnp.bfloat16)
        final = mid + (
            lax.dot_general(hidden_low, down_t, nt, preferred_element_type=jnp.float32)
            + biases_now[5]
        )
        rows_out = final.astype(jnp.bfloat16)

        grad_final = cotangent.astype(jnp.float32)
        down_grad_t = lax.dot_general(cotangent, hidden_low, tn, preferred_element_type=jnp.float32)
        grad_hidden = jnp.dot(cotangent, down_t, preferred_element_type=jnp.float32) * gelu_slope(
            hidden_pre
        )
        grad_hidden_low = grad_hidden.astype(jnp.bfloat16)
        up_grad_t = lax.dot_general(grad_hidden_low, act_two, tn, preferred_element_type=jnp.float32)
        up_bias_grad = jnp.sum(grad_hidden_low.astype(jnp.float32), axis=0)
        grad_act_two = jnp.dot(grad_hidden_low, up_t, preferred_element_type=jnp.float32)
        grad_norm_two, gain_two_grad, shift_two_grad = norm_backward(
            grad_act_two, normed_two, inv_two, gains_now[1]
        )
        grad_mid = grad_final + grad_norm_two
        grad_branch_low = grad_mid.astype(jnp.bfloat16)
        out_grad_t = lax.dot_general(
            grad_branch_low, attended_low, tn, preferred_element_type=jnp.float32
        )
        late_rows = jnp.concatenate(
            [
                out_grad_t.reshape(chips, 2, -1, model_width),
                up_grad_t.reshape(chips, 2, -1, model_width),
            ],
            axis=2,
        )
        late = ring_reduce_steps(
            ring, [(late_rows, "both"), (down_grad_t.reshape((chips, 2, -1) + down_grad_t.shape[1:]), "both")]
        )
        grad_attended = jnp.dot(grad_branch_low, out_t, preferred_element_type=jnp.float32).astype(
            jnp.bfloat16
        )
        kernel_count = tables[0].shape[0]
        start_sums = (
            jnp.zeros((kernel_count, head_count), jnp.float32),
            jnp.zeros((kernel_count,), jnp.float32),
            jnp.zeros((kernel_count,), jnp.float32),
            jnp.zeros((ATOM_TYPES, ATOM_TYPES), jnp.float32),
            jnp.zeros((ATOM_TYPES, ATOM_TYPES), jnp.float32),
        )
        kernel_sums = start_sums
        q_grads, k_grads, v_grads = [], [], []
        grad_attended_blocks = grad_attended.reshape(split_shape)
        stepper = Stepper(late)
        for b in range(blocks):
            gate = stepper.tie(grad_attended_blocks[b])
            kernel_sums, (qg, kg, vg) = block_backward(
                kernel_sums,
                (
                    queries[b],
                    key_rows[b],
                    value_rows[b],
                    gate,
                    log_sums[b],
                    pos_blocks[b],
                    type_blocks[b],
                    mol_blocks[b],
                    pad_blocks[b],
                ),
                tables=tables,
                kernel_heads=heads_full,
                tile_rows=tile_rows,
                hook=stepper.tie,
            )
            q_grads.append(qg)
            k_grads.append(kg)
            v_grads.append(vg)
        queries_grad = jnp.stack(q_grads)
        keys_grad = jnp.stack(k_grads)
        values_grad = jnp.stack(v_grads)
        grad_projected = jnp.concatenate(
            [
                queries_grad.reshape(row_count, model_width),
                keys_grad.reshape(row_count, model_width),
                values_grad.reshape(row_count, model_width),
            ],
            axis=1,
        ).astype(jnp.bfloat16)
        in_grad_t = lax.dot_general(grad_projected, act_one, tn, preferred_element_type=jnp.float32)
        grad_act_one = jnp.dot(grad_projected, in_t, preferred_element_type=jnp.float32)
        grad_norm_one, gain_one_grad, shift_one_grad = norm_backward(
            grad_act_one, normed_one, inv_one, gains_now[0]
        )
        inputs_grad = grad_mid + grad_norm_one
        projected_sums = jnp.sum(grad_projected.astype(jnp.float32), axis=0)
        heads_grad, means_grad, widths_grad, scale_grad, shift_grad = kernel_sums
        small_grads = [
            jnp.stack([gain_one_grad, gain_two_grad]),
            jnp.stack(
                [
                    shift_one_grad,
                    shift_two_grad,
                    projected_sums[:model_width],
                    projected_sums[2 * model_width :],
                    jnp.sum(grad_branch_low.astype(jnp.float32), axis=0),
                    jnp.sum(grad_final, axis=0),
                ]
            ),
            up_bias_grad,
            means_grad,
            widths_grad,
            scale_grad,
            shift_grad,
            heads_grad,
        ]
        late_owned = stepper.finish()
        out_owned = late_owned[0][:out_rows]
        up_owned = late_owned[0][out_rows:]
        down_owned = late_owned[1]
        last = jnp.concatenate(
            [
                in_grad_t.reshape((chips, 2, -1) + in_grad_t.shape[1:]),
                pack_small_grads(small_grads, fsdp, chips),
            ],
            axis=2,
        )
        (last_owned,) = run_steps(ring_reduce_steps(ring, [(last, "both")]))
        in_rows = in_grad_t.shape[0] // fsdp
        in_owned = last_owned[:in_rows]
        small_owned = last_owned[in_rows:]
        sg = unpack_small_owned(small_owned, offsets)
        return (
            rows_out,
            inputs_grad,
            sg[0],
            sg[1],
            sg[2],
            in_owned.T,
            out_owned.T,
            up_owned.T,
            down_owned.T,
            sg[3],
            sg[4],
            sg[5],
            sg[6],
            sg[7],
        )

    return body


def solution(mesh):
    reps, fsdp = mesh.devices.shape
    chips = fsdp // 2
    grid = Mesh(mesh.devices.reshape(reps, chips, 2), ("rep", "chip", "core"))
    chips_x = 1
    try:
        coords = [tuple(d.coords) for d in mesh.devices[0, ::2]]
        xs = sorted({c[0] for c in coords})
        chips_x = len(xs)
        flat_ok = all(
            coords[i][0] == xs[i % chips_x] for i in range(chips)
        )
        if not flat_ok:
            chips_x = 1
    except Exception:
        chips_x = 1
    ring = None
    if chips <= 8:
        ring = Ring(snake_ring(chips_x, chips // chips_x))
    atoms = ("rep", "chip", "core")
    cols = ("chip", "core")
    placed = (
        P(atoms, None),
        P(atoms),
        P(None, atoms),
        P(atoms),
        P(atoms),
        P(atoms),
        P(atoms, None),
        P(None, cols),
        P(None, cols),
        P(cols),
        P(None, cols),
        P(None, cols),
        P(None, cols),
        P(None, cols),
        P(cols),
        P(cols),
        P(cols),
        P(cols),
        P(cols, None),
    )
    return jax.shard_map(
        make_body(ring, chips),
        mesh=grid,
        in_specs=placed,
        out_specs=(
            P(atoms, None),
            P(atoms, None),
            P(None, cols),
            P(None, cols),
            P(cols),
            P(None, cols),
            P(None, cols),
            P(None, cols),
            P(None, cols),
            P(cols),
            P(cols),
            P(cols),
            P(cols),
            P(cols, None),
        ),
        check_vma=False,
    )
```

```python
from functools import partial
import math

import jax
import jax.numpy as jnp
from jax import lax
from jax.sharding import Mesh, PartitionSpec as P
import numpy as np

ATOM_TYPES = 64


epsilon = 1e-05
masked_score = -1000000000.0
time_scale = 1000.0
root_two_pi = math.sqrt(2.0 * math.pi)
highest = lax.Precision.HIGHEST


def time_embedding(times, model_width):
    half_width = model_width // 2
    counter = jnp.arange(half_width, dtype=jnp.float32)
    frequency = jnp.exp(counter * (-math.log(10000.0) / half_width))
    angles = (time_scale * times)[:, None] * frequency[None, :]
    return jnp.concatenate([jnp.sin(angles), jnp.cos(angles)], axis=1)


def layer_norm(values, gain_row, shift_row):
    center = values - jnp.mean(values, axis=1, keepdims=True)
    inv_std = lax.rsqrt(jnp.mean(center * center, axis=1, keepdims=True) + epsilon)
    normed = center * inv_std
    return (normed * gain_row + shift_row, normed, inv_std)


def norm_backward(grad_out, normed, inv_std, gain_row):
    grad_normed = grad_out * gain_row
    first_mean = jnp.mean(grad_normed, axis=1, keepdims=True)
    second_mean = jnp.mean(grad_normed * normed, axis=1, keepdims=True)
    grad_input = inv_std * (grad_normed - first_mean - normed * second_mean)
    return (grad_input, jnp.sum(grad_out * normed, axis=0), jnp.sum(grad_out, axis=0))


def gelu_value(values):
    return values * (0.5 + 0.5 * lax.erf(values * math.sqrt(0.5)))


def gelu_slope(values):
    return (
        0.5
        + 0.5 * lax.erf(values * math.sqrt(0.5))
        + values * jnp.exp(-0.5 * values * values) / root_two_pi
    )


def pair_terms(pos_rows, pos_cols, type_rows, type_cols, tables):
    kernel_means, kernel_widths, scale_table, shift_table = tables
    offsets = pos_rows[:, :, None] - pos_cols[:, None, :]
    distance = jnp.sqrt(jnp.sum(offsets * offsets, axis=0))
    type_range = jnp.arange(ATOM_TYPES, dtype=jnp.int32)
    hot_rows = (type_rows[:, None] == type_range[None, :]).astype(jnp.float32)
    hot_cols = (type_cols[:, None] == type_range[None, :]).astype(jnp.float32)
    scale_pair = jnp.dot(
        jnp.dot(hot_rows, scale_table, precision=highest), hot_cols.T, precision=highest
    )
    shift_pair = jnp.dot(
        jnp.dot(hot_rows, shift_table, precision=highest), hot_cols.T, precision=highest
    )
    stretched = scale_pair * distance + shift_pair
    kernel_gap = (stretched[:, :, None] - kernel_means) / kernel_widths
    kernels = jnp.exp(-0.5 * kernel_gap * kernel_gap) / (root_two_pi * kernel_widths)
    return (distance, hot_rows, hot_cols, kernel_gap, kernels)


def allowed_pairs(row_ids, col_ids, mol_rows, mol_cols, pad_cols):
    same_mol = mol_rows[:, None] == mol_cols[None, :]
    key_live = (pad_cols[None, :] == 1) | (row_ids[:, None] == col_ids[None, :])
    return same_mol & key_live


def tile_scores(q_tile, key_block, kernels_low, kernel_heads, allowed, score_scale):
    pair_bias = jnp.einsum(
        "ijk,kh->hij", kernels_low, kernel_heads, preferred_element_type=jnp.float32
    )
    raw_scores = jnp.einsum("ihd,jhd->hij", q_tile, key_block, preferred_element_type=jnp.float32)
    return jnp.where(allowed[None], raw_scores * score_scale + pair_bias, masked_score)


def block_forward(pieces, tables, kernel_heads, tile_rows):
    queries, key_block, value_block, positions, types, mols, pads = pieces
    block_rows = queries.shape[0]
    score_scale = 1.0 / math.sqrt(queries.shape[2])
    col_ids = jnp.arange(block_rows, dtype=jnp.int32)

    def one_tile(running, tile_index):
        first_row = tile_index * tile_rows
        row_ids = first_row + jnp.arange(tile_rows, dtype=jnp.int32)
        terms = pair_terms(positions, positions, types, types, tables)
        kernels_low = terms[4].astype(jnp.bfloat16)
        allowed = allowed_pairs(row_ids, col_ids, mols, mols, pads)
        scores = tile_scores(queries, key_block, kernels_low, kernel_heads, allowed, score_scale)
        row_max = jnp.max(scores, axis=2, keepdims=True)
        exponent = jnp.exp(scores - row_max)
        row_sum = jnp.sum(exponent, axis=2, keepdims=True)
        probs_low = (exponent / row_sum).astype(jnp.bfloat16)
        attended = jnp.einsum(
            "hij,jhd->ihd", probs_low, value_block, preferred_element_type=jnp.float32
        )
        return (running, (attended, (row_max + jnp.log(row_sum))[:, :, 0]))

    count = block_rows // tile_rows
    if count == 1:
        _, (attended, log_sums) = one_tile(None, 0)
        return (attended.reshape(block_rows, -1), log_sums)
    _, (attended, log_sums) = lax.scan(one_tile, None, jnp.arange(count, dtype=jnp.int32))
    attended = attended.reshape(block_rows, -1)
    log_sums = jnp.transpose(log_sums, (1, 0, 2)).reshape(log_sums.shape[1], block_rows)
    return (attended, log_sums)


def block_backward(running, pieces, tables, kernel_heads, tile_rows, hook=None):
    queries, key_block, value_block, grad_attended, log_sums, positions, types, mols, pads = pieces
    kernel_widths = tables[1]
    block_rows = queries.shape[0]
    score_scale = 1.0 / math.sqrt(queries.shape[2])
    col_ids = jnp.arange(block_rows, dtype=jnp.int32)

    def one_tile(partial_sums, tile_index):
        keys_grad, values_grad, heads_grad, means_grad, widths_grad, scale_grad, shift_grad = (
            partial_sums
        )
        first_row = tile_index * tile_rows
        row_ids = first_row + jnp.arange(tile_rows, dtype=jnp.int32)
        distance, hot_rows, hot_cols, kernel_gap, kernels = pair_terms(
            positions, positions, types, types, tables
        )
        kernels_low = kernels.astype(jnp.bfloat16)
        allowed = allowed_pairs(row_ids, col_ids, mols, mols, pads)
        scores = tile_scores(queries, key_block, kernels_low, kernel_heads, allowed, score_scale)
        attn_probs = jnp.exp(scores - log_sums[:, :, None])
        grad_probs = jnp.einsum(
            "ihd,jhd->hij", grad_attended, value_block, preferred_element_type=jnp.float32
        )
        values_grad = values_grad + jnp.einsum(
            "hij,ihd->jhd",
            attn_probs.astype(jnp.bfloat16),
            grad_attended,
            preferred_element_type=jnp.float32,
        )
        probs_dot = jnp.sum(attn_probs * grad_probs, axis=2, keepdims=True)
        grad_scores = (attn_probs * (grad_probs - probs_dot)).astype(jnp.bfloat16)
        if hook is not None:
            grad_scores = hook(grad_scores)
        query_grad = (
            jnp.einsum("hij,jhd->ihd", grad_scores, key_block, preferred_element_type=jnp.float32)
            * score_scale
        )
        keys_grad = (
            keys_grad
            + jnp.einsum("hij,ihd->jhd", grad_scores, queries, preferred_element_type=jnp.float32)
            * score_scale
        )
        heads_grad = heads_grad + jnp.einsum(
            "ijk,hij->kh", kernels_low, grad_scores, preferred_element_type=jnp.float32
        )
        grad_kernels = jnp.einsum(
            "hij,kh->ijk", grad_scores, kernel_heads, preferred_element_type=jnp.float32
        )
        spread = grad_kernels * kernels
        mean_part = spread * kernel_gap / kernel_widths
        means_grad = means_grad + jnp.sum(mean_part, axis=(0, 1))
        widths_grad = widths_grad + jnp.sum(
            spread * (kernel_gap * kernel_gap - 1.0) / kernel_widths, axis=(0, 1)
        )
        grad_stretched = -jnp.sum(mean_part, axis=2)
        scale_grad = scale_grad + jnp.dot(
            jnp.dot(hot_rows.T, grad_stretched * distance, precision=highest),
            hot_cols,
            precision=highest,
        )
        shift_grad = shift_grad + jnp.dot(
            jnp.dot(hot_rows.T, grad_stretched, precision=highest), hot_cols, precision=highest
        )
        return (
            (keys_grad, values_grad, heads_grad, means_grad, widths_grad, scale_grad, shift_grad),
            query_grad,
        )

    zero_block = jnp.zeros(key_block.shape, jnp.float32)
    count = block_rows // tile_rows
    if count == 1:
        sums_out, query_grads = one_tile((zero_block, zero_block) + tuple(running), 0)
        return (sums_out[2:], (query_grads.reshape(key_block.shape), sums_out[0], sums_out[1]))
    sums_out, query_grads = lax.scan(
        one_tile, (zero_block, zero_block) + tuple(running), jnp.arange(count, dtype=jnp.int32)
    )
    query_grads = query_grads.reshape(key_block.shape)
    return (sums_out[2:], (query_grads, sums_out[0], sums_out[1]))


def snake_ring(chips_x, chips_other):
    if chips_x == 2 and chips_other >= 2:
        return [2 * z for z in range(chips_other)] + [
            2 * z + 1 for z in reversed(range(chips_other))
        ]
    return list(range(chips_x * chips_other))


class Ring:
    def __init__(self, order):
        self.order = order
        self.n = len(order)
        pos = np.zeros(self.n, np.int32)
        for i, c in enumerate(order):
            pos[c] = i
        self.pos = pos
        self.cw = [(order[i], order[(i + 1) % self.n]) for i in range(self.n)]
        self.ccw = [(order[i], order[(i - 1) % self.n]) for i in range(self.n)]

    def here(self):
        chip = lax.axis_index("chip")
        core = lax.axis_index("core")
        return chip, core, jnp.asarray(self.pos)[chip]

    def chip_at(self, position):
        return jnp.asarray(np.array(self.order, np.int32))[position % self.n]


SWAP = [(0, 1), (1, 0)]


def _halves(x, axis):
    size = x.shape[axis] // 2
    return (
        lax.slice_in_dim(x, 0, size, axis=axis),
        lax.slice_in_dim(x, size, 2 * size, axis=axis),
    )


def ring_gather(ring, pieces, chips):
    if ring is None:
        return [
            lax.all_gather(x, ("chip", "core"), axis=0, tiled=False).reshape((chips, 2) + x.shape)
            for x, _ in pieces
        ]
    chip, core, p = ring.here()
    n = ring.n
    bufs, fronts = [], []
    for x, axis in pieces:
        buf = jnp.zeros((n, 2) + x.shape, x.dtype)
        buf = lax.dynamic_update_slice(buf, x[None, None], (chip, core) + (0,) * x.ndim)
        bufs.append(buf)
        if axis is None:
            fronts.append([x, None])
        else:
            fronts.append(list(_halves(x, axis)))
    partner = lax.ppermute([x for x, _ in pieces], "core", SWAP)
    for i, x in enumerate(partner):
        bufs[i] = lax.dynamic_update_slice(
            bufs[i], x[None, None], (chip, 1 - core) + (0,) * x.ndim
        )
    for step in range(1, n):
        going = [f[0] for f in fronts]
        coming = [f[1] for f in fronts if f[1] is not None]
        going = lax.ppermute(going, "chip", ring.cw)
        coming = lax.ppermute(coming, "chip", ring.ccw) if coming else []
        from_cw = ring.chip_at(p - step)
        from_ccw = ring.chip_at(p + step)
        both = lax.ppermute([going, coming], "core", SWAP)
        j = 0
        for i, (x, axis) in enumerate(pieces):
            fronts[i][0] = going[i]
            parts = [(going[i], both[0][i], from_cw, 0)]
            if axis is not None:
                fronts[i][1] = coming[j]
                parts.append((coming[j], both[1][j], from_ccw, x.shape[axis] // 2))
                j += 1
            for mine, theirs, source, offset in parts:
                start = [0] * x.ndim
                if axis is not None:
                    start[axis] = offset
                bufs[i] = lax.dynamic_update_slice(
                    bufs[i], mine[None, None], (source, core) + tuple(start)
                )
                bufs[i] = lax.dynamic_update_slice(
                    bufs[i], theirs[None, None], (source, 1 - core) + tuple(start)
                )
    return bufs


def ring_reduce_steps(ring, pieces, send=jnp.bfloat16):
    if ring is None:
        owned = []
        for g, _ in pieces:
            flat = g.reshape((-1,) + g.shape[3:])
            part = lax.psum_scatter(flat, ("chip", "core"), scatter_dimension=0, tiled=True)
            owned.append(lax.psum(part.astype(send), "rep").astype(jnp.float32))
        yield owned
        return owned
    chip, core, p = ring.here()
    n = ring.n
    mine, theirs = [], []
    for g, _ in pieces:
        mine.append(lax.dynamic_index_in_dim(g, core, axis=1, keepdims=False))
        theirs.append(lax.dynamic_index_in_dim(g, 1 - core, axis=1, keepdims=False).astype(send))
    got = lax.ppermute(theirs, "core", SWAP)
    yield got
    flows = []
    for i, (g, way) in enumerate(pieces):
        if way == "both":
            flows.append((i, 1, n // 2, mine[i], got[i]))
            flows.append((i, -1, (n - 1) // 2, mine[i], got[i]))
        elif isinstance(way, tuple):
            axis = way[1] + 1
            for d, (m, t) in zip((1, -1), zip(_halves(mine[i], axis), _halves(got[i], axis))):
                flows.append((i, d, n - 1, m, t))
        else:
            flows.append((i, way, n - 1, mine[i], got[i]))

    def contribution(m, t, position):
        at = ring.chip_at(position)
        own = lax.dynamic_index_in_dim(m, at, axis=0, keepdims=False)
        other = lax.dynamic_index_in_dim(t, at, axis=0, keepdims=False)
        return own + other.astype(jnp.float32)

    acc = [contribution(m, t, p + d * hops) for _, d, hops, m, t in flows]
    for step in range(1, max(f[2] for f in flows) + 1):
        moved = []
        for d in (1, -1):
            chosen = [k for k, f in enumerate(flows) if f[1] == d and f[2] >= step]
            if chosen:
                out = lax.ppermute([acc[k].astype(send) for k in chosen], "chip", ring.cw if d == 1 else ring.ccw)
                for k, o in zip(chosen, out):
                    acc[k] = o.astype(jnp.float32)
                moved.extend(out)
        yield moved
        for k, (_, d, hops, m, t) in enumerate(flows):
            if hops > step:
                acc[k] = acc[k] + contribution(m, t, p + d * (hops - step))
    owned = []
    for i, (g, way) in enumerate(pieces):
        parts = [(a, f) for a, f in zip(acc, flows) if f[0] == i]
        if way == "both":
            total = contribution(parts[0][1][3], parts[0][1][4], p) + parts[0][0] + parts[1][0]
        else:
            total = [a + contribution(f[3], f[4], p) for a, f in parts]
            total = total[0] if len(total) == 1 else jnp.concatenate(total, axis=way[1])
        owned.append(total)
    other = lax.ppermute([o.astype(send) for o in owned], "rep", SWAP)
    yield other
    return [o + t.astype(jnp.float32) for o, t in zip(owned, other)]


class Stepper:
    def __init__(self, gen):
        self.gen = gen
        self.result = None
        self.over = False

    def tie(self, value):
        if self.over:
            return value
        try:
            ready = next(self.gen)
        except StopIteration as done:
            self.result, self.over = done.value, True
            return value
        _, value = lax.optimization_barrier((ready, value))
        return value

    def finish(self):
        if not self.over:
            self.result, self.over = run_steps(self.gen), True
        return self.result


def run_steps(gen):
    while True:
        try:
            next(gen)
        except StopIteration as done:
            return done.value


SMALL_ROWS, SMALL_LANES = 16, 768


def small_layout(fsdp):
    d = 768 // fsdp
    sizes = [2 * d, 6 * d, 3072 // fsdp, 128 // fsdp, 128 // fsdp, 4096 // fsdp, 4096 // fsdp, (128 // fsdp) * 32]
    offsets, at = [], 0
    for size in sizes:
        offsets.append((at, size))
        at += size
    assert at <= SMALL_ROWS * SMALL_LANES
    return offsets


def pack_small(parts):
    flat = jnp.concatenate([part.reshape(-1) for part in parts])
    flat = jnp.pad(flat, (0, SMALL_ROWS * SMALL_LANES - flat.shape[0]))
    return flat.reshape(SMALL_ROWS, SMALL_LANES)


def unpack_small_full(gathered, offsets, fsdp):
    flat = gathered.reshape(fsdp, -1).astype(jnp.float32)
    take = [flat[:, at : at + size] for at, size in offsets]
    d = 768 // fsdp
    return [
        take[0].reshape(fsdp, 2, d).transpose(1, 0, 2).reshape(2, -1),
        take[1].reshape(fsdp, 6, d).transpose(1, 0, 2).reshape(6, -1),
        take[2].reshape(-1),
        take[3].reshape(-1),
        take[4].reshape(-1),
        take[5].reshape(ATOM_TYPES, ATOM_TYPES),
        take[6].reshape(ATOM_TYPES, ATOM_TYPES),
        take[7].reshape(-1, 32),
    ]


def pack_small_grads(grads, fsdp, chips):
    d = 768 // fsdp
    blocks = [
        grads[0].reshape(2, fsdp, d).transpose(1, 0, 2),
        grads[1].reshape(6, fsdp, d).transpose(1, 0, 2),
    ] + [g.reshape(-1) for g in grads[2:]]
    flat = jnp.concatenate([blk.reshape(fsdp, -1) for blk in blocks], axis=1)
    flat = jnp.pad(flat, ((0, 0), (0, SMALL_ROWS * SMALL_LANES - flat.shape[1])))
    return flat.reshape(chips, 2, SMALL_ROWS, SMALL_LANES)


def unpack_small_owned(block, offsets):
    flat = block.reshape(-1)
    take = [flat[at : at + size] for at, size in offsets]
    return [
        take[0].reshape(2, -1),
        take[1].reshape(6, -1),
        take[2],
        take[3],
        take[4],
        take[5],
        take[6],
        take[7].reshape(-1, 32),
    ]


def make_body(ring, chips):
    fsdp = 2 * chips

    def body(
        inputs,
        times,
        positions,
        atom_types,
        molecule_ids,
        pad_mask,
        cotangent,
        norm_gains,
        bias_rows,
        up_bias,
        input_weight,
        output_weight,
        up_weight,
        down_weight,
        kernel_means,
        kernel_widths,
        pair_scale,
        pair_shift,
        kernel_heads,
    ):
        offsets = small_layout(fsdp)
        small = jnp.concatenate(
            [
                part.reshape(-1)
                for part in (norm_gains, bias_rows, up_bias, kernel_means, kernel_widths, pair_scale, pair_shift, kernel_heads)
            ]
        )
        small = jnp.pad(small, (0, -small.shape[0] % 128))
        width = input_weight.shape[0]
        small_all = lax.all_gather(small, ("chip", "core"), axis=0, tiled=False)
        in_t = lax.all_gather(input_weight.T, ("chip", "core"), axis=0, tiled=True)
        down_rows = down_weight.shape[1]
        down_packed = (
            down_weight.T.reshape(down_rows, -1, width).transpose(1, 0, 2).reshape(-1, width)
        )
        second = jnp.concatenate([output_weight.T, up_weight.T, down_packed], axis=0)
        second_all = lax.all_gather(second, ("chip", "core"), axis=0, tiled=False)
        params = unpack_small_full(small_all, offsets, fsdp)
        out_rows = output_weight.shape[1]
        up_rows = up_weight.shape[1]
        out_t = second_all[:, :out_rows].reshape(-1, width)
        up_t = second_all[:, out_rows : out_rows + up_rows].reshape(-1, width)
        down_t = (
            second_all[:, out_rows + up_rows :]
            .reshape(fsdp, -1, down_rows, width)
            .transpose(0, 2, 1, 3)
            .reshape(-1, down_weight.shape[0])
        )
        gains_now, biases_now, up_shift = params[0], params[1], params[2]
        tables = (params[3], params[4], params[5], params[6])
        heads_full = params[7].astype(jnp.bfloat16)

        row_count = inputs.shape[0]
        model_width = inputs.shape[1]
        head_count = heads_full.shape[1]
        head_size = model_width // head_count
        block_rows = min(128, row_count)
        blocks = row_count // block_rows
        tile_rows = min(128, block_rows)
        nt = (((1,), (1,)), ((), ()))
        tn = (((0,), (0,)), ((), ()))

        stream = inputs.astype(jnp.float32) + time_embedding(times, model_width)
        normed_out, normed_one, inv_one = layer_norm(stream, gains_now[0], biases_now[0])
        act_one = normed_out.astype(jnp.bfloat16)
        qkv_shift = jnp.concatenate([biases_now[2], jnp.zeros_like(biases_now[2]), biases_now[3]])
        projected = (
            lax.dot_general(act_one, in_t, nt, preferred_element_type=jnp.float32) + qkv_shift
        ).astype(jnp.bfloat16)
        split_shape = (blocks, block_rows, head_count, head_size)
        queries = projected[:, :model_width].reshape(split_shape)
        key_rows = projected[:, model_width : 2 * model_width].reshape(split_shape)
        value_rows = projected[:, 2 * model_width :].reshape(split_shape)
        pos_blocks = jnp.transpose(positions.reshape(3, blocks, block_rows), (1, 0, 2))
        type_blocks = atom_types.reshape(blocks, block_rows)
        mol_blocks = molecule_ids.reshape(blocks, block_rows)
        pad_blocks = pad_mask.reshape(blocks, block_rows)
        fwd = [
            block_forward(
                (queries[b], key_rows[b], value_rows[b], pos_blocks[b], type_blocks[b], mol_blocks[b], pad_blocks[b]),
                tables=tables,
                kernel_heads=heads_full,
                tile_rows=tile_rows,
            )
            for b in range(blocks)
        ]
        attended = jnp.stack([f[0] for f in fwd])
        log_sums = [f[1] for f in fwd]
        attended_low = attended.reshape(row_count, model_width).astype(jnp.bfloat16)
        mid = stream + (
            lax.dot_general(attended_low, out_t, nt, preferred_element_type=jnp.float32)
            + biases_now[4]
        )
        normed_out_two, normed_two, inv_two = layer_norm(mid, gains_now[1], biases_now[1])
        act_two = normed_out_two.astype(jnp.bfloat16)
        hidden_pre = (
            lax.dot_general(act_two, up_t, nt, preferred_element_type=jnp.float32) + up_shift
        )
        hidden_low = gelu_value(hidden_pre).astype(jnp.bfloat16)
        final = mid + (
            lax.dot_general(hidden_low, down_t, nt, preferred_element_type=jnp.float32)
            + biases_now[5]
        )
        rows_out = final.astype(jnp.bfloat16)

        grad_final = cotangent.astype(jnp.float32)
        down_grad_t = lax.dot_general(cotangent, hidden_low, tn, preferred_element_type=jnp.float32)
        grad_hidden = jnp.dot(cotangent, down_t, preferred_element_type=jnp.float32) * gelu_slope(
            hidden_pre
        )
        grad_hidden_low = grad_hidden.astype(jnp.bfloat16)
        up_grad_t = lax.dot_general(grad_hidden_low, act_two, tn, preferred_element_type=jnp.float32)
        up_bias_grad = jnp.sum(grad_hidden_low.astype(jnp.float32), axis=0)
        grad_act_two = jnp.dot(grad_hidden_low, up_t, preferred_element_type=jnp.float32)
        grad_norm_two, gain_two_grad, shift_two_grad = norm_backward(
            grad_act_two, normed_two, inv_two, gains_now[1]
        )
        grad_mid = grad_final + grad_norm_two
        grad_branch_low = grad_mid.astype(jnp.bfloat16)
        out_grad_t = lax.dot_general(
            grad_branch_low, attended_low, tn, preferred_element_type=jnp.float32
        )
        late_rows = jnp.concatenate(
            [
                out_grad_t.reshape(chips, 2, -1, model_width),
                up_grad_t.reshape(chips, 2, -1, model_width),
            ],
            axis=2,
        )
        late = ring_reduce_steps(
            ring, [(late_rows, "both"), (down_grad_t.reshape((chips, 2, -1) + down_grad_t.shape[1:]), "both")]
        )
        grad_attended = jnp.dot(grad_branch_low, out_t, preferred_element_type=jnp.float32).astype(
            jnp.bfloat16
        )
        kernel_count = tables[0].shape[0]
        start_sums = (
            jnp.zeros((kernel_count, head_count), jnp.float32),
            jnp.zeros((kernel_count,), jnp.float32),
            jnp.zeros((kernel_count,), jnp.float32),
            jnp.zeros((ATOM_TYPES, ATOM_TYPES), jnp.float32),
            jnp.zeros((ATOM_TYPES, ATOM_TYPES), jnp.float32),
        )
        kernel_sums = start_sums
        q_grads, k_grads, v_grads = [], [], []
        grad_attended_blocks = grad_attended.reshape(split_shape)
        stepper = Stepper(late)
        for b in range(blocks):
            gate = stepper.tie(grad_attended_blocks[b])
            kernel_sums, (qg, kg, vg) = block_backward(
                kernel_sums,
                (
                    queries[b],
                    key_rows[b],
                    value_rows[b],
                    gate,
                    log_sums[b],
                    pos_blocks[b],
                    type_blocks[b],
                    mol_blocks[b],
                    pad_blocks[b],
                ),
                tables=tables,
                kernel_heads=heads_full,
                tile_rows=tile_rows,
                hook=stepper.tie,
            )
            q_grads.append(qg)
            k_grads.append(kg)
            v_grads.append(vg)
        queries_grad = jnp.stack(q_grads)
        keys_grad = jnp.stack(k_grads)
        values_grad = jnp.stack(v_grads)
        grad_projected = jnp.concatenate(
            [
                queries_grad.reshape(row_count, model_width),
                keys_grad.reshape(row_count, model_width),
                values_grad.reshape(row_count, model_width),
            ],
            axis=1,
        ).astype(jnp.bfloat16)
        in_grad_t = lax.dot_general(grad_projected, act_one, tn, preferred_element_type=jnp.float32)
        grad_act_one = jnp.dot(grad_projected, in_t, preferred_element_type=jnp.float32)
        grad_norm_one, gain_one_grad, shift_one_grad = norm_backward(
            grad_act_one, normed_one, inv_one, gains_now[0]
        )
        inputs_grad = grad_mid + grad_norm_one
        projected_sums = jnp.sum(grad_projected.astype(jnp.float32), axis=0)
        heads_grad, means_grad, widths_grad, scale_grad, shift_grad = kernel_sums
        small_grads = [
            jnp.stack([gain_one_grad, gain_two_grad]),
            jnp.stack(
                [
                    shift_one_grad,
                    shift_two_grad,
                    projected_sums[:model_width],
                    projected_sums[2 * model_width :],
                    jnp.sum(grad_branch_low.astype(jnp.float32), axis=0),
                    jnp.sum(grad_final, axis=0),
                ]
            ),
            up_bias_grad,
            means_grad,
            widths_grad,
            scale_grad,
            shift_grad,
            heads_grad,
        ]
        late_owned = stepper.finish()
        out_owned = late_owned[0][:out_rows]
        up_owned = late_owned[0][out_rows:]
        down_owned = late_owned[1]
        last = jnp.concatenate(
            [
                in_grad_t.reshape((chips, 2, -1) + in_grad_t.shape[1:]),
                pack_small_grads(small_grads, fsdp, chips),
            ],
            axis=2,
        )
        (last_owned,) = run_steps(ring_reduce_steps(ring, [(last, "both")]))
        in_rows = in_grad_t.shape[0] // fsdp
        in_owned = last_owned[:in_rows]
        small_owned = last_owned[in_rows:]
        sg = unpack_small_owned(small_owned, offsets)
        return (
            rows_out,
            inputs_grad,
            sg[0],
            sg[1],
            sg[2],
            in_owned.T,
            out_owned.T,
            up_owned.T,
            down_owned.T,
            sg[3],
            sg[4],
            sg[5],
            sg[6],
            sg[7],
        )

    return body


def solution(mesh):
    reps, fsdp = mesh.devices.shape
    chips = fsdp // 2
    grid = Mesh(mesh.devices.reshape(reps, chips, 2), ("rep", "chip", "core"))
    chips_x = 1
    try:
        coords = [tuple(d.coords) for d in mesh.devices[0, ::2]]
        xs = sorted({c[0] for c in coords})
        chips_x = len(xs)
        flat_ok = all(
            coords[i][0] == xs[i % chips_x] for i in range(chips)
        )
        if not flat_ok:
            chips_x = 1
    except Exception:
        chips_x = 1
    ring = None
    if chips <= 8:
        ring = Ring(snake_ring(chips_x, chips // chips_x))
    atoms = ("rep", "chip", "core")
    cols = ("chip", "core")
    placed = (
        P(atoms, None),
        P(atoms),
        P(None, atoms),
        P(atoms),
        P(atoms),
        P(atoms),
        P(atoms, None),
        P(None, cols),
        P(None, cols),
        P(cols),
        P(None, cols),
        P(None, cols),
        P(None, cols),
        P(None, cols),
        P(cols),
        P(cols),
        P(cols),
        P(cols),
        P(cols, None),
    )
    return jax.shard_map(
        make_body(ring, chips),
        mesh=grid,
        in_specs=placed,
        out_specs=(
            P(atoms, None),
            P(atoms, None),
            P(None, cols),
            P(None, cols),
            P(cols),
            P(None, cols),
            P(None, cols),
            P(None, cols),
            P(None, cols),
            P(cols),
            P(cols),
            P(cols),
            P(cols),
            P(cols, None),
        ),
        check_vma=False,
    )
```

```python
from functools import partial
import math

import jax
import jax.numpy as jnp
from jax import lax
from jax.sharding import Mesh, PartitionSpec as P
import numpy as np

ATOM_TYPES = 64


epsilon = 1e-05
masked_score = -1000000000.0
time_scale = 1000.0
root_two_pi = math.sqrt(2.0 * math.pi)
highest = lax.Precision.HIGHEST


def time_embedding(times, model_width):
    half_width = model_width // 2
    counter = jnp.arange(half_width, dtype=jnp.float32)
    frequency = jnp.exp(counter * (-math.log(10000.0) / half_width))
    angles = (time_scale * times)[:, None] * frequency[None, :]
    return jnp.concatenate([jnp.sin(angles), jnp.cos(angles)], axis=1)


def layer_norm(values, gain_row, shift_row):
    center = values - jnp.mean(values, axis=1, keepdims=True)
    inv_std = lax.rsqrt(jnp.mean(center * center, axis=1, keepdims=True) + epsilon)
    normed = center * inv_std
    return (normed * gain_row + shift_row, normed, inv_std)


def norm_backward(grad_out, normed, inv_std, gain_row):
    grad_normed = grad_out * gain_row
    first_mean = jnp.mean(grad_normed, axis=1, keepdims=True)
    second_mean = jnp.mean(grad_normed * normed, axis=1, keepdims=True)
    grad_input = inv_std * (grad_normed - first_mean - normed * second_mean)
    return (grad_input, jnp.sum(grad_out * normed, axis=0), jnp.sum(grad_out, axis=0))


def gelu_value(values):
    return values * (0.5 + 0.5 * lax.erf(values * math.sqrt(0.5)))


def gelu_slope(values):
    return (
        0.5
        + 0.5 * lax.erf(values * math.sqrt(0.5))
        + values * jnp.exp(-0.5 * values * values) / root_two_pi
    )


def pair_terms(pos_rows, pos_cols, type_rows, type_cols, tables):
    kernel_means, kernel_widths, scale_table, shift_table = tables
    offsets = pos_rows[:, :, None] - pos_cols[:, None, :]
    distance = jnp.sqrt(jnp.sum(offsets * offsets, axis=0))
    type_range = jnp.arange(ATOM_TYPES, dtype=jnp.int32)
    hot_rows = (type_rows[:, None] == type_range[None, :]).astype(jnp.float32)
    hot_cols = (type_cols[:, None] == type_range[None, :]).astype(jnp.float32)
    scale_pair = jnp.dot(
        jnp.dot(hot_rows, scale_table, precision=highest), hot_cols.T, precision=highest
    )
    shift_pair = jnp.dot(
        jnp.dot(hot_rows, shift_table, precision=highest), hot_cols.T, precision=highest
    )
    stretched = scale_pair * distance + shift_pair
    kernel_gap = (stretched[:, :, None] - kernel_means) / kernel_widths
    kernels = jnp.exp(-0.5 * kernel_gap * kernel_gap) / (root_two_pi * kernel_widths)
    return (distance, hot_rows, hot_cols, kernel_gap, kernels)


def allowed_pairs(row_ids, col_ids, mol_rows, mol_cols, pad_cols):
    same_mol = mol_rows[:, None] == mol_cols[None, :]
    key_live = (pad_cols[None, :] == 1) | (row_ids[:, None] == col_ids[None, :])
    return same_mol & key_live


def tile_scores(q_tile, key_block, kernels_low, kernel_heads, allowed, score_scale):
    pair_bias = jnp.einsum(
        "ijk,kh->hij", kernels_low, kernel_heads, preferred_element_type=jnp.float32
    )
    raw_scores = jnp.einsum("ihd,jhd->hij", q_tile, key_block, preferred_element_type=jnp.float32)
    return jnp.where(allowed[None], raw_scores * score_scale + pair_bias, masked_score)


def block_forward(pieces, tables, kernel_heads, tile_rows):
    queries, key_block, value_block, positions, types, mols, pads = pieces
    block_rows = queries.shape[0]
    score_scale = 1.0 / math.sqrt(queries.shape[2])
    col_ids = jnp.arange(block_rows, dtype=jnp.int32)

    def one_tile(running, tile_index):
        first_row = tile_index * tile_rows
        row_ids = first_row + jnp.arange(tile_rows, dtype=jnp.int32)
        terms = pair_terms(positions, positions, types, types, tables)
        kernels_low = terms[4].astype(jnp.bfloat16)
        allowed = allowed_pairs(row_ids, col_ids, mols, mols, pads)
        pair_bias = jnp.einsum(
            "ijk,kh->ihj", kernels_low, kernel_heads, preferred_element_type=jnp.float32
        )
        raw_scores = jnp.einsum("ihd,jhd->ihj", queries, key_block, preferred_element_type=jnp.float32)
        scores = jnp.where(allowed[:, None, :], raw_scores * score_scale + pair_bias, masked_score)
        row_max = jnp.max(scores, axis=2, keepdims=True)
        exponent = jnp.exp(scores - row_max)
        row_sum = jnp.sum(exponent, axis=2, keepdims=True)
        probs_low = (exponent / row_sum).astype(jnp.bfloat16)
        attended = jnp.einsum(
            "ihj,jhd->ihd", probs_low, value_block, preferred_element_type=jnp.float32
        )
        return (running, (attended, (row_max + jnp.log(row_sum))[:, :, 0].T))

    count = block_rows // tile_rows
    if count == 1:
        _, (attended, log_sums) = one_tile(None, 0)
        return (attended.reshape(block_rows, -1), log_sums)
    _, (attended, log_sums) = lax.scan(one_tile, None, jnp.arange(count, dtype=jnp.int32))
    attended = attended.reshape(block_rows, -1)
    log_sums = jnp.transpose(log_sums, (1, 0, 2)).reshape(log_sums.shape[1], block_rows)
    return (attended, log_sums)


def block_backward(running, pieces, tables, kernel_heads, tile_rows, hook=None):
    queries, key_block, value_block, grad_attended, log_sums, positions, types, mols, pads = pieces
    kernel_widths = tables[1]
    block_rows = queries.shape[0]
    score_scale = 1.0 / math.sqrt(queries.shape[2])
    col_ids = jnp.arange(block_rows, dtype=jnp.int32)

    def one_tile(partial_sums, tile_index):
        keys_grad, values_grad, heads_grad, means_grad, widths_grad, scale_grad, shift_grad = (
            partial_sums
        )
        first_row = tile_index * tile_rows
        row_ids = first_row + jnp.arange(tile_rows, dtype=jnp.int32)
        distance, hot_rows, hot_cols, kernel_gap, kernels = pair_terms(
            positions, positions, types, types, tables
        )
        kernels_low = kernels.astype(jnp.bfloat16)
        allowed = allowed_pairs(row_ids, col_ids, mols, mols, pads)
        scores = tile_scores(queries, key_block, kernels_low, kernel_heads, allowed, score_scale)
        attn_probs = jnp.exp(scores - log_sums[:, :, None])
        grad_probs = jnp.einsum(
            "ihd,jhd->hij", grad_attended, value_block, preferred_element_type=jnp.float32
        )
        values_grad = values_grad + jnp.einsum(
            "hij,ihd->jhd",
            attn_probs.astype(jnp.bfloat16),
            grad_attended,
            preferred_element_type=jnp.float32,
        )
        probs_dot = jnp.sum(attn_probs * grad_probs, axis=2, keepdims=True)
        grad_scores = (attn_probs * (grad_probs - probs_dot)).astype(jnp.bfloat16)
        if hook is not None:
            grad_scores = hook(grad_scores)
        query_grad = (
            jnp.einsum("hij,jhd->ihd", grad_scores, key_block, preferred_element_type=jnp.float32)
            * score_scale
        )
        keys_grad = (
            keys_grad
            + jnp.einsum("hij,ihd->jhd", grad_scores, queries, preferred_element_type=jnp.float32)
            * score_scale
        )
        heads_grad = heads_grad + jnp.einsum(
            "ijk,hij->kh", kernels_low, grad_scores, preferred_element_type=jnp.float32
        )
        grad_kernels = jnp.einsum(
            "hij,kh->ijk", grad_scores, kernel_heads, preferred_element_type=jnp.float32
        )
        spread = grad_kernels * kernels
        mean_part = spread * kernel_gap / kernel_widths
        means_grad = means_grad + jnp.sum(mean_part, axis=(0, 1))
        widths_grad = widths_grad + jnp.sum(
            spread * (kernel_gap * kernel_gap - 1.0) / kernel_widths, axis=(0, 1)
        )
        grad_stretched = -jnp.sum(mean_part, axis=2)
        scale_grad = scale_grad + jnp.dot(
            jnp.dot(hot_rows.T, grad_stretched * distance, precision=highest),
            hot_cols,
            precision=highest,
        )
        shift_grad = shift_grad + jnp.dot(
            jnp.dot(hot_rows.T, grad_stretched, precision=highest), hot_cols, precision=highest
        )
        return (
            (keys_grad, values_grad, heads_grad, means_grad, widths_grad, scale_grad, shift_grad),
            query_grad,
        )

    zero_block = jnp.zeros(key_block.shape, jnp.float32)
    count = block_rows // tile_rows
    if count == 1:
        sums_out, query_grads = one_tile((zero_block, zero_block) + tuple(running), 0)
        return (sums_out[2:], (query_grads.reshape(key_block.shape), sums_out[0], sums_out[1]))
    sums_out, query_grads = lax.scan(
        one_tile, (zero_block, zero_block) + tuple(running), jnp.arange(count, dtype=jnp.int32)
    )
    query_grads = query_grads.reshape(key_block.shape)
    return (sums_out[2:], (query_grads, sums_out[0], sums_out[1]))


def snake_ring(chips_x, chips_other):
    if chips_x == 2 and chips_other >= 2:
        return [2 * z for z in range(chips_other)] + [
            2 * z + 1 for z in reversed(range(chips_other))
        ]
    return list(range(chips_x * chips_other))


class Ring:
    def __init__(self, order):
        self.order = order
        self.n = len(order)
        pos = np.zeros(self.n, np.int32)
        for i, c in enumerate(order):
            pos[c] = i
        self.pos = pos
        self.cw = [(order[i], order[(i + 1) % self.n]) for i in range(self.n)]
        self.ccw = [(order[i], order[(i - 1) % self.n]) for i in range(self.n)]

    def here(self):
        chip = lax.axis_index("chip")
        core = lax.axis_index("core")
        return chip, core, jnp.asarray(self.pos)[chip]

    def chip_at(self, position):
        return jnp.asarray(np.array(self.order, np.int32))[position % self.n]


SWAP = [(0, 1), (1, 0)]


def _halves(x, axis):
    size = x.shape[axis] // 2
    return (
        lax.slice_in_dim(x, 0, size, axis=axis),
        lax.slice_in_dim(x, size, 2 * size, axis=axis),
    )


def ring_gather(ring, pieces, chips):
    if ring is None:
        return [
            lax.all_gather(x, ("chip", "core"), axis=0, tiled=False).reshape((chips, 2) + x.shape)
            for x, _ in pieces
        ]
    chip, core, p = ring.here()
    n = ring.n
    bufs, fronts = [], []
    for x, axis in pieces:
        buf = jnp.zeros((n, 2) + x.shape, x.dtype)
        buf = lax.dynamic_update_slice(buf, x[None, None], (chip, core) + (0,) * x.ndim)
        bufs.append(buf)
        if axis is None:
            fronts.append([x, None])
        else:
            fronts.append(list(_halves(x, axis)))
    partner = lax.ppermute([x for x, _ in pieces], "core", SWAP)
    for i, x in enumerate(partner):
        bufs[i] = lax.dynamic_update_slice(
            bufs[i], x[None, None], (chip, 1 - core) + (0,) * x.ndim
        )
    for step in range(1, n):
        going = [f[0] for f in fronts]
        coming = [f[1] for f in fronts if f[1] is not None]
        going = lax.ppermute(going, "chip", ring.cw)
        coming = lax.ppermute(coming, "chip", ring.ccw) if coming else []
        from_cw = ring.chip_at(p - step)
        from_ccw = ring.chip_at(p + step)
        both = lax.ppermute([going, coming], "core", SWAP)
        j = 0
        for i, (x, axis) in enumerate(pieces):
            fronts[i][0] = going[i]
            parts = [(going[i], both[0][i], from_cw, 0)]
            if axis is not None:
                fronts[i][1] = coming[j]
                parts.append((coming[j], both[1][j], from_ccw, x.shape[axis] // 2))
                j += 1
            for mine, theirs, source, offset in parts:
                start = [0] * x.ndim
                if axis is not None:
                    start[axis] = offset
                bufs[i] = lax.dynamic_update_slice(
                    bufs[i], mine[None, None], (source, core) + tuple(start)
                )
                bufs[i] = lax.dynamic_update_slice(
                    bufs[i], theirs[None, None], (source, 1 - core) + tuple(start)
                )
    return bufs


def ring_reduce_steps(ring, pieces, send=jnp.bfloat16):
    if ring is None:
        owned = []
        for g, _ in pieces:
            flat = g.reshape((-1,) + g.shape[3:])
            part = lax.psum_scatter(flat, ("chip", "core"), scatter_dimension=0, tiled=True)
            owned.append(lax.psum(part.astype(send), "rep").astype(jnp.float32))
        yield owned
        return owned
    chip, core, p = ring.here()
    n = ring.n
    mine, theirs = [], []
    for g, _ in pieces:
        mine.append(lax.dynamic_index_in_dim(g, core, axis=1, keepdims=False))
        theirs.append(lax.dynamic_index_in_dim(g, 1 - core, axis=1, keepdims=False).astype(send))
    got = lax.ppermute(theirs, "core", SWAP)
    yield got
    flows = []
    for i, (g, way) in enumerate(pieces):
        if way == "both":
            flows.append((i, 1, n // 2, mine[i], got[i]))
            flows.append((i, -1, (n - 1) // 2, mine[i], got[i]))
        elif isinstance(way, tuple):
            axis = way[1] + 1
            for d, (m, t) in zip((1, -1), zip(_halves(mine[i], axis), _halves(got[i], axis))):
                flows.append((i, d, n - 1, m, t))
        else:
            flows.append((i, way, n - 1, mine[i], got[i]))

    def contribution(m, t, position):
        at = ring.chip_at(position)
        own = lax.dynamic_index_in_dim(m, at, axis=0, keepdims=False)
        other = lax.dynamic_index_in_dim(t, at, axis=0, keepdims=False)
        return own + other.astype(jnp.float32)

    acc = [contribution(m, t, p + d * hops) for _, d, hops, m, t in flows]
    for step in range(1, max(f[2] for f in flows) + 1):
        moved = []
        for d in (1, -1):
            chosen = [k for k, f in enumerate(flows) if f[1] == d and f[2] >= step]
            if chosen:
                out = lax.ppermute([acc[k].astype(send) for k in chosen], "chip", ring.cw if d == 1 else ring.ccw)
                for k, o in zip(chosen, out):
                    acc[k] = o.astype(jnp.float32)
                moved.extend(out)
        yield moved
        for k, (_, d, hops, m, t) in enumerate(flows):
            if hops > step:
                acc[k] = acc[k] + contribution(m, t, p + d * (hops - step))
    owned = []
    for i, (g, way) in enumerate(pieces):
        parts = [(a, f) for a, f in zip(acc, flows) if f[0] == i]
        if way == "both":
            total = contribution(parts[0][1][3], parts[0][1][4], p) + parts[0][0] + parts[1][0]
        else:
            total = [a + contribution(f[3], f[4], p) for a, f in parts]
            total = total[0] if len(total) == 1 else jnp.concatenate(total, axis=way[1])
        owned.append(total)
    other = lax.ppermute([o.astype(send) for o in owned], "rep", SWAP)
    yield other
    return [o + t.astype(jnp.float32) for o, t in zip(owned, other)]


class Stepper:
    def __init__(self, gen):
        self.gen = gen
        self.result = None
        self.over = False

    def tie(self, value):
        if self.over:
            return value
        try:
            ready = next(self.gen)
        except StopIteration as done:
            self.result, self.over = done.value, True
            return value
        _, value = lax.optimization_barrier((ready, value))
        return value

    def finish(self):
        if not self.over:
            self.result, self.over = run_steps(self.gen), True
        return self.result


def run_steps(gen):
    while True:
        try:
            next(gen)
        except StopIteration as done:
            return done.value


SMALL_ROWS, SMALL_LANES = 16, 768


def small_layout(fsdp):
    d = 768 // fsdp
    sizes = [2 * d, 6 * d, 3072 // fsdp, 128 // fsdp, 128 // fsdp, 4096 // fsdp, 4096 // fsdp, (128 // fsdp) * 32]
    offsets, at = [], 0
    for size in sizes:
        offsets.append((at, size))
        at += size
    assert at <= SMALL_ROWS * SMALL_LANES
    return offsets


def pack_small(parts):
    flat = jnp.concatenate([part.reshape(-1) for part in parts])
    flat = jnp.pad(flat, (0, SMALL_ROWS * SMALL_LANES - flat.shape[0]))
    return flat.reshape(SMALL_ROWS, SMALL_LANES)


def unpack_small_full(gathered, offsets, fsdp):
    flat = gathered.reshape(fsdp, -1).astype(jnp.float32)
    take = [flat[:, at : at + size] for at, size in offsets]
    d = 768 // fsdp
    return [
        take[0].reshape(fsdp, 2, d).transpose(1, 0, 2).reshape(2, -1),
        take[1].reshape(fsdp, 6, d).transpose(1, 0, 2).reshape(6, -1),
        take[2].reshape(-1),
        take[3].reshape(-1),
        take[4].reshape(-1),
        take[5].reshape(ATOM_TYPES, ATOM_TYPES),
        take[6].reshape(ATOM_TYPES, ATOM_TYPES),
        take[7].reshape(-1, 32),
    ]


def pack_small_grads(grads, fsdp, chips):
    d = 768 // fsdp
    blocks = [
        grads[0].reshape(2, fsdp, d).transpose(1, 0, 2),
        grads[1].reshape(6, fsdp, d).transpose(1, 0, 2),
    ] + [g.reshape(-1) for g in grads[2:]]
    flat = jnp.concatenate([blk.reshape(fsdp, -1) for blk in blocks], axis=1)
    flat = jnp.pad(flat, ((0, 0), (0, SMALL_ROWS * SMALL_LANES - flat.shape[1])))
    return flat.reshape(chips, 2, SMALL_ROWS, SMALL_LANES)


def unpack_small_owned(block, offsets):
    flat = block.reshape(-1)
    take = [flat[at : at + size] for at, size in offsets]
    return [
        take[0].reshape(2, -1),
        take[1].reshape(6, -1),
        take[2],
        take[3],
        take[4],
        take[5],
        take[6],
        take[7].reshape(-1, 32),
    ]


def make_body(ring, chips):
    fsdp = 2 * chips

    def body(
        inputs,
        times,
        positions,
        atom_types,
        molecule_ids,
        pad_mask,
        cotangent,
        norm_gains,
        bias_rows,
        up_bias,
        input_weight,
        output_weight,
        up_weight,
        down_weight,
        kernel_means,
        kernel_widths,
        pair_scale,
        pair_shift,
        kernel_heads,
    ):
        offsets = small_layout(fsdp)
        small = jnp.concatenate(
            [
                part.reshape(-1)
                for part in (norm_gains, bias_rows, up_bias, kernel_means, kernel_widths, pair_scale, pair_shift, kernel_heads)
            ]
        )
        small = jnp.pad(small, (0, -small.shape[0] % 128))
        width = input_weight.shape[0]
        small_all = lax.all_gather(small, ("chip", "core"), axis=0, tiled=False)
        in_t = lax.all_gather(input_weight.T, ("chip", "core"), axis=0, tiled=True)
        down_rows = down_weight.shape[1]
        down_packed = (
            down_weight.T.reshape(down_rows, -1, width).transpose(1, 0, 2).reshape(-1, width)
        )
        second = jnp.concatenate([output_weight.T, up_weight.T, down_packed], axis=0)
        second_all = lax.all_gather(second, ("chip", "core"), axis=0, tiled=False)
        params = unpack_small_full(small_all, offsets, fsdp)
        out_rows = output_weight.shape[1]
        up_rows = up_weight.shape[1]
        out_t = second_all[:, :out_rows].reshape(-1, width)
        up_t = second_all[:, out_rows : out_rows + up_rows].reshape(-1, width)
        down_t = (
            second_all[:, out_rows + up_rows :]
            .reshape(fsdp, -1, down_rows, width)
            .transpose(0, 2, 1, 3)
            .reshape(-1, down_weight.shape[0])
        )
        gains_now, biases_now, up_shift = params[0], params[1], params[2]
        tables = (params[3], params[4], params[5], params[6])
        heads_full = params[7].astype(jnp.bfloat16)

        row_count = inputs.shape[0]
        model_width = inputs.shape[1]
        head_count = heads_full.shape[1]
        head_size = model_width // head_count
        block_rows = min(128, row_count)
        blocks = row_count // block_rows
        tile_rows = min(128, block_rows)
        nt = (((1,), (1,)), ((), ()))
        tn = (((0,), (0,)), ((), ()))

        stream = inputs.astype(jnp.float32) + time_embedding(times, model_width)
        normed_out, normed_one, inv_one = layer_norm(stream, gains_now[0], biases_now[0])
        act_one = normed_out.astype(jnp.bfloat16)
        qkv_shift = jnp.concatenate([biases_now[2], jnp.zeros_like(biases_now[2]), biases_now[3]])
        projected = (
            lax.dot_general(act_one, in_t, nt, preferred_element_type=jnp.float32) + qkv_shift
        ).astype(jnp.bfloat16)
        split_shape = (blocks, block_rows, head_count, head_size)
        queries = projected[:, :model_width].reshape(split_shape)
        key_rows = projected[:, model_width : 2 * model_width].reshape(split_shape)
        value_rows = projected[:, 2 * model_width :].reshape(split_shape)
        pos_blocks = jnp.transpose(positions.reshape(3, blocks, block_rows), (1, 0, 2))
        type_blocks = atom_types.reshape(blocks, block_rows)
        mol_blocks = molecule_ids.reshape(blocks, block_rows)
        pad_blocks = pad_mask.reshape(blocks, block_rows)
        fwd = [
            block_forward(
                (queries[b], key_rows[b], value_rows[b], pos_blocks[b], type_blocks[b], mol_blocks[b], pad_blocks[b]),
                tables=tables,
                kernel_heads=heads_full,
                tile_rows=tile_rows,
            )
            for b in range(blocks)
        ]
        attended = jnp.stack([f[0] for f in fwd])
        log_sums = [f[1] for f in fwd]
        attended_low = attended.reshape(row_count, model_width).astype(jnp.bfloat16)
        mid = stream + (
            lax.dot_general(attended_low, out_t, nt, preferred_element_type=jnp.float32)
            + biases_now[4]
        )
        normed_out_two, normed_two, inv_two = layer_norm(mid, gains_now[1], biases_now[1])
        act_two = normed_out_two.astype(jnp.bfloat16)
        hidden_pre = (
            lax.dot_general(act_two, up_t, nt, preferred_element_type=jnp.float32) + up_shift
        )
        hidden_low = gelu_value(hidden_pre).astype(jnp.bfloat16)
        final = mid + (
            lax.dot_general(hidden_low, down_t, nt, preferred_element_type=jnp.float32)
            + biases_now[5]
        )
        rows_out = final.astype(jnp.bfloat16)

        grad_final = cotangent.astype(jnp.float32)
        down_grad_t = lax.dot_general(cotangent, hidden_low, tn, preferred_element_type=jnp.float32)
        grad_hidden = jnp.dot(cotangent, down_t, preferred_element_type=jnp.float32) * gelu_slope(
            hidden_pre
        )
        grad_hidden_low = grad_hidden.astype(jnp.bfloat16)
        up_grad_t = lax.dot_general(grad_hidden_low, act_two, tn, preferred_element_type=jnp.float32)
        up_bias_grad = jnp.sum(grad_hidden_low.astype(jnp.float32), axis=0)
        grad_act_two = jnp.dot(grad_hidden_low, up_t, preferred_element_type=jnp.float32)
        grad_norm_two, gain_two_grad, shift_two_grad = norm_backward(
            grad_act_two, normed_two, inv_two, gains_now[1]
        )
        grad_mid = grad_final + grad_norm_two
        grad_branch_low = grad_mid.astype(jnp.bfloat16)
        out_grad_t = lax.dot_general(
            grad_branch_low, attended_low, tn, preferred_element_type=jnp.float32
        )
        late_rows = jnp.concatenate(
            [
                out_grad_t.reshape(chips, 2, -1, model_width),
                up_grad_t.reshape(chips, 2, -1, model_width),
            ],
            axis=2,
        )
        late = ring_reduce_steps(
            ring, [(late_rows, "both"), (down_grad_t.reshape((chips, 2, -1) + down_grad_t.shape[1:]), "both")]
        )
        grad_attended = jnp.dot(grad_branch_low, out_t, preferred_element_type=jnp.float32).astype(
            jnp.bfloat16
        )
        kernel_count = tables[0].shape[0]
        start_sums = (
            jnp.zeros((kernel_count, head_count), jnp.float32),
            jnp.zeros((kernel_count,), jnp.float32),
            jnp.zeros((kernel_count,), jnp.float32),
            jnp.zeros((ATOM_TYPES, ATOM_TYPES), jnp.float32),
            jnp.zeros((ATOM_TYPES, ATOM_TYPES), jnp.float32),
        )
        kernel_sums = start_sums
        q_grads, k_grads, v_grads = [], [], []
        grad_attended_blocks = grad_attended.reshape(split_shape)
        stepper = Stepper(late)
        for b in range(blocks):
            gate = stepper.tie(grad_attended_blocks[b])
            kernel_sums, (qg, kg, vg) = block_backward(
                kernel_sums,
                (
                    queries[b],
                    key_rows[b],
                    value_rows[b],
                    gate,
                    log_sums[b],
                    pos_blocks[b],
                    type_blocks[b],
                    mol_blocks[b],
                    pad_blocks[b],
                ),
                tables=tables,
                kernel_heads=heads_full,
                tile_rows=tile_rows,
                hook=stepper.tie,
            )
            q_grads.append(qg)
            k_grads.append(kg)
            v_grads.append(vg)
        queries_grad = jnp.stack(q_grads)
        keys_grad = jnp.stack(k_grads)
        values_grad = jnp.stack(v_grads)
        grad_projected = jnp.concatenate(
            [
                queries_grad.reshape(row_count, model_width),
                keys_grad.reshape(row_count, model_width),
                values_grad.reshape(row_count, model_width),
            ],
            axis=1,
        ).astype(jnp.bfloat16)
        in_grad_t = lax.dot_general(grad_projected, act_one, tn, preferred_element_type=jnp.float32)
        grad_act_one = jnp.dot(grad_projected, in_t, preferred_element_type=jnp.float32)
        grad_norm_one, gain_one_grad, shift_one_grad = norm_backward(
            grad_act_one, normed_one, inv_one, gains_now[0]
        )
        inputs_grad = grad_mid + grad_norm_one
        projected_sums = jnp.sum(grad_projected.astype(jnp.float32), axis=0)
        heads_grad, means_grad, widths_grad, scale_grad, shift_grad = kernel_sums
        small_grads = [
            jnp.stack([gain_one_grad, gain_two_grad]),
            jnp.stack(
                [
                    shift_one_grad,
                    shift_two_grad,
                    projected_sums[:model_width],
                    projected_sums[2 * model_width :],
                    jnp.sum(grad_branch_low.astype(jnp.float32), axis=0),
                    jnp.sum(grad_final, axis=0),
                ]
            ),
            up_bias_grad,
            means_grad,
            widths_grad,
            scale_grad,
            shift_grad,
            heads_grad,
        ]
        late_owned = stepper.finish()
        out_owned = late_owned[0][:out_rows]
        up_owned = late_owned[0][out_rows:]
        down_owned = late_owned[1]
        last = jnp.concatenate(
            [
                in_grad_t.reshape((chips, 2, -1) + in_grad_t.shape[1:]),
                pack_small_grads(small_grads, fsdp, chips),
            ],
            axis=2,
        )
        (last_owned,) = run_steps(ring_reduce_steps(ring, [(last, "both")]))
        in_rows = in_grad_t.shape[0] // fsdp
        in_owned = last_owned[:in_rows]
        small_owned = last_owned[in_rows:]
        sg = unpack_small_owned(small_owned, offsets)
        return (
            rows_out,
            inputs_grad,
            sg[0],
            sg[1],
            sg[2],
            in_owned.T,
            out_owned.T,
            up_owned.T,
            down_owned.T,
            sg[3],
            sg[4],
            sg[5],
            sg[6],
            sg[7],
        )

    return body


def solution(mesh):
    reps, fsdp = mesh.devices.shape
    chips = fsdp // 2
    grid = Mesh(mesh.devices.reshape(reps, chips, 2), ("rep", "chip", "core"))
    chips_x = 1
    try:
        coords = [tuple(d.coords) for d in mesh.devices[0, ::2]]
        xs = sorted({c[0] for c in coords})
        chips_x = len(xs)
        flat_ok = all(
            coords[i][0] == xs[i % chips_x] for i in range(chips)
        )
        if not flat_ok:
            chips_x = 1
    except Exception:
        chips_x = 1
    ring = None
    if chips <= 8:
        ring = Ring(snake_ring(chips_x, chips // chips_x))
    atoms = ("rep", "chip", "core")
    cols = ("chip", "core")
    placed = (
        P(atoms, None),
        P(atoms),
        P(None, atoms),
        P(atoms),
        P(atoms),
        P(atoms),
        P(atoms, None),
        P(None, cols),
        P(None, cols),
        P(cols),
        P(None, cols),
        P(None, cols),
        P(None, cols),
        P(None, cols),
        P(cols),
        P(cols),
        P(cols),
        P(cols),
        P(cols, None),
    )
    return jax.shard_map(
        make_body(ring, chips),
        mesh=grid,
        in_specs=placed,
        out_specs=(
            P(atoms, None),
            P(atoms, None),
            P(None, cols),
            P(None, cols),
            P(cols),
            P(None, cols),
            P(None, cols),
            P(None, cols),
            P(None, cols),
            P(cols),
            P(cols),
            P(cols),
            P(cols),
            P(cols, None),
        ),
        check_vma=False,
    )
```

```python
from functools import partial
import math

import jax
import jax.numpy as jnp
from jax import lax
from jax.sharding import Mesh, PartitionSpec as P
import numpy as np

ATOM_TYPES = 64


epsilon = 1e-05
masked_score = -1000000000.0
time_scale = 1000.0
root_two_pi = math.sqrt(2.0 * math.pi)
highest = lax.Precision.HIGHEST


def time_embedding(times, model_width):
    half_width = model_width // 2
    counter = jnp.arange(half_width, dtype=jnp.float32)
    frequency = jnp.exp(counter * (-math.log(10000.0) / half_width))
    angles = (time_scale * times)[:, None] * frequency[None, :]
    return jnp.concatenate([jnp.sin(angles), jnp.cos(angles)], axis=1)


def layer_norm(values, gain_row, shift_row):
    center = values - jnp.mean(values, axis=1, keepdims=True)
    inv_std = lax.rsqrt(jnp.mean(center * center, axis=1, keepdims=True) + epsilon)
    normed = center * inv_std
    return (normed * gain_row + shift_row, normed, inv_std)


def norm_backward(grad_out, normed, inv_std, gain_row):
    grad_normed = grad_out * gain_row
    first_mean = jnp.mean(grad_normed, axis=1, keepdims=True)
    second_mean = jnp.mean(grad_normed * normed, axis=1, keepdims=True)
    grad_input = inv_std * (grad_normed - first_mean - normed * second_mean)
    return (grad_input, jnp.sum(grad_out * normed, axis=0), jnp.sum(grad_out, axis=0))


def gelu_value(values):
    return values * (0.5 + 0.5 * lax.erf(values * math.sqrt(0.5)))


def gelu_slope(values):
    return (
        0.5
        + 0.5 * lax.erf(values * math.sqrt(0.5))
        + values * jnp.exp(-0.5 * values * values) / root_two_pi
    )


def pair_terms(pos_rows, pos_cols, type_rows, type_cols, tables):
    kernel_means, kernel_widths, scale_table, shift_table = tables
    offsets = pos_rows[:, :, None] - pos_cols[:, None, :]
    distance = jnp.sqrt(jnp.sum(offsets * offsets, axis=0))
    type_range = jnp.arange(ATOM_TYPES, dtype=jnp.int32)
    hot_rows = (type_rows[:, None] == type_range[None, :]).astype(jnp.float32)
    hot_cols = (type_cols[:, None] == type_range[None, :]).astype(jnp.float32)
    scale_pair = jnp.dot(
        jnp.dot(hot_rows, scale_table, precision=highest), hot_cols.T, precision=highest
    )
    shift_pair = jnp.dot(
        jnp.dot(hot_rows, shift_table, precision=highest), hot_cols.T, precision=highest
    )
    stretched = scale_pair * distance + shift_pair
    kernel_gap = (stretched[:, :, None] - kernel_means) / kernel_widths
    kernels = jnp.exp(-0.5 * kernel_gap * kernel_gap) / (root_two_pi * kernel_widths)
    return (distance, hot_rows, hot_cols, kernel_gap, kernels)


def allowed_pairs(row_ids, col_ids, mol_rows, mol_cols, pad_cols):
    same_mol = mol_rows[:, None] == mol_cols[None, :]
    key_live = (pad_cols[None, :] == 1) | (row_ids[:, None] == col_ids[None, :])
    return same_mol & key_live


def tile_scores(q_tile, key_block, kernels_low, kernel_heads, allowed, score_scale):
    pair_bias = jnp.einsum(
        "ijk,kh->hij", kernels_low, kernel_heads, preferred_element_type=jnp.float32
    )
    raw_scores = jnp.einsum("ihd,jhd->hij", q_tile, key_block, preferred_element_type=jnp.float32)
    return jnp.where(allowed[None], raw_scores * score_scale + pair_bias, masked_score)


def block_forward(pieces, tables, kernel_heads, tile_rows):
    queries, key_block, value_block, positions, types, mols, pads = pieces
    block_rows = queries.shape[0]
    score_scale = 1.0 / math.sqrt(queries.shape[2])
    col_ids = jnp.arange(block_rows, dtype=jnp.int32)

    def one_tile(running, tile_index):
        first_row = tile_index * tile_rows
        row_ids = first_row + jnp.arange(tile_rows, dtype=jnp.int32)
        terms = pair_terms(positions, positions, types, types, tables)
        kernels_low = terms[4].astype(jnp.bfloat16)
        allowed = allowed_pairs(row_ids, col_ids, mols, mols, pads)
        scores = tile_scores(queries, key_block, kernels_low, kernel_heads, allowed, score_scale)
        row_max = jnp.max(scores, axis=2, keepdims=True)
        exponent = jnp.exp(scores - row_max)
        row_sum = jnp.sum(exponent, axis=2, keepdims=True)
        probs_low = (exponent / row_sum).astype(jnp.bfloat16)
        attended = jnp.einsum(
            "hij,jhd->ihd", probs_low, value_block, preferred_element_type=jnp.float32
        )
        return (running, (attended, (row_max + jnp.log(row_sum))[:, :, 0]))

    count = block_rows // tile_rows
    if count == 1:
        _, (attended, log_sums) = one_tile(None, 0)
        return (attended.reshape(block_rows, -1), log_sums)
    _, (attended, log_sums) = lax.scan(one_tile, None, jnp.arange(count, dtype=jnp.int32))
    attended = attended.reshape(block_rows, -1)
    log_sums = jnp.transpose(log_sums, (1, 0, 2)).reshape(log_sums.shape[1], block_rows)
    return (attended, log_sums)


def block_backward(running, pieces, tables, kernel_heads, tile_rows, hook=None):
    queries, key_block, value_block, grad_attended, log_sums, positions, types, mols, pads = pieces
    kernel_widths = tables[1]
    block_rows = queries.shape[0]
    score_scale = 1.0 / math.sqrt(queries.shape[2])
    col_ids = jnp.arange(block_rows, dtype=jnp.int32)

    def one_tile(partial_sums, tile_index):
        keys_grad, values_grad, heads_grad, means_grad, widths_grad, scale_grad, shift_grad = (
            partial_sums
        )
        first_row = tile_index * tile_rows
        row_ids = first_row + jnp.arange(tile_rows, dtype=jnp.int32)
        distance, hot_rows, hot_cols, kernel_gap, kernels = pair_terms(
            positions, positions, types, types, tables
        )
        kernels_low = kernels.astype(jnp.bfloat16)
        allowed = allowed_pairs(row_ids, col_ids, mols, mols, pads)
        scores = tile_scores(queries, key_block, kernels_low, kernel_heads, allowed, score_scale)
        attn_probs = jnp.exp(scores - log_sums[:, :, None])
        grad_probs = jnp.einsum(
            "ihd,jhd->hij", grad_attended, value_block, preferred_element_type=jnp.float32
        )
        values_grad = values_grad + jnp.einsum(
            "hij,ihd->jhd",
            attn_probs.astype(jnp.bfloat16),
            grad_attended,
            preferred_element_type=jnp.float32,
        )
        probs_dot = jnp.sum(attn_probs * grad_probs, axis=2, keepdims=True)
        grad_scores = (attn_probs * (grad_probs - probs_dot)).astype(jnp.bfloat16)
        if hook is not None:
            grad_scores = hook(grad_scores)
        query_grad = (
            jnp.einsum("hij,jhd->ihd", grad_scores, key_block, preferred_element_type=jnp.float32)
            * score_scale
        )
        keys_grad = (
            keys_grad
            + jnp.einsum("hij,ihd->jhd", grad_scores, queries, preferred_element_type=jnp.float32)
            * score_scale
        )
        heads_grad = heads_grad + jnp.einsum(
            "ijk,hij->kh", kernels_low, grad_scores, preferred_element_type=jnp.float32
        )
        grad_kernels = jnp.einsum(
            "hij,kh->ijk", grad_scores, kernel_heads, preferred_element_type=jnp.float32
        )
        spread = grad_kernels * kernels
        mean_part = spread * kernel_gap / kernel_widths
        means_grad = means_grad + jnp.sum(mean_part, axis=(0, 1))
        widths_grad = widths_grad + jnp.sum(
            spread * (kernel_gap * kernel_gap - 1.0) / kernel_widths, axis=(0, 1)
        )
        grad_stretched = -jnp.sum(mean_part, axis=2)
        scale_grad = scale_grad + jnp.dot(
            jnp.dot(hot_rows.T, grad_stretched * distance, precision=highest),
            hot_cols,
            precision=highest,
        )
        shift_grad = shift_grad + jnp.dot(
            jnp.dot(hot_rows.T, grad_stretched, precision=highest), hot_cols, precision=highest
        )
        return (
            (keys_grad, values_grad, heads_grad, means_grad, widths_grad, scale_grad, shift_grad),
            query_grad,
        )

    zero_block = jnp.zeros(key_block.shape, jnp.float32)
    count = block_rows // tile_rows
    if count == 1:
        sums_out, query_grads = one_tile((zero_block, zero_block) + tuple(running), 0)
        return (sums_out[2:], (query_grads.reshape(key_block.shape), sums_out[0], sums_out[1]))
    sums_out, query_grads = lax.scan(
        one_tile, (zero_block, zero_block) + tuple(running), jnp.arange(count, dtype=jnp.int32)
    )
    query_grads = query_grads.reshape(key_block.shape)
    return (sums_out[2:], (query_grads, sums_out[0], sums_out[1]))


def snake_ring(chips_x, chips_other):
    if chips_x == 2 and chips_other >= 2:
        return [2 * z for z in range(chips_other)] + [
            2 * z + 1 for z in reversed(range(chips_other))
        ]
    return list(range(chips_x * chips_other))


class Ring:
    def __init__(self, order):
        self.order = order
        self.n = len(order)
        pos = np.zeros(self.n, np.int32)
        for i, c in enumerate(order):
            pos[c] = i
        self.pos = pos
        self.cw = [(order[i], order[(i + 1) % self.n]) for i in range(self.n)]
        self.ccw = [(order[i], order[(i - 1) % self.n]) for i in range(self.n)]

    def here(self):
        chip = lax.axis_index("chip")
        core = lax.axis_index("core")
        return chip, core, jnp.asarray(self.pos)[chip]

    def chip_at(self, position):
        return jnp.asarray(np.array(self.order, np.int32))[position % self.n]


SWAP = [(0, 1), (1, 0)]


def _halves(x, axis):
    size = x.shape[axis] // 2
    return (
        lax.slice_in_dim(x, 0, size, axis=axis),
        lax.slice_in_dim(x, size, 2 * size, axis=axis),
    )


def ring_gather(ring, pieces, chips):
    if ring is None:
        return [
            lax.all_gather(x, ("chip", "core"), axis=0, tiled=False).reshape((chips, 2) + x.shape)
            for x, _ in pieces
        ]
    chip, core, p = ring.here()
    n = ring.n
    bufs, fronts = [], []
    for x, axis in pieces:
        buf = jnp.zeros((n, 2) + x.shape, x.dtype)
        buf = lax.dynamic_update_slice(buf, x[None, None], (chip, core) + (0,) * x.ndim)
        bufs.append(buf)
        if axis is None:
            fronts.append([x, None])
        else:
            fronts.append(list(_halves(x, axis)))
    partner = lax.ppermute([x for x, _ in pieces], "core", SWAP)
    for i, x in enumerate(partner):
        bufs[i] = lax.dynamic_update_slice(
            bufs[i], x[None, None], (chip, 1 - core) + (0,) * x.ndim
        )
    for step in range(1, n):
        going = [f[0] for f in fronts]
        coming = [f[1] for f in fronts if f[1] is not None]
        going = lax.ppermute(going, "chip", ring.cw)
        coming = lax.ppermute(coming, "chip", ring.ccw) if coming else []
        from_cw = ring.chip_at(p - step)
        from_ccw = ring.chip_at(p + step)
        both = lax.ppermute([going, coming], "core", SWAP)
        j = 0
        for i, (x, axis) in enumerate(pieces):
            fronts[i][0] = going[i]
            parts = [(going[i], both[0][i], from_cw, 0)]
            if axis is not None:
                fronts[i][1] = coming[j]
                parts.append((coming[j], both[1][j], from_ccw, x.shape[axis] // 2))
                j += 1
            for mine, theirs, source, offset in parts:
                start = [0] * x.ndim
                if axis is not None:
                    start[axis] = offset
                bufs[i] = lax.dynamic_update_slice(
                    bufs[i], mine[None, None], (source, core) + tuple(start)
                )
                bufs[i] = lax.dynamic_update_slice(
                    bufs[i], theirs[None, None], (source, 1 - core) + tuple(start)
                )
    return bufs


def ring_reduce_steps(ring, pieces, send=jnp.bfloat16):
    if ring is None:
        owned = []
        for g, _ in pieces:
            flat = g.reshape((-1,) + g.shape[3:])
            part = lax.psum_scatter(flat, ("chip", "core"), scatter_dimension=0, tiled=True)
            owned.append(lax.psum(part.astype(send), "rep").astype(jnp.float32))
        yield owned
        return owned
    chip, core, p = ring.here()
    n = ring.n
    mine, theirs = [], []
    for g, _ in pieces:
        mine.append(lax.dynamic_index_in_dim(g, core, axis=1, keepdims=False))
        theirs.append(lax.dynamic_index_in_dim(g, 1 - core, axis=1, keepdims=False).astype(send))
    got = lax.ppermute(theirs, "core", SWAP)
    yield got
    flows = []
    for i, (g, way) in enumerate(pieces):
        if way == "both":
            flows.append((i, 1, n // 2, mine[i], got[i]))
            flows.append((i, -1, (n - 1) // 2, mine[i], got[i]))
        elif isinstance(way, tuple):
            axis = way[1] + 1
            for d, (m, t) in zip((1, -1), zip(_halves(mine[i], axis), _halves(got[i], axis))):
                flows.append((i, d, n - 1, m, t))
        else:
            flows.append((i, way, n - 1, mine[i], got[i]))

    def contribution(m, t, position):
        at = ring.chip_at(position)
        own = lax.dynamic_index_in_dim(m, at, axis=0, keepdims=False)
        other = lax.dynamic_index_in_dim(t, at, axis=0, keepdims=False)
        return own + other.astype(jnp.float32)

    acc = [contribution(m, t, p + d * hops) for _, d, hops, m, t in flows]
    for step in range(1, max(f[2] for f in flows) + 1):
        moved = []
        for d in (1, -1):
            chosen = [k for k, f in enumerate(flows) if f[1] == d and f[2] >= step]
            if chosen:
                out = lax.ppermute([acc[k].astype(send) for k in chosen], "chip", ring.cw if d == 1 else ring.ccw)
                for k, o in zip(chosen, out):
                    acc[k] = o.astype(jnp.float32)
                moved.extend(out)
        yield moved
        for k, (_, d, hops, m, t) in enumerate(flows):
            if hops > step:
                acc[k] = acc[k] + contribution(m, t, p + d * (hops - step))
    owned = []
    for i, (g, way) in enumerate(pieces):
        parts = [(a, f) for a, f in zip(acc, flows) if f[0] == i]
        if way == "both":
            total = contribution(parts[0][1][3], parts[0][1][4], p) + parts[0][0] + parts[1][0]
        else:
            total = [a + contribution(f[3], f[4], p) for a, f in parts]
            total = total[0] if len(total) == 1 else jnp.concatenate(total, axis=way[1])
        owned.append(total)
    other = lax.ppermute([o.astype(send) for o in owned], "rep", SWAP)
    yield other
    return [o + t.astype(jnp.float32) for o, t in zip(owned, other)]


class Stepper:
    def __init__(self, gen):
        self.gen = gen
        self.result = None
        self.over = False

    def tie(self, value):
        if self.over:
            return value
        try:
            ready = next(self.gen)
        except StopIteration as done:
            self.result, self.over = done.value, True
            return value
        _, value = lax.optimization_barrier((ready, value))
        return value

    def finish(self):
        if not self.over:
            self.result, self.over = run_steps(self.gen), True
        return self.result


def run_steps(gen):
    while True:
        try:
            next(gen)
        except StopIteration as done:
            return done.value


SMALL_ROWS, SMALL_LANES = 16, 768
GRAD_ROWS = 8


def small_layout(fsdp):
    d = 768 // fsdp
    sizes = [2 * d, 6 * d, 3072 // fsdp, 128 // fsdp, 128 // fsdp, 4096 // fsdp, 4096 // fsdp, (128 // fsdp) * 32]
    offsets, at = [], 0
    for size in sizes:
        offsets.append((at, size))
        at += size
    assert at <= SMALL_ROWS * SMALL_LANES
    return offsets


def pack_small(parts):
    flat = jnp.concatenate([part.reshape(-1) for part in parts])
    flat = jnp.pad(flat, (0, SMALL_ROWS * SMALL_LANES - flat.shape[0]))
    return flat.reshape(SMALL_ROWS, SMALL_LANES)


def unpack_small_full(gathered, offsets, fsdp):
    flat = gathered.reshape(fsdp, -1).astype(jnp.float32)
    take = [flat[:, at : at + size] for at, size in offsets]
    d = 768 // fsdp
    return [
        take[0].reshape(fsdp, 2, d).transpose(1, 0, 2).reshape(2, -1),
        take[1].reshape(fsdp, 6, d).transpose(1, 0, 2).reshape(6, -1),
        take[2].reshape(-1),
        take[3].reshape(-1),
        take[4].reshape(-1),
        take[5].reshape(ATOM_TYPES, ATOM_TYPES),
        take[6].reshape(ATOM_TYPES, ATOM_TYPES),
        take[7].reshape(-1, 32),
    ]


def pack_small_grads(grads, fsdp, chips):
    d = 768 // fsdp
    blocks = [
        grads[0].reshape(2, fsdp, d).transpose(1, 0, 2),
        grads[1].reshape(6, fsdp, d).transpose(1, 0, 2),
    ] + [g.reshape(-1) for g in grads[2:]]
    flat = jnp.concatenate([blk.reshape(fsdp, -1) for blk in blocks], axis=1)
    flat = jnp.pad(flat, ((0, 0), (0, GRAD_ROWS * SMALL_LANES - flat.shape[1])))
    return flat.reshape(chips, 2, GRAD_ROWS, SMALL_LANES)


def unpack_small_owned(block, offsets):
    flat = block.reshape(-1)
    take = [flat[at : at + size] for at, size in offsets]
    return [
        take[0].reshape(2, -1),
        take[1].reshape(6, -1),
        take[2],
        take[3],
        take[4],
        take[5],
        take[6],
        take[7].reshape(-1, 32),
    ]


def make_body(ring, chips):
    fsdp = 2 * chips

    def body(
        inputs,
        times,
        positions,
        atom_types,
        molecule_ids,
        pad_mask,
        cotangent,
        norm_gains,
        bias_rows,
        up_bias,
        input_weight,
        output_weight,
        up_weight,
        down_weight,
        kernel_means,
        kernel_widths,
        pair_scale,
        pair_shift,
        kernel_heads,
    ):
        offsets = small_layout(fsdp)
        small = jnp.concatenate(
            [
                part.reshape(-1)
                for part in (norm_gains, bias_rows, up_bias, kernel_means, kernel_widths, pair_scale, pair_shift, kernel_heads)
            ]
        )
        small = jnp.pad(small, (0, -small.shape[0] % 128))
        width = input_weight.shape[0]
        small_all = lax.all_gather(small, ("chip", "core"), axis=0, tiled=False)
        in_t = lax.all_gather(input_weight.T, ("chip", "core"), axis=0, tiled=True)
        down_rows = down_weight.shape[1]
        down_packed = (
            down_weight.T.reshape(down_rows, -1, width).transpose(1, 0, 2).reshape(-1, width)
        )
        second = jnp.concatenate([output_weight.T, up_weight.T, down_packed], axis=0)
        second_all = lax.all_gather(second, ("chip", "core"), axis=0, tiled=False)
        params = unpack_small_full(small_all, offsets, fsdp)
        out_rows = output_weight.shape[1]
        up_rows = up_weight.shape[1]
        out_t = second_all[:, :out_rows].reshape(-1, width)
        up_t = second_all[:, out_rows : out_rows + up_rows].reshape(-1, width)
        down_t = (
            second_all[:, out_rows + up_rows :]
            .reshape(fsdp, -1, down_rows, width)
            .transpose(0, 2, 1, 3)
            .reshape(-1, down_weight.shape[0])
        )
        gains_now, biases_now, up_shift = params[0], params[1], params[2]
        tables = (params[3], params[4], params[5], params[6])
        heads_full = params[7].astype(jnp.bfloat16)

        row_count = inputs.shape[0]
        model_width = inputs.shape[1]
        head_count = heads_full.shape[1]
        head_size = model_width // head_count
        block_rows = min(128, row_count)
        blocks = row_count // block_rows
        tile_rows = min(128, block_rows)
        nt = (((1,), (1,)), ((), ()))
        tn = (((0,), (0,)), ((), ()))

        stream = inputs.astype(jnp.float32) + time_embedding(times, model_width)
        normed_out, normed_one, inv_one = layer_norm(stream, gains_now[0], biases_now[0])
        act_one = normed_out.astype(jnp.bfloat16)
        qkv_shift = jnp.concatenate([biases_now[2], jnp.zeros_like(biases_now[2]), biases_now[3]])
        projected = (
            lax.dot_general(act_one, in_t, nt, preferred_element_type=jnp.float32) + qkv_shift
        ).astype(jnp.bfloat16)
        split_shape = (blocks, block_rows, head_count, head_size)
        queries = projected[:, :model_width].reshape(split_shape)
        key_rows = projected[:, model_width : 2 * model_width].reshape(split_shape)
        value_rows = projected[:, 2 * model_width :].reshape(split_shape)
        pos_blocks = jnp.transpose(positions.reshape(3, blocks, block_rows), (1, 0, 2))
        type_blocks = atom_types.reshape(blocks, block_rows)
        mol_blocks = molecule_ids.reshape(blocks, block_rows)
        pad_blocks = pad_mask.reshape(blocks, block_rows)
        fwd = [
            block_forward(
                (queries[b], key_rows[b], value_rows[b], pos_blocks[b], type_blocks[b], mol_blocks[b], pad_blocks[b]),
                tables=tables,
                kernel_heads=heads_full,
                tile_rows=tile_rows,
            )
            for b in range(blocks)
        ]
        attended = jnp.stack([f[0] for f in fwd])
        log_sums = [f[1] for f in fwd]
        attended_low = attended.reshape(row_count, model_width).astype(jnp.bfloat16)
        mid = stream + (
            lax.dot_general(attended_low, out_t, nt, preferred_element_type=jnp.float32)
            + biases_now[4]
        )
        normed_out_two, normed_two, inv_two = layer_norm(mid, gains_now[1], biases_now[1])
        act_two = normed_out_two.astype(jnp.bfloat16)
        hidden_pre = (
            lax.dot_general(act_two, up_t, nt, preferred_element_type=jnp.float32) + up_shift
        )
        hidden_low = gelu_value(hidden_pre).astype(jnp.bfloat16)
        final = mid + (
            lax.dot_general(hidden_low, down_t, nt, preferred_element_type=jnp.float32)
            + biases_now[5]
        )
        rows_out = final.astype(jnp.bfloat16)

        grad_final = cotangent.astype(jnp.float32)
        down_grad_t = lax.dot_general(cotangent, hidden_low, tn, preferred_element_type=jnp.float32)
        grad_hidden = jnp.dot(cotangent, down_t, preferred_element_type=jnp.float32) * gelu_slope(
            hidden_pre
        )
        grad_hidden_low = grad_hidden.astype(jnp.bfloat16)
        up_grad_t = lax.dot_general(grad_hidden_low, act_two, tn, preferred_element_type=jnp.float32)
        up_bias_grad = jnp.sum(grad_hidden_low.astype(jnp.float32), axis=0)
        grad_act_two = jnp.dot(grad_hidden_low, up_t, preferred_element_type=jnp.float32)
        grad_norm_two, gain_two_grad, shift_two_grad = norm_backward(
            grad_act_two, normed_two, inv_two, gains_now[1]
        )
        grad_mid = grad_final + grad_norm_two
        grad_branch_low = grad_mid.astype(jnp.bfloat16)
        out_grad_t = lax.dot_general(
            grad_branch_low, attended_low, tn, preferred_element_type=jnp.float32
        )
        late_rows = jnp.concatenate(
            [
                out_grad_t.reshape(chips, 2, -1, model_width),
                up_grad_t.reshape(chips, 2, -1, model_width),
            ],
            axis=2,
        )
        late = ring_reduce_steps(
            ring, [(late_rows, "both"), (down_grad_t.reshape((chips, 2, -1) + down_grad_t.shape[1:]), "both")]
        )
        grad_attended = jnp.dot(grad_branch_low, out_t, preferred_element_type=jnp.float32).astype(
            jnp.bfloat16
        )
        kernel_count = tables[0].shape[0]
        start_sums = (
            jnp.zeros((kernel_count, head_count), jnp.float32),
            jnp.zeros((kernel_count,), jnp.float32),
            jnp.zeros((kernel_count,), jnp.float32),
            jnp.zeros((ATOM_TYPES, ATOM_TYPES), jnp.float32),
            jnp.zeros((ATOM_TYPES, ATOM_TYPES), jnp.float32),
        )
        kernel_sums = start_sums
        q_grads, k_grads, v_grads = [], [], []
        grad_attended_blocks = grad_attended.reshape(split_shape)
        stepper = Stepper(late)
        for b in range(blocks):
            gate = stepper.tie(grad_attended_blocks[b])
            kernel_sums, (qg, kg, vg) = block_backward(
                kernel_sums,
                (
                    queries[b],
                    key_rows[b],
                    value_rows[b],
                    gate,
                    log_sums[b],
                    pos_blocks[b],
                    type_blocks[b],
                    mol_blocks[b],
                    pad_blocks[b],
                ),
                tables=tables,
                kernel_heads=heads_full,
                tile_rows=tile_rows,
                hook=stepper.tie,
            )
            q_grads.append(qg)
            k_grads.append(kg)
            v_grads.append(vg)
        queries_grad = jnp.stack(q_grads)
        keys_grad = jnp.stack(k_grads)
        values_grad = jnp.stack(v_grads)
        grad_projected = jnp.concatenate(
            [
                queries_grad.reshape(row_count, model_width),
                keys_grad.reshape(row_count, model_width),
                values_grad.reshape(row_count, model_width),
            ],
            axis=1,
        ).astype(jnp.bfloat16)
        in_grad_t = lax.dot_general(grad_projected, act_one, tn, preferred_element_type=jnp.float32)
        grad_act_one = jnp.dot(grad_projected, in_t, preferred_element_type=jnp.float32)
        grad_norm_one, gain_one_grad, shift_one_grad = norm_backward(
            grad_act_one, normed_one, inv_one, gains_now[0]
        )
        inputs_grad = grad_mid + grad_norm_one
        projected_sums = jnp.sum(grad_projected.astype(jnp.float32), axis=0)
        heads_grad, means_grad, widths_grad, scale_grad, shift_grad = kernel_sums
        small_grads = [
            jnp.stack([gain_one_grad, gain_two_grad]),
            jnp.stack(
                [
                    shift_one_grad,
                    shift_two_grad,
                    projected_sums[:model_width],
                    projected_sums[2 * model_width :],
                    jnp.sum(grad_branch_low.astype(jnp.float32), axis=0),
                    jnp.sum(grad_final, axis=0),
                ]
            ),
            up_bias_grad,
            means_grad,
            widths_grad,
            scale_grad,
            shift_grad,
            heads_grad,
        ]
        late_owned = stepper.finish()
        out_owned = late_owned[0][:out_rows]
        up_owned = late_owned[0][out_rows:]
        down_owned = late_owned[1]
        last = jnp.concatenate(
            [
                in_grad_t.reshape((chips, 2, -1) + in_grad_t.shape[1:]),
                pack_small_grads(small_grads, fsdp, chips),
            ],
            axis=2,
        )
        (last_owned,) = run_steps(ring_reduce_steps(ring, [(last, "both")]))
        in_rows = in_grad_t.shape[0] // fsdp
        in_owned = last_owned[:in_rows]
        small_owned = last_owned[in_rows:]
        sg = unpack_small_owned(small_owned, offsets)
        return (
            rows_out,
            inputs_grad,
            sg[0],
            sg[1],
            sg[2],
            in_owned.T,
            out_owned.T,
            up_owned.T,
            down_owned.T,
            sg[3],
            sg[4],
            sg[5],
            sg[6],
            sg[7],
        )

    return body


def solution(mesh):
    reps, fsdp = mesh.devices.shape
    chips = fsdp // 2
    grid = Mesh(mesh.devices.reshape(reps, chips, 2), ("rep", "chip", "core"))
    chips_x = 1
    try:
        coords = [tuple(d.coords) for d in mesh.devices[0, ::2]]
        xs = sorted({c[0] for c in coords})
        chips_x = len(xs)
        flat_ok = all(
            coords[i][0] == xs[i % chips_x] for i in range(chips)
        )
        if not flat_ok:
            chips_x = 1
    except Exception:
        chips_x = 1
    ring = None
    if chips <= 8:
        ring = Ring(snake_ring(chips_x, chips // chips_x))
    atoms = ("rep", "chip", "core")
    cols = ("chip", "core")
    placed = (
        P(atoms, None),
        P(atoms),
        P(None, atoms),
        P(atoms),
        P(atoms),
        P(atoms),
        P(atoms, None),
        P(None, cols),
        P(None, cols),
        P(cols),
        P(None, cols),
        P(None, cols),
        P(None, cols),
        P(None, cols),
        P(cols),
        P(cols),
        P(cols),
        P(cols),
        P(cols, None),
    )
    return jax.shard_map(
        make_body(ring, chips),
        mesh=grid,
        in_specs=placed,
        out_specs=(
            P(atoms, None),
            P(atoms, None),
            P(None, cols),
            P(None, cols),
            P(cols),
            P(None, cols),
            P(None, cols),
            P(None, cols),
            P(None, cols),
            P(cols),
            P(cols),
            P(cols),
            P(cols),
            P(cols, None),
        ),
        check_vma=False,
    )
```
